256 devices in a mesh: cast: 64 (over z, x, core), width: 4 (over y).
Axes of the slice: x: 4, y: 4, z: 8, core: 2. Of those that a mesh axis runs over, the one named last changes fastest.
Arguments:
- stored_caloric_content: float32 [64, 512, 512], P(None, 'cast', 'width'), may hold values from -6 to 6
- zones: int32 [2, 512, 512], P(None, 'cast', 'width'), may hold values from 0 to 9
- spray_coef: float32 [10], replicated, may hold values from 0.2 to 5
Outputs:
- new_enthalpy: float32 [64, 512, 512], P(None, 'cast', 'width')
The draws below stay inside these ranges and needn't reach their ends.
All inputs are finite; a program needn't handle non-finite values.
Results may differ from the reference program's by a relative error of at most 0.0018.
Values sent between devices are 32-bit elements; how exact they have to be, the bound alone decides.
No kernel may reach another device: no remote copies, remote signals or barrier semaphores. Data moves between devices by JAX's collectives and lax.ppermute only.
A program may use at most 64 MiB of HBM per device.

```python
import math
import jax
import jax.numpy as jnp
from jax import lax

CX = 8
CY = 128
CZ = 64
ZONES = 10
NX = 512
NY = 512


def draw_stored_caloric_content(key, part):
    key_noise = jax.random.fold_in(key, 0)
    noise_field = jnp.clip(jax.random.normal(key_noise, (CZ, NX, NY), jnp.float32), -4.0, 4.0)
    return noise_field


def draw_zones(key, part):
    key_cast, key_width, key_stray, key_pick = jax.random.split(key, 4)
    offset_cast = jax.random.randint(key_cast, (), 0, NX)
    offset_width = jax.random.randint(key_width, (2, 1, 1), 0, NY)
    cast_place = (jnp.arange(NX, dtype=jnp.int32)[None, :, None] + offset_cast) % NX
    width_place = (jnp.arange(NY, dtype=jnp.int32)[None, None, :] + offset_width) % NY
    segment = cast_place * (ZONES // 2) // NX
    side_half = width_place * 2 // NY
    layout = segment * 2 + side_half
    stray_mask = jax.random.randint(key_stray, (2, NX, NY), 0, 8) == 0
    random_zone = jax.random.randint(key_pick, (2, NX, NY), 0, ZONES)
    return jnp.where(stray_mask, random_zone, layout).astype(jnp.int32)


def setup_inputs(seed: int = 0) -> dict:
    keys = jax.random.split(jax.random.key(seed), 4)
    stored_caloric_content = draw_stored_caloric_content(jax.random.fold_in(keys[3], 71), 0)
    zones = draw_zones(jax.random.fold_in(keys[3], 71), 0)
    spray_coef = jnp.clip(jnp.exp(jax.random.uniform(keys[2], (ZONES,), jnp.float32, math.log(0.2), math.log(5.0))), 0.2, 5.0)
    return dict(stored_caloric_content=stored_caloric_content, zones=zones, spray_coef=spray_coef)


solidification_release = 0.4
quench_medium_hotness = -2.0


def medium_parameters(caloric_content_mesh):
    phase_change_threshold = jnp.tanh(caloric_content_mesh)
    hotness_mesh = caloric_content_mesh - solidification_release * phase_change_threshold
    transport_modulus = 1.5 - 0.5 * jnp.tanh(hotness_mesh)
    caloric_content_incline = (1.0 - solidification_release) + solidification_release * phase_change_threshold * phase_change_threshold
    return hotness_mesh, transport_modulus, caloric_content_incline


def face_pair(cond_first, gain):
    middle_faces = gain * 0.5 * (cond_first[1:] + cond_first[:-1])
    zero_face = jnp.zeros_like(cond_first[:1])
    return jnp.concatenate([zero_face, middle_faces], 0), jnp.concatenate([middle_faces, zero_face], 0)


def displaced_entries_list(caloric_content_mesh):
    before = jnp.concatenate([caloric_content_mesh[:1], caloric_content_mesh[:-1]], 0)
    after = jnp.concatenate([caloric_content_mesh[1:], caloric_content_mesh[-1:]], 0)
    return before, after


def thomas(lower, middle, upper, source):
    zeros_line = jnp.zeros(lower.shape[1:], lower.dtype)

    def forward(carry, row_vals):
        cprime, dprime = carry
        lower_row, middle_row, upper_row, source_row = row_vals
        pivot = middle_row - lower_row * cprime
        new_c = upper_row / pivot
        new_d = (source_row - lower_row * dprime) / pivot
        return (new_c, new_d), (new_c, new_d)

    _, (cprimes, dprimes) = lax.scan(forward, (zeros_line, zeros_line), (lower, middle, upper, source))

    def backward(after_val, row_vals):
        cprime, dprime = row_vals
        value = dprime - cprime * after_val
        return value, value

    _, values = lax.scan(backward, zeros_line, (cprimes, dprimes), reverse=True)
    return values


def line_solve(rhs, transport_modulus, caloric_content_incline, exchange_rim_relation, storage_index_order, gain):
    cond_first = jnp.moveaxis(transport_modulus, storage_index_order, 0)
    slope_first = jnp.moveaxis(caloric_content_incline, storage_index_order, 0)
    bottom_surface_exchange, top_surface_exchange = face_pair(cond_first, gain)
    slope_before, slope_after = displaced_entries_list(slope_first)
    lower = -bottom_surface_exchange * slope_before
    upper = -top_surface_exchange * slope_after
    if storage_index_order == 0:
        middle = 1.0 + slope_first * (bottom_surface_exchange + top_surface_exchange + exchange_rim_relation)
    else:
        middle = 1.0 + slope_first * (bottom_surface_exchange + top_surface_exchange)
    shape_first = lower.shape
    flat_rows = shape_first[0]
    solved = thomas(lower.reshape(flat_rows, -1), middle.reshape(flat_rows, -1), upper.reshape(flat_rows, -1),
                    jnp.moveaxis(rhs, storage_index_order, 0).reshape(flat_rows, -1))
    return jnp.moveaxis(solved.reshape(shape_first), 0, storage_index_order)


def reference(stored_caloric_content, zones, spray_coef):
    hotness_mesh, transport_modulus, caloric_content_incline = medium_parameters(stored_caloric_content)
    surface = spray_coef[zones] * (CZ * CZ / 8.0)
    inner_zero = jnp.zeros((CZ - 2, NX, NY), jnp.float32)
    exchange_rim_relation = jnp.concatenate([surface[0:1], inner_zero, surface[1:2]], 0)
    gains = [(1, CX * CX * 4.0), (2, CY * CY / 4.0), (0, CZ * CZ / 4.0)]
    known_side_increment = exchange_rim_relation * (quench_medium_hotness - hotness_mesh)
    for storage_index_order, gain in gains:
        cond_first = jnp.moveaxis(transport_modulus, storage_index_order, 0)
        hotness_leading_sweep = jnp.moveaxis(hotness_mesh, storage_index_order, 0)
        bottom_surface_exchange, top_surface_exchange = face_pair(cond_first, gain)
        hotness_earlier_step, hotness_later_step = displaced_entries_list(hotness_leading_sweep)
        transport_stream = top_surface_exchange * (hotness_later_step - hotness_leading_sweep) - bottom_surface_exchange * (hotness_leading_sweep - hotness_earlier_step)
        known_side_increment = known_side_increment + jnp.moveaxis(transport_stream, 0, storage_index_order)
    increment = known_side_increment
    for storage_index_order, gain in gains:
        increment = line_solve(increment, transport_modulus, caloric_content_incline, exchange_rim_relation, storage_index_order, gain)
    return stored_caloric_content + increment
```

```python
import functools

import jax
import jax.numpy as jnp
from jax import lax
from jax.experimental import pallas as pl
from jax.experimental.pallas import tpu as pltpu
from jax.sharding import PartitionSpec as P

F32 = jnp.float32
solidification_release = 0.4
quench_medium_hotness = -2.0


def _spike_kernel(with_vw, unroll, a_ref, b_ref, c_ref, d_ref, *refs):
    if with_vw:
        y_ref, v_ref, w_ref, cp_ref = refs
    else:
        y_ref, cp_ref = refs
    n = a_ref.shape[0]
    zero = jnp.zeros(a_ref.shape[1:], F32)
    one = jnp.ones(a_ref.shape[1:], F32)

    def fwd(i, carry):
        cprev, dprev, vprev = carry
        a = a_ref[i]
        r = 1.0 / (b_ref[i] - a * cprev)
        cn = c_ref[i] * r
        dn = (d_ref[i] - a * dprev) * r
        cp_ref[i] = cn
        y_ref[i] = dn
        if with_vw:
            vprev = -(a * vprev) * r
            v_ref[i] = vprev
        return cn, dn, vprev

    cl, dl, vl = lax.fori_loop(0, n, fwd, (zero, zero, one), unroll=unroll)
    if with_vw:
        w_ref[n - 1] = -cl

    def bwd(j, carry):
        i = n - 2 - j
        yn, vn, wn = carry
        cp = cp_ref[i]
        yn = y_ref[i] - cp * yn
        y_ref[i] = yn
        if with_vw:
            vn = v_ref[i] - cp * vn
            wn = -cp * wn
            v_ref[i] = vn
            w_ref[i] = wn
        return yn, vn, wn

    lax.fori_loop(0, n - 1, bwd, (dl, vl, -cl), unroll=unroll)


def spike(a, b, c, d, with_vw, unroll):
    nout = 3 if with_vw else 1
    out = pl.pallas_call(
        functools.partial(_spike_kernel, with_vw, unroll),
        out_shape=[jax.ShapeDtypeStruct(a.shape, F32)] * nout,
        scratch_shapes=[pltpu.VMEM(a.shape, F32)],
    )(a, b, c, d)
    return out


def _reduced_kernel(s_ref, lr_ref, st_ref):
    nb = s_ref.shape[1]
    zero = jnp.zeros((1,) + s_ref.shape[2:], F32)
    pp, qq = zero, zero
    for p in range(nb):
        y0, v0, w0, yn, vn, wn = (s_ref[k, p : p + 1] for k in range(6))
        rd = 1.0 / (1.0 - v0 * qq)
        fa = (y0 + v0 * pp) * rd
        fb = w0 * rd
        st_ref[0, p : p + 1] = fa
        st_ref[1, p : p + 1] = fb
        st_ref[2, p : p + 1] = pp
        st_ref[3, p : p + 1] = qq
        pp, qq = yn + vn * (pp + qq * fa), wn + vn * qq * fb
    f_next = zero
    for p in range(nb - 1, -1, -1):
        f = st_ref[0, p : p + 1] + st_ref[1, p : p + 1] * f_next
        lr_ref[0, p : p + 1] = st_ref[2, p : p + 1] + st_ref[3, p : p + 1] * f
        lr_ref[1, p : p + 1] = f_next
        f_next = f


def reduced(s):
    return pl.pallas_call(
        _reduced_kernel,
        out_shape=jax.ShapeDtypeStruct((2,) + s.shape[1:], F32),
        scratch_shapes=[pltpu.VMEM((4,) + s.shape[1:], F32)],
    )(s)


def medium_parameters(x):
    t = jnp.tanh(x)
    hot = x - solidification_release * t
    cond = 1.5 - 0.5 * jnp.tanh(hot)
    slope = (1.0 - solidification_release) + solidification_release * t * t
    return hot, cond, slope


def summary(y, v, w):
    return jnp.stack([y[0], v[0], w[0], y[-1], v[-1], w[-1]])


def shards(h, zones, spray_coef):
    nt, ncl, nwl = h.shape
    nc, nw = lax.axis_size("cast"), lax.axis_size("width")
    ci, wi = lax.axis_index("cast"), lax.axis_index("width")
    up_c = [(i, i + 1) for i in range(nc - 1)]
    up_w = [(i, i + 1) for i in range(nw - 1)]
    h_cl = lax.ppermute(h[:, -1:, :], "cast", up_c)
    h_ch = lax.ppermute(h[:, :1, :], "cast", [(b, a) for a, b in up_c])
    h_wl = lax.ppermute(h[:, :, -1:], "width", up_w)
    h_wh = lax.ppermute(h[:, :, :1], "width", [(b, a) for a, b in up_w])

    T, k, s = medium_parameters(h)
    T_cl, k_cl, s_cl = medium_parameters(h_cl)
    T_ch, k_ch, s_ch = medium_parameters(h_ch)
    T_wl, k_wl, s_wl = medium_parameters(h_wl)
    T_wh, k_wh, s_wh = medium_parameters(h_wh)

    cast_low = (ci > 0).astype(F32)
    cast_high = (ci < nc - 1).astype(F32)
    width_low = (wi > 0).astype(F32)
    width_high = (wi < nw - 1).astype(F32)

    kc = jnp.concatenate([k_cl, k, k_ch], 1)
    Tc = jnp.concatenate([T_cl, T, T_ch], 1)
    sc = jnp.concatenate([s_cl, s, s_ch], 1)
    edge_c = jnp.ones((ncl + 1,), F32).at[0].set(cast_low).at[-1].set(cast_high)
    fc = (ncl * ncl * 4.0) * 0.5 * (kc[:, 1:] + kc[:, :-1]) * edge_c[None, :, None]
    gcl, gch = fc[:, :-1], fc[:, 1:]
    kw = jnp.concatenate([k_wl, k, k_wh], 2)
    Tw = jnp.concatenate([T_wl, T, T_wh], 2)
    sw = jnp.concatenate([s_wl, s, s_wh], 2)
    edge_w = jnp.ones((nwl + 1,), F32).at[0].set(width_low).at[-1].set(width_high)
    fw = (nwl * nwl / 4.0) * 0.5 * (kw[:, :, 1:] + kw[:, :, :-1]) * edge_w[None, None, :]
    gwl, gwh = fw[:, :, :-1], fw[:, :, 1:]
    mid = (nt * nt / 4.0) * 0.5 * (k[1:] + k[:-1])
    zf = jnp.zeros((1, ncl, nwl), F32)
    gtl = jnp.concatenate([zf, mid], 0)
    gth = jnp.concatenate([mid, zf], 0)

    surf = jnp.zeros(zones.shape, F32)
    for z in range(spray_coef.shape[0]):
        surf = jnp.where(zones == z, spray_coef[z], surf)
    surf = surf * (nt * nt / 8.0)
    rim = jnp.concatenate([surf[0:1], jnp.zeros((nt - 2, ncl, nwl), F32), surf[1:2]], 0)

    T_prev = jnp.concatenate([T[:1], T[:-1]], 0)
    T_next = jnp.concatenate([T[1:], T[-1:]], 0)
    explicit = rim * (quench_medium_hotness - T)
    explicit = explicit + (gch * (Tc[:, 2:] - T) - gcl * (T - Tc[:, :-2]))
    explicit = explicit + (gwh * (Tw[:, :, 2:] - T) - gwl * (T - Tw[:, :, :-2]))
    explicit = explicit + (gth * (T_next - T) - gtl * (T - T_prev))

    def ctw(x):
        return jnp.transpose(x, (1, 0, 2))

    lo = -gcl * sc[:, :-2]
    hi = -gch * sc[:, 2:]
    md = 1.0 + s * (gcl + gch)
    y, v, w = spike(ctw(lo), ctw(md), ctw(hi), ctw(explicit), True, True)
    summ = summary(y, v, w).reshape(6, nc, -1)
    recv = lax.all_to_all(summ, "cast", 1, 1, tiled=True)
    lr = reduced(recv)
    back = lax.all_to_all(lr, "cast", 1, 1, tiled=True).reshape(2, nt, nwl)
    step_cast = y + v * back[0][None] + w * back[1][None]

    lines = nt * ncl

    def wl(x):
        return jnp.transpose(x, (2, 0, 1)).reshape(nwl, lines // 128, 128)

    lo = -gwl * sw[:, :, :-2]
    hi = -gwh * sw[:, :, 2:]
    md = 1.0 + s * (gwl + gwh)
    rhs = jnp.transpose(step_cast, (2, 1, 0)).reshape(nwl, lines // 128, 128)
    y, v, w = spike(wl(lo), wl(md), wl(hi), rhs, True, 8)
    summ = summary(y, v, w)
    gath = lax.all_gather(summ, "width", axis=1)
    lr = reduced(gath)
    mine = lax.dynamic_index_in_dim(lr, wi, axis=1, keepdims=False)
    step_width = y + v * mine[0][None] + w * mine[1][None]
    step_width = step_width.reshape(nwl, nt, ncl).transpose(1, 2, 0)

    s_prev = jnp.concatenate([s[:1], s[:-1]], 0)
    s_next = jnp.concatenate([s[1:], s[-1:]], 0)
    lo = -gtl * s_prev
    hi = -gth * s_next
    md = 1.0 + s * (gtl + gth + rim)
    (step_thick,) = spike(lo, md, hi, step_width, False, 8)
    return h + step_thick


def solution(mesh):
    spec = P(None, "cast", "width")
    return jax.shard_map(
        shards, mesh=mesh, in_specs=(spec, spec, P()), out_specs=spec, check_vma=False
    )
```

```python
import functools

import jax
import jax.numpy as jnp
from jax import lax
from jax.experimental import pallas as pl
from jax.experimental.pallas import tpu as pltpu
from jax.sharding import PartitionSpec as P

F32 = jnp.float32
solidification_release = 0.4
quench_medium_hotness = -2.0
SMEM_SPEC = pl.BlockSpec(memory_space=pltpu.SMEM)


def _sweep(n, ld, st, a_ref, b_ref, c_ref, d_ref, y_ref, v_ref, w_ref, cp_ref, unroll, shape):
    with_vw = v_ref is not None
    zero = jnp.zeros(shape, F32)
    one = jnp.ones(shape, F32)

    def fwd(i, carry):
        cprev, dprev, vprev = carry
        a = ld(a_ref, i)
        r = 1.0 / (ld(b_ref, i) - a * cprev)
        cn = ld(c_ref, i) * r
        dn = (ld(d_ref, i) - a * dprev) * r
        st(cp_ref, i, cn)
        st(y_ref, i, dn)
        if with_vw:
            vprev = -(a * vprev) * r
            st(v_ref, i, vprev)
        return cn, dn, vprev

    if unroll is True:
        carry = (zero, zero, one)
        for i in range(n):
            carry = fwd(i, carry)
    else:
        carry = lax.fori_loop(0, n, fwd, (zero, zero, one), unroll=unroll)
    cl, dl, vl = carry
    if with_vw:
        st(w_ref, n - 1, -cl)

    def bwd(j, carry):
        i = n - 2 - j
        yn, vn, wn = carry
        cp = ld(cp_ref, i)
        yn = ld(y_ref, i) - cp * yn
        st(y_ref, i, yn)
        if with_vw:
            vn = ld(v_ref, i) - cp * vn
            wn = -cp * wn
            st(v_ref, i, vn)
            st(w_ref, i, wn)
        return yn, vn, wn

    carry = (dl, vl, -cl)
    if unroll is True:
        for j in range(n - 1):
            carry = bwd(j, carry)
    else:
        lax.fori_loop(0, n - 1, bwd, carry, unroll=unroll)


def _put_summary(sm_ref, ld, n, y_ref, v_ref, w_ref):
    for k, (ref, i) in enumerate(
        [(y_ref, 0), (v_ref, 0), (w_ref, 0), (y_ref, n - 1), (v_ref, n - 1), (w_ref, n - 1)]
    ):
        sm_ref[k] = ld(ref, i)


def _cast_kernel(n, a_ref, b_ref, c_ref, d_ref, y_ref, v_ref, w_ref, sm_ref, cp_ref):
    m = a_ref.shape[0] // n

    def ld(ref, i):
        return ref[pl.ds(i, m, stride=n), :]

    def st(ref, i, val):
        ref[pl.ds(i, m, stride=n), :] = val

    shape = (m, a_ref.shape[1])
    _sweep(n, ld, st, a_ref, b_ref, c_ref, d_ref, y_ref, v_ref, w_ref, cp_ref, True, shape)
    _put_summary(sm_ref, ld, n, y_ref, v_ref, w_ref)


def _lead_ld(ref, i):
    return ref[i]


def _lead_st(ref, i, val):
    ref[i] = val


def _width_kernel(a_ref, b_ref, c_ref, d_ref, y_ref, v_ref, w_ref, sm_ref, cp_ref):
    n = a_ref.shape[0]
    shape = a_ref.shape[1:]
    _sweep(n, _lead_ld, _lead_st, a_ref, b_ref, c_ref, d_ref, y_ref, v_ref, w_ref, cp_ref, 8, shape)
    _put_summary(sm_ref, _lead_ld, n, y_ref, v_ref, w_ref)


def _thick_kernel(a_ref, b_ref, c_ref, d_ref, h_ref, o_ref, y_ref, cp_ref):
    n = a_ref.shape[0]
    shape = a_ref.shape[1:]
    _sweep(n, _lead_ld, _lead_st, a_ref, b_ref, c_ref, d_ref, y_ref, None, None, cp_ref, 8, shape)
    o_ref[...] = h_ref[...] + y_ref[...]


def cast_solve(a, b, c, d, n):
    shp = jax.ShapeDtypeStruct(a.shape, F32)
    m = a.shape[0] // n
    return pl.pallas_call(
        functools.partial(_cast_kernel, n),
        out_shape=[shp, shp, shp, jax.ShapeDtypeStruct((6, m, a.shape[1]), F32)],
        scratch_shapes=[pltpu.VMEM(a.shape, F32)],
    )(a, b, c, d)


def width_solve(a, b, c, d):
    shp = jax.ShapeDtypeStruct(a.shape, F32)
    return pl.pallas_call(
        _width_kernel,
        out_shape=[shp, shp, shp, jax.ShapeDtypeStruct((6,) + a.shape[1:], F32)],
        scratch_shapes=[pltpu.VMEM(a.shape, F32)],
    )(a, b, c, d)


def thick_solve(a, b, c, d, h):
    return pl.pallas_call(
        _thick_kernel,
        out_shape=jax.ShapeDtypeStruct(a.shape, F32),
        scratch_shapes=[pltpu.VMEM(a.shape, F32), pltpu.VMEM(a.shape, F32)],
    )(a, b, c, d, h)


def _reduce_blocks(nb, blk, emit, zero):
    pp, qq = zero, zero
    saved = []
    for p in range(nb):
        y0, v0, w0, yn, vn, wn = blk(p)
        rd = 1.0 / (1.0 - v0 * qq)
        fa = (y0 + v0 * pp) * rd
        fb = w0 * rd
        saved.append((fa, fb, pp, qq))
        pp, qq = yn + vn * (pp + qq * fa), wn + vn * qq * fb
    f_next = zero
    for p in range(nb - 1, -1, -1):
        fa, fb, pp, qq = saved[p]
        f = fa + fb * f_next
        emit(p, pp + qq * f, f_next)
        f_next = f


def _cast_reduced_kernel(s_ref, lr_ref):
    nb = s_ref.shape[1]

    def blk(p):
        return tuple(s_ref[k, p : p + 1] for k in range(6))

    def emit(p, left, right):
        lr_ref[0, p : p + 1] = left
        lr_ref[1, p : p + 1] = right

    _reduce_blocks(nb, blk, emit, jnp.zeros((1, s_ref.shape[2]), F32))


def _width_reduced_kernel(me_ref, r_ref, lr_ref):
    nb = r_ref.shape[0]
    me = me_ref[0]

    def blk(p):
        k = (me - p + nb) % nb
        return tuple(r_ref[k, q] for q in range(6))

    def emit(p, left, right):
        @pl.when(me == p)
        def _():
            lr_ref[0] = left
            lr_ref[1] = right

    _reduce_blocks(nb, blk, emit, jnp.zeros(r_ref.shape[2:], F32))


def _surface_kernel(scale, z_ref, sp_ref, o_ref):
    z = z_ref[...]
    acc = jnp.zeros(z.shape, F32)
    for q in range(sp_ref.shape[0]):
        acc = jnp.where(z == q, sp_ref[q], acc)
    o_ref[...] = acc * scale


def medium_parameters(x):
    t = jnp.tanh(x)
    hot = x - solidification_release * t
    cond = 1.5 - 0.5 * jnp.tanh(hot)
    slope = (1.0 - solidification_release) + solidification_release * t * t
    return hot, cond, slope


def shards(h, zones, spray_coef):
    nt, ncl, nwl = h.shape
    nc, nw = lax.axis_size("cast"), lax.axis_size("width")
    ci, wi = lax.axis_index("cast"), lax.axis_index("width")
    up_c = [(i, i + 1) for i in range(nc - 1)]
    up_w = [(i, i + 1) for i in range(nw - 1)]
    h_cl = lax.ppermute(h[:, -1, :], "cast", up_c)[:, None, :]
    h_ch = lax.ppermute(h[:, 0, :], "cast", [(b, a) for a, b in up_c])[:, None, :]
    h_wl = lax.ppermute(h[:, :, -1], "width", up_w)[:, :, None]
    h_wh = lax.ppermute(h[:, :, 0], "width", [(b, a) for a, b in up_w])[:, :, None]

    surf = pl.pallas_call(
        functools.partial(_surface_kernel, nt * nt / 8.0),
        out_shape=jax.ShapeDtypeStruct((2 * ncl, nwl), F32),
        in_specs=[pl.BlockSpec(memory_space=pltpu.VMEM), SMEM_SPEC],
    )(zones.reshape(2 * ncl, nwl), spray_coef).reshape(2, ncl, nwl)

    T, k, s = medium_parameters(h)
    T_cl, k_cl, s_cl = medium_parameters(h_cl)
    T_ch, k_ch, s_ch = medium_parameters(h_ch)
    T_wl, k_wl, s_wl = medium_parameters(h_wl)
    T_wh, k_wh, s_wh = medium_parameters(h_wh)

    cast_low = (ci > 0).astype(F32)
    cast_high = (ci < nc - 1).astype(F32)
    width_low = (wi > 0).astype(F32)
    width_high = (wi < nw - 1).astype(F32)

    kc = jnp.concatenate([k_cl, k, k_ch], 1)
    Tc = jnp.concatenate([T_cl, T, T_ch], 1)
    sc = jnp.concatenate([s_cl, s, s_ch], 1)
    edge_c = jnp.ones((ncl + 1,), F32).at[0].set(cast_low).at[-1].set(cast_high)
    fc = (ncl * ncl * 4.0) * 0.5 * (kc[:, 1:] + kc[:, :-1]) * edge_c[None, :, None]
    gcl, gch = fc[:, :-1], fc[:, 1:]
    kw = jnp.concatenate([k_wl, k, k_wh], 2)
    Tw = jnp.concatenate([T_wl, T, T_wh], 2)
    sw = jnp.concatenate([s_wl, s, s_wh], 2)
    edge_w = jnp.ones((nwl + 1,), F32).at[0].set(width_low).at[-1].set(width_high)
    fw = (nwl * nwl / 4.0) * 0.5 * (kw[:, :, 1:] + kw[:, :, :-1]) * edge_w[None, None, :]
    gwl, gwh = fw[:, :, :-1], fw[:, :, 1:]
    mid = (nt * nt / 4.0) * 0.5 * (k[1:] + k[:-1])
    zf = jnp.zeros((1, ncl, nwl), F32)
    gtl = jnp.concatenate([zf, mid], 0)
    gth = jnp.concatenate([mid, zf], 0)
    rim = jnp.concatenate([surf[0:1], jnp.zeros((nt - 2, ncl, nwl), F32), surf[1:2]], 0)

    T_prev = jnp.concatenate([T[:1], T[:-1]], 0)
    T_next = jnp.concatenate([T[1:], T[-1:]], 0)
    explicit = rim * (quench_medium_hotness - T)
    explicit = explicit + (gch * (Tc[:, 2:] - T) - gcl * (T - Tc[:, :-2]))
    explicit = explicit + (gwh * (Tw[:, :, 2:] - T) - gwl * (T - Tw[:, :, :-2]))
    explicit = explicit + (gth * (T_next - T) - gtl * (T - T_prev))

    def flat(x):
        return x.reshape(nt * ncl, nwl)

    lo = -gcl * sc[:, :-2]
    hi = -gch * sc[:, 2:]
    md = 1.0 + s * (gcl + gch)
    y, v, w, summ = cast_solve(flat(lo), flat(md), flat(hi), flat(explicit), ncl)
    recv = lax.all_to_all(summ.reshape(6, nc, -1), "cast", 1, 1, tiled=True)
    lr = pl.pallas_call(
        _cast_reduced_kernel, out_shape=jax.ShapeDtypeStruct((2,) + recv.shape[1:], F32)
    )(recv)
    back = lax.all_to_all(lr, "cast", 1, 1, tiled=True).reshape(2, nt, 1, nwl)
    y, v, w = (x.reshape(nt, ncl, nwl) for x in (y, v, w))
    step_cast = y + v * back[0] + w * back[1]

    lines = nt * ncl

    def wl(x):
        return jnp.transpose(x, (2, 0, 1)).reshape(nwl, lines // 128, 128)

    lo = -gwl * sw[:, :, :-2]
    hi = -gwh * sw[:, :, 2:]
    md = 1.0 + s * (gwl + gwh)
    y, v, w, summ = width_solve(wl(lo), wl(md), wl(hi), wl(step_cast))
    got = [summ] + [
        lax.ppermute(summ, "width", [(i, (i + q) % nw) for i in range(nw)]) for q in range(1, nw)
    ]
    lr = pl.pallas_call(
        _width_reduced_kernel,
        out_shape=jax.ShapeDtypeStruct((2,) + summ.shape[1:], F32),
        in_specs=[SMEM_SPEC, pl.BlockSpec(memory_space=pltpu.VMEM)],
    )(wi.astype(jnp.int32).reshape(1), jnp.stack(got))
    step_width = y + v * lr[0][None] + w * lr[1][None]
    step_width = step_width.reshape(nwl, nt, ncl).transpose(1, 2, 0)

    s_prev = jnp.concatenate([s[:1], s[:-1]], 0)
    s_next = jnp.concatenate([s[1:], s[-1:]], 0)
    lo = -gtl * s_prev
    hi = -gth * s_next
    md = 1.0 + s * (gtl + gth + rim)
    return thick_solve(lo, md, hi, step_width, h)


def solution(mesh):
    spec = P(None, "cast", "width")
    return jax.shard_map(
        shards, mesh=mesh, in_specs=(spec, spec, P()), out_specs=spec, check_vma=False
    )
```

```python
import functools

import jax
import jax.numpy as jnp
from jax import lax
from jax.experimental import pallas as pl
from jax.experimental.pallas import tpu as pltpu
from jax.sharding import PartitionSpec as P

F32 = jnp.float32
solidification_release = 0.4
quench_medium_hotness = -2.0
SMEM_SPEC = pl.BlockSpec(memory_space=pltpu.SMEM)


def _sweep(n, subs, ld, st, a_ref, b_ref, c_ref, d_ref, y_ref, v_ref, w_ref, cp_ref, unroll, shape):
    with_vw = v_ref is not None
    zero = jnp.zeros(shape, F32)
    one = jnp.ones(shape, F32)

    def fwd(i, carries):
        out = []
        for s0, (cprev, dprev, vprev) in zip(subs, carries):
            j = s0 + i
            a = ld(a_ref, j)
            r = 1.0 / (ld(b_ref, j) - a * cprev)
            cn = ld(c_ref, j) * r
            dn = (ld(d_ref, j) - a * dprev) * r
            st(cp_ref, j, cn)
            st(y_ref, j, dn)
            if with_vw:
                vprev = -(a * vprev) * r
                st(v_ref, j, vprev)
            out.append((cn, dn, vprev))
        return tuple(out)

    carries = tuple((zero, zero, one) for _ in subs)
    if unroll is True:
        for i in range(n):
            carries = fwd(i, carries)
    else:
        carries = lax.fori_loop(0, n, fwd, carries, unroll=unroll)
    if with_vw:
        for s0, (cl, _, _) in zip(subs, carries):
            st(w_ref, s0 + n - 1, -cl)

    def bwd(jj, carries):
        i = n - 2 - jj
        out = []
        for s0, (yn, vn, wn) in zip(subs, carries):
            j = s0 + i
            cp = ld(cp_ref, j)
            yn = ld(y_ref, j) - cp * yn
            st(y_ref, j, yn)
            if with_vw:
                vn = ld(v_ref, j) - cp * vn
                wn = -cp * wn
                st(v_ref, j, vn)
                st(w_ref, j, wn)
            out.append((yn, vn, wn))
        return tuple(out)

    carries = tuple((dl, vl, -cl) for cl, dl, vl in carries)
    if unroll is True:
        for jj in range(n - 1):
            carries = bwd(jj, carries)
    else:
        lax.fori_loop(0, n - 1, bwd, carries, unroll=unroll)


def _summary_rows(ld, s0, n, y_ref, v_ref, w_ref):
    return [ld(y_ref, s0), ld(v_ref, s0), ld(w_ref, s0),
            ld(y_ref, s0 + n - 1), ld(v_ref, s0 + n - 1), ld(w_ref, s0 + n - 1)]


def _cast_kernel(n, a_ref, b_ref, c_ref, d_ref, y_ref, v_ref, w_ref, sm_ref, cp_ref):
    m = a_ref.shape[0] // n

    def ld(ref, i):
        return ref[pl.ds(i, m, stride=n), :]

    def st(ref, i, val):
        ref[pl.ds(i, m, stride=n), :] = val

    shape = (m, a_ref.shape[1])
    _sweep(n, [0], ld, st, a_ref, b_ref, c_ref, d_ref, y_ref, v_ref, w_ref, cp_ref, True, shape)
    rows = _summary_rows(ld, 0, n, y_ref, v_ref, w_ref)
    rows += [jnp.zeros(shape, F32)] * (8 - len(rows))
    for k, val in enumerate(rows):
        sm_ref[pl.ds(k, m, stride=8), :] = val


def _lead_ld(ref, i):
    return ref[i]


def _lead_st(ref, i, val):
    ref[i] = val


def _width_kernel(nsub, a_ref, b_ref, c_ref, d_ref, y_ref, v_ref, w_ref, sm_ref, cp_ref):
    n = a_ref.shape[0] // nsub
    subs = [q * n for q in range(nsub)]
    shape = a_ref.shape[1:]
    _sweep(n, subs, _lead_ld, _lead_st, a_ref, b_ref, c_ref, d_ref, y_ref, v_ref, w_ref, cp_ref, 4, shape)
    for q, s0 in enumerate(subs):
        for k, val in enumerate(_summary_rows(_lead_ld, s0, n, y_ref, v_ref, w_ref)):
            sm_ref[q, k] = val


def _thick_kernel(a_ref, b_ref, c_ref, d_ref, h_ref, o_ref, y_ref, cp_ref):
    n = a_ref.shape[0]
    shape = a_ref.shape[1:]
    _sweep(n, [0], _lead_ld, _lead_st, a_ref, b_ref, c_ref, d_ref, y_ref, None, None, cp_ref, 8, shape)
    o_ref[...] = h_ref[...] + y_ref[...]


def cast_solve(a, b, c, d, n):
    shp = jax.ShapeDtypeStruct(a.shape, F32)
    m = a.shape[0] // n
    return pl.pallas_call(
        functools.partial(_cast_kernel, n),
        out_shape=[shp, shp, shp, jax.ShapeDtypeStruct((m * 8, a.shape[1]), F32)],
        scratch_shapes=[pltpu.VMEM(a.shape, F32)],
    )(a, b, c, d)


def width_solve(a, b, c, d, nsub):
    shp = jax.ShapeDtypeStruct(a.shape, F32)
    return pl.pallas_call(
        functools.partial(_width_kernel, nsub),
        out_shape=[shp, shp, shp, jax.ShapeDtypeStruct((nsub, 6) + a.shape[1:], F32)],
        scratch_shapes=[pltpu.VMEM(a.shape, F32)],
    )(a, b, c, d)


def thick_solve(a, b, c, d, h):
    return pl.pallas_call(
        _thick_kernel,
        out_shape=jax.ShapeDtypeStruct(a.shape, F32),
        scratch_shapes=[pltpu.VMEM(a.shape, F32), pltpu.VMEM(a.shape, F32)],
    )(a, b, c, d, h)


def _reduce_blocks(nb, blk, emit, zero):
    pp, qq = zero, zero
    saved = []
    for p in range(nb):
        y0, v0, w0, yn, vn, wn = blk(p)
        rd = 1.0 / (1.0 - v0 * qq)
        fa = (y0 + v0 * pp) * rd
        fb = w0 * rd
        saved.append((fa, fb, pp, qq))
        pp, qq = yn + vn * (pp + qq * fa), wn + vn * qq * fb
    f_next = zero
    for p in range(nb - 1, -1, -1):
        fa, fb, pp, qq = saved[p]
        f = fa + fb * f_next
        emit(p, pp + qq * f, f_next)
        f_next = f


def _cast_reduced_kernel(s_ref, lr_ref):
    nb = s_ref.shape[0]
    lr_ref[...] = jnp.zeros(lr_ref.shape, F32)

    def blk(p):
        return tuple(s_ref[p, :, k, :] for k in range(6))

    def emit(p, left, right):
        lr_ref[p, :, 0, :] = left
        lr_ref[p, :, 1, :] = right

    _reduce_blocks(nb, blk, emit, jnp.zeros((s_ref.shape[1], s_ref.shape[3]), F32))


def _width_reduced_kernel(me_ref, *refs):
    *r_refs, lr_ref = refs
    nw = len(r_refs)
    nsub = r_refs[0].shape[0]
    me = me_ref[0]

    def blk(b):
        dev, q = divmod(b, nsub)
        kk = (me - dev + nw) % nw
        vals = []
        for k6 in range(6):
            val = r_refs[0][q, k6]
            for k in range(1, nw):
                val = jnp.where(kk == k, r_refs[k][q, k6], val)
            vals.append(val)
        return tuple(vals)

    def emit(b, left, right):
        dev, q = divmod(b, nsub)

        @pl.when(me == dev)
        def _():
            lr_ref[q, 0] = left
            lr_ref[q, 1] = right

    _reduce_blocks(nw * nsub, blk, emit, jnp.zeros(r_refs[0].shape[2:], F32))


def _surface_kernel(scale, z_ref, sp_ref, o_ref):
    z = z_ref[...]
    acc = jnp.zeros(z.shape, F32)
    for q in range(sp_ref.shape[0]):
        acc = jnp.where(z == q, sp_ref[q], acc)
    o_ref[...] = acc * scale


def medium_parameters(x):
    t = jnp.tanh(x)
    hot = x - solidification_release * t
    cond = 1.5 - 0.5 * jnp.tanh(hot)
    slope = (1.0 - solidification_release) + solidification_release * t * t
    return hot, cond, slope


def shards(h, zones, spray_coef):
    nt, ncl, nwl = h.shape
    nc, nw = lax.axis_size("cast"), lax.axis_size("width")
    ci, wi = lax.axis_index("cast"), lax.axis_index("width")
    up_c = [(i, i + 1) for i in range(nc - 1)]
    up_w = [(i, i + 1) for i in range(nw - 1)]
    h_cl = lax.ppermute(h[:, -1, :], "cast", up_c)[:, None, :]
    h_ch = lax.ppermute(h[:, 0, :], "cast", [(b, a) for a, b in up_c])[:, None, :]
    h_wl = lax.ppermute(h[:, :, -1], "width", up_w)[:, :, None]
    h_wh = lax.ppermute(h[:, :, 0], "width", [(b, a) for a, b in up_w])[:, :, None]

    surf = pl.pallas_call(
        functools.partial(_surface_kernel, nt * nt / 8.0),
        out_shape=jax.ShapeDtypeStruct((2 * ncl, nwl), F32),
        in_specs=[pl.BlockSpec(memory_space=pltpu.VMEM), SMEM_SPEC],
    )(zones.reshape(2 * ncl, nwl), spray_coef).reshape(2, ncl, nwl)

    T, k, s = medium_parameters(h)
    T_cl, k_cl, s_cl = medium_parameters(h_cl)
    T_ch, k_ch, s_ch = medium_parameters(h_ch)
    T_wl, k_wl, s_wl = medium_parameters(h_wl)
    T_wh, k_wh, s_wh = medium_parameters(h_wh)

    cast_low = (ci > 0).astype(F32)
    cast_high = (ci < nc - 1).astype(F32)
    width_low = (wi > 0).astype(F32)
    width_high = (wi < nw - 1).astype(F32)

    kc = jnp.concatenate([k_cl, k, k_ch], 1)
    Tc = jnp.concatenate([T_cl, T, T_ch], 1)
    sc = jnp.concatenate([s_cl, s, s_ch], 1)
    edge_c = jnp.ones((ncl + 1,), F32).at[0].set(cast_low).at[-1].set(cast_high)
    fc = (ncl * ncl * 4.0) * 0.5 * (kc[:, 1:] + kc[:, :-1]) * edge_c[None, :, None]
    gcl, gch = fc[:, :-1], fc[:, 1:]
    kw = jnp.concatenate([k_wl, k, k_wh], 2)
    Tw = jnp.concatenate([T_wl, T, T_wh], 2)
    sw = jnp.concatenate([s_wl, s, s_wh], 2)
    edge_w = jnp.ones((nwl + 1,), F32).at[0].set(width_low).at[-1].set(width_high)
    fw = (nwl * nwl / 4.0) * 0.5 * (kw[:, :, 1:] + kw[:, :, :-1]) * edge_w[None, None, :]
    gwl, gwh = fw[:, :, :-1], fw[:, :, 1:]
    mid = (nt * nt / 4.0) * 0.5 * (k[1:] + k[:-1])
    zf = jnp.zeros((1, ncl, nwl), F32)
    gtl = jnp.concatenate([zf, mid], 0)
    gth = jnp.concatenate([mid, zf], 0)
    rim = jnp.concatenate([surf[0:1], jnp.zeros((nt - 2, ncl, nwl), F32), surf[1:2]], 0)

    T_prev = jnp.concatenate([T[:1], T[:-1]], 0)
    T_next = jnp.concatenate([T[1:], T[-1:]], 0)
    explicit = rim * (quench_medium_hotness - T)
    explicit = explicit + (gch * (Tc[:, 2:] - T) - gcl * (T - Tc[:, :-2]))
    explicit = explicit + (gwh * (Tw[:, :, 2:] - T) - gwl * (T - Tw[:, :, :-2]))
    explicit = explicit + (gth * (T_next - T) - gtl * (T - T_prev))

    def flat(x):
        return x.reshape(nt * ncl, nwl)

    lo = -gcl * sc[:, :-2]
    hi = -gch * sc[:, 2:]
    md = 1.0 + s * (gcl + gch)
    y, v, w, summ = cast_solve(flat(lo), flat(md), flat(hi), flat(explicit), ncl)
    recv = lax.all_to_all(summ.reshape(nc, nt // nc, 8, nwl), "cast", 0, 0, tiled=True)
    lr = pl.pallas_call(_cast_reduced_kernel, out_shape=jax.ShapeDtypeStruct(recv.shape, F32))(recv)
    back = lax.all_to_all(lr, "cast", 0, 0, tiled=True).reshape(nt, 8, nwl)
    y, v, w = (x.reshape(nt, ncl, nwl) for x in (y, v, w))
    step_cast = y + v * back[:, 0:1] + w * back[:, 1:2]

    lines = nt * ncl
    nsub = 4

    def wl(x):
        return jnp.transpose(x, (2, 0, 1)).reshape(nwl, lines // 128, 128)

    lo = -gwl * sw[:, :, :-2]
    hi = -gwh * sw[:, :, 2:]
    md = 1.0 + s * (gwl + gwh)
    y, v, w, summ = width_solve(wl(lo), wl(md), wl(hi), wl(step_cast), nsub)
    got = [summ] + [
        lax.ppermute(summ, "width", [(i, (i + q) % nw) for i in range(nw)]) for q in range(1, nw)
    ]
    lr = pl.pallas_call(
        _width_reduced_kernel,
        out_shape=jax.ShapeDtypeStruct((nsub, 2) + summ.shape[2:], F32),
        in_specs=[SMEM_SPEC] + [pl.BlockSpec(memory_space=pltpu.VMEM)] * nw,
    )(wi.astype(jnp.int32).reshape(1), *got)
    sub = (nsub, nwl // nsub) + y.shape[1:]
    y, v, w = (x.reshape(sub) for x in (y, v, w))
    step_width = y + v * lr[:, 0:1] + w * lr[:, 1:2]
    step_width = step_width.reshape(nwl, nt, ncl).transpose(1, 2, 0)

    s_prev = jnp.concatenate([s[:1], s[:-1]], 0)
    s_next = jnp.concatenate([s[1:], s[-1:]], 0)
    lo = -gtl * s_prev
    hi = -gth * s_next
    md = 1.0 + s * (gtl + gth + rim)
    return thick_solve(lo, md, hi, step_width, h)


def solution(mesh):
    spec = P(None, "cast", "width")
    return jax.shard_map(
        shards, mesh=mesh, in_specs=(spec, spec, P()), out_specs=spec, check_vma=False
    )
```

```python
import functools

import jax
import jax.numpy as jnp
from jax import lax
from jax.experimental import pallas as pl
from jax.experimental.pallas import tpu as pltpu
from jax.sharding import PartitionSpec as P

F32 = jnp.float32
solidification_release = 0.4
quench_medium_hotness = -2.0
SMEM_SPEC = pl.BlockSpec(memory_space=pltpu.SMEM)


def _sweep(n, subs, ld, st, a_ref, b_ref, c_ref, d_ref, y_ref, v_ref, w_ref, cp_ref, unroll, shape):
    with_vw = v_ref is not None
    zero = jnp.zeros(shape, F32)
    one = jnp.ones(shape, F32)

    def fwd(i, carries):
        out = []
        for s0, (cprev, dprev, vprev) in zip(subs, carries):
            j = s0 + i
            a = ld(a_ref, j)
            r = 1.0 / (ld(b_ref, j) - a * cprev)
            cn = ld(c_ref, j) * r
            dn = (ld(d_ref, j) - a * dprev) * r
            st(cp_ref, j, cn)
            st(y_ref, j, dn)
            if with_vw:
                vprev = -(a * vprev) * r
                st(v_ref, j, vprev)
            out.append((cn, dn, vprev))
        return tuple(out)

    carries = tuple((zero, zero, one) for _ in subs)
    if unroll is True:
        for i in range(n):
            carries = fwd(i, carries)
    else:
        carries = lax.fori_loop(0, n, fwd, carries, unroll=unroll)
    if with_vw:
        for s0, (cl, _, _) in zip(subs, carries):
            st(w_ref, s0 + n - 1, -cl)

    def bwd(jj, carries):
        i = n - 2 - jj
        out = []
        for s0, (yn, vn, wn) in zip(subs, carries):
            j = s0 + i
            cp = ld(cp_ref, j)
            yn = ld(y_ref, j) - cp * yn
            st(y_ref, j, yn)
            if with_vw:
                vn = ld(v_ref, j) - cp * vn
                wn = -cp * wn
                st(v_ref, j, vn)
                st(w_ref, j, wn)
            out.append((yn, vn, wn))
        return tuple(out)

    carries = tuple((dl, vl, -cl) for cl, dl, vl in carries)
    if unroll is True:
        for jj in range(n - 1):
            carries = bwd(jj, carries)
    else:
        lax.fori_loop(0, n - 1, bwd, carries, unroll=unroll)


def _summary_rows(ld, s0, n, y_ref, v_ref, w_ref):
    return [ld(y_ref, s0), ld(v_ref, s0), ld(w_ref, s0),
            ld(y_ref, s0 + n - 1), ld(v_ref, s0 + n - 1), ld(w_ref, s0 + n - 1)]


def _cast_kernel(n, a_ref, b_ref, c_ref, d_ref, y_ref, v_ref, w_ref, sm_ref, cp_ref):
    m = a_ref.shape[0] // n

    def ld(ref, i):
        return ref[pl.ds(i, m, stride=n), :]

    def st(ref, i, val):
        ref[pl.ds(i, m, stride=n), :] = val

    shape = (m, a_ref.shape[1])
    _sweep(n, [0], ld, st, a_ref, b_ref, c_ref, d_ref, y_ref, v_ref, w_ref, cp_ref, True, shape)
    rows = _summary_rows(ld, 0, n, y_ref, v_ref, w_ref)
    rows += [jnp.zeros(shape, F32)] * (8 - len(rows))
    for k, val in enumerate(rows):
        sm_ref[pl.ds(k, m, stride=8), :] = val


def _lead_ld(ref, i):
    return ref[i]


def _lead_st(ref, i, val):
    ref[i] = val


def _width_kernel(nsub, yc_ref, vc_ref, wc_ref, bk_ref, a_ref, b_ref, c_ref,
                  y_ref, v_ref, w_ref, sm_ref, cp_ref, d_ref):
    sc = yc_ref[...] + vc_ref[...] * bk_ref[:, 0:1, :] + wc_ref[...] * bk_ref[:, 1:2, :]
    nt, ncl, nwl = sc.shape
    sc = sc.reshape(nt * ncl, nwl)
    for q in range(d_ref.shape[1]):
        d_ref[:, q, :] = sc[q * 128 : (q + 1) * 128, :].T
    n = a_ref.shape[0] // nsub
    subs = [q * n for q in range(nsub)]
    shape = a_ref.shape[1:]
    _sweep(n, subs, _lead_ld, _lead_st, a_ref, b_ref, c_ref, d_ref, y_ref, v_ref, w_ref, cp_ref, 4, shape)
    for q, s0 in enumerate(subs):
        for k, val in enumerate(_summary_rows(_lead_ld, s0, n, y_ref, v_ref, w_ref)):
            sm_ref[q, k] = val


def _thick_kernel(nsub, yw_ref, vw_ref, ww_ref, lr_ref, a_ref, b_ref, c_ref, h_ref,
                  o_ref, sw_ref, d_ref, y_ref, cp_ref):
    m = yw_ref.shape[0] // nsub
    for q in range(nsub):
        sl = slice(q * m, (q + 1) * m)
        sw_ref[sl] = yw_ref[sl] + vw_ref[sl] * lr_ref[q, 0] + ww_ref[sl] * lr_ref[q, 1]
    nt, ncl, nwl = a_ref.shape
    per_q = 128 // ncl
    for q in range(sw_ref.shape[1]):
        d_ref[q * per_q : (q + 1) * per_q] = sw_ref[:, q, :].T.reshape(per_q, ncl, nwl)
    shape = a_ref.shape[1:]
    _sweep(nt, [0], _lead_ld, _lead_st, a_ref, b_ref, c_ref, d_ref, y_ref, None, None, cp_ref, 8, shape)
    o_ref[...] = h_ref[...] + y_ref[...]


def cast_solve(a, b, c, d, n):
    shp = jax.ShapeDtypeStruct(a.shape, F32)
    m = a.shape[0] // n
    return pl.pallas_call(
        functools.partial(_cast_kernel, n),
        out_shape=[shp, shp, shp, jax.ShapeDtypeStruct((m * 8, a.shape[1]), F32)],
        scratch_shapes=[pltpu.VMEM(a.shape, F32)],
    )(a, b, c, d)


def width_solve(yc, vc, wc, bk, a, b, c, nsub):
    shp = jax.ShapeDtypeStruct(a.shape, F32)
    return pl.pallas_call(
        functools.partial(_width_kernel, nsub),
        out_shape=[shp, shp, shp, jax.ShapeDtypeStruct((nsub, 6) + a.shape[1:], F32)],
        scratch_shapes=[pltpu.VMEM(a.shape, F32), pltpu.VMEM(a.shape, F32)],
    )(yc, vc, wc, bk, a, b, c)


def thick_solve(yw, vw, ww, lr, a, b, c, h, nsub):
    return pl.pallas_call(
        functools.partial(_thick_kernel, nsub),
        out_shape=jax.ShapeDtypeStruct(a.shape, F32),
        scratch_shapes=[pltpu.VMEM(yw.shape, F32)] + [pltpu.VMEM(a.shape, F32)] * 3,
    )(yw, vw, ww, lr, a, b, c, h)


def _reduce_blocks(nb, blk, emit, zero):
    pp, qq = zero, zero
    saved = []
    for p in range(nb):
        y0, v0, w0, yn, vn, wn = blk(p)
        rd = 1.0 / (1.0 - v0 * qq)
        fa = (y0 + v0 * pp) * rd
        fb = w0 * rd
        saved.append((fa, fb, pp, qq))
        pp, qq = yn + vn * (pp + qq * fa), wn + vn * qq * fb
    f_next = zero
    for p in range(nb - 1, -1, -1):
        fa, fb, pp, qq = saved[p]
        f = fa + fb * f_next
        emit(p, pp + qq * f, f_next)
        f_next = f


def _cast_reduced_kernel(s_ref, lr_ref):
    nb = s_ref.shape[0]
    def blk(p):
        return tuple(s_ref[p, :, k, :] for k in range(6))

    def emit(p, left, right):
        lr_ref[p, :, 0:1, :] = left[:, None]
        lr_ref[p, :, 1:2, :] = right[:, None]

    _reduce_blocks(nb, blk, emit, jnp.zeros((s_ref.shape[1], s_ref.shape[3]), F32))


def _width_reduced_kernel(me_ref, *refs):
    *r_refs, lr_ref = refs
    nw = len(r_refs)
    nsub = r_refs[0].shape[0]
    me = me_ref[0]

    def blk(b):
        dev, q = divmod(b, nsub)
        kk = (me - dev + nw) % nw
        vals = []
        for k6 in range(6):
            val = r_refs[0][q, k6]
            for k in range(1, nw):
                val = jnp.where(kk == k, r_refs[k][q, k6], val)
            vals.append(val)
        return tuple(vals)

    def emit(b, left, right):
        dev, q = divmod(b, nsub)

        @pl.when(me == dev)
        def _():
            lr_ref[q, 0] = left
            lr_ref[q, 1] = right

    _reduce_blocks(nw * nsub, blk, emit, jnp.zeros(r_refs[0].shape[2:], F32))


def _surface_kernel(scale, z_ref, sp_ref, o_ref):
    z = z_ref[...]
    acc = jnp.zeros(z.shape, F32)
    for q in range(sp_ref.shape[0]):
        acc = jnp.where(z == q, sp_ref[q], acc)
    o_ref[...] = acc * scale


def medium_parameters(x):
    t = jnp.tanh(x)
    hot = x - solidification_release * t
    cond = 1.5 - 0.5 * jnp.tanh(hot)
    slope = (1.0 - solidification_release) + solidification_release * t * t
    return hot, cond, slope


def shards(h, zones, spray_coef):
    nt, ncl, nwl = h.shape
    nc, nw = lax.axis_size("cast"), lax.axis_size("width")
    ci, wi = lax.axis_index("cast"), lax.axis_index("width")
    up_c = [(i, i + 1) for i in range(nc - 1)]
    up_w = [(i, i + 1) for i in range(nw - 1)]
    h_cl = lax.ppermute(h[:, -1, :], "cast", up_c)[:, None, :]
    h_ch = lax.ppermute(h[:, 0, :], "cast", [(b, a) for a, b in up_c])[:, None, :]
    h_wl = lax.ppermute(h[:, :, -1], "width", up_w)[:, :, None]
    h_wh = lax.ppermute(h[:, :, 0], "width", [(b, a) for a, b in up_w])[:, :, None]

    surf = pl.pallas_call(
        functools.partial(_surface_kernel, nt * nt / 8.0),
        out_shape=jax.ShapeDtypeStruct((2 * ncl, nwl), F32),
        in_specs=[pl.BlockSpec(memory_space=pltpu.VMEM), SMEM_SPEC],
    )(zones.reshape(2 * ncl, nwl), spray_coef).reshape(2, ncl, nwl)

    T, k, s = medium_parameters(h)
    T_cl, k_cl, s_cl = medium_parameters(h_cl)
    T_ch, k_ch, s_ch = medium_parameters(h_ch)
    T_wl, k_wl, s_wl = medium_parameters(h_wl)
    T_wh, k_wh, s_wh = medium_parameters(h_wh)

    cast_low = (ci > 0).astype(F32)
    cast_high = (ci < nc - 1).astype(F32)
    width_low = (wi > 0).astype(F32)
    width_high = (wi < nw - 1).astype(F32)

    kc = jnp.concatenate([k_cl, k, k_ch], 1)
    Tc = jnp.concatenate([T_cl, T, T_ch], 1)
    sc = jnp.concatenate([s_cl, s, s_ch], 1)
    edge_c = jnp.ones((ncl + 1,), F32).at[0].set(cast_low).at[-1].set(cast_high)
    fc = (ncl * ncl * 4.0) * 0.5 * (kc[:, 1:] + kc[:, :-1]) * edge_c[None, :, None]
    gcl, gch = fc[:, :-1], fc[:, 1:]
    kw = jnp.concatenate([k_wl, k, k_wh], 2)
    Tw = jnp.concatenate([T_wl, T, T_wh], 2)
    sw = jnp.concatenate([s_wl, s, s_wh], 2)
    edge_w = jnp.ones((nwl + 1,), F32).at[0].set(width_low).at[-1].set(width_high)
    fw = (nwl * nwl / 4.0) * 0.5 * (kw[:, :, 1:] + kw[:, :, :-1]) * edge_w[None, None, :]
    gwl, gwh = fw[:, :, :-1], fw[:, :, 1:]
    mid = (nt * nt / 4.0) * 0.5 * (k[1:] + k[:-1])
    zf = jnp.zeros((1, ncl, nwl), F32)
    gtl = jnp.concatenate([zf, mid], 0)
    gth = jnp.concatenate([mid, zf], 0)
    rim = jnp.concatenate([surf[0:1], jnp.zeros((nt - 2, ncl, nwl), F32), surf[1:2]], 0)

    T_prev = jnp.concatenate([T[:1], T[:-1]], 0)
    T_next = jnp.concatenate([T[1:], T[-1:]], 0)
    explicit = rim * (quench_medium_hotness - T)
    explicit = explicit + (gch * (Tc[:, 2:] - T) - gcl * (T - Tc[:, :-2]))
    explicit = explicit + (gwh * (Tw[:, :, 2:] - T) - gwl * (T - Tw[:, :, :-2]))
    explicit = explicit + (gth * (T_next - T) - gtl * (T - T_prev))

    def flat(x):
        return x.reshape(nt * ncl, nwl)

    lo = -gcl * sc[:, :-2]
    hi = -gch * sc[:, 2:]
    md = 1.0 + s * (gcl + gch)
    y, v, w, summ = cast_solve(flat(lo), flat(md), flat(hi), flat(explicit), ncl)
    recv = lax.all_to_all(summ.reshape(nc, nt // nc, 8, nwl), "cast", 0, 0, tiled=True)
    lr_shape = recv.shape[:2] + (2, nwl)
    lr = pl.pallas_call(_cast_reduced_kernel, out_shape=jax.ShapeDtypeStruct(lr_shape, F32))(recv)
    back = lax.all_to_all(lr, "cast", 0, 0, tiled=True).reshape(nt, 2, nwl)
    y, v, w = (x.reshape(nt, ncl, nwl) for x in (y, v, w))

    lines = nt * ncl
    nsub = 4

    def wl(x):
        return jnp.transpose(x, (2, 0, 1)).reshape(nwl, lines // 128, 128)

    lo = -gwl * sw[:, :, :-2]
    hi = -gwh * sw[:, :, 2:]
    md = 1.0 + s * (gwl + gwh)
    y, v, w, summ = width_solve(y, v, w, back, wl(lo), wl(md), wl(hi), nsub)
    got = [summ] + [
        lax.ppermute(summ, "width", [(i, (i + q) % nw) for i in range(nw)]) for q in range(1, nw)
    ]
    lr = pl.pallas_call(
        _width_reduced_kernel,
        out_shape=jax.ShapeDtypeStruct((nsub, 2) + summ.shape[2:], F32),
        in_specs=[SMEM_SPEC] + [pl.BlockSpec(memory_space=pltpu.VMEM)] * nw,
    )(wi.astype(jnp.int32).reshape(1), *got)
    s_prev = jnp.concatenate([s[:1], s[:-1]], 0)
    s_next = jnp.concatenate([s[1:], s[-1:]], 0)
    lo = -gtl * s_prev
    hi = -gth * s_next
    md = 1.0 + s * (gtl + gth + rim)
    return thick_solve(y, v, w, lr, lo, md, hi, h, nsub)


def solution(mesh):
    spec = P(None, "cast", "width")
    return jax.shard_map(
        shards, mesh=mesh, in_specs=(spec, spec, P()), out_specs=spec, check_vma=False
    )
```

```python
import functools

import jax
import jax.numpy as jnp
from jax import lax
from jax.experimental import pallas as pl
from jax.experimental.pallas import tpu as pltpu
from jax.sharding import PartitionSpec as P

F32 = jnp.float32
solidification_release = 0.4
quench_medium_hotness = -2.0
SMEM_SPEC = pl.BlockSpec(memory_space=pltpu.SMEM)


def _sweep(n, subs, ld, st, a_ref, b_ref, c_ref, d_ref, y_ref, v_ref, w_ref, cp_ref, unroll, shape):
    with_vw = v_ref is not None
    zero = jnp.zeros(shape, F32)
    one = jnp.ones(shape, F32)

    def fwd(i, carries):
        out = []
        for s0, (cprev, dprev, vprev) in zip(subs, carries):
            j = s0 + i
            a = ld(a_ref, j)
            r = 1.0 / (ld(b_ref, j) - a * cprev)
            cn = ld(c_ref, j) * r
            dn = (ld(d_ref, j) - a * dprev) * r
            st(cp_ref, j, cn)
            st(y_ref, j, dn)
            if with_vw:
                vprev = -(a * vprev) * r
                st(v_ref, j, vprev)
            out.append((cn, dn, vprev))
        return tuple(out)

    carries = tuple((zero, zero, one) for _ in subs)
    if unroll is True:
        for i in range(n):
            carries = fwd(i, carries)
    else:
        carries = lax.fori_loop(0, n, fwd, carries, unroll=unroll)
    if with_vw:
        for s0, (cl, _, _) in zip(subs, carries):
            st(w_ref, s0 + n - 1, -cl)

    def bwd(jj, carries):
        i = n - 2 - jj
        out = []
        for s0, (yn, vn, wn) in zip(subs, carries):
            j = s0 + i
            cp = ld(cp_ref, j)
            yn = ld(y_ref, j) - cp * yn
            st(y_ref, j, yn)
            if with_vw:
                vn = ld(v_ref, j) - cp * vn
                wn = -cp * wn
                st(v_ref, j, vn)
                st(w_ref, j, wn)
            out.append((yn, vn, wn))
        return tuple(out)

    carries = tuple((dl, vl, -cl) for cl, dl, vl in carries)
    if unroll is True:
        for jj in range(n - 1):
            carries = bwd(jj, carries)
    else:
        lax.fori_loop(0, n - 1, bwd, carries, unroll=unroll)


def _summary_rows(ld, s0, n, y_ref, v_ref, w_ref):
    return [ld(y_ref, s0), ld(v_ref, s0), ld(w_ref, s0),
            ld(y_ref, s0 + n - 1), ld(v_ref, s0 + n - 1), ld(w_ref, s0 + n - 1)]


def _cast_kernel(n, a_ref, b_ref, c_ref, d_ref, y_ref, v_ref, w_ref, sm_ref, cp_ref):
    m = a_ref.shape[0] // n

    def ld(ref, i):
        return ref[pl.ds(i, m, stride=n), :]

    def st(ref, i, val):
        ref[pl.ds(i, m, stride=n), :] = val

    shape = (m, a_ref.shape[1])
    _sweep(n, [0], ld, st, a_ref, b_ref, c_ref, d_ref, y_ref, v_ref, w_ref, cp_ref, True, shape)
    rows = _summary_rows(ld, 0, n, y_ref, v_ref, w_ref)
    rows += [jnp.zeros(shape, F32)] * (8 - len(rows))
    for k, val in enumerate(rows):
        sm_ref[pl.ds(k, m, stride=8), :] = val


def _lead_ld(ref, i):
    return ref[i]


def _lead_st(ref, i, val):
    ref[i] = val


def _width_kernel(nsub, yc_ref, vc_ref, wc_ref, bk_ref, a_ref, b_ref, c_ref,
                  y_ref, v_ref, w_ref, sm_ref, cp_ref, d_ref):
    sc = yc_ref[...] + vc_ref[...] * bk_ref[:, 0:1, :] + wc_ref[...] * bk_ref[:, 1:2, :]
    nt, ncl, nwl = sc.shape
    sc = sc.reshape(nt * ncl, nwl)
    for q in range(d_ref.shape[1]):
        d_ref[:, q, :] = sc[q * 128 : (q + 1) * 128, :].T
    n = a_ref.shape[0] // nsub
    subs = [q * n for q in range(nsub)]
    shape = a_ref.shape[1:]
    _sweep(n, subs, _lead_ld, _lead_st, a_ref, b_ref, c_ref, d_ref, y_ref, v_ref, w_ref, cp_ref, 4, shape)
    for q, s0 in enumerate(subs):
        for k, val in enumerate(_summary_rows(_lead_ld, s0, n, y_ref, v_ref, w_ref)):
            sm_ref[q, k] = val


def _thick_kernel(nsub, tsub, yw_ref, vw_ref, ww_ref, lr_ref, a_ref, b_ref, c_ref, h_ref,
                  o_ref, sw_ref, d_ref, y_ref, v_ref, w_ref, cp_ref):
    m = yw_ref.shape[0] // nsub
    for q in range(nsub):
        sl = slice(q * m, (q + 1) * m)
        sw_ref[sl] = yw_ref[sl] + vw_ref[sl] * lr_ref[q, 0] + ww_ref[sl] * lr_ref[q, 1]
    nt, ncl, nwl = a_ref.shape
    per_q = 128 // ncl
    for q in range(sw_ref.shape[1]):
        d_ref[q * per_q : (q + 1) * per_q] = sw_ref[:, q, :].T.reshape(per_q, ncl, nwl)
    n = nt // tsub
    subs = [q * n for q in range(tsub)]
    shape = a_ref.shape[1:]
    _sweep(n, subs, _lead_ld, _lead_st, a_ref, b_ref, c_ref, d_ref, y_ref, v_ref, w_ref, cp_ref, 4, shape)
    sums = [tuple(_summary_rows(_lead_ld, s0, n, y_ref, v_ref, w_ref)) for s0 in subs]
    lrs = [None] * tsub

    def emit(p, left, right):
        lrs[p] = (left, right)

    _reduce_blocks(tsub, lambda p: sums[p], emit, jnp.zeros(shape, F32))
    for q, s0 in enumerate(subs):
        sl = slice(s0, s0 + n)
        left, right = lrs[q]
        o_ref[sl] = h_ref[sl] + (y_ref[sl] + v_ref[sl] * left + w_ref[sl] * right)


def cast_solve(a, b, c, d, n):
    shp = jax.ShapeDtypeStruct(a.shape, F32)
    m = a.shape[0] // n
    return pl.pallas_call(
        functools.partial(_cast_kernel, n),
        out_shape=[shp, shp, shp, jax.ShapeDtypeStruct((m * 8, a.shape[1]), F32)],
        scratch_shapes=[pltpu.VMEM(a.shape, F32)],
    )(a, b, c, d)


def width_solve(yc, vc, wc, bk, a, b, c, nsub):
    shp = jax.ShapeDtypeStruct(a.shape, F32)
    return pl.pallas_call(
        functools.partial(_width_kernel, nsub),
        out_shape=[shp, shp, shp, jax.ShapeDtypeStruct((nsub, 6) + a.shape[1:], F32)],
        scratch_shapes=[pltpu.VMEM(a.shape, F32), pltpu.VMEM(a.shape, F32)],
    )(yc, vc, wc, bk, a, b, c)


def thick_solve(yw, vw, ww, lr, a, b, c, h, nsub, tsub):
    return pl.pallas_call(
        functools.partial(_thick_kernel, nsub, tsub),
        out_shape=jax.ShapeDtypeStruct(a.shape, F32),
        scratch_shapes=[pltpu.VMEM(yw.shape, F32)] + [pltpu.VMEM(a.shape, F32)] * 5,
    )(yw, vw, ww, lr, a, b, c, h)


def _reduce_blocks(nb, blk, emit, zero):
    pp, qq = zero, zero
    saved = []
    for p in range(nb):
        y0, v0, w0, yn, vn, wn = blk(p)
        rd = 1.0 / (1.0 - v0 * qq)
        fa = (y0 + v0 * pp) * rd
        fb = w0 * rd
        saved.append((fa, fb, pp, qq))
        pp, qq = yn + vn * (pp + qq * fa), wn + vn * qq * fb
    f_next = zero
    for p in range(nb - 1, -1, -1):
        fa, fb, pp, qq = saved[p]
        f = fa + fb * f_next
        emit(p, pp + qq * f, f_next)
        f_next = f


def _cast_reduced_kernel(s_ref, lr_ref):
    nb = s_ref.shape[0]
    def blk(p):
        return tuple(s_ref[p, :, k, :] for k in range(6))

    def emit(p, left, right):
        lr_ref[p, :, 0:1, :] = left[:, None]
        lr_ref[p, :, 1:2, :] = right[:, None]

    _reduce_blocks(nb, blk, emit, jnp.zeros((s_ref.shape[1], s_ref.shape[3]), F32))


def _width_reduced_kernel(me_ref, *refs):
    *r_refs, lr_ref = refs
    nw = len(r_refs)
    nsub = r_refs[0].shape[0]
    me = me_ref[0]

    def blk(b):
        dev, q = divmod(b, nsub)
        kk = (me - dev + nw) % nw
        vals = []
        for k6 in range(6):
            val = r_refs[0][q, k6]
            for k in range(1, nw):
                val = jnp.where(kk == k, r_refs[k][q, k6], val)
            vals.append(val)
        return tuple(vals)

    def emit(b, left, right):
        dev, q = divmod(b, nsub)

        @pl.when(me == dev)
        def _():
            lr_ref[q, 0] = left
            lr_ref[q, 1] = right

    _reduce_blocks(nw * nsub, blk, emit, jnp.zeros(r_refs[0].shape[2:], F32))


def _surface_kernel(scale, z_ref, sp_ref, o_ref):
    z = z_ref[...]
    acc = jnp.zeros(z.shape, F32)
    for q in range(sp_ref.shape[0]):
        acc = jnp.where(z == q, sp_ref[q], acc)
    o_ref[...] = acc * scale


def medium_parameters(x):
    t = jnp.tanh(x)
    hot = x - solidification_release * t
    cond = 1.5 - 0.5 * jnp.tanh(hot)
    slope = (1.0 - solidification_release) + solidification_release * t * t
    return hot, cond, slope


def shards(h, zones, spray_coef):
    nt, ncl, nwl = h.shape
    nc, nw = lax.axis_size("cast"), lax.axis_size("width")
    ci, wi = lax.axis_index("cast"), lax.axis_index("width")
    up_c = [(i, i + 1) for i in range(nc - 1)]
    up_w = [(i, i + 1) for i in range(nw - 1)]
    h_cl = lax.ppermute(h[:, -1, :], "cast", up_c)[:, None, :]
    h_ch = lax.ppermute(h[:, 0, :], "cast", [(b, a) for a, b in up_c])[:, None, :]
    h_wl = lax.ppermute(h[:, :, -1], "width", up_w)[:, :, None]
    h_wh = lax.ppermute(h[:, :, 0], "width", [(b, a) for a, b in up_w])[:, :, None]

    surf = pl.pallas_call(
        functools.partial(_surface_kernel, nt * nt / 8.0),
        out_shape=jax.ShapeDtypeStruct((2 * ncl, nwl), F32),
        in_specs=[pl.BlockSpec(memory_space=pltpu.VMEM), SMEM_SPEC],
    )(zones.reshape(2 * ncl, nwl), spray_coef).reshape(2, ncl, nwl)

    T, k, s = medium_parameters(h)
    T_cl, k_cl, s_cl = medium_parameters(h_cl)
    T_ch, k_ch, s_ch = medium_parameters(h_ch)
    T_wl, k_wl, s_wl = medium_parameters(h_wl)
    T_wh, k_wh, s_wh = medium_parameters(h_wh)

    cast_low = (ci > 0).astype(F32)
    cast_high = (ci < nc - 1).astype(F32)
    width_low = (wi > 0).astype(F32)
    width_high = (wi < nw - 1).astype(F32)

    kc = jnp.concatenate([k_cl, k, k_ch], 1)
    Tc = jnp.concatenate([T_cl, T, T_ch], 1)
    sc = jnp.concatenate([s_cl, s, s_ch], 1)
    edge_c = jnp.ones((ncl + 1,), F32).at[0].set(cast_low).at[-1].set(cast_high)
    fc = (ncl * ncl * 4.0) * 0.5 * (kc[:, 1:] + kc[:, :-1]) * edge_c[None, :, None]
    gcl, gch = fc[:, :-1], fc[:, 1:]
    kw = jnp.concatenate([k_wl, k, k_wh], 2)
    Tw = jnp.concatenate([T_wl, T, T_wh], 2)
    sw = jnp.concatenate([s_wl, s, s_wh], 2)
    edge_w = jnp.ones((nwl + 1,), F32).at[0].set(width_low).at[-1].set(width_high)
    fw = (nwl * nwl / 4.0) * 0.5 * (kw[:, :, 1:] + kw[:, :, :-1]) * edge_w[None, None, :]
    gwl, gwh = fw[:, :, :-1], fw[:, :, 1:]
    mid = (nt * nt / 4.0) * 0.5 * (k[1:] + k[:-1])
    zf = jnp.zeros((1, ncl, nwl), F32)
    gtl = jnp.concatenate([zf, mid], 0)
    gth = jnp.concatenate([mid, zf], 0)
    rim = jnp.concatenate([surf[0:1], jnp.zeros((nt - 2, ncl, nwl), F32), surf[1:2]], 0)

    T_prev = jnp.concatenate([T[:1], T[:-1]], 0)
    T_next = jnp.concatenate([T[1:], T[-1:]], 0)
    explicit = rim * (quench_medium_hotness - T)
    explicit = explicit + (gch * (Tc[:, 2:] - T) - gcl * (T - Tc[:, :-2]))
    explicit = explicit + (gwh * (Tw[:, :, 2:] - T) - gwl * (T - Tw[:, :, :-2]))
    explicit = explicit + (gth * (T_next - T) - gtl * (T - T_prev))

    def flat(x):
        return x.reshape(nt * ncl, nwl)

    lo = -gcl * sc[:, :-2]
    hi = -gch * sc[:, 2:]
    md = 1.0 + s * (gcl + gch)
    y, v, w, summ = cast_solve(flat(lo), flat(md), flat(hi), flat(explicit), ncl)
    recv = lax.all_to_all(summ.reshape(nc, nt // nc, 8, nwl), "cast", 0, 0, tiled=True)
    lr_shape = recv.shape[:2] + (2, nwl)
    lr = pl.pallas_call(_cast_reduced_kernel, out_shape=jax.ShapeDtypeStruct(lr_shape, F32))(recv)
    back = lax.all_to_all(lr, "cast", 0, 0, tiled=True).reshape(nt, 2, nwl)
    y, v, w = (x.reshape(nt, ncl, nwl) for x in (y, v, w))

    lines = nt * ncl
    nsub = 4

    def wl(x):
        return jnp.transpose(x, (2, 0, 1)).reshape(nwl, lines // 128, 128)

    lo = -gwl * sw[:, :, :-2]
    hi = -gwh * sw[:, :, 2:]
    md = 1.0 + s * (gwl + gwh)
    y, v, w, summ = width_solve(y, v, w, back, wl(lo), wl(md), wl(hi), nsub)
    got = [summ] + [
        lax.ppermute(summ, "width", [(i, (i + q) % nw) for i in range(nw)]) for q in range(1, nw)
    ]
    lr = pl.pallas_call(
        _width_reduced_kernel,
        out_shape=jax.ShapeDtypeStruct((nsub, 2) + summ.shape[2:], F32),
        in_specs=[SMEM_SPEC] + [pl.BlockSpec(memory_space=pltpu.VMEM)] * nw,
    )(wi.astype(jnp.int32).reshape(1), *got)
    s_prev = jnp.concatenate([s[:1], s[:-1]], 0)
    s_next = jnp.concatenate([s[1:], s[-1:]], 0)
    lo = -gtl * s_prev
    hi = -gth * s_next
    md = 1.0 + s * (gtl + gth + rim)
    return thick_solve(y, v, w, lr, lo, md, hi, h, nsub, 4)


def solution(mesh):
    spec = P(None, "cast", "width")
    return jax.shard_map(
        shards, mesh=mesh, in_specs=(spec, spec, P()), out_specs=spec, check_vma=False
    )
```

```python
import functools

import jax
import jax.numpy as jnp
from jax import lax
from jax.experimental import pallas as pl
from jax.experimental.pallas import tpu as pltpu
from jax.sharding import PartitionSpec as P

F32 = jnp.float32
solidification_release = 0.4
quench_medium_hotness = -2.0
SMEM_SPEC = pl.BlockSpec(memory_space=pltpu.SMEM)


def _sweep(n, subs, ld, st, a_ref, b_ref, c_ref, d_ref, y_ref, v_ref, w_ref, cp_ref, unroll, shape):
    with_vw = v_ref is not None
    zero = jnp.zeros(shape, F32)
    one = jnp.ones(shape, F32)

    def fwd(i, carries):
        out = []
        for s0, (cprev, dprev, vprev) in zip(subs, carries):
            j = s0 + i
            a = ld(a_ref, j)
            r = 1.0 / (ld(b_ref, j) - a * cprev)
            cn = ld(c_ref, j) * r
            dn = (ld(d_ref, j) - a * dprev) * r
            st(cp_ref, j, cn)
            st(y_ref, j, dn)
            if with_vw:
                vprev = -(a * vprev) * r
                st(v_ref, j, vprev)
            out.append((cn, dn, vprev))
        return tuple(out)

    carries = tuple((zero, zero, one) for _ in subs)
    if unroll is True:
        for i in range(n):
            carries = fwd(i, carries)
    else:
        carries = lax.fori_loop(0, n, fwd, carries, unroll=unroll)
    if with_vw:
        for s0, (cl, _, _) in zip(subs, carries):
            st(w_ref, s0 + n - 1, -cl)

    def bwd(jj, carries):
        i = n - 2 - jj
        out = []
        for s0, (yn, vn, wn) in zip(subs, carries):
            j = s0 + i
            cp = ld(cp_ref, j)
            yn = ld(y_ref, j) - cp * yn
            st(y_ref, j, yn)
            if with_vw:
                vn = ld(v_ref, j) - cp * vn
                wn = -cp * wn
                st(v_ref, j, vn)
                st(w_ref, j, wn)
            out.append((yn, vn, wn))
        return tuple(out)

    carries = tuple((dl, vl, -cl) for cl, dl, vl in carries)
    if unroll is True:
        for jj in range(n - 1):
            carries = bwd(jj, carries)
    else:
        lax.fori_loop(0, n - 1, bwd, carries, unroll=unroll)


def _summary_rows(ld, s0, n, y_ref, v_ref, w_ref):
    return [ld(y_ref, s0), ld(v_ref, s0), ld(w_ref, s0),
            ld(y_ref, s0 + n - 1), ld(v_ref, s0 + n - 1), ld(w_ref, s0 + n - 1)]


def _cast_kernel(n, a_ref, b_ref, c_ref, d_ref, y_ref, v_ref, w_ref, sm_ref, cp_ref):
    m = a_ref.shape[0] // n

    def ld(ref, i):
        return ref[pl.ds(i, m, stride=n), :]

    def st(ref, i, val):
        ref[pl.ds(i, m, stride=n), :] = val

    shape = (m, a_ref.shape[1])
    _sweep(n, [0], ld, st, a_ref, b_ref, c_ref, d_ref, y_ref, v_ref, w_ref, cp_ref, True, shape)
    rows = _summary_rows(ld, 0, n, y_ref, v_ref, w_ref)
    rows += [jnp.zeros(shape, F32)] * (8 - len(rows))
    for k, val in enumerate(rows):
        sm_ref[pl.ds(k, m, stride=8), :] = val


def _lead_ld(ref, i):
    return ref[i]


def _lead_st(ref, i, val):
    ref[i] = val


def _prep_kernel(n, h_ref, hcl_ref, hch_ref, hwl_ref, hwh_ref, z_ref, sp_ref, fl_ref,
                 y_ref, v_ref, w_ref, sm_ref, wa_ref, wb_ref, wc_ref, ta_ref, tb_ref, tc_ref,
                 tp_ref, kp_ref, sp2_ref, a_ref, b_ref, c_ref, d_ref, cp_ref):
    rows, nwl = h_ref.shape
    nt = rows // n
    hot, cond, slope = medium_parameters(h_ref[...])
    zpad = jnp.zeros((n, nwl), F32)
    for ref, val in ((tp_ref, hot), (kp_ref, cond), (sp2_ref, slope)):
        ref[0:n] = zpad
        ref[n : n + rows] = val
        ref[n + rows : 2 * n + rows] = zpad

    def row(ref, off):
        return ref[pl.ds(off, nt, stride=n), :]

    lane = lax.broadcasted_iota(jnp.int32, (nt, nwl), 1)
    tix = lax.broadcasted_iota(jnp.int32, (nt, nwl), 0)
    cast_lo = medium_parameters(hcl_ref[...])
    cast_hi = medium_parameters(hch_ref[...])
    g_c = n * n * 4.0 * 0.5
    g_w = nwl * nwl / 4.0 * 0.5
    g_t = nt * nt / 4.0 * 0.5
    edge_wl = jnp.where(lane == 0, fl_ref[2], 1.0)
    edge_wh = jnp.where(lane == nwl - 1, fl_ref[3], 1.0)
    nz = sp_ref.shape[0]

    def surf_row(zr):
        acc = jnp.zeros(zr.shape, F32)
        for q in range(nz):
            acc = jnp.where(zr == q, sp_ref[q], acc)
        return acc * (nt * nt / 8.0)

    for c in range(n):
        T0, k0, s0 = (row(r, n + c) for r in (tp_ref, kp_ref, sp2_ref))
        if c == 0:
            Tm, km, sm = cast_lo
        else:
            Tm, km, sm = (row(r, n + c - 1) for r in (tp_ref, kp_ref, sp2_ref))
        if c == n - 1:
            Tq, kq, sq = cast_hi
        else:
            Tq, kq, sq = (row(r, n + c + 1) for r in (tp_ref, kp_ref, sp2_ref))
        Ttm, ktm, stm = (row(r, c) for r in (tp_ref, kp_ref, sp2_ref))
        Ttp, ktp, stp = (row(r, 2 * n + c) for r in (tp_ref, kp_ref, sp2_ref))
        wlo = medium_parameters(hwl_ref[c])
        whi = medium_parameters(hwh_ref[c])
        Twm, kwm, swm = (jnp.where(lane == 0, b, pltpu.roll(f, 1, 1)) for f, b in zip((T0, k0, s0), wlo))
        Twp, kwp, swp = (
            jnp.where(lane == nwl - 1, b, pltpu.roll(f, nwl - 1, 1)) for f, b in zip((T0, k0, s0), whi)
        )
        gcl = g_c * (k0 + km)
        if c == 0:
            gcl = gcl * fl_ref[0]
        gch = g_c * (kq + k0)
        if c == n - 1:
            gch = gch * fl_ref[1]
        gwl = g_w * (k0 + kwm) * edge_wl
        gwh = g_w * (kwp + k0) * edge_wh
        gtl = jnp.where(tix == 0, 0.0, g_t * (k0 + ktm))
        gth = jnp.where(tix == nt - 1, 0.0, g_t * (ktp + k0))
        s_lo = surf_row(z_ref[c : c + 1, :])
        s_hi = surf_row(z_ref[n + c : n + c + 1, :])
        rim = jnp.where(tix == 0, s_lo, jnp.where(tix == nt - 1, s_hi, 0.0))
        ex = rim * (quench_medium_hotness - T0)
        ex = ex + (gch * (Tq - T0) - gcl * (T0 - Tm))
        ex = ex + (gwh * (Twp - T0) - gwl * (T0 - Twm))
        ex = ex + (gth * (Ttp - T0) - gtl * (T0 - Ttm))
        sel = pl.ds(c, nt, stride=n)
        a_ref[sel, :] = -gcl * sm
        c_ref[sel, :] = -gch * sq
        b_ref[sel, :] = 1.0 + s0 * (gcl + gch)
        d_ref[sel, :] = ex
        wa_ref[sel, :] = -gwl * swm
        wc_ref[sel, :] = -gwh * swp
        wb_ref[sel, :] = 1.0 + s0 * (gwl + gwh)
        ta_ref[sel, :] = -gtl * stm
        tc_ref[sel, :] = -gth * stp
        tb_ref[sel, :] = 1.0 + s0 * (gtl + gth + rim)

    def ld(ref, i):
        return ref[pl.ds(i, nt, stride=n), :]

    def st(ref, i, val):
        ref[pl.ds(i, nt, stride=n), :] = val

    shape = (nt, nwl)
    _sweep(n, [0], ld, st, a_ref, b_ref, c_ref, d_ref, y_ref, v_ref, w_ref, cp_ref, True, shape)
    rws = _summary_rows(ld, 0, n, y_ref, v_ref, w_ref)
    rws += [jnp.zeros(shape, F32)] * (8 - len(rws))
    for k, val in enumerate(rws):
        sm_ref[pl.ds(k, nt, stride=8), :] = val


def prep_solve(h2, hcl, hch, hwl, hwh, z2, spray, flags, n):
    rows, nwl = h2.shape
    nt = rows // n
    shp = jax.ShapeDtypeStruct(h2.shape, F32)
    vm = pl.BlockSpec(memory_space=pltpu.VMEM)
    pad = pltpu.VMEM((rows + 2 * n, nwl), F32)
    return pl.pallas_call(
        functools.partial(_prep_kernel, n),
        out_shape=[shp] * 3 + [jax.ShapeDtypeStruct((nt * 8, nwl), F32)] + [shp] * 6,
        in_specs=[vm] * 6 + [SMEM_SPEC, SMEM_SPEC],
        scratch_shapes=[pad, pad, pad] + [pltpu.VMEM(h2.shape, F32)] * 5,
    )(h2, hcl, hch, hwl, hwh, z2, spray, flags)


def _width_kernel(nsub, yc_ref, vc_ref, wc_ref, bk_ref, a_ref, b_ref, c_ref,
                  y_ref, v_ref, w_ref, sm_ref, cp_ref, d_ref):
    sc = yc_ref[...] + vc_ref[...] * bk_ref[:, 0:1, :] + wc_ref[...] * bk_ref[:, 1:2, :]
    nt, ncl, nwl = sc.shape
    sc = sc.reshape(nt * ncl, nwl)
    for q in range(d_ref.shape[1]):
        d_ref[:, q, :] = sc[q * 128 : (q + 1) * 128, :].T
    n = a_ref.shape[0] // nsub
    subs = [q * n for q in range(nsub)]
    shape = a_ref.shape[1:]
    _sweep(n, subs, _lead_ld, _lead_st, a_ref, b_ref, c_ref, d_ref, y_ref, v_ref, w_ref, cp_ref, 4, shape)
    for q, s0 in enumerate(subs):
        for k, val in enumerate(_summary_rows(_lead_ld, s0, n, y_ref, v_ref, w_ref)):
            sm_ref[q, k] = val


def _thick_kernel(nsub, tsub, yw_ref, vw_ref, ww_ref, lr_ref, a_ref, b_ref, c_ref, h_ref,
                  o_ref, sw_ref, d_ref, y_ref, v_ref, w_ref, cp_ref):
    m = yw_ref.shape[0] // nsub
    for q in range(nsub):
        sl = slice(q * m, (q + 1) * m)
        sw_ref[sl] = yw_ref[sl] + vw_ref[sl] * lr_ref[q, 0] + ww_ref[sl] * lr_ref[q, 1]
    nt, ncl, nwl = a_ref.shape
    per_q = 128 // ncl
    for q in range(sw_ref.shape[1]):
        d_ref[q * per_q : (q + 1) * per_q] = sw_ref[:, q, :].T.reshape(per_q, ncl, nwl)
    n = nt // tsub
    subs = [q * n for q in range(tsub)]
    shape = a_ref.shape[1:]
    _sweep(n, subs, _lead_ld, _lead_st, a_ref, b_ref, c_ref, d_ref, y_ref, v_ref, w_ref, cp_ref, 4, shape)
    sums = [tuple(_summary_rows(_lead_ld, s0, n, y_ref, v_ref, w_ref)) for s0 in subs]
    lrs = [None] * tsub

    def emit(p, left, right):
        lrs[p] = (left, right)

    _reduce_blocks(tsub, lambda p: sums[p], emit, jnp.zeros(shape, F32))
    for q, s0 in enumerate(subs):
        sl = slice(s0, s0 + n)
        left, right = lrs[q]
        o_ref[sl] = h_ref[sl] + (y_ref[sl] + v_ref[sl] * left + w_ref[sl] * right)


def cast_solve(a, b, c, d, n):
    shp = jax.ShapeDtypeStruct(a.shape, F32)
    m = a.shape[0] // n
    return pl.pallas_call(
        functools.partial(_cast_kernel, n),
        out_shape=[shp, shp, shp, jax.ShapeDtypeStruct((m * 8, a.shape[1]), F32)],
        scratch_shapes=[pltpu.VMEM(a.shape, F32)],
    )(a, b, c, d)


def width_solve(yc, vc, wc, bk, a, b, c, nsub):
    shp = jax.ShapeDtypeStruct(a.shape, F32)
    return pl.pallas_call(
        functools.partial(_width_kernel, nsub),
        out_shape=[shp, shp, shp, jax.ShapeDtypeStruct((nsub, 6) + a.shape[1:], F32)],
        scratch_shapes=[pltpu.VMEM(a.shape, F32), pltpu.VMEM(a.shape, F32)],
    )(yc, vc, wc, bk, a, b, c)


def thick_solve(yw, vw, ww, lr, a, b, c, h, nsub, tsub):
    return pl.pallas_call(
        functools.partial(_thick_kernel, nsub, tsub),
        out_shape=jax.ShapeDtypeStruct(a.shape, F32),
        scratch_shapes=[pltpu.VMEM(yw.shape, F32)] + [pltpu.VMEM(a.shape, F32)] * 5,
    )(yw, vw, ww, lr, a, b, c, h)


def _reduce_blocks(nb, blk, emit, zero):
    pp, qq = zero, zero
    saved = []
    for p in range(nb):
        y0, v0, w0, yn, vn, wn = blk(p)
        rd = 1.0 / (1.0 - v0 * qq)
        fa = (y0 + v0 * pp) * rd
        fb = w0 * rd
        saved.append((fa, fb, pp, qq))
        pp, qq = yn + vn * (pp + qq * fa), wn + vn * qq * fb
    f_next = zero
    for p in range(nb - 1, -1, -1):
        fa, fb, pp, qq = saved[p]
        f = fa + fb * f_next
        emit(p, pp + qq * f, f_next)
        f_next = f


def _cast_reduced_kernel(s_ref, lr_ref):
    nb = s_ref.shape[0]
    def blk(p):
        return tuple(s_ref[p, :, k, :] for k in range(6))

    def emit(p, left, right):
        lr_ref[p, :, 0:1, :] = left[:, None]
        lr_ref[p, :, 1:2, :] = right[:, None]

    _reduce_blocks(nb, blk, emit, jnp.zeros((s_ref.shape[1], s_ref.shape[3]), F32))


def _width_reduced_kernel(me_ref, *refs):
    *r_refs, lr_ref = refs
    nw = len(r_refs)
    nsub = r_refs[0].shape[0]
    me = me_ref[0]

    def blk(b):
        dev, q = divmod(b, nsub)
        kk = (me - dev + nw) % nw
        vals = []
        for k6 in range(6):
            val = r_refs[0][q, k6]
            for k in range(1, nw):
                val = jnp.where(kk == k, r_refs[k][q, k6], val)
            vals.append(val)
        return tuple(vals)

    def emit(b, left, right):
        dev, q = divmod(b, nsub)

        @pl.when(me == dev)
        def _():
            lr_ref[q, 0] = left
            lr_ref[q, 1] = right

    _reduce_blocks(nw * nsub, blk, emit, jnp.zeros(r_refs[0].shape[2:], F32))


def _surface_kernel(scale, z_ref, sp_ref, o_ref):
    z = z_ref[...]
    acc = jnp.zeros(z.shape, F32)
    for q in range(sp_ref.shape[0]):
        acc = jnp.where(z == q, sp_ref[q], acc)
    o_ref[...] = acc * scale


def medium_parameters(x):
    t = jnp.tanh(x)
    hot = x - solidification_release * t
    cond = 1.5 - 0.5 * jnp.tanh(hot)
    slope = (1.0 - solidification_release) + solidification_release * t * t
    return hot, cond, slope


def shards(h, zones, spray_coef):
    nt, ncl, nwl = h.shape
    nc, nw = lax.axis_size("cast"), lax.axis_size("width")
    ci, wi = lax.axis_index("cast"), lax.axis_index("width")
    up_c = [(i, i + 1) for i in range(nc - 1)]
    up_w = [(i, i + 1) for i in range(nw - 1)]
    h_cl = lax.ppermute(h[:, -1, :], "cast", up_c)
    h_ch = lax.ppermute(h[:, 0, :], "cast", [(b, a) for a, b in up_c])
    h_wl = lax.ppermute(h[:, :, -1], "width", up_w)[:, :, None]
    h_wh = lax.ppermute(h[:, :, 0], "width", [(b, a) for a, b in up_w])[:, :, None]

    cast_low = (ci > 0).astype(F32)
    cast_high = (ci < nc - 1).astype(F32)
    width_low = (wi > 0).astype(F32)
    width_high = (wi < nw - 1).astype(F32)
    flags = jnp.stack([cast_low, cast_high, width_low, width_high])
    outs = prep_solve(
        h.reshape(nt * ncl, nwl), h_cl, h_ch,
        jnp.transpose(h_wl, (1, 0, 2)), jnp.transpose(h_wh, (1, 0, 2)),
        zones.reshape(2 * ncl, nwl), spray_coef, flags, ncl,
    )
    y, v, w, summ = outs[:4]
    wlo, wmd, whi, tlo, tmd, thi = (x.reshape(nt, ncl, nwl) for x in outs[4:])
    recv = lax.all_to_all(summ.reshape(nc, nt // nc, 8, nwl), "cast", 0, 0, tiled=True)
    lr_shape = recv.shape[:2] + (2, nwl)
    lr = pl.pallas_call(_cast_reduced_kernel, out_shape=jax.ShapeDtypeStruct(lr_shape, F32))(recv)
    back = lax.all_to_all(lr, "cast", 0, 0, tiled=True).reshape(nt, 2, nwl)
    y, v, w = (x.reshape(nt, ncl, nwl) for x in (y, v, w))

    lines = nt * ncl
    nsub = 4

    def wl(x):
        return jnp.transpose(x, (2, 0, 1)).reshape(nwl, lines // 128, 128)

    y, v, w, summ = width_solve(y, v, w, back, wl(wlo), wl(wmd), wl(whi), nsub)
    got = [summ] + [
        lax.ppermute(summ, "width", [(i, (i + q) % nw) for i in range(nw)]) for q in range(1, nw)
    ]
    lr = pl.pallas_call(
        _width_reduced_kernel,
        out_shape=jax.ShapeDtypeStruct((nsub, 2) + summ.shape[2:], F32),
        in_specs=[SMEM_SPEC] + [pl.BlockSpec(memory_space=pltpu.VMEM)] * nw,
    )(wi.astype(jnp.int32).reshape(1), *got)
    return thick_solve(y, v, w, lr, tlo, tmd, thi, h, nsub, 4)


def solution(mesh):
    spec = P(None, "cast", "width")
    return jax.shard_map(
        shards, mesh=mesh, in_specs=(spec, spec, P()), out_specs=spec, check_vma=False
    )
```

```python
import functools

import jax
import jax.numpy as jnp
from jax import lax
from jax.experimental import pallas as pl
from jax.experimental.pallas import tpu as pltpu
from jax.sharding import PartitionSpec as P

F32 = jnp.float32
solidification_release = 0.4
quench_medium_hotness = -2.0
SMEM_SPEC = pl.BlockSpec(memory_space=pltpu.SMEM)


def _sweep(n, subs, ld, st, a_ref, b_ref, c_ref, d_ref, y_ref, v_ref, w_ref, cp_ref, unroll, shape):
    with_vw = v_ref is not None
    zero = jnp.zeros(shape, F32)
    one = jnp.ones(shape, F32)

    def fwd(i, carries):
        out = []
        for s0, (cprev, dprev, vprev) in zip(subs, carries):
            j = s0 + i
            a = ld(a_ref, j)
            r = 1.0 / (ld(b_ref, j) - a * cprev)
            cn = ld(c_ref, j) * r
            dn = (ld(d_ref, j) - a * dprev) * r
            st(cp_ref, j, cn)
            st(y_ref, j, dn)
            if with_vw:
                vprev = -(a * vprev) * r
                st(v_ref, j, vprev)
            out.append((cn, dn, vprev))
        return tuple(out)

    carries = tuple((zero, zero, one) for _ in subs)
    if unroll is True:
        for i in range(n):
            carries = fwd(i, carries)
    else:
        carries = lax.fori_loop(0, n, fwd, carries, unroll=unroll)
    if with_vw:
        for s0, (cl, _, _) in zip(subs, carries):
            st(w_ref, s0 + n - 1, -cl)

    def bwd(jj, carries):
        i = n - 2 - jj
        out = []
        for s0, (yn, vn, wn) in zip(subs, carries):
            j = s0 + i
            cp = ld(cp_ref, j)
            yn = ld(y_ref, j) - cp * yn
            st(y_ref, j, yn)
            if with_vw:
                vn = ld(v_ref, j) - cp * vn
                wn = -cp * wn
                st(v_ref, j, vn)
                st(w_ref, j, wn)
            out.append((yn, vn, wn))
        return tuple(out)

    carries = tuple((dl, vl, -cl) for cl, dl, vl in carries)
    if unroll is True:
        for jj in range(n - 1):
            carries = bwd(jj, carries)
    else:
        lax.fori_loop(0, n - 1, bwd, carries, unroll=unroll)


def _summary_rows(ld, s0, n, y_ref, v_ref, w_ref):
    return [ld(y_ref, s0), ld(v_ref, s0), ld(w_ref, s0),
            ld(y_ref, s0 + n - 1), ld(v_ref, s0 + n - 1), ld(w_ref, s0 + n - 1)]


def _cast_kernel(n, a_ref, b_ref, c_ref, d_ref, y_ref, v_ref, w_ref, sm_ref, cp_ref):
    m = a_ref.shape[0] // n

    def ld(ref, i):
        return ref[pl.ds(i, m, stride=n), :]

    def st(ref, i, val):
        ref[pl.ds(i, m, stride=n), :] = val

    shape = (m, a_ref.shape[1])
    _sweep(n, [0], ld, st, a_ref, b_ref, c_ref, d_ref, y_ref, v_ref, w_ref, cp_ref, True, shape)
    rows = _summary_rows(ld, 0, n, y_ref, v_ref, w_ref)
    rows += [jnp.zeros(shape, F32)] * (8 - len(rows))
    for k, val in enumerate(rows):
        sm_ref[pl.ds(k, m, stride=8), :] = val


def _lead_ld(ref, i):
    return ref[i]


def _lead_st(ref, i, val):
    ref[i] = val


def _prep_kernel(n, h_ref, hcl_ref, hch_ref, hwl_ref, hwh_ref, z_ref, sp_ref, fl_ref,
                 y_ref, v_ref, w_ref, sm_ref, wa_ref, wb_ref, wc_ref, ta_ref, tb_ref, tc_ref,
                 tp_ref, kp_ref, sp2_ref, a_ref, b_ref, c_ref, d_ref, cp_ref):
    rows, nwl = h_ref.shape
    nt = rows // n
    hot, cond, slope = medium_parameters(h_ref[...])
    zpad = jnp.zeros((n, nwl), F32)
    for ref, val in ((tp_ref, hot), (kp_ref, cond), (sp2_ref, slope)):
        ref[0:n] = zpad
        ref[n : n + rows] = val
        ref[n + rows : 2 * n + rows] = zpad

    def row(ref, off):
        return ref[pl.ds(off, nt, stride=n), :]

    lane = lax.broadcasted_iota(jnp.int32, (nt, nwl), 1)
    tix = lax.broadcasted_iota(jnp.int32, (nt, nwl), 0)
    even = fl_ref[4] > 0.5
    got_a, got_b = hcl_ref[...], hch_ref[...]
    cast_lo = medium_parameters(jnp.where(even, got_b, got_a))
    cast_hi = medium_parameters(jnp.where(even, got_a, got_b))
    g_c = n * n * 4.0 * 0.5
    g_w = nwl * nwl / 4.0 * 0.5
    g_t = nt * nt / 4.0 * 0.5
    edge_wl = jnp.where(lane == 0, fl_ref[2], 1.0)
    edge_wh = jnp.where(lane == nwl - 1, fl_ref[3], 1.0)
    nz = sp_ref.shape[0]

    def surf_row(zr):
        acc = jnp.zeros(zr.shape, F32)
        for q in range(nz):
            acc = jnp.where(zr == q, sp_ref[q], acc)
        return acc * (nt * nt / 8.0)

    for c in range(n):
        T0, k0, s0 = (row(r, n + c) for r in (tp_ref, kp_ref, sp2_ref))
        if c == 0:
            Tm, km, sm = cast_lo
        else:
            Tm, km, sm = (row(r, n + c - 1) for r in (tp_ref, kp_ref, sp2_ref))
        if c == n - 1:
            Tq, kq, sq = cast_hi
        else:
            Tq, kq, sq = (row(r, n + c + 1) for r in (tp_ref, kp_ref, sp2_ref))
        Ttm, ktm, stm = (row(r, c) for r in (tp_ref, kp_ref, sp2_ref))
        Ttp, ktp, stp = (row(r, 2 * n + c) for r in (tp_ref, kp_ref, sp2_ref))
        wlo = medium_parameters(hwl_ref[:, c : c + 1])
        whi = medium_parameters(hwh_ref[:, c : c + 1])
        Twm, kwm, swm = (jnp.where(lane == 0, b, pltpu.roll(f, 1, 1)) for f, b in zip((T0, k0, s0), wlo))
        Twp, kwp, swp = (
            jnp.where(lane == nwl - 1, b, pltpu.roll(f, nwl - 1, 1)) for f, b in zip((T0, k0, s0), whi)
        )
        gcl = g_c * (k0 + km)
        if c == 0:
            gcl = gcl * fl_ref[0]
        gch = g_c * (kq + k0)
        if c == n - 1:
            gch = gch * fl_ref[1]
        gwl = g_w * (k0 + kwm) * edge_wl
        gwh = g_w * (kwp + k0) * edge_wh
        gtl = jnp.where(tix == 0, 0.0, g_t * (k0 + ktm))
        gth = jnp.where(tix == nt - 1, 0.0, g_t * (ktp + k0))
        s_lo = surf_row(z_ref[c : c + 1, :])
        s_hi = surf_row(z_ref[n + c : n + c + 1, :])
        rim = jnp.where(tix == 0, s_lo, jnp.where(tix == nt - 1, s_hi, 0.0))
        ex = rim * (quench_medium_hotness - T0)
        ex = ex + (gch * (Tq - T0) - gcl * (T0 - Tm))
        ex = ex + (gwh * (Twp - T0) - gwl * (T0 - Twm))
        ex = ex + (gth * (Ttp - T0) - gtl * (T0 - Ttm))
        sel = pl.ds(c, nt, stride=n)
        a_ref[sel, :] = -gcl * sm
        c_ref[sel, :] = -gch * sq
        b_ref[sel, :] = 1.0 + s0 * (gcl + gch)
        d_ref[sel, :] = ex
        wa_ref[sel, :] = -gwl * swm
        wc_ref[sel, :] = -gwh * swp
        wb_ref[sel, :] = 1.0 + s0 * (gwl + gwh)
        ta_ref[sel, :] = -gtl * stm
        tc_ref[sel, :] = -gth * stp
        tb_ref[sel, :] = 1.0 + s0 * (gtl + gth + rim)

    def ld(ref, i):
        return ref[pl.ds(i, nt, stride=n), :]

    def st(ref, i, val):
        ref[pl.ds(i, nt, stride=n), :] = val

    shape = (nt, nwl)
    _sweep(n, [0], ld, st, a_ref, b_ref, c_ref, d_ref, y_ref, v_ref, w_ref, cp_ref, True, shape)
    rws = _summary_rows(ld, 0, n, y_ref, v_ref, w_ref)
    rws += [jnp.zeros(shape, F32)] * (8 - len(rws))
    for k, val in enumerate(rws):
        sm_ref[pl.ds(k, nt, stride=8), :] = val


def prep_solve(h2, hcl, hch, hwl, hwh, z2, spray, flags, n):
    rows, nwl = h2.shape
    nt = rows // n
    shp = jax.ShapeDtypeStruct(h2.shape, F32)
    vm = pl.BlockSpec(memory_space=pltpu.VMEM)
    pad = pltpu.VMEM((rows + 2 * n, nwl), F32)
    return pl.pallas_call(
        functools.partial(_prep_kernel, n),
        out_shape=[shp] * 3 + [jax.ShapeDtypeStruct((nt * 8, nwl), F32)] + [shp] * 6,
        in_specs=[vm] * 6 + [SMEM_SPEC, SMEM_SPEC],
        scratch_shapes=[pad, pad, pad] + [pltpu.VMEM(h2.shape, F32)] * 5,
    )(h2, hcl, hch, hwl, hwh, z2, spray, flags)


def _width_kernel(nsub, yc_ref, vc_ref, wc_ref, bk_ref, a_ref, b_ref, c_ref,
                  y_ref, v_ref, w_ref, sm_ref, cp_ref, d_ref):
    sc = yc_ref[...] + vc_ref[...] * bk_ref[:, 0:1, :] + wc_ref[...] * bk_ref[:, 1:2, :]
    nt, ncl, nwl = sc.shape
    sc = sc.reshape(nt * ncl, nwl)
    for q in range(d_ref.shape[1]):
        d_ref[:, q, :] = sc[q * 128 : (q + 1) * 128, :].T
    n = a_ref.shape[0] // nsub
    subs = [q * n for q in range(nsub)]
    shape = a_ref.shape[1:]
    _sweep(n, subs, _lead_ld, _lead_st, a_ref, b_ref, c_ref, d_ref, y_ref, v_ref, w_ref, cp_ref, 4, shape)
    for q, s0 in enumerate(subs):
        for k, val in enumerate(_summary_rows(_lead_ld, s0, n, y_ref, v_ref, w_ref)):
            sm_ref[q, k] = val


def _thick_kernel(nsub, tsub, yw_ref, vw_ref, ww_ref, lr_ref, a_ref, b_ref, c_ref, h_ref,
                  o_ref, sw_ref, d_ref, y_ref, v_ref, w_ref, cp_ref):
    m = yw_ref.shape[0] // nsub
    for q in range(nsub):
        sl = slice(q * m, (q + 1) * m)
        sw_ref[sl] = yw_ref[sl] + vw_ref[sl] * lr_ref[q, 0] + ww_ref[sl] * lr_ref[q, 1]
    nt, ncl, nwl = a_ref.shape
    per_q = 128 // ncl
    for q in range(sw_ref.shape[1]):
        d_ref[q * per_q : (q + 1) * per_q] = sw_ref[:, q, :].T.reshape(per_q, ncl, nwl)
    n = nt // tsub
    subs = [q * n for q in range(tsub)]
    shape = a_ref.shape[1:]
    _sweep(n, subs, _lead_ld, _lead_st, a_ref, b_ref, c_ref, d_ref, y_ref, v_ref, w_ref, cp_ref, 4, shape)
    sums = [tuple(_summary_rows(_lead_ld, s0, n, y_ref, v_ref, w_ref)) for s0 in subs]
    lrs = [None] * tsub

    def emit(p, left, right):
        lrs[p] = (left, right)

    _reduce_blocks(tsub, lambda p: sums[p], emit, jnp.zeros(shape, F32))
    for q, s0 in enumerate(subs):
        sl = slice(s0, s0 + n)
        left, right = lrs[q]
        o_ref[sl] = h_ref[sl] + (y_ref[sl] + v_ref[sl] * left + w_ref[sl] * right)


def cast_solve(a, b, c, d, n):
    shp = jax.ShapeDtypeStruct(a.shape, F32)
    m = a.shape[0] // n
    return pl.pallas_call(
        functools.partial(_cast_kernel, n),
        out_shape=[shp, shp, shp, jax.ShapeDtypeStruct((m * 8, a.shape[1]), F32)],
        scratch_shapes=[pltpu.VMEM(a.shape, F32)],
    )(a, b, c, d)


def width_solve(yc, vc, wc, bk, a, b, c, nsub):
    shp = jax.ShapeDtypeStruct(a.shape, F32)
    return pl.pallas_call(
        functools.partial(_width_kernel, nsub),
        out_shape=[shp, shp, shp, jax.ShapeDtypeStruct((nsub, 6) + a.shape[1:], F32)],
        scratch_shapes=[pltpu.VMEM(a.shape, F32), pltpu.VMEM(a.shape, F32)],
    )(yc, vc, wc, bk, a, b, c)


def thick_solve(yw, vw, ww, lr, a, b, c, h, nsub, tsub):
    return pl.pallas_call(
        functools.partial(_thick_kernel, nsub, tsub),
        out_shape=jax.ShapeDtypeStruct(a.shape, F32),
        scratch_shapes=[pltpu.VMEM(yw.shape, F32)] + [pltpu.VMEM(a.shape, F32)] * 5,
    )(yw, vw, ww, lr, a, b, c, h)


def _reduce_blocks(nb, blk, emit, zero):
    pp, qq = zero, zero
    saved = []
    for p in range(nb):
        y0, v0, w0, yn, vn, wn = blk(p)
        rd = 1.0 / (1.0 - v0 * qq)
        fa = (y0 + v0 * pp) * rd
        fb = w0 * rd
        saved.append((fa, fb, pp, qq))
        pp, qq = yn + vn * (pp + qq * fa), wn + vn * qq * fb
    f_next = zero
    for p in range(nb - 1, -1, -1):
        fa, fb, pp, qq = saved[p]
        f = fa + fb * f_next
        emit(p, pp + qq * f, f_next)
        f_next = f


def _cast_reduced_kernel(s_ref, lr_ref):
    nb = s_ref.shape[0]
    def blk(p):
        return tuple(s_ref[p, :, k, :] for k in range(6))

    def emit(p, left, right):
        lr_ref[p, :, 0:1, :] = left[:, None]
        lr_ref[p, :, 1:2, :] = right[:, None]

    _reduce_blocks(nb, blk, emit, jnp.zeros((s_ref.shape[1], s_ref.shape[3]), F32))


def _width_reduced_kernel(me_ref, *refs):
    *r_refs, lr_ref = refs
    nw = len(r_refs)
    nsub = r_refs[0].shape[0]
    me = me_ref[0]

    def blk(b):
        dev, q = divmod(b, nsub)
        kk = (me - dev + nw) % nw
        vals = []
        for k6 in range(6):
            val = r_refs[0][q, k6]
            for k in range(1, nw):
                val = jnp.where(kk == k, r_refs[k][q, k6], val)
            vals.append(val)
        return tuple(vals)

    def emit(b, left, right):
        dev, q = divmod(b, nsub)

        @pl.when(me == dev)
        def _():
            lr_ref[q, 0] = left
            lr_ref[q, 1] = right

    _reduce_blocks(nw * nsub, blk, emit, jnp.zeros(r_refs[0].shape[2:], F32))


def _surface_kernel(scale, z_ref, sp_ref, o_ref):
    z = z_ref[...]
    acc = jnp.zeros(z.shape, F32)
    for q in range(sp_ref.shape[0]):
        acc = jnp.where(z == q, sp_ref[q], acc)
    o_ref[...] = acc * scale


def medium_parameters(x):
    t = jnp.tanh(x)
    hot = x - solidification_release * t
    cond = 1.5 - 0.5 * jnp.tanh(hot)
    slope = (1.0 - solidification_release) + solidification_release * t * t
    return hot, cond, slope


def shards(h, zones, spray_coef):
    nt, ncl, nwl = h.shape
    nc, nw = lax.axis_size("cast"), lax.axis_size("width")
    ci, wi = lax.axis_index("cast"), lax.axis_index("width")
    up_c = [(i, i + 1) for i in range(nc - 1)]
    up_w = [(i, i + 1) for i in range(nw - 1)]
    even = ci % 2 == 0
    first, last = h[:, 0, :], h[:, -1, :]
    in_chip = [(i, i ^ 1) for i in range(nc)]
    across = [(i, i + 1) for i in range(1, nc - 1, 2)] + [(i + 1, i) for i in range(1, nc - 1, 2)]
    got_a = lax.ppermute(jnp.where(even, last, first), "cast", in_chip)
    got_b = lax.ppermute(jnp.where(even, first, last), "cast", across)
    h_wl = lax.ppermute(h[:, :, -1], "width", up_w)
    h_wh = lax.ppermute(h[:, :, 0], "width", [(b, a) for a, b in up_w])

    cast_low = (ci > 0).astype(F32)
    cast_high = (ci < nc - 1).astype(F32)
    width_low = (wi > 0).astype(F32)
    width_high = (wi < nw - 1).astype(F32)
    flags = jnp.stack([cast_low, cast_high, width_low, width_high, even.astype(F32)])
    outs = prep_solve(
        h.reshape(nt * ncl, nwl), got_a, got_b,
        h_wl, h_wh,
        zones.reshape(2 * ncl, nwl), spray_coef, flags, ncl,
    )
    y, v, w, summ = outs[:4]
    wlo, wmd, whi, tlo, tmd, thi = (x.reshape(nt, ncl, nwl) for x in outs[4:])
    recv = lax.all_to_all(summ.reshape(nc, nt // nc, 8, nwl), "cast", 0, 0, tiled=True)
    lr_shape = recv.shape[:2] + (2, nwl)
    lr = pl.pallas_call(_cast_reduced_kernel, out_shape=jax.ShapeDtypeStruct(lr_shape, F32))(recv)
    back = lax.all_to_all(lr, "cast", 0, 0, tiled=True).reshape(nt, 2, nwl)
    y, v, w = (x.reshape(nt, ncl, nwl) for x in (y, v, w))

    lines = nt * ncl
    nsub = 4

    def wl(x):
        return jnp.transpose(x, (2, 0, 1)).reshape(nwl, lines // 128, 128)

    y, v, w, summ = width_solve(y, v, w, back, wl(wlo), wl(wmd), wl(whi), nsub)
    got = [summ] + [
        lax.ppermute(summ, "width", [(i, (i + q) % nw) for i in range(nw)]) for q in range(1, nw)
    ]
    lr = pl.pallas_call(
        _width_reduced_kernel,
        out_shape=jax.ShapeDtypeStruct((nsub, 2) + summ.shape[2:], F32),
        in_specs=[SMEM_SPEC] + [pl.BlockSpec(memory_space=pltpu.VMEM)] * nw,
    )(wi.astype(jnp.int32).reshape(1), *got)
    return thick_solve(y, v, w, lr, tlo, tmd, thi, h, nsub, 4)


def solution(mesh):
    spec = P(None, "cast", "width")
    return jax.shard_map(
        shards, mesh=mesh, in_specs=(spec, spec, P()), out_specs=spec, check_vma=False
    )
```

```python
import functools

import jax
import jax.numpy as jnp
from jax import lax
from jax.experimental import pallas as pl
from jax.experimental.pallas import tpu as pltpu
from jax.sharding import PartitionSpec as P

F32 = jnp.float32
solidification_release = 0.4
quench_medium_hotness = -2.0
SMEM_SPEC = pl.BlockSpec(memory_space=pltpu.SMEM)


def _sweep(n, subs, ld, st, a_ref, b_ref, c_ref, d_ref, y_ref, v_ref, w_ref, cp_ref, unroll, shape):
    with_vw = v_ref is not None
    zero = jnp.zeros(shape, F32)
    one = jnp.ones(shape, F32)

    def fwd(i, carries):
        out = []
        for s0, (cprev, dprev, vprev) in zip(subs, carries):
            j = s0 + i
            a = ld(a_ref, j)
            r = 1.0 / (ld(b_ref, j) - a * cprev)
            cn = ld(c_ref, j) * r
            dn = (ld(d_ref, j) - a * dprev) * r
            st(cp_ref, j, cn)
            st(y_ref, j, dn)
            if with_vw:
                vprev = -(a * vprev) * r
                st(v_ref, j, vprev)
            out.append((cn, dn, vprev))
        return tuple(out)

    carries = tuple((zero, zero, one) for _ in subs)
    if unroll is True:
        for i in range(n):
            carries = fwd(i, carries)
    else:
        carries = lax.fori_loop(0, n, fwd, carries, unroll=unroll)
    if with_vw:
        for s0, (cl, _, _) in zip(subs, carries):
            st(w_ref, s0 + n - 1, -cl)

    def bwd(jj, carries):
        i = n - 2 - jj
        out = []
        for s0, (yn, vn, wn) in zip(subs, carries):
            j = s0 + i
            cp = ld(cp_ref, j)
            yn = ld(y_ref, j) - cp * yn
            st(y_ref, j, yn)
            if with_vw:
                vn = ld(v_ref, j) - cp * vn
                wn = -cp * wn
                st(v_ref, j, vn)
                st(w_ref, j, wn)
            out.append((yn, vn, wn))
        return tuple(out)

    carries = tuple((dl, vl, -cl) for cl, dl, vl in carries)
    if unroll is True:
        for jj in range(n - 1):
            carries = bwd(jj, carries)
    else:
        lax.fori_loop(0, n - 1, bwd, carries, unroll=unroll)


def _summary_rows(ld, s0, n, y_ref, v_ref, w_ref):
    return [ld(y_ref, s0), ld(v_ref, s0), ld(w_ref, s0),
            ld(y_ref, s0 + n - 1), ld(v_ref, s0 + n - 1), ld(w_ref, s0 + n - 1)]


def _cast_kernel(n, a_ref, b_ref, c_ref, d_ref, y_ref, v_ref, w_ref, sm_ref, cp_ref):
    m = a_ref.shape[0] // n

    def ld(ref, i):
        return ref[pl.ds(i, m, stride=n), :]

    def st(ref, i, val):
        ref[pl.ds(i, m, stride=n), :] = val

    shape = (m, a_ref.shape[1])
    _sweep(n, [0], ld, st, a_ref, b_ref, c_ref, d_ref, y_ref, v_ref, w_ref, cp_ref, True, shape)
    rows = _summary_rows(ld, 0, n, y_ref, v_ref, w_ref)
    rows += [jnp.zeros(shape, F32)] * (8 - len(rows))
    for k, val in enumerate(rows):
        sm_ref[pl.ds(k, m, stride=8), :] = val


def _lead_ld(ref, i):
    return ref[i]


def _lead_st(ref, i, val):
    ref[i] = val


def _prep_kernel(n, h_ref, hcl_ref, hch_ref, hwl_ref, hwh_ref, z_ref, sp_ref, fl_ref,
                 y_ref, v_ref, w_ref, sm_ref, wa_ref, wb_ref, wc_ref, ta_ref, tb_ref, tc_ref,
                 tp_ref, kp_ref, sp2_ref, a_ref, b_ref, c_ref, d_ref, cp_ref):
    rows, nwl = h_ref.shape
    nt = rows // n
    hot, cond, slope = medium_parameters(h_ref[...])
    zpad = jnp.zeros((n, nwl), F32)
    for ref, val in ((tp_ref, hot), (kp_ref, cond), (sp2_ref, slope)):
        ref[0:n] = zpad
        ref[n : n + rows] = val
        ref[n + rows : 2 * n + rows] = zpad

    def row(ref, off):
        return ref[pl.ds(off, nt, stride=n), :]

    lane = lax.broadcasted_iota(jnp.int32, (nt, nwl), 1)
    tix = lax.broadcasted_iota(jnp.int32, (nt, nwl), 0)
    even = fl_ref[4] > 0.5
    got_a, got_b = hcl_ref[...], hch_ref[...]
    cast_lo = medium_parameters(jnp.where(even, got_b, got_a))
    cast_hi = medium_parameters(jnp.where(even, got_a, got_b))
    g_c = n * n * 4.0 * 0.5
    g_w = nwl * nwl / 4.0 * 0.5
    g_t = nt * nt / 4.0 * 0.5
    edge_wl = jnp.where(lane == 0, fl_ref[2], 1.0)
    edge_wh = jnp.where(lane == nwl - 1, fl_ref[3], 1.0)
    nz = sp_ref.shape[0]

    def surf_row(zr):
        acc = jnp.zeros(zr.shape, F32)
        for q in range(nz):
            acc = jnp.where(zr == q, sp_ref[q], acc)
        return acc * (nt * nt / 8.0)

    for c in range(n):
        T0, k0, s0 = (row(r, n + c) for r in (tp_ref, kp_ref, sp2_ref))
        if c == 0:
            Tm, km, sm = cast_lo
        else:
            Tm, km, sm = (row(r, n + c - 1) for r in (tp_ref, kp_ref, sp2_ref))
        if c == n - 1:
            Tq, kq, sq = cast_hi
        else:
            Tq, kq, sq = (row(r, n + c + 1) for r in (tp_ref, kp_ref, sp2_ref))
        Ttm, ktm, stm = (row(r, c) for r in (tp_ref, kp_ref, sp2_ref))
        Ttp, ktp, stp = (row(r, 2 * n + c) for r in (tp_ref, kp_ref, sp2_ref))
        wlo = medium_parameters(hwl_ref[:, c : c + 1])
        whi = medium_parameters(hwh_ref[:, c : c + 1])
        Twm, kwm, swm = (jnp.where(lane == 0, b, pltpu.roll(f, 1, 1)) for f, b in zip((T0, k0, s0), wlo))
        Twp, kwp, swp = (
            jnp.where(lane == nwl - 1, b, pltpu.roll(f, nwl - 1, 1)) for f, b in zip((T0, k0, s0), whi)
        )
        gcl = g_c * (k0 + km)
        if c == 0:
            gcl = gcl * fl_ref[0]
        gch = g_c * (kq + k0)
        if c == n - 1:
            gch = gch * fl_ref[1]
        gwl = g_w * (k0 + kwm) * edge_wl
        gwh = g_w * (kwp + k0) * edge_wh
        gtl = jnp.where(tix == 0, 0.0, g_t * (k0 + ktm))
        gth = jnp.where(tix == nt - 1, 0.0, g_t * (ktp + k0))
        s_lo = surf_row(z_ref[c : c + 1, :])
        s_hi = surf_row(z_ref[n + c : n + c + 1, :])
        rim = jnp.where(tix == 0, s_lo, jnp.where(tix == nt - 1, s_hi, 0.0))
        ex = rim * (quench_medium_hotness - T0)
        ex = ex + (gch * (Tq - T0) - gcl * (T0 - Tm))
        ex = ex + (gwh * (Twp - T0) - gwl * (T0 - Twm))
        ex = ex + (gth * (Ttp - T0) - gtl * (T0 - Ttm))
        sel = pl.ds(c, nt, stride=n)
        a_ref[sel, :] = -gcl * sm
        c_ref[sel, :] = -gch * sq
        b_ref[sel, :] = 1.0 + s0 * (gcl + gch)
        d_ref[sel, :] = ex
        wa_ref[sel, :] = -gwl * swm
        wc_ref[sel, :] = -gwh * swp
        wb_ref[sel, :] = 1.0 + s0 * (gwl + gwh)
        ta_ref[sel, :] = -gtl * stm
        tc_ref[sel, :] = -gth * stp
        tb_ref[sel, :] = 1.0 + s0 * (gtl + gth + rim)

    def ld(ref, i):
        return ref[pl.ds(i, nt, stride=n), :]

    def st(ref, i, val):
        ref[pl.ds(i, nt, stride=n), :] = val

    shape = (nt, nwl)
    _sweep(n, [0], ld, st, a_ref, b_ref, c_ref, d_ref, y_ref, v_ref, w_ref, cp_ref, True, shape)
    rws = _summary_rows(ld, 0, n, y_ref, v_ref, w_ref)
    rws += [jnp.zeros(shape, F32)] * (8 - len(rws))
    for k, val in enumerate(rws):
        sm_ref[pl.ds(k, nt, stride=8), :] = val


def prep_solve(h2, hcl, hch, hwl, hwh, z2, spray, flags, n):
    rows, nwl = h2.shape
    nt = rows // n
    shp = jax.ShapeDtypeStruct(h2.shape, F32)
    vm = pl.BlockSpec(memory_space=pltpu.VMEM)
    pad = pltpu.VMEM((rows + 2 * n, nwl), F32)
    return pl.pallas_call(
        functools.partial(_prep_kernel, n),
        out_shape=[shp] * 3 + [jax.ShapeDtypeStruct((nt * 8, nwl), F32)] + [shp] * 6,
        in_specs=[vm] * 6 + [SMEM_SPEC, SMEM_SPEC],
        scratch_shapes=[pad, pad, pad] + [pltpu.VMEM(h2.shape, F32)] * 5,
    )(h2, hcl, hch, hwl, hwh, z2, spray, flags)


def _width_kernel(nsub, yc_ref, vc_ref, wc_ref, bk_ref, a_ref, b_ref, c_ref,
                  y_ref, v_ref, w_ref, sm_ref, cp_ref, d_ref):
    sc = yc_ref[...] + vc_ref[...] * bk_ref[:, 0:1, :] + wc_ref[...] * bk_ref[:, 1:2, :]
    nt, ncl, nwl = sc.shape
    sc = sc.reshape(nt * ncl, nwl)
    for q in range(d_ref.shape[1]):
        d_ref[:, q, :] = sc[q * 128 : (q + 1) * 128, :].T
    n = a_ref.shape[0] // nsub
    subs = [q * n for q in range(nsub)]
    shape = a_ref.shape[1:]
    _sweep(n, subs, _lead_ld, _lead_st, a_ref, b_ref, c_ref, d_ref, y_ref, v_ref, w_ref, cp_ref, 4, shape)
    for q, s0 in enumerate(subs):
        for k, val in enumerate(_summary_rows(_lead_ld, s0, n, y_ref, v_ref, w_ref)):
            sm_ref[q, k] = val


def _thick_kernel(nsub, tsub, nw, me_ref, *refs):
    r_refs = refs[:nw]
    (yw_ref, vw_ref, ww_ref, a_ref, b_ref, c_ref, h_ref,
     o_ref, sw_ref, d_ref, y_ref, v_ref, w_ref, cp_ref) = refs[nw:]
    lrw = _width_reduce(me_ref[0], r_refs)
    m = yw_ref.shape[0] // nsub
    for q in range(nsub):
        sl = slice(q * m, (q + 1) * m)
        sw_ref[sl] = yw_ref[sl] + vw_ref[sl] * lrw[q][0] + ww_ref[sl] * lrw[q][1]
    nt, ncl, nwl = a_ref.shape
    per_q = 128 // ncl
    for q in range(sw_ref.shape[1]):
        d_ref[q * per_q : (q + 1) * per_q] = sw_ref[:, q, :].T.reshape(per_q, ncl, nwl)
    n = nt // tsub
    subs = [q * n for q in range(tsub)]
    shape = a_ref.shape[1:]
    _sweep(n, subs, _lead_ld, _lead_st, a_ref, b_ref, c_ref, d_ref, y_ref, v_ref, w_ref, cp_ref, 4, shape)
    sums = [tuple(_summary_rows(_lead_ld, s0, n, y_ref, v_ref, w_ref)) for s0 in subs]
    lrs = [None] * tsub

    def emit(p, left, right):
        lrs[p] = (left, right)

    _reduce_blocks(tsub, lambda p: sums[p], emit, jnp.zeros(shape, F32))
    for q, s0 in enumerate(subs):
        sl = slice(s0, s0 + n)
        left, right = lrs[q]
        o_ref[sl] = h_ref[sl] + (y_ref[sl] + v_ref[sl] * left + w_ref[sl] * right)


def cast_solve(a, b, c, d, n):
    shp = jax.ShapeDtypeStruct(a.shape, F32)
    m = a.shape[0] // n
    return pl.pallas_call(
        functools.partial(_cast_kernel, n),
        out_shape=[shp, shp, shp, jax.ShapeDtypeStruct((m * 8, a.shape[1]), F32)],
        scratch_shapes=[pltpu.VMEM(a.shape, F32)],
    )(a, b, c, d)


def width_solve(yc, vc, wc, bk, a, b, c, nsub):
    shp = jax.ShapeDtypeStruct(a.shape, F32)
    return pl.pallas_call(
        functools.partial(_width_kernel, nsub),
        out_shape=[shp, shp, shp, jax.ShapeDtypeStruct((nsub, 6) + a.shape[1:], F32)],
        scratch_shapes=[pltpu.VMEM(a.shape, F32), pltpu.VMEM(a.shape, F32)],
    )(yc, vc, wc, bk, a, b, c)


def thick_solve(me, got, yw, vw, ww, a, b, c, h, nsub, tsub):
    vm = pl.BlockSpec(memory_space=pltpu.VMEM)
    return pl.pallas_call(
        functools.partial(_thick_kernel, nsub, tsub, len(got)),
        out_shape=jax.ShapeDtypeStruct(a.shape, F32),
        in_specs=[SMEM_SPEC] + [vm] * (len(got) + 7),
        scratch_shapes=[pltpu.VMEM(yw.shape, F32)] + [pltpu.VMEM(a.shape, F32)] * 5,
    )(me, *got, yw, vw, ww, a, b, c, h)


def _reduce_blocks(nb, blk, emit, zero):
    pp, qq = zero, zero
    saved = []
    for p in range(nb):
        y0, v0, w0, yn, vn, wn = blk(p)
        rd = 1.0 / (1.0 - v0 * qq)
        fa = (y0 + v0 * pp) * rd
        fb = w0 * rd
        saved.append((fa, fb, pp, qq))
        pp, qq = yn + vn * (pp + qq * fa), wn + vn * qq * fb
    f_next = zero
    for p in range(nb - 1, -1, -1):
        fa, fb, pp, qq = saved[p]
        f = fa + fb * f_next
        emit(p, pp + qq * f, f_next)
        f_next = f


def _cast_reduced_kernel(s_ref, lr_ref):
    nb = s_ref.shape[0]
    def blk(p):
        return tuple(s_ref[p, :, k, :] for k in range(6))

    def emit(p, left, right):
        lr_ref[p, :, 0:1, :] = left[:, None]
        lr_ref[p, :, 1:2, :] = right[:, None]

    _reduce_blocks(nb, blk, emit, jnp.zeros((s_ref.shape[1], s_ref.shape[3]), F32))


def _width_reduce(me, r_refs):
    nw = len(r_refs)
    nsub = r_refs[0].shape[0]
    out = [[None, None] for _ in range(nsub)]

    def blk(b):
        dev, q = divmod(b, nsub)
        kk = (me - dev + nw) % nw
        vals = []
        for k6 in range(6):
            val = r_refs[0][q, k6]
            for k in range(1, nw):
                val = jnp.where(kk == k, r_refs[k][q, k6], val)
            vals.append(val)
        return tuple(vals)

    def emit(b, left, right):
        dev, q = divmod(b, nsub)
        mine = me == dev
        for j, val in enumerate((left, right)):
            out[q][j] = val if out[q][j] is None else jnp.where(mine, val, out[q][j])

    _reduce_blocks(nw * nsub, blk, emit, jnp.zeros(r_refs[0].shape[2:], F32))
    return out


def _surface_kernel(scale, z_ref, sp_ref, o_ref):
    z = z_ref[...]
    acc = jnp.zeros(z.shape, F32)
    for q in range(sp_ref.shape[0]):
        acc = jnp.where(z == q, sp_ref[q], acc)
    o_ref[...] = acc * scale


def medium_parameters(x):
    t = jnp.tanh(x)
    hot = x - solidification_release * t
    cond = 1.5 - 0.5 * jnp.tanh(hot)
    slope = (1.0 - solidification_release) + solidification_release * t * t
    return hot, cond, slope


def shards(h, zones, spray_coef):
    nt, ncl, nwl = h.shape
    nc, nw = lax.axis_size("cast"), lax.axis_size("width")
    ci, wi = lax.axis_index("cast"), lax.axis_index("width")
    up_c = [(i, i + 1) for i in range(nc - 1)]
    up_w = [(i, i + 1) for i in range(nw - 1)]
    even = ci % 2 == 0
    first, last = h[:, 0, :], h[:, -1, :]
    in_chip = [(i, i ^ 1) for i in range(nc)]
    across = [(i, i + 1) for i in range(1, nc - 1, 2)] + [(i + 1, i) for i in range(1, nc - 1, 2)]
    got_a = lax.ppermute(jnp.where(even, last, first), "cast", in_chip)
    got_b = lax.ppermute(jnp.where(even, first, last), "cast", across)
    h_wl = lax.ppermute(h[:, :, -1], "width", up_w)
    h_wh = lax.ppermute(h[:, :, 0], "width", [(b, a) for a, b in up_w])

    cast_low = (ci > 0).astype(F32)
    cast_high = (ci < nc - 1).astype(F32)
    width_low = (wi > 0).astype(F32)
    width_high = (wi < nw - 1).astype(F32)
    flags = jnp.stack([cast_low, cast_high, width_low, width_high, even.astype(F32)])
    outs = prep_solve(
        h.reshape(nt * ncl, nwl), got_a, got_b,
        h_wl, h_wh,
        zones.reshape(2 * ncl, nwl), spray_coef, flags, ncl,
    )
    y, v, w, summ = outs[:4]
    wlo, wmd, whi, tlo, tmd, thi = (x.reshape(nt, ncl, nwl) for x in outs[4:])
    recv = lax.all_to_all(summ.reshape(nc, nt // nc, 8, nwl), "cast", 0, 0, tiled=True)
    lr_shape = recv.shape[:2] + (2, nwl)
    lr = pl.pallas_call(_cast_reduced_kernel, out_shape=jax.ShapeDtypeStruct(lr_shape, F32))(recv)
    back = lax.all_to_all(lr, "cast", 0, 0, tiled=True).reshape(nt, 2, nwl)
    y, v, w = (x.reshape(nt, ncl, nwl) for x in (y, v, w))

    lines = nt * ncl
    nsub = 4

    def wl(x):
        return jnp.transpose(x, (2, 0, 1)).reshape(nwl, lines // 128, 128)

    y, v, w, summ = width_solve(y, v, w, back, wl(wlo), wl(wmd), wl(whi), nsub)
    got = [summ] + [
        lax.ppermute(summ, "width", [(i, (i + q) % nw) for i in range(nw)]) for q in range(1, nw)
    ]
    me = wi.astype(jnp.int32).reshape(1)
    return thick_solve(me, got, y, v, w, tlo, tmd, thi, h, nsub, 4)


def solution(mesh):
    spec = P(None, "cast", "width")
    return jax.shard_map(
        shards, mesh=mesh, in_specs=(spec, spec, P()), out_specs=spec, check_vma=False
    )
```

```python
import functools

import jax
import jax.numpy as jnp
from jax import lax
from jax.experimental import pallas as pl
from jax.experimental.pallas import tpu as pltpu
from jax.sharding import PartitionSpec as P

F32 = jnp.float32
solidification_release = 0.4
quench_medium_hotness = -2.0
SMEM_SPEC = pl.BlockSpec(memory_space=pltpu.SMEM)


def _sweep(n, subs, ld, st, a_ref, b_ref, c_ref, d_ref, y_ref, v_ref, w_ref, cp_ref, unroll, shape):
    with_vw = v_ref is not None
    zero = jnp.zeros(shape, F32)
    one = jnp.ones(shape, F32)

    def fwd(i, carries):
        out = []
        for s0, (cprev, dprev, vprev) in zip(subs, carries):
            j = s0 + i
            a = ld(a_ref, j)
            r = 1.0 / (ld(b_ref, j) - a * cprev)
            cn = ld(c_ref, j) * r
            dn = (ld(d_ref, j) - a * dprev) * r
            st(cp_ref, j, cn)
            st(y_ref, j, dn)
            if with_vw:
                vprev = -(a * vprev) * r
                st(v_ref, j, vprev)
            out.append((cn, dn, vprev))
        return tuple(out)

    carries = tuple((zero, zero, one) for _ in subs)
    if unroll is True:
        for i in range(n):
            carries = fwd(i, carries)
    else:
        carries = lax.fori_loop(0, n, fwd, carries, unroll=unroll)
    if with_vw:
        for s0, (cl, _, _) in zip(subs, carries):
            st(w_ref, s0 + n - 1, -cl)

    def bwd(jj, carries):
        i = n - 2 - jj
        out = []
        for s0, (yn, vn, wn) in zip(subs, carries):
            j = s0 + i
            cp = ld(cp_ref, j)
            yn = ld(y_ref, j) - cp * yn
            st(y_ref, j, yn)
            if with_vw:
                vn = ld(v_ref, j) - cp * vn
                wn = -cp * wn
                st(v_ref, j, vn)
                st(w_ref, j, wn)
            out.append((yn, vn, wn))
        return tuple(out)

    carries = tuple((dl, vl, -cl) for cl, dl, vl in carries)
    if unroll is True:
        for jj in range(n - 1):
            carries = bwd(jj, carries)
    else:
        lax.fori_loop(0, n - 1, bwd, carries, unroll=unroll)


def _summary_rows(ld, s0, n, y_ref, v_ref, w_ref):
    return [ld(y_ref, s0), ld(v_ref, s0), ld(w_ref, s0),
            ld(y_ref, s0 + n - 1), ld(v_ref, s0 + n - 1), ld(w_ref, s0 + n - 1)]


def _cast_kernel(n, a_ref, b_ref, c_ref, d_ref, y_ref, v_ref, w_ref, sm_ref, cp_ref):
    m = a_ref.shape[0] // n

    def ld(ref, i):
        return ref[pl.ds(i, m, stride=n), :]

    def st(ref, i, val):
        ref[pl.ds(i, m, stride=n), :] = val

    shape = (m, a_ref.shape[1])
    _sweep(n, [0], ld, st, a_ref, b_ref, c_ref, d_ref, y_ref, v_ref, w_ref, cp_ref, True, shape)
    rows = _summary_rows(ld, 0, n, y_ref, v_ref, w_ref)
    rows += [jnp.zeros(shape, F32)] * (8 - len(rows))
    for k, val in enumerate(rows):
        sm_ref[pl.ds(k, m, stride=8), :] = val


def _lead_ld(ref, i):
    return ref[i]


def _lead_st(ref, i, val):
    ref[i] = val


def _prep_kernel(n, h_ref, hcl_ref, hch_ref, hwl_ref, hwh_ref, z_ref, sp_ref, fl_ref,
                 y_ref, v_ref, w_ref, sm_ref, wa_ref, wb_ref, wc_ref, ta_ref, tb_ref, tc_ref,
                 tp_ref, kp_ref, sp2_ref, a_ref, b_ref, c_ref, d_ref, cp_ref):
    rows, nwl = h_ref.shape
    nt = rows // n
    hot, cond, slope = medium_parameters(h_ref[...])
    zpad = jnp.zeros((n, nwl), F32)
    for ref, val in ((tp_ref, hot), (kp_ref, cond), (sp2_ref, slope)):
        ref[0:n] = zpad
        ref[n : n + rows] = val
        ref[n + rows : 2 * n + rows] = zpad

    def row(ref, off):
        return ref[pl.ds(off, nt, stride=n), :]

    lane = lax.broadcasted_iota(jnp.int32, (nt, nwl), 1)
    tix = lax.broadcasted_iota(jnp.int32, (nt, nwl), 0)
    even = fl_ref[4] > 0.5
    got_a, got_b = hcl_ref[...], hch_ref[...]
    cast_lo = medium_parameters(jnp.where(even, got_b, got_a))
    cast_hi = medium_parameters(jnp.where(even, got_a, got_b))
    g_c = n * n * 4.0 * 0.5
    g_w = nwl * nwl / 4.0 * 0.5
    g_t = nt * nt / 4.0 * 0.5
    edge_wl = jnp.where(lane == 0, fl_ref[2], 1.0)
    edge_wh = jnp.where(lane == nwl - 1, fl_ref[3], 1.0)
    nz = sp_ref.shape[0]

    def surf_row(zr):
        acc = jnp.zeros(zr.shape, F32)
        for q in range(nz):
            acc = jnp.where(zr == q, sp_ref[q], acc)
        return acc * (nt * nt / 8.0)

    for c in range(n):
        T0, k0, s0 = (row(r, n + c) for r in (tp_ref, kp_ref, sp2_ref))
        if c == 0:
            Tm, km, sm = cast_lo
        else:
            Tm, km, sm = (row(r, n + c - 1) for r in (tp_ref, kp_ref, sp2_ref))
        if c == n - 1:
            Tq, kq, sq = cast_hi
        else:
            Tq, kq, sq = (row(r, n + c + 1) for r in (tp_ref, kp_ref, sp2_ref))
        Ttm, ktm, stm = (row(r, c) for r in (tp_ref, kp_ref, sp2_ref))
        Ttp, ktp, stp = (row(r, 2 * n + c) for r in (tp_ref, kp_ref, sp2_ref))
        wlo = medium_parameters(hwl_ref[:, c : c + 1])
        whi = medium_parameters(hwh_ref[:, c : c + 1])
        Twm, kwm, swm = (jnp.where(lane == 0, b, pltpu.roll(f, 1, 1)) for f, b in zip((T0, k0, s0), wlo))
        Twp, kwp, swp = (
            jnp.where(lane == nwl - 1, b, pltpu.roll(f, nwl - 1, 1)) for f, b in zip((T0, k0, s0), whi)
        )
        gcl = g_c * (k0 + km)
        if c == 0:
            gcl = gcl * fl_ref[0]
        gch = g_c * (kq + k0)
        if c == n - 1:
            gch = gch * fl_ref[1]
        gwl = g_w * (k0 + kwm) * edge_wl
        gwh = g_w * (kwp + k0) * edge_wh
        gtl = jnp.where(tix == 0, 0.0, g_t * (k0 + ktm))
        gth = jnp.where(tix == nt - 1, 0.0, g_t * (ktp + k0))
        s_lo = surf_row(z_ref[c : c + 1, :])
        s_hi = surf_row(z_ref[n + c : n + c + 1, :])
        rim = jnp.where(tix == 0, s_lo, jnp.where(tix == nt - 1, s_hi, 0.0))
        ex = rim * (quench_medium_hotness - T0)
        ex = ex + (gch * (Tq - T0) - gcl * (T0 - Tm))
        ex = ex + (gwh * (Twp - T0) - gwl * (T0 - Twm))
        ex = ex + (gth * (Ttp - T0) - gtl * (T0 - Ttm))
        sel = pl.ds(c, nt, stride=n)
        a_ref[sel, :] = -gcl * sm
        c_ref[sel, :] = -gch * sq
        b_ref[sel, :] = 1.0 + s0 * (gcl + gch)
        d_ref[sel, :] = ex
        wa_ref[sel, :] = -gwl * swm
        wc_ref[sel, :] = -gwh * swp
        wb_ref[sel, :] = 1.0 + s0 * (gwl + gwh)
        ta_ref[sel, :] = -gtl * stm
        tc_ref[sel, :] = -gth * stp
        tb_ref[sel, :] = 1.0 + s0 * (gtl + gth + rim)

    def ld(ref, i):
        return ref[pl.ds(i, nt, stride=n), :]

    def st(ref, i, val):
        ref[pl.ds(i, nt, stride=n), :] = val

    shape = (nt, nwl)
    _sweep(n, [0], ld, st, a_ref, b_ref, c_ref, d_ref, y_ref, v_ref, w_ref, cp_ref, True, shape)
    rws = _summary_rows(ld, 0, n, y_ref, v_ref, w_ref)
    rws += [jnp.zeros(shape, F32)] * (8 - len(rws))
    for k, val in enumerate(rws):
        sm_ref[pl.ds(k, nt, stride=8), :] = val


def prep_solve(h2, hcl, hch, hwl, hwh, z2, spray, flags, n):
    rows, nwl = h2.shape
    nt = rows // n
    shp = jax.ShapeDtypeStruct(h2.shape, F32)
    vm = pl.BlockSpec(memory_space=pltpu.VMEM)
    pad = pltpu.VMEM((rows + 2 * n, nwl), F32)
    return pl.pallas_call(
        functools.partial(_prep_kernel, n),
        out_shape=[shp] * 3 + [jax.ShapeDtypeStruct((nt * 8, nwl), F32)] + [shp] * 6,
        in_specs=[vm] * 6 + [SMEM_SPEC, SMEM_SPEC],
        scratch_shapes=[pad, pad, pad] + [pltpu.VMEM(h2.shape, F32)] * 5,
    )(h2, hcl, hch, hwl, hwh, z2, spray, flags)


def _factor(n, subs, ld, st, a_ref, b_ref, c_ref, r_ref, cp_ref, v_ref, w_ref, unroll, shape):
    zero = jnp.zeros(shape, F32)
    one = jnp.ones(shape, F32)

    def fwd(i, carries):
        out = []
        for s0, (cprev, vprev) in zip(subs, carries):
            j = s0 + i
            a = ld(a_ref, j)
            r = 1.0 / (ld(b_ref, j) - a * cprev)
            cn = ld(c_ref, j) * r
            vprev = -(a * vprev) * r
            st(r_ref, j, r)
            st(cp_ref, j, cn)
            st(v_ref, j, vprev)
            out.append((cn, vprev))
        return tuple(out)

    carries = lax.fori_loop(0, n, fwd, tuple((zero, one) for _ in subs), unroll=unroll)
    for s0, (cl, _) in zip(subs, carries):
        st(w_ref, s0 + n - 1, -cl)

    def bwd(jj, carries):
        i = n - 2 - jj
        out = []
        for s0, (vn, wn) in zip(subs, carries):
            j = s0 + i
            cp = ld(cp_ref, j)
            vn = ld(v_ref, j) - cp * vn
            wn = -cp * wn
            st(v_ref, j, vn)
            st(w_ref, j, wn)
            out.append((vn, wn))
        return tuple(out)

    lax.fori_loop(0, n - 1, bwd, tuple((vl, -cl) for cl, vl in carries), unroll=unroll)


def _solve_rhs(n, subs, ld, st, a_ref, r_ref, cp_ref, d_ref, y_ref, unroll, shape):
    zero = jnp.zeros(shape, F32)

    def fwd(i, carries):
        out = []
        for s0, dprev in zip(subs, carries):
            j = s0 + i
            dn = (ld(d_ref, j) - ld(a_ref, j) * dprev) * ld(r_ref, j)
            st(y_ref, j, dn)
            out.append(dn)
        return tuple(out)

    carries = lax.fori_loop(0, n, fwd, tuple(zero for _ in subs), unroll=unroll)

    def bwd(jj, carries):
        i = n - 2 - jj
        out = []
        for s0, yn in zip(subs, carries):
            j = s0 + i
            yn = ld(y_ref, j) - ld(cp_ref, j) * yn
            st(y_ref, j, yn)
            out.append(yn)
        return tuple(out)

    lax.fori_loop(0, n - 1, bwd, carries, unroll=unroll)


def _factor_kernel(nsub, a_ref, b_ref, c_ref, r_ref, cp_ref, v_ref, w_ref):
    n = a_ref.shape[0] // nsub
    subs = [q * n for q in range(nsub)]
    _factor(n, subs, _lead_ld, _lead_st, a_ref, b_ref, c_ref, r_ref, cp_ref, v_ref, w_ref, 4, a_ref.shape[1:])


def factor(a, b, c, nsub):
    shp = jax.ShapeDtypeStruct(a.shape, F32)
    return pl.pallas_call(functools.partial(_factor_kernel, nsub), out_shape=[shp] * 4)(a, b, c)


def _width_kernel(nsub, yc_ref, vc_ref, wc_ref, bk_ref, a_ref, r_ref, cp_ref, v_ref, w_ref,
                  y_ref, sm_ref, d_ref):
    sc = yc_ref[...] + vc_ref[...] * bk_ref[:, 0:1, :] + wc_ref[...] * bk_ref[:, 1:2, :]
    nt, ncl, nwl = sc.shape
    sc = sc.reshape(nt * ncl, nwl)
    for q in range(d_ref.shape[1]):
        d_ref[:, q, :] = sc[q * 128 : (q + 1) * 128, :].T
    n = a_ref.shape[0] // nsub
    subs = [q * n for q in range(nsub)]
    _solve_rhs(n, subs, _lead_ld, _lead_st, a_ref, r_ref, cp_ref, d_ref, y_ref, 4, a_ref.shape[1:])
    for q, s0 in enumerate(subs):
        for k, val in enumerate(_summary_rows(_lead_ld, s0, n, y_ref, v_ref, w_ref)):
            sm_ref[q, k] = val


def _thick_kernel(nsub, tsub, nw, me_ref, *refs):
    r_refs = refs[:nw]
    (yw_ref, vw_ref, ww_ref, a_ref, r_ref, cp_ref, v_ref, w_ref, h_ref,
     o_ref, sw_ref, d_ref, y_ref) = refs[nw:]
    lrw = _width_reduce(me_ref[0], r_refs)
    m = yw_ref.shape[0] // nsub
    for q in range(nsub):
        sl = slice(q * m, (q + 1) * m)
        sw_ref[sl] = yw_ref[sl] + vw_ref[sl] * lrw[q][0] + ww_ref[sl] * lrw[q][1]
    nt, ncl, nwl = a_ref.shape
    per_q = 128 // ncl
    for q in range(sw_ref.shape[1]):
        d_ref[q * per_q : (q + 1) * per_q] = sw_ref[:, q, :].T.reshape(per_q, ncl, nwl)
    n = nt // tsub
    subs = [q * n for q in range(tsub)]
    shape = a_ref.shape[1:]
    _solve_rhs(n, subs, _lead_ld, _lead_st, a_ref, r_ref, cp_ref, d_ref, y_ref, 4, shape)
    sums = [tuple(_summary_rows(_lead_ld, s0, n, y_ref, v_ref, w_ref)) for s0 in subs]
    lrs = [None] * tsub

    def emit(p, left, right):
        lrs[p] = (left, right)

    _reduce_blocks(tsub, lambda p: sums[p], emit, jnp.zeros(shape, F32))
    for q, s0 in enumerate(subs):
        sl = slice(s0, s0 + n)
        left, right = lrs[q]
        o_ref[sl] = h_ref[sl] + (y_ref[sl] + v_ref[sl] * left + w_ref[sl] * right)


def cast_solve(a, b, c, d, n):
    shp = jax.ShapeDtypeStruct(a.shape, F32)
    m = a.shape[0] // n
    return pl.pallas_call(
        functools.partial(_cast_kernel, n),
        out_shape=[shp, shp, shp, jax.ShapeDtypeStruct((m * 8, a.shape[1]), F32)],
        scratch_shapes=[pltpu.VMEM(a.shape, F32)],
    )(a, b, c, d)


def width_solve(yc, vc, wc, bk, a, fac, nsub):
    shp = jax.ShapeDtypeStruct(a.shape, F32)
    return pl.pallas_call(
        functools.partial(_width_kernel, nsub),
        out_shape=[shp, jax.ShapeDtypeStruct((nsub, 6) + a.shape[1:], F32)],
        scratch_shapes=[pltpu.VMEM(a.shape, F32)],
    )(yc, vc, wc, bk, a, *fac)


def thick_solve(me, got, yw, vw, ww, a, fac, h, nsub, tsub):
    vm = pl.BlockSpec(memory_space=pltpu.VMEM)
    return pl.pallas_call(
        functools.partial(_thick_kernel, nsub, tsub, len(got)),
        out_shape=jax.ShapeDtypeStruct(a.shape, F32),
        in_specs=[SMEM_SPEC] + [vm] * (len(got) + 9),
        scratch_shapes=[pltpu.VMEM(yw.shape, F32)] + [pltpu.VMEM(a.shape, F32)] * 2,
    )(me, *got, yw, vw, ww, a, *fac, h)


def _reduce_blocks(nb, blk, emit, zero):
    pp, qq = zero, zero
    saved = []
    for p in range(nb):
        y0, v0, w0, yn, vn, wn = blk(p)
        rd = 1.0 / (1.0 - v0 * qq)
        fa = (y0 + v0 * pp) * rd
        fb = w0 * rd
        saved.append((fa, fb, pp, qq))
        pp, qq = yn + vn * (pp + qq * fa), wn + vn * qq * fb
    f_next = zero
    for p in range(nb - 1, -1, -1):
        fa, fb, pp, qq = saved[p]
        f = fa + fb * f_next
        emit(p, pp + qq * f, f_next)
        f_next = f


def _cast_reduced_kernel(s_ref, lr_ref):
    nb = s_ref.shape[0]
    def blk(p):
        return tuple(s_ref[p, :, k, :] for k in range(6))

    def emit(p, left, right):
        lr_ref[p, :, 0:1, :] = left[:, None]
        lr_ref[p, :, 1:2, :] = right[:, None]

    _reduce_blocks(nb, blk, emit, jnp.zeros((s_ref.shape[1], s_ref.shape[3]), F32))


def _width_reduce(me, r_refs):
    nw = len(r_refs)
    nsub = r_refs[0].shape[0]
    out = [[None, None] for _ in range(nsub)]

    def blk(b):
        dev, q = divmod(b, nsub)
        kk = (me - dev + nw) % nw
        vals = []
        for k6 in range(6):
            val = r_refs[0][q, k6]
            for k in range(1, nw):
                val = jnp.where(kk == k, r_refs[k][q, k6], val)
            vals.append(val)
        return tuple(vals)

    def emit(b, left, right):
        dev, q = divmod(b, nsub)
        mine = me == dev
        for j, val in enumerate((left, right)):
            out[q][j] = val if out[q][j] is None else jnp.where(mine, val, out[q][j])

    _reduce_blocks(nw * nsub, blk, emit, jnp.zeros(r_refs[0].shape[2:], F32))
    return out


def _surface_kernel(scale, z_ref, sp_ref, o_ref):
    z = z_ref[...]
    acc = jnp.zeros(z.shape, F32)
    for q in range(sp_ref.shape[0]):
        acc = jnp.where(z == q, sp_ref[q], acc)
    o_ref[...] = acc * scale


def medium_parameters(x):
    t = jnp.tanh(x)
    hot = x - solidification_release * t
    cond = 1.5 - 0.5 * jnp.tanh(hot)
    slope = (1.0 - solidification_release) + solidification_release * t * t
    return hot, cond, slope


def shards(h, zones, spray_coef):
    nt, ncl, nwl = h.shape
    nc, nw = lax.axis_size("cast"), lax.axis_size("width")
    ci, wi = lax.axis_index("cast"), lax.axis_index("width")
    up_c = [(i, i + 1) for i in range(nc - 1)]
    up_w = [(i, i + 1) for i in range(nw - 1)]
    even = ci % 2 == 0
    first, last = h[:, 0, :], h[:, -1, :]
    in_chip = [(i, i ^ 1) for i in range(nc)]
    across = [(i, i + 1) for i in range(1, nc - 1, 2)] + [(i + 1, i) for i in range(1, nc - 1, 2)]
    got_a = lax.ppermute(jnp.where(even, last, first), "cast", in_chip)
    got_b = lax.ppermute(jnp.where(even, first, last), "cast", across)
    h_wl = lax.ppermute(h[:, :, -1], "width", up_w)
    h_wh = lax.ppermute(h[:, :, 0], "width", [(b, a) for a, b in up_w])

    cast_low = (ci > 0).astype(F32)
    cast_high = (ci < nc - 1).astype(F32)
    width_low = (wi > 0).astype(F32)
    width_high = (wi < nw - 1).astype(F32)
    flags = jnp.stack([cast_low, cast_high, width_low, width_high, even.astype(F32)])
    outs = prep_solve(
        h.reshape(nt * ncl, nwl), got_a, got_b,
        h_wl, h_wh,
        zones.reshape(2 * ncl, nwl), spray_coef, flags, ncl,
    )
    y, v, w, summ = outs[:4]
    wlo, wmd, whi, tlo, tmd, thi = (x.reshape(nt, ncl, nwl) for x in outs[4:])
    recv = lax.all_to_all(summ.reshape(nc, nt // nc, 8, nwl), "cast", 0, 0, tiled=True)
    lr_shape = recv.shape[:2] + (2, nwl)
    lr = pl.pallas_call(_cast_reduced_kernel, out_shape=jax.ShapeDtypeStruct(lr_shape, F32))(recv)
    back = lax.all_to_all(lr, "cast", 0, 0, tiled=True).reshape(nt, 2, nwl)
    y, v, w = (x.reshape(nt, ncl, nwl) for x in (y, v, w))

    lines = nt * ncl
    nsub = 4

    def wl(x):
        return jnp.transpose(x, (2, 0, 1)).reshape(nwl, lines // 128, 128)

    wa = wl(wlo)
    wfac = factor(wa, wl(wmd), wl(whi), nsub)
    tfac = factor(tlo, tmd, thi, 4)
    yw, summ = width_solve(y, v, w, back, wa, wfac, nsub)
    got = [summ] + [
        lax.ppermute(summ, "width", [(i, (i + q) % nw) for i in range(nw)]) for q in range(1, nw)
    ]
    me = wi.astype(jnp.int32).reshape(1)
    return thick_solve(me, got, yw, wfac[2], wfac[3], tlo, tfac, h, nsub, 4)


def solution(mesh):
    spec = P(None, "cast", "width")
    return jax.shard_map(
        shards, mesh=mesh, in_specs=(spec, spec, P()), out_specs=spec, check_vma=False
    )
```

```python
import functools

import jax
import jax.numpy as jnp
from jax import lax
from jax.experimental import pallas as pl
from jax.experimental.pallas import tpu as pltpu
from jax.sharding import PartitionSpec as P

F32 = jnp.float32
solidification_release = 0.4
quench_medium_hotness = -2.0
SMEM_SPEC = pl.BlockSpec(memory_space=pltpu.SMEM)


def _sweep(n, subs, ld, st, a_ref, b_ref, c_ref, d_ref, y_ref, v_ref, w_ref, cp_ref, unroll, shape):
    with_vw = v_ref is not None
    zero = jnp.zeros(shape, F32)
    one = jnp.ones(shape, F32)

    def fwd(i, carries):
        out = []
        for s0, (cprev, dprev, vprev) in zip(subs, carries):
            j = s0 + i
            a = ld(a_ref, j)
            r = 1.0 / (ld(b_ref, j) - a * cprev)
            cn = ld(c_ref, j) * r
            dn = (ld(d_ref, j) - a * dprev) * r
            st(cp_ref, j, cn)
            st(y_ref, j, dn)
            if with_vw:
                vprev = -(a * vprev) * r
                st(v_ref, j, vprev)
            out.append((cn, dn, vprev))
        return tuple(out)

    carries = tuple((zero, zero, one) for _ in subs)
    if unroll is True:
        for i in range(n):
            carries = fwd(i, carries)
    else:
        carries = lax.fori_loop(0, n, fwd, carries, unroll=unroll)
    if with_vw:
        for s0, (cl, _, _) in zip(subs, carries):
            st(w_ref, s0 + n - 1, -cl)

    def bwd(jj, carries):
        i = n - 2 - jj
        out = []
        for s0, (yn, vn, wn) in zip(subs, carries):
            j = s0 + i
            cp = ld(cp_ref, j)
            yn = ld(y_ref, j) - cp * yn
            st(y_ref, j, yn)
            if with_vw:
                vn = ld(v_ref, j) - cp * vn
                wn = -cp * wn
                st(v_ref, j, vn)
                st(w_ref, j, wn)
            out.append((yn, vn, wn))
        return tuple(out)

    carries = tuple((dl, vl, -cl) for cl, dl, vl in carries)
    if unroll is True:
        for jj in range(n - 1):
            carries = bwd(jj, carries)
    else:
        lax.fori_loop(0, n - 1, bwd, carries, unroll=unroll)


def _summary_rows(ld, s0, n, y_ref, v_ref, w_ref):
    return [ld(y_ref, s0), ld(v_ref, s0), ld(w_ref, s0),
            ld(y_ref, s0 + n - 1), ld(v_ref, s0 + n - 1), ld(w_ref, s0 + n - 1)]


def _cast_kernel(n, a_ref, b_ref, c_ref, d_ref, y_ref, v_ref, w_ref, sm_ref, cp_ref):
    m = a_ref.shape[0] // n

    def ld(ref, i):
        return ref[pl.ds(i, m, stride=n), :]

    def st(ref, i, val):
        ref[pl.ds(i, m, stride=n), :] = val

    shape = (m, a_ref.shape[1])
    _sweep(n, [0], ld, st, a_ref, b_ref, c_ref, d_ref, y_ref, v_ref, w_ref, cp_ref, True, shape)
    rows = _summary_rows(ld, 0, n, y_ref, v_ref, w_ref)
    rows += [jnp.zeros(shape, F32)] * (8 - len(rows))
    for k, val in enumerate(rows):
        sm_ref[pl.ds(k, m, stride=8), :] = val


def _lead_ld(ref, i):
    return ref[i]


def _lead_st(ref, i, val):
    ref[i] = val


def _loop(n, body, carry, unroll):
    if unroll is True:
        for i in range(n):
            carry = body(i, carry)
        return carry
    return lax.fori_loop(0, n, body, carry, unroll=unroll)


def _factor(n, subs, ld, st, a_ref, b_ref, c_ref, r_ref, cp_ref, v_ref, w_ref, unroll, shape):
    zero = jnp.zeros(shape, F32)
    one = jnp.ones(shape, F32)

    def fwd(i, carries):
        out = []
        for s0, (cprev, vprev) in zip(subs, carries):
            j = s0 + i
            a = ld(a_ref, j)
            r = 1.0 / (ld(b_ref, j) - a * cprev)
            cn = ld(c_ref, j) * r
            vprev = -(a * vprev) * r
            st(r_ref, j, r)
            st(cp_ref, j, cn)
            st(v_ref, j, vprev)
            out.append((cn, vprev))
        return tuple(out)

    carries = _loop(n, fwd, tuple((zero, one) for _ in subs), unroll)
    for s0, (cl, _) in zip(subs, carries):
        st(w_ref, s0 + n - 1, -cl)

    def bwd(jj, carries):
        i = n - 2 - jj
        out = []
        for s0, (vn, wn) in zip(subs, carries):
            j = s0 + i
            cp = ld(cp_ref, j)
            vn = ld(v_ref, j) - cp * vn
            wn = -cp * wn
            st(v_ref, j, vn)
            st(w_ref, j, wn)
            out.append((vn, wn))
        return tuple(out)

    _loop(n - 1, bwd, tuple((vl, -cl) for cl, vl in carries), unroll)


def _solve_rhs(n, subs, ld, st, a_ref, r_ref, cp_ref, d_ref, y_ref, unroll, shape):
    zero = jnp.zeros(shape, F32)

    def fwd(i, carries):
        out = []
        for s0, dprev in zip(subs, carries):
            j = s0 + i
            dn = (ld(d_ref, j) - ld(a_ref, j) * dprev) * ld(r_ref, j)
            st(y_ref, j, dn)
            out.append(dn)
        return tuple(out)

    carries = _loop(n, fwd, tuple(zero for _ in subs), unroll)

    def bwd(jj, carries):
        i = n - 2 - jj
        out = []
        for s0, yn in zip(subs, carries):
            j = s0 + i
            yn = ld(y_ref, j) - ld(cp_ref, j) * yn
            st(y_ref, j, yn)
            out.append(yn)
        return tuple(out)

    _loop(n - 1, bwd, carries, unroll)


def _factor_kernel(nsub, a_ref, b_ref, c_ref, r_ref, cp_ref, v_ref, w_ref):
    n = a_ref.shape[0] // nsub
    subs = [q * n for q in range(nsub)]
    _factor(n, subs, _lead_ld, _lead_st, a_ref, b_ref, c_ref, r_ref, cp_ref, v_ref, w_ref, 4, a_ref.shape[1:])


def factor(a, b, c, nsub):
    shp = jax.ShapeDtypeStruct(a.shape, F32)
    return pl.pallas_call(functools.partial(_factor_kernel, nsub), out_shape=[shp] * 4)(a, b, c)


def _width_faces(n, c, T0, k0, s0, lane, wlo, whi, fl_ref):
    nwl = T0.shape[1]
    g_w = nwl * nwl / 4.0 * 0.5
    if wlo is None:
        wlo = (T0, k0, s0)
        whi = (T0, k0, s0)
        e_lo, e_hi = 0.0, 0.0
    else:
        e_lo, e_hi = fl_ref[2], fl_ref[3]
    Twm, kwm, swm = (jnp.where(lane == 0, b, pltpu.roll(f, 1, 1)) for f, b in zip((T0, k0, s0), wlo))
    Twp, kwp, swp = (
        jnp.where(lane == nwl - 1, b, pltpu.roll(f, nwl - 1, 1)) for f, b in zip((T0, k0, s0), whi)
    )
    gwl = g_w * (k0 + kwm) * jnp.where(lane == 0, e_lo, 1.0)
    gwh = g_w * (kwp + k0) * jnp.where(lane == nwl - 1, e_hi, 1.0)
    return Twm, swm, Twp, swp, gwl, gwh


def _prep_kernel(n, h_ref, hcl_ref, hch_ref, z_ref, sp_ref, fl_ref,
                 y_ref, v_ref, w_ref, sm_ref, a_ref, r_ref, cp_ref, ta_ref, tb_ref, tc_ref,
                 tp_ref, kp_ref, sp2_ref, b_ref, c_ref, d_ref):
    rows, nwl = h_ref.shape
    nt = rows // n
    hot, cond, slope = medium_parameters(h_ref[...])
    zpad = jnp.zeros((n, nwl), F32)
    for ref, val in ((tp_ref, hot), (kp_ref, cond), (sp2_ref, slope)):
        ref[0:n] = zpad
        ref[n : n + rows] = val
        ref[n + rows : 2 * n + rows] = zpad

    def row(ref, off):
        return ref[pl.ds(off, nt, stride=n), :]

    lane = lax.broadcasted_iota(jnp.int32, (nt, nwl), 1)
    tix = lax.broadcasted_iota(jnp.int32, (nt, nwl), 0)
    even = fl_ref[4] > 0.5
    got_a, got_b = hcl_ref[...], hch_ref[...]
    cast_lo = medium_parameters(jnp.where(even, got_b, got_a))
    cast_hi = medium_parameters(jnp.where(even, got_a, got_b))
    g_c = n * n * 4.0 * 0.5
    g_t = nt * nt / 4.0 * 0.5
    nz = sp_ref.shape[0]

    def surf_row(zr):
        acc = jnp.zeros(zr.shape, F32)
        for q in range(nz):
            acc = jnp.where(zr == q, sp_ref[q], acc)
        return acc * (nt * nt / 8.0)

    for c in range(n):
        T0, k0, s0 = (row(r, n + c) for r in (tp_ref, kp_ref, sp2_ref))
        if c == 0:
            Tm, km, sm = cast_lo
        else:
            Tm, km, sm = (row(r, n + c - 1) for r in (tp_ref, kp_ref, sp2_ref))
        if c == n - 1:
            Tq, kq, sq = cast_hi
        else:
            Tq, kq, sq = (row(r, n + c + 1) for r in (tp_ref, kp_ref, sp2_ref))
        Ttm, ktm, stm = (row(r, c) for r in (tp_ref, kp_ref, sp2_ref))
        Ttp, ktp, stp = (row(r, 2 * n + c) for r in (tp_ref, kp_ref, sp2_ref))
        Twm, _, Twp, _, gwl, gwh = _width_faces(n, c, T0, k0, s0, lane, None, None, fl_ref)
        gcl = g_c * (k0 + km)
        if c == 0:
            gcl = gcl * fl_ref[0]
        gch = g_c * (kq + k0)
        if c == n - 1:
            gch = gch * fl_ref[1]
        gtl = jnp.where(tix == 0, 0.0, g_t * (k0 + ktm))
        gth = jnp.where(tix == nt - 1, 0.0, g_t * (ktp + k0))
        s_lo = surf_row(z_ref[c : c + 1, :])
        s_hi = surf_row(z_ref[n + c : n + c + 1, :])
        rim = jnp.where(tix == 0, s_lo, jnp.where(tix == nt - 1, s_hi, 0.0))
        ex = rim * (quench_medium_hotness - T0)
        ex = ex + (gch * (Tq - T0) - gcl * (T0 - Tm))
        ex = ex + (gwh * (Twp - T0) - gwl * (T0 - Twm))
        ex = ex + (gth * (Ttp - T0) - gtl * (T0 - Ttm))
        sel = pl.ds(c, nt, stride=n)
        a_ref[sel, :] = -gcl * sm
        c_ref[sel, :] = -gch * sq
        b_ref[sel, :] = 1.0 + s0 * (gcl + gch)
        d_ref[sel, :] = ex
        ta_ref[sel, :] = -gtl * stm
        tc_ref[sel, :] = -gth * stp
        tb_ref[sel, :] = 1.0 + s0 * (gtl + gth + rim)

    def ld(ref, i):
        return ref[pl.ds(i, nt, stride=n), :]

    def st(ref, i, val):
        ref[pl.ds(i, nt, stride=n), :] = val

    shape = (nt, nwl)
    _factor(n, [0], ld, st, a_ref, b_ref, c_ref, r_ref, cp_ref, v_ref, w_ref, True, shape)
    _solve_rhs(n, [0], ld, st, a_ref, r_ref, cp_ref, d_ref, y_ref, True, shape)
    rws = _summary_rows(ld, 0, n, y_ref, v_ref, w_ref)
    rws += [jnp.zeros(shape, F32)] * (8 - len(rws))
    for k, val in enumerate(rws):
        sm_ref[pl.ds(k, nt, stride=8), :] = val


def prep_solve(h2, hcl, hch, z2, spray, flags, n):
    rows, nwl = h2.shape
    nt = rows // n
    shp = jax.ShapeDtypeStruct(h2.shape, F32)
    vm = pl.BlockSpec(memory_space=pltpu.VMEM)
    pad = pltpu.VMEM((rows + 2 * n, nwl), F32)
    return pl.pallas_call(
        functools.partial(_prep_kernel, n),
        out_shape=[shp] * 3 + [jax.ShapeDtypeStruct((nt * 8, nwl), F32)] + [shp] * 6,
        in_specs=[vm] * 4 + [SMEM_SPEC, SMEM_SPEC],
        scratch_shapes=[pad, pad, pad] + [pltpu.VMEM(h2.shape, F32)] * 3,
    )(h2, hcl, hch, z2, spray, flags)


def _edge_kernel(n, h_ref, hwl_ref, hwh_ref, fl_ref, a_ref, r_ref, cp_ref, y_ref, sm_ref,
                 yo_ref, smo_ref, d_ref, e_ref):
    rows, nwl = h_ref.shape
    nt = rows // n
    lane = lax.broadcasted_iota(jnp.int32, (nt, nwl), 1)
    for c in range(n):
        sel = pl.ds(c, nt, stride=n)
        T0, k0, s0 = medium_parameters(h_ref[sel, :])
        wlo = medium_parameters(hwl_ref[:, c : c + 1])
        whi = medium_parameters(hwh_ref[:, c : c + 1])
        Twm, _, Twp, _, gwl, gwh = _width_faces(n, c, T0, k0, s0, lane, wlo, whi, fl_ref)
        edge = jnp.where(lane == 0, -gwl * (T0 - Twm), jnp.where(lane == nwl - 1, gwh * (Twp - T0), 0.0))
        d_ref[sel, :] = edge

    def ld(ref, i):
        return ref[pl.ds(i, nt, stride=n), :]

    def st(ref, i, val):
        ref[pl.ds(i, nt, stride=n), :] = val

    _solve_rhs(n, [0], ld, st, a_ref, r_ref, cp_ref, d_ref, e_ref, True, (nt, nwl))
    yo_ref[...] = y_ref[...] + e_ref[...]
    smo_ref[...] = sm_ref[...]
    smo_ref[pl.ds(0, nt, stride=8), :] = sm_ref[pl.ds(0, nt, stride=8), :] + ld(e_ref, 0)
    smo_ref[pl.ds(3, nt, stride=8), :] = sm_ref[pl.ds(3, nt, stride=8), :] + ld(e_ref, n - 1)


def edge_solve(h2, hwl, hwh, flags, a, r, cp, y, sm, n):
    vm = pl.BlockSpec(memory_space=pltpu.VMEM)
    return pl.pallas_call(
        functools.partial(_edge_kernel, n),
        out_shape=[jax.ShapeDtypeStruct(y.shape, F32), jax.ShapeDtypeStruct(sm.shape, F32)],
        in_specs=[vm] * 3 + [SMEM_SPEC] + [vm] * 5,
        scratch_shapes=[pltpu.VMEM(y.shape, F32)] * 2,
    )(h2, hwl, hwh, flags, a, r, cp, y, sm)


def _wfactor_kernel(n, nsub, h_ref, hwl_ref, hwh_ref, fl_ref, a_ref, r_ref, cp_ref, v_ref, w_ref,
                    at_ref, bt_ref, ct_ref, b_ref, c_ref):
    rows, nwl = h_ref.shape
    nt = rows // n
    lane = lax.broadcasted_iota(jnp.int32, (nt, nwl), 1)
    for c in range(n):
        sel = pl.ds(c, nt, stride=n)
        T0, k0, s0 = medium_parameters(h_ref[sel, :])
        wlo = medium_parameters(hwl_ref[:, c : c + 1])
        whi = medium_parameters(hwh_ref[:, c : c + 1])
        _, swm, _, swp, gwl, gwh = _width_faces(n, c, T0, k0, s0, lane, wlo, whi, fl_ref)
        at_ref[sel, :] = -gwl * swm
        ct_ref[sel, :] = -gwh * swp
        bt_ref[sel, :] = 1.0 + s0 * (gwl + gwh)
    for src, dst in ((at_ref, a_ref), (bt_ref, b_ref), (ct_ref, c_ref)):
        for q in range(dst.shape[1]):
            dst[:, q, :] = src[q * 128 : (q + 1) * 128, :].T
    m = a_ref.shape[0] // nsub
    subs = [q * m for q in range(nsub)]
    _factor(m, subs, _lead_ld, _lead_st, a_ref, b_ref, c_ref, r_ref, cp_ref, v_ref, w_ref, 4, a_ref.shape[1:])


def wfactor(h2, hwl, hwh, flags, n, nsub):
    rows, nwl = h2.shape
    wshape = (nwl, rows // 128, 128)
    shp = jax.ShapeDtypeStruct(wshape, F32)
    vm = pl.BlockSpec(memory_space=pltpu.VMEM)
    return pl.pallas_call(
        functools.partial(_wfactor_kernel, n, nsub),
        out_shape=[shp] * 5,
        in_specs=[vm] * 3 + [SMEM_SPEC],
        scratch_shapes=[pltpu.VMEM(h2.shape, F32)] * 3 + [pltpu.VMEM(wshape, F32)] * 2,
    )(h2, hwl, hwh, flags)


def _width_kernel(nsub, yc_ref, vc_ref, wc_ref, bk_ref, a_ref, r_ref, cp_ref, v_ref, w_ref,
                  y_ref, sm_ref, d_ref):
    sc = yc_ref[...] + vc_ref[...] * bk_ref[:, 0:1, :] + wc_ref[...] * bk_ref[:, 1:2, :]
    nt, ncl, nwl = sc.shape
    sc = sc.reshape(nt * ncl, nwl)
    for q in range(d_ref.shape[1]):
        d_ref[:, q, :] = sc[q * 128 : (q + 1) * 128, :].T
    n = a_ref.shape[0] // nsub
    subs = [q * n for q in range(nsub)]
    _solve_rhs(n, subs, _lead_ld, _lead_st, a_ref, r_ref, cp_ref, d_ref, y_ref, 4, a_ref.shape[1:])
    for q, s0 in enumerate(subs):
        for k, val in enumerate(_summary_rows(_lead_ld, s0, n, y_ref, v_ref, w_ref)):
            sm_ref[q, k] = val


def _thick_kernel(nsub, tsub, nw, me_ref, *refs):
    r_refs = refs[:nw]
    (yw_ref, vw_ref, ww_ref, a_ref, r_ref, cp_ref, v_ref, w_ref, h_ref,
     o_ref, sw_ref, d_ref, y_ref) = refs[nw:]
    lrw = _width_reduce(me_ref[0], r_refs)
    m = yw_ref.shape[0] // nsub
    for q in range(nsub):
        sl = slice(q * m, (q + 1) * m)
        sw_ref[sl] = yw_ref[sl] + vw_ref[sl] * lrw[q][0] + ww_ref[sl] * lrw[q][1]
    nt, ncl, nwl = a_ref.shape
    per_q = 128 // ncl
    for q in range(sw_ref.shape[1]):
        d_ref[q * per_q : (q + 1) * per_q] = sw_ref[:, q, :].T.reshape(per_q, ncl, nwl)
    n = nt // tsub
    subs = [q * n for q in range(tsub)]
    shape = a_ref.shape[1:]
    _solve_rhs(n, subs, _lead_ld, _lead_st, a_ref, r_ref, cp_ref, d_ref, y_ref, 4, shape)
    sums = [tuple(_summary_rows(_lead_ld, s0, n, y_ref, v_ref, w_ref)) for s0 in subs]
    lrs = [None] * tsub

    def emit(p, left, right):
        lrs[p] = (left, right)

    _reduce_blocks(tsub, lambda p: sums[p], emit, jnp.zeros(shape, F32))
    for q, s0 in enumerate(subs):
        sl = slice(s0, s0 + n)
        left, right = lrs[q]
        o_ref[sl] = h_ref[sl] + (y_ref[sl] + v_ref[sl] * left + w_ref[sl] * right)


def cast_solve(a, b, c, d, n):
    shp = jax.ShapeDtypeStruct(a.shape, F32)
    m = a.shape[0] // n
    return pl.pallas_call(
        functools.partial(_cast_kernel, n),
        out_shape=[shp, shp, shp, jax.ShapeDtypeStruct((m * 8, a.shape[1]), F32)],
        scratch_shapes=[pltpu.VMEM(a.shape, F32)],
    )(a, b, c, d)


def width_solve(yc, vc, wc, bk, a, fac, nsub):
    shp = jax.ShapeDtypeStruct(a.shape, F32)
    return pl.pallas_call(
        functools.partial(_width_kernel, nsub),
        out_shape=[shp, jax.ShapeDtypeStruct((nsub, 6) + a.shape[1:], F32)],
        scratch_shapes=[pltpu.VMEM(a.shape, F32)],
    )(yc, vc, wc, bk, a, *fac)


def thick_solve(me, got, yw, vw, ww, a, fac, h, nsub, tsub):
    vm = pl.BlockSpec(memory_space=pltpu.VMEM)
    return pl.pallas_call(
        functools.partial(_thick_kernel, nsub, tsub, len(got)),
        out_shape=jax.ShapeDtypeStruct(a.shape, F32),
        in_specs=[SMEM_SPEC] + [vm] * (len(got) + 9),
        scratch_shapes=[pltpu.VMEM(yw.shape, F32)] + [pltpu.VMEM(a.shape, F32)] * 2,
    )(me, *got, yw, vw, ww, a, *fac, h)


def _reduce_blocks(nb, blk, emit, zero):
    pp, qq = zero, zero
    saved = []
    for p in range(nb):
        y0, v0, w0, yn, vn, wn = blk(p)
        rd = 1.0 / (1.0 - v0 * qq)
        fa = (y0 + v0 * pp) * rd
        fb = w0 * rd
        saved.append((fa, fb, pp, qq))
        pp, qq = yn + vn * (pp + qq * fa), wn + vn * qq * fb
    f_next = zero
    for p in range(nb - 1, -1, -1):
        fa, fb, pp, qq = saved[p]
        f = fa + fb * f_next
        emit(p, pp + qq * f, f_next)
        f_next = f


def _cast_reduced_kernel(s_ref, lr_ref):
    nb = s_ref.shape[0]
    def blk(p):
        return tuple(s_ref[p, :, k, :] for k in range(6))

    def emit(p, left, right):
        lr_ref[p, :, 0:1, :] = left[:, None]
        lr_ref[p, :, 1:2, :] = right[:, None]

    _reduce_blocks(nb, blk, emit, jnp.zeros((s_ref.shape[1], s_ref.shape[3]), F32))


def _width_reduce(me, r_refs):
    nw = len(r_refs)
    nsub = r_refs[0].shape[0]
    out = [[None, None] for _ in range(nsub)]

    def blk(b):
        dev, q = divmod(b, nsub)
        kk = (me - dev + nw) % nw
        vals = []
        for k6 in range(6):
            val = r_refs[0][q, k6]
            for k in range(1, nw):
                val = jnp.where(kk == k, r_refs[k][q, k6], val)
            vals.append(val)
        return tuple(vals)

    def emit(b, left, right):
        dev, q = divmod(b, nsub)
        mine = me == dev
        for j, val in enumerate((left, right)):
            out[q][j] = val if out[q][j] is None else jnp.where(mine, val, out[q][j])

    _reduce_blocks(nw * nsub, blk, emit, jnp.zeros(r_refs[0].shape[2:], F32))
    return out


def _surface_kernel(scale, z_ref, sp_ref, o_ref):
    z = z_ref[...]
    acc = jnp.zeros(z.shape, F32)
    for q in range(sp_ref.shape[0]):
        acc = jnp.where(z == q, sp_ref[q], acc)
    o_ref[...] = acc * scale


def medium_parameters(x):
    t = jnp.tanh(x)
    hot = x - solidification_release * t
    cond = 1.5 - 0.5 * jnp.tanh(hot)
    slope = (1.0 - solidification_release) + solidification_release * t * t
    return hot, cond, slope


def shards(h, zones, spray_coef):
    nt, ncl, nwl = h.shape
    nc, nw = lax.axis_size("cast"), lax.axis_size("width")
    ci, wi = lax.axis_index("cast"), lax.axis_index("width")
    up_c = [(i, i + 1) for i in range(nc - 1)]
    up_w = [(i, i + 1) for i in range(nw - 1)]
    even = ci % 2 == 0
    first, last = h[:, 0, :], h[:, -1, :]
    in_chip = [(i, i ^ 1) for i in range(nc)]
    across = [(i, i + 1) for i in range(1, nc - 1, 2)] + [(i + 1, i) for i in range(1, nc - 1, 2)]
    got_a = lax.ppermute(jnp.where(even, last, first), "cast", in_chip)
    got_b = lax.ppermute(jnp.where(even, first, last), "cast", across)
    h_wl = lax.ppermute(h[:, :, -1], "width", up_w)
    h_wh = lax.ppermute(h[:, :, 0], "width", [(b, a) for a, b in up_w])

    cast_low = (ci > 0).astype(F32)
    cast_high = (ci < nc - 1).astype(F32)
    width_low = (wi > 0).astype(F32)
    width_high = (wi < nw - 1).astype(F32)
    flags = jnp.stack([cast_low, cast_high, width_low, width_high, even.astype(F32)])
    h2 = h.reshape(nt * ncl, nwl)
    outs = prep_solve(h2, got_a, got_b, zones.reshape(2 * ncl, nwl), spray_coef, flags, ncl)
    y, v, w, summ, a_c, r_c, cp_c = outs[:7]
    tlo, tmd, thi = (x.reshape(nt, ncl, nwl) for x in outs[7:])
    y, summ = edge_solve(h2, h_wl, h_wh, flags, a_c, r_c, cp_c, y, summ, ncl)
    recv = lax.all_to_all(summ.reshape(nc, nt // nc, 8, nwl), "cast", 0, 0, tiled=True)
    lr_shape = recv.shape[:2] + (2, nwl)
    lr = pl.pallas_call(_cast_reduced_kernel, out_shape=jax.ShapeDtypeStruct(lr_shape, F32))(recv)
    back = lax.all_to_all(lr, "cast", 0, 0, tiled=True).reshape(nt, 2, nwl)
    y, v, w = (x.reshape(nt, ncl, nwl) for x in (y, v, w))

    lines = nt * ncl
    nsub = 4

    def wl(x):
        return jnp.transpose(x, (2, 0, 1)).reshape(nwl, lines // 128, 128)

    wa, *wfac = wfactor(h2, h_wl, h_wh, flags, ncl, nsub)
    tfac = factor(tlo, tmd, thi, 4)
    yw, summ = width_solve(y, v, w, back, wa, wfac, nsub)
    got = [summ] + [
        lax.ppermute(summ, "width", [(i, (i + q) % nw) for i in range(nw)]) for q in range(1, nw)
    ]
    me = wi.astype(jnp.int32).reshape(1)
    return thick_solve(me, got, yw, wfac[2], wfac[3], tlo, tfac, h, nsub, 4)


def solution(mesh):
    spec = P(None, "cast", "width")
    return jax.shard_map(
        shards, mesh=mesh, in_specs=(spec, spec, P()), out_specs=spec, check_vma=False
    )
```

```python
import functools

import jax
import jax.numpy as jnp
from jax import lax
from jax.experimental import pallas as pl
from jax.experimental.pallas import tpu as pltpu
from jax.sharding import PartitionSpec as P


F32 = jnp.float32
solidification_release = 0.4
quench_medium_hotness = -2.0
SMEM_SPEC = pl.BlockSpec(memory_space=pltpu.SMEM)


def _summary_rows(ld, s0, n, y_ref, v_ref, w_ref):
    return [ld(y_ref, s0), ld(v_ref, s0), ld(w_ref, s0),
            ld(y_ref, s0 + n - 1), ld(v_ref, s0 + n - 1), ld(w_ref, s0 + n - 1)]


def _lead_ld(ref, i):
    return ref[i]


def _lead_st(ref, i, val):
    ref[i] = val


def _loop(n, body, carry, unroll):
    if unroll is True:
        for i in range(n):
            carry = body(i, carry)
        return carry
    return lax.fori_loop(0, n, body, carry, unroll=unroll)


def _factor(n, subs, ld, st, a_ref, b_ref, c_ref, r_ref, cp_ref, v_ref, w_ref, unroll, shape):
    zero = jnp.zeros(shape, F32)
    one = jnp.ones(shape, F32)

    def fwd(i, carries):
        out = []
        for s0, (cprev, vprev) in zip(subs, carries):
            j = s0 + i
            a = ld(a_ref, j)
            r = 1.0 / (ld(b_ref, j) - a * cprev)
            cn = ld(c_ref, j) * r
            vprev = -(a * vprev) * r
            st(r_ref, j, r)
            st(cp_ref, j, cn)
            st(v_ref, j, vprev)
            out.append((cn, vprev))
        return tuple(out)

    carries = _loop(n, fwd, tuple((zero, one) for _ in subs), unroll)
    for s0, (cl, _) in zip(subs, carries):
        st(w_ref, s0 + n - 1, -cl)

    def bwd(jj, carries):
        i = n - 2 - jj
        out = []
        for s0, (vn, wn) in zip(subs, carries):
            j = s0 + i
            cp = ld(cp_ref, j)
            vn = ld(v_ref, j) - cp * vn
            wn = -cp * wn
            st(v_ref, j, vn)
            st(w_ref, j, wn)
            out.append((vn, wn))
        return tuple(out)

    _loop(n - 1, bwd, tuple((vl, -cl) for cl, vl in carries), unroll)


def _solve_rhs(n, subs, ld, st, a_ref, r_ref, cp_ref, d_ref, y_ref, unroll, shape):
    zero = jnp.zeros(shape, F32)

    def fwd(i, carries):
        out = []
        for s0, dprev in zip(subs, carries):
            j = s0 + i
            dn = (ld(d_ref, j) - ld(a_ref, j) * dprev) * ld(r_ref, j)
            st(y_ref, j, dn)
            out.append(dn)
        return tuple(out)

    carries = _loop(n, fwd, tuple(zero for _ in subs), unroll)

    def bwd(jj, carries):
        i = n - 2 - jj
        out = []
        for s0, yn in zip(subs, carries):
            j = s0 + i
            yn = ld(y_ref, j) - ld(cp_ref, j) * yn
            st(y_ref, j, yn)
            out.append(yn)
        return tuple(out)

    _loop(n - 1, bwd, carries, unroll)


def _factor_kernel(nsub, a_ref, b_ref, c_ref, r_ref, cp_ref, v_ref, w_ref):
    n = a_ref.shape[0] // nsub
    subs = [q * n for q in range(nsub)]
    _factor(n, subs, _lead_ld, _lead_st, a_ref, b_ref, c_ref, r_ref, cp_ref, v_ref, w_ref, 4, a_ref.shape[1:])


def factor(a, b, c, nsub):
    shp = jax.ShapeDtypeStruct(a.shape, F32)
    return pl.pallas_call(functools.partial(_factor_kernel, nsub), out_shape=[shp] * 4)(a, b, c)


def _width_faces(T0, k0, s0, lane, wlo, whi, fl_ref):
    nwl = T0.shape[1]
    g_w = nwl * nwl / 4.0 * 0.5
    if wlo is None:
        wlo = (T0, k0, s0)
        whi = (T0, k0, s0)
        e_lo, e_hi = 0.0, 0.0
    else:
        e_lo, e_hi = fl_ref[2], fl_ref[3]
    Twm, kwm, swm = (jnp.where(lane == 0, b, pltpu.roll(f, 1, 1)) for f, b in zip((T0, k0, s0), wlo))
    Twp, kwp, swp = (
        jnp.where(lane == nwl - 1, b, pltpu.roll(f, nwl - 1, 1)) for f, b in zip((T0, k0, s0), whi)
    )
    gwl = g_w * (k0 + kwm) * jnp.where(lane == 0, e_lo, 1.0)
    gwh = g_w * (kwp + k0) * jnp.where(lane == nwl - 1, e_hi, 1.0)
    return Twm, swm, Twp, swp, gwl, gwh


def _prep_kernel(n, h_ref, hcl_ref, hch_ref, z_ref, sp_ref, fl_ref,
                 y_ref, v_ref, w_ref, sm_ref, a_ref, r_ref, cp_ref, ta_ref, tb_ref, tc_ref,
                 tp_ref, kp_ref, sp2_ref, b_ref, c_ref, d_ref):
    rows, nwl = h_ref.shape
    nt = rows // n
    hot, cond, slope = medium_parameters(h_ref[...])
    zpad = jnp.zeros((n, nwl), F32)
    for ref, val in ((tp_ref, hot), (kp_ref, cond), (sp2_ref, slope)):
        ref[0:n] = zpad
        ref[n : n + rows] = val
        ref[n + rows : 2 * n + rows] = zpad

    def row(ref, off):
        return ref[pl.ds(off, nt, stride=n), :]

    lane = lax.broadcasted_iota(jnp.int32, (nt, nwl), 1)
    tix = lax.broadcasted_iota(jnp.int32, (nt, nwl), 0)
    even = fl_ref[4] > 0.5
    got_a, got_b = hcl_ref[...], hch_ref[...]
    cast_lo = medium_parameters(jnp.where(even, got_b, got_a))
    cast_hi = medium_parameters(jnp.where(even, got_a, got_b))
    g_c = n * n * 4.0 * 0.5
    g_t = nt * nt / 4.0 * 0.5
    nz = sp_ref.shape[0]

    def surf_row(zr):
        acc = jnp.zeros(zr.shape, F32)
        for q in range(nz):
            acc = jnp.where(zr == q, sp_ref[q], acc)
        return acc * (nt * nt / 8.0)

    for c in range(n):
        T0, k0, s0 = (row(r, n + c) for r in (tp_ref, kp_ref, sp2_ref))
        if c == 0:
            Tm, km, sm = cast_lo
        else:
            Tm, km, sm = (row(r, n + c - 1) for r in (tp_ref, kp_ref, sp2_ref))
        if c == n - 1:
            Tq, kq, sq = cast_hi
        else:
            Tq, kq, sq = (row(r, n + c + 1) for r in (tp_ref, kp_ref, sp2_ref))
        Ttm, ktm, stm = (row(r, c) for r in (tp_ref, kp_ref, sp2_ref))
        Ttp, ktp, stp = (row(r, 2 * n + c) for r in (tp_ref, kp_ref, sp2_ref))
        Twm, _, Twp, _, gwl, gwh = _width_faces(T0, k0, s0, lane, None, None, fl_ref)
        gcl = g_c * (k0 + km)
        if c == 0:
            gcl = gcl * fl_ref[0]
        gch = g_c * (kq + k0)
        if c == n - 1:
            gch = gch * fl_ref[1]
        gtl = jnp.where(tix == 0, 0.0, g_t * (k0 + ktm))
        gth = jnp.where(tix == nt - 1, 0.0, g_t * (ktp + k0))
        s_lo = surf_row(z_ref[c : c + 1, :])
        s_hi = surf_row(z_ref[n + c : n + c + 1, :])
        rim = jnp.where(tix == 0, s_lo, jnp.where(tix == nt - 1, s_hi, 0.0))
        ex = rim * (quench_medium_hotness - T0)
        ex = ex + (gch * (Tq - T0) - gcl * (T0 - Tm))
        ex = ex + (gwh * (Twp - T0) - gwl * (T0 - Twm))
        ex = ex + (gth * (Ttp - T0) - gtl * (T0 - Ttm))
        sel = pl.ds(c, nt, stride=n)
        a_ref[sel, :] = -gcl * sm
        c_ref[sel, :] = -gch * sq
        b_ref[sel, :] = 1.0 + s0 * (gcl + gch)
        d_ref[sel, :] = ex
        ta_ref[sel, :] = -gtl * stm
        tc_ref[sel, :] = -gth * stp
        tb_ref[sel, :] = 1.0 + s0 * (gtl + gth + rim)

    def ld(ref, i):
        return ref[pl.ds(i, nt, stride=n), :]

    def st(ref, i, val):
        ref[pl.ds(i, nt, stride=n), :] = val

    shape = (nt, nwl)
    _factor(n, [0], ld, st, a_ref, b_ref, c_ref, r_ref, cp_ref, v_ref, w_ref, True, shape)
    _solve_rhs(n, [0], ld, st, a_ref, r_ref, cp_ref, d_ref, y_ref, True, shape)
    rws = _summary_rows(ld, 0, n, y_ref, v_ref, w_ref)
    rws += [jnp.zeros(shape, F32)] * (8 - len(rws))
    for k, val in enumerate(rws):
        sm_ref[pl.ds(k, nt, stride=8), :] = val


def prep_solve(h2, hcl, hch, z2, spray, flags, n):
    rows, nwl = h2.shape
    nt = rows // n
    shp = jax.ShapeDtypeStruct(h2.shape, F32)
    vm = pl.BlockSpec(memory_space=pltpu.VMEM)
    pad = pltpu.VMEM((rows + 2 * n, nwl), F32)
    return pl.pallas_call(
        functools.partial(_prep_kernel, n),
        out_shape=[shp] * 3 + [jax.ShapeDtypeStruct((nt * 8, nwl), F32)] + [shp] * 6,
        in_specs=[vm] * 4 + [SMEM_SPEC, SMEM_SPEC],
        scratch_shapes=[pad, pad, pad] + [pltpu.VMEM(h2.shape, F32)] * 3,
    )(h2, hcl, hch, z2, spray, flags)


def _edge_kernel(n, h_ref, hwl_ref, hwh_ref, fl_ref, a_ref, r_ref, cp_ref, y_ref, sm_ref,
                 yo_ref, smo_ref, d_ref, e_ref):
    rows, nwl = h_ref.shape
    nt = rows // n
    lane = lax.broadcasted_iota(jnp.int32, (nt, nwl), 1)
    for c in range(n):
        sel = pl.ds(c, nt, stride=n)
        T0, k0, s0 = medium_parameters(h_ref[sel, :])
        wlo = medium_parameters(hwl_ref[:, c : c + 1])
        whi = medium_parameters(hwh_ref[:, c : c + 1])
        Twm, _, Twp, _, gwl, gwh = _width_faces(T0, k0, s0, lane, wlo, whi, fl_ref)
        edge = jnp.where(lane == 0, -gwl * (T0 - Twm), jnp.where(lane == nwl - 1, gwh * (Twp - T0), 0.0))
        d_ref[sel, :] = edge

    def ld(ref, i):
        return ref[pl.ds(i, nt, stride=n), :]

    def st(ref, i, val):
        ref[pl.ds(i, nt, stride=n), :] = val

    _solve_rhs(n, [0], ld, st, a_ref, r_ref, cp_ref, d_ref, e_ref, True, (nt, nwl))
    yo_ref[...] = y_ref[...] + e_ref[...]
    smo_ref[...] = sm_ref[...]
    smo_ref[pl.ds(0, nt, stride=8), :] = sm_ref[pl.ds(0, nt, stride=8), :] + ld(e_ref, 0)
    smo_ref[pl.ds(3, nt, stride=8), :] = sm_ref[pl.ds(3, nt, stride=8), :] + ld(e_ref, n - 1)


def edge_solve(h2, hwl, hwh, flags, a, r, cp, y, sm, n):
    vm = pl.BlockSpec(memory_space=pltpu.VMEM)
    return pl.pallas_call(
        functools.partial(_edge_kernel, n),
        out_shape=[jax.ShapeDtypeStruct(y.shape, F32), jax.ShapeDtypeStruct(sm.shape, F32)],
        in_specs=[vm] * 3 + [SMEM_SPEC] + [vm] * 5,
        scratch_shapes=[pltpu.VMEM(y.shape, F32)] * 2,
    )(h2, hwl, hwh, flags, a, r, cp, y, sm)


def _wfactor_kernel(n, nsub, h_ref, hwl_ref, hwh_ref, fl_ref, a_ref, r_ref, cp_ref, v_ref, w_ref,
                    at_ref, bt_ref, ct_ref, b_ref, c_ref):
    rows, nwl = h_ref.shape
    nt = rows // n
    lane = lax.broadcasted_iota(jnp.int32, (nt, nwl), 1)
    for c in range(n):
        sel = pl.ds(c, nt, stride=n)
        T0, k0, s0 = medium_parameters(h_ref[sel, :])
        wlo = medium_parameters(hwl_ref[:, c : c + 1])
        whi = medium_parameters(hwh_ref[:, c : c + 1])
        _, swm, _, swp, gwl, gwh = _width_faces(T0, k0, s0, lane, wlo, whi, fl_ref)
        at_ref[sel, :] = -gwl * swm
        ct_ref[sel, :] = -gwh * swp
        bt_ref[sel, :] = 1.0 + s0 * (gwl + gwh)
    for src, dst in ((at_ref, a_ref), (bt_ref, b_ref), (ct_ref, c_ref)):
        for q in range(dst.shape[1]):
            dst[:, q, :] = src[q * 128 : (q + 1) * 128, :].T
    m = a_ref.shape[0] // nsub
    subs = [q * m for q in range(nsub)]
    _factor(m, subs, _lead_ld, _lead_st, a_ref, b_ref, c_ref, r_ref, cp_ref, v_ref, w_ref, 4, a_ref.shape[1:])


def wfactor(h2, hwl, hwh, flags, n, nsub):
    rows, nwl = h2.shape
    wshape = (nwl, rows // 128, 128)
    shp = jax.ShapeDtypeStruct(wshape, F32)
    vm = pl.BlockSpec(memory_space=pltpu.VMEM)
    return pl.pallas_call(
        functools.partial(_wfactor_kernel, n, nsub),
        out_shape=[shp] * 5,
        in_specs=[vm] * 3 + [SMEM_SPEC],
        scratch_shapes=[pltpu.VMEM(h2.shape, F32)] * 3 + [pltpu.VMEM(wshape, F32)] * 2,
    )(h2, hwl, hwh, flags)


def _width_kernel(nsub, yc_ref, vc_ref, wc_ref, bk_ref, a_ref, r_ref, cp_ref, v_ref, w_ref,
                  y_ref, sm_ref, d_ref):
    sc = yc_ref[...] + vc_ref[...] * bk_ref[:, 0:1, :] + wc_ref[...] * bk_ref[:, 1:2, :]
    nt, ncl, nwl = sc.shape
    sc = sc.reshape(nt * ncl, nwl)
    for q in range(d_ref.shape[1]):
        d_ref[:, q, :] = sc[q * 128 : (q + 1) * 128, :].T
    n = a_ref.shape[0] // nsub
    subs = [q * n for q in range(nsub)]
    _solve_rhs(n, subs, _lead_ld, _lead_st, a_ref, r_ref, cp_ref, d_ref, y_ref, 4, a_ref.shape[1:])
    for q, s0 in enumerate(subs):
        for k, val in enumerate(_summary_rows(_lead_ld, s0, n, y_ref, v_ref, w_ref)):
            sm_ref[q, k] = val


def _thick_kernel(nsub, tsub, nw, me_ref, *refs):
    r_refs = refs[:nw]
    (yw_ref, vw_ref, ww_ref, a_ref, r_ref, cp_ref, v_ref, w_ref, h_ref,
     o_ref, sw_ref, d_ref, y_ref) = refs[nw:]
    lrw = _width_reduce(me_ref[0], r_refs)
    m = yw_ref.shape[0] // nsub
    for q in range(nsub):
        sl = slice(q * m, (q + 1) * m)
        sw_ref[sl] = yw_ref[sl] + vw_ref[sl] * lrw[q][0] + ww_ref[sl] * lrw[q][1]
    nt, ncl, nwl = a_ref.shape
    per_q = 128 // ncl
    for q in range(sw_ref.shape[1]):
        d_ref[q * per_q : (q + 1) * per_q] = sw_ref[:, q, :].T.reshape(per_q, ncl, nwl)
    n = nt // tsub
    subs = [q * n for q in range(tsub)]
    shape = a_ref.shape[1:]
    _solve_rhs(n, subs, _lead_ld, _lead_st, a_ref, r_ref, cp_ref, d_ref, y_ref, 4, shape)
    sums = [tuple(_summary_rows(_lead_ld, s0, n, y_ref, v_ref, w_ref)) for s0 in subs]
    lrs = [None] * tsub

    def emit(p, left, right):
        lrs[p] = (left, right)

    _reduce_blocks(tsub, lambda p: sums[p], emit, jnp.zeros(shape, F32))
    for q, s0 in enumerate(subs):
        sl = slice(s0, s0 + n)
        left, right = lrs[q]
        o_ref[sl] = h_ref[sl] + (y_ref[sl] + v_ref[sl] * left + w_ref[sl] * right)


def width_solve(yc, vc, wc, bk, a, fac, nsub):
    shp = jax.ShapeDtypeStruct(a.shape, F32)
    return pl.pallas_call(
        functools.partial(_width_kernel, nsub),
        out_shape=[shp, jax.ShapeDtypeStruct((nsub, 6) + a.shape[1:], F32)],
        scratch_shapes=[pltpu.VMEM(a.shape, F32)],
    )(yc, vc, wc, bk, a, *fac)


def thick_solve(me, got, yw, vw, ww, a, fac, h, nsub, tsub):
    vm = pl.BlockSpec(memory_space=pltpu.VMEM)
    return pl.pallas_call(
        functools.partial(_thick_kernel, nsub, tsub, len(got)),
        out_shape=jax.ShapeDtypeStruct(a.shape, F32),
        in_specs=[SMEM_SPEC] + [vm] * (len(got) + 9),
        scratch_shapes=[pltpu.VMEM(yw.shape, F32)] + [pltpu.VMEM(a.shape, F32)] * 2,
    )(me, *got, yw, vw, ww, a, *fac, h)


def _reduce_blocks(nb, blk, emit, zero):
    pp, qq = zero, zero
    saved = []
    for p in range(nb):
        y0, v0, w0, yn, vn, wn = blk(p)
        rd = 1.0 / (1.0 - v0 * qq)
        fa = (y0 + v0 * pp) * rd
        fb = w0 * rd
        saved.append((fa, fb, pp, qq))
        pp, qq = yn + vn * (pp + qq * fa), wn + vn * qq * fb
    f_next = zero
    for p in range(nb - 1, -1, -1):
        fa, fb, pp, qq = saved[p]
        f = fa + fb * f_next
        emit(p, pp + qq * f, f_next)
        f_next = f


def _cast_reduced_kernel(s_ref, lr_ref):
    nb = s_ref.shape[0]

    def blk(p):
        return tuple(s_ref[p, :, k, :] for k in range(6))

    def emit(p, left, right):
        lr_ref[p, :, 0:1, :] = left[:, None]
        lr_ref[p, :, 1:2, :] = right[:, None]

    _reduce_blocks(nb, blk, emit, jnp.zeros((s_ref.shape[1], s_ref.shape[3]), F32))


def _width_reduce(me, r_refs):
    nw = len(r_refs)
    nsub = r_refs[0].shape[0]
    out = [[None, None] for _ in range(nsub)]

    def blk(b):
        dev, q = divmod(b, nsub)
        kk = (me - dev + nw) % nw
        vals = []
        for k6 in range(6):
            val = r_refs[0][q, k6]
            for k in range(1, nw):
                val = jnp.where(kk == k, r_refs[k][q, k6], val)
            vals.append(val)
        return tuple(vals)

    def emit(b, left, right):
        dev, q = divmod(b, nsub)
        mine = me == dev
        for j, val in enumerate((left, right)):
            out[q][j] = val if out[q][j] is None else jnp.where(mine, val, out[q][j])

    _reduce_blocks(nw * nsub, blk, emit, jnp.zeros(r_refs[0].shape[2:], F32))
    return out


def medium_parameters(x):
    t = jnp.tanh(x)
    hot = x - solidification_release * t
    cond = 1.5 - 0.5 * jnp.tanh(hot)
    slope = (1.0 - solidification_release) + solidification_release * t * t
    return hot, cond, slope


def _shards(h, zones, spray_coef):
    nt, ncl, nwl = h.shape
    nc, nw = lax.axis_size("cast"), lax.axis_size("width")
    ci, wi = lax.axis_index("cast"), lax.axis_index("width")
    up_w = [(i, i + 1) for i in range(nw - 1)]
    even = ci % 2 == 0
    first, last = h[:, 0, :], h[:, -1, :]
    in_chip = [(i, i ^ 1) for i in range(nc)]
    across = [(i, i + 1) for i in range(1, nc - 1, 2)] + [(i + 1, i) for i in range(1, nc - 1, 2)]
    got_a = lax.ppermute(jnp.where(even, last, first), "cast", in_chip)
    got_b = lax.ppermute(jnp.where(even, first, last), "cast", across)
    h_wl = lax.ppermute(h[:, :, -1], "width", up_w)
    h_wh = lax.ppermute(h[:, :, 0], "width", [(b, a) for a, b in up_w])

    cast_low = (ci > 0).astype(F32)
    cast_high = (ci < nc - 1).astype(F32)
    width_low = (wi > 0).astype(F32)
    width_high = (wi < nw - 1).astype(F32)
    flags = jnp.stack([cast_low, cast_high, width_low, width_high, even.astype(F32)])
    h2 = h.reshape(nt * ncl, nwl)
    outs = prep_solve(h2, got_a, got_b, zones.reshape(2 * ncl, nwl), spray_coef, flags, ncl)
    y, v, w, summ, a_c, r_c, cp_c = outs[:7]
    tlo, tmd, thi = (x.reshape(nt, ncl, nwl) for x in outs[7:])
    y, summ = edge_solve(h2, h_wl, h_wh, flags, a_c, r_c, cp_c, y, summ, ncl)
    recv = lax.all_to_all(summ.reshape(nc, nt // nc, 8, nwl), "cast", 0, 0, tiled=True)
    lr_shape = recv.shape[:2] + (2, nwl)
    lr = pl.pallas_call(_cast_reduced_kernel, out_shape=jax.ShapeDtypeStruct(lr_shape, F32))(recv)
    back = lax.all_to_all(lr, "cast", 0, 0, tiled=True).reshape(nt, 2, nwl)
    y, v, w = (x.reshape(nt, ncl, nwl) for x in (y, v, w))

    nsub = 4

    wa, *wfac = wfactor(h2, h_wl, h_wh, flags, ncl, nsub)
    tfac = factor(tlo, tmd, thi, 4)
    yw, summ = width_solve(y, v, w, back, wa, wfac, nsub)
    got = [summ] + [
        lax.ppermute(summ, "width", [(i, (i + q) % nw) for i in range(nw)]) for q in range(1, nw)
    ]
    me = wi.astype(jnp.int32).reshape(1)
    return thick_solve(me, got, yw, wfac[2], wfac[3], tlo, tfac, h, nsub, 4)


def solution(mesh):
    spec = P(None, "cast", "width")
    return jax.shard_map(
        _shards, mesh=mesh, in_specs=(spec, spec, P()), out_specs=spec, check_vma=False
    )
```

```python
import functools

import jax
import jax.numpy as jnp
from jax import lax
from jax.experimental import pallas as pl
from jax.experimental.pallas import tpu as pltpu
from jax.sharding import PartitionSpec as P

F32 = jnp.float32
solidification_release = 0.4
quench_medium_hotness = -2.0
SMEM_SPEC = pl.BlockSpec(memory_space=pltpu.SMEM)
PARAMS = pltpu.CompilerParams()


def _sweep(n, subs, ld, st, a_ref, b_ref, c_ref, d_ref, y_ref, v_ref, w_ref, cp_ref, unroll, shape):
    with_vw = v_ref is not None
    zero = jnp.zeros(shape, F32)
    one = jnp.ones(shape, F32)

    def fwd(i, carries):
        out = []
        for s0, (cprev, dprev, vprev) in zip(subs, carries):
            j = s0 + i
            a = ld(a_ref, j)
            r = 1.0 / (ld(b_ref, j) - a * cprev)
            cn = ld(c_ref, j) * r
            dn = (ld(d_ref, j) - a * dprev) * r
            st(cp_ref, j, cn)
            st(y_ref, j, dn)
            if with_vw:
                vprev = -(a * vprev) * r
                st(v_ref, j, vprev)
            out.append((cn, dn, vprev))
        return tuple(out)

    carries = tuple((zero, zero, one) for _ in subs)
    if unroll is True:
        for i in range(n):
            carries = fwd(i, carries)
    else:
        carries = lax.fori_loop(0, n, fwd, carries, unroll=unroll)
    if with_vw:
        for s0, (cl, _, _) in zip(subs, carries):
            st(w_ref, s0 + n - 1, -cl)

    def bwd(jj, carries):
        i = n - 2 - jj
        out = []
        for s0, (yn, vn, wn) in zip(subs, carries):
            j = s0 + i
            cp = ld(cp_ref, j)
            yn = ld(y_ref, j) - cp * yn
            st(y_ref, j, yn)
            if with_vw:
                vn = ld(v_ref, j) - cp * vn
                wn = -cp * wn
                st(v_ref, j, vn)
                st(w_ref, j, wn)
            out.append((yn, vn, wn))
        return tuple(out)

    carries = tuple((dl, vl, -cl) for cl, dl, vl in carries)
    if unroll is True:
        for jj in range(n - 1):
            carries = bwd(jj, carries)
    else:
        lax.fori_loop(0, n - 1, bwd, carries, unroll=unroll)


def _summary_rows(ld, s0, n, y_ref, v_ref, w_ref):
    return [ld(y_ref, s0), ld(v_ref, s0), ld(w_ref, s0),
            ld(y_ref, s0 + n - 1), ld(v_ref, s0 + n - 1), ld(w_ref, s0 + n - 1)]


def _cast_kernel(n, a_ref, b_ref, c_ref, d_ref, y_ref, v_ref, w_ref, sm_ref, cp_ref):
    m = a_ref.shape[0] // n

    def ld(ref, i):
        return ref[pl.ds(i, m, stride=n), :]

    def st(ref, i, val):
        ref[pl.ds(i, m, stride=n), :] = val

    shape = (m, a_ref.shape[1])
    _sweep(n, [0], ld, st, a_ref, b_ref, c_ref, d_ref, y_ref, v_ref, w_ref, cp_ref, True, shape)
    rows = _summary_rows(ld, 0, n, y_ref, v_ref, w_ref)
    rows += [jnp.zeros(shape, F32)] * (8 - len(rows))
    for k, val in enumerate(rows):
        sm_ref[pl.ds(k, m, stride=8), :] = val


def _lead_ld(ref, i):
    return ref[i]


def _lead_st(ref, i, val):
    ref[i] = val


def _loop(n, body, carry, unroll):
    if unroll is True:
        for i in range(n):
            carry = body(i, carry)
        return carry
    return lax.fori_loop(0, n, body, carry, unroll=unroll)


def _factor(n, subs, ld, st, a_ref, b_ref, c_ref, r_ref, cp_ref, v_ref, w_ref, unroll, shape):
    zero = jnp.zeros(shape, F32)
    one = jnp.ones(shape, F32)

    def fwd(i, carries):
        out = []
        for s0, (cprev, vprev) in zip(subs, carries):
            j = s0 + i
            a = ld(a_ref, j)
            r = 1.0 / (ld(b_ref, j) - a * cprev)
            cn = ld(c_ref, j) * r
            vprev = -(a * vprev) * r
            st(r_ref, j, r)
            st(cp_ref, j, cn)
            st(v_ref, j, vprev)
            out.append((cn, vprev))
        return tuple(out)

    carries = _loop(n, fwd, tuple((zero, one) for _ in subs), unroll)
    for s0, (cl, _) in zip(subs, carries):
        st(w_ref, s0 + n - 1, -cl)

    def bwd(jj, carries):
        i = n - 2 - jj
        out = []
        for s0, (vn, wn) in zip(subs, carries):
            j = s0 + i
            cp = ld(cp_ref, j)
            vn = ld(v_ref, j) - cp * vn
            wn = -cp * wn
            st(v_ref, j, vn)
            st(w_ref, j, wn)
            out.append((vn, wn))
        return tuple(out)

    _loop(n - 1, bwd, tuple((vl, -cl) for cl, vl in carries), unroll)


def _solve_rhs(n, subs, ld, st, a_ref, r_ref, cp_ref, d_ref, y_ref, unroll, shape):
    zero = jnp.zeros(shape, F32)

    def fwd(i, carries):
        out = []
        for s0, dprev in zip(subs, carries):
            j = s0 + i
            dn = (ld(d_ref, j) - ld(a_ref, j) * dprev) * ld(r_ref, j)
            st(y_ref, j, dn)
            out.append(dn)
        return tuple(out)

    carries = _loop(n, fwd, tuple(zero for _ in subs), unroll)

    def bwd(jj, carries):
        i = n - 2 - jj
        out = []
        for s0, yn in zip(subs, carries):
            j = s0 + i
            yn = ld(y_ref, j) - ld(cp_ref, j) * yn
            st(y_ref, j, yn)
            out.append(yn)
        return tuple(out)

    _loop(n - 1, bwd, carries, unroll)


def _factor_kernel(nsub, a_ref, b_ref, c_ref, r_ref, cp_ref, v_ref, w_ref):
    n = a_ref.shape[0] // nsub
    subs = [q * n for q in range(nsub)]
    _factor(n, subs, _lead_ld, _lead_st, a_ref, b_ref, c_ref, r_ref, cp_ref, v_ref, w_ref, 4, a_ref.shape[1:])


def factor(a, b, c, nsub):
    shp = jax.ShapeDtypeStruct(a.shape, F32)
    return pl.pallas_call(compiler_params=PARAMS, kernel=functools.partial(_factor_kernel, nsub), out_shape=[shp] * 4)(a, b, c)


def _width_faces(n, c, T0, k0, s0, lane, wlo, whi, fl_ref):
    nwl = T0.shape[1]
    g_w = nwl * nwl / 4.0 * 0.5
    if wlo is None:
        wlo = (T0, k0, s0)
        whi = (T0, k0, s0)
        e_lo, e_hi = 0.0, 0.0
    else:
        e_lo, e_hi = fl_ref[2], fl_ref[3]
    Twm, kwm, swm = (jnp.where(lane == 0, b, pltpu.roll(f, 1, 1)) for f, b in zip((T0, k0, s0), wlo))
    Twp, kwp, swp = (
        jnp.where(lane == nwl - 1, b, pltpu.roll(f, nwl - 1, 1)) for f, b in zip((T0, k0, s0), whi)
    )
    gwl = g_w * (k0 + kwm) * jnp.where(lane == 0, e_lo, 1.0)
    gwh = g_w * (kwp + k0) * jnp.where(lane == nwl - 1, e_hi, 1.0)
    return Twm, swm, Twp, swp, gwl, gwh


def _prep_kernel(n, h_ref, hcl_ref, hch_ref, z_ref, sp_ref, fl_ref,
                 y_ref, v_ref, w_ref, sm_ref, a_ref, r_ref, cp_ref, ta_ref, tb_ref, tc_ref,
                 tp_ref, kp_ref, sp2_ref, b_ref, c_ref, d_ref):
    rows, nwl = h_ref.shape
    nt = rows // n
    hot, cond, slope = medium_parameters(h_ref[...])
    zpad = jnp.zeros((n, nwl), F32)
    for ref, val in ((tp_ref, hot), (kp_ref, cond), (sp2_ref, slope)):
        ref[0:n] = zpad
        ref[n : n + rows] = val
        ref[n + rows : 2 * n + rows] = zpad

    def row(ref, off):
        return ref[pl.ds(off, nt, stride=n), :]

    lane = lax.broadcasted_iota(jnp.int32, (nt, nwl), 1)
    tix = lax.broadcasted_iota(jnp.int32, (nt, nwl), 0)
    even = fl_ref[4] > 0.5
    got_a, got_b = hcl_ref[...], hch_ref[...]
    cast_lo = medium_parameters(jnp.where(even, got_b, got_a))
    cast_hi = medium_parameters(jnp.where(even, got_a, got_b))
    g_c = n * n * 4.0 * 0.5
    g_t = nt * nt / 4.0 * 0.5
    nz = sp_ref.shape[0]

    def surf_row(zr):
        acc = jnp.zeros(zr.shape, F32)
        for q in range(nz):
            acc = jnp.where(zr == q, sp_ref[q], acc)
        return acc * (nt * nt / 8.0)

    for c in range(n):
        T0, k0, s0 = (row(r, n + c) for r in (tp_ref, kp_ref, sp2_ref))
        if c == 0:
            Tm, km, sm = cast_lo
        else:
            Tm, km, sm = (row(r, n + c - 1) for r in (tp_ref, kp_ref, sp2_ref))
        if c == n - 1:
            Tq, kq, sq = cast_hi
        else:
            Tq, kq, sq = (row(r, n + c + 1) for r in (tp_ref, kp_ref, sp2_ref))
        Ttm, ktm, stm = (row(r, c) for r in (tp_ref, kp_ref, sp2_ref))
        Ttp, ktp, stp = (row(r, 2 * n + c) for r in (tp_ref, kp_ref, sp2_ref))
        Twm, _, Twp, _, gwl, gwh = _width_faces(n, c, T0, k0, s0, lane, None, None, fl_ref)
        gcl = g_c * (k0 + km)
        if c == 0:
            gcl = gcl * fl_ref[0]
        gch = g_c * (kq + k0)
        if c == n - 1:
            gch = gch * fl_ref[1]
        gtl = jnp.where(tix == 0, 0.0, g_t * (k0 + ktm))
        gth = jnp.where(tix == nt - 1, 0.0, g_t * (ktp + k0))
        s_lo = surf_row(z_ref[c : c + 1, :])
        s_hi = surf_row(z_ref[n + c : n + c + 1, :])
        rim = jnp.where(tix == 0, s_lo, jnp.where(tix == nt - 1, s_hi, 0.0))
        ex = rim * (quench_medium_hotness - T0)
        ex = ex + (gch * (Tq - T0) - gcl * (T0 - Tm))
        ex = ex + (gwh * (Twp - T0) - gwl * (T0 - Twm))
        ex = ex + (gth * (Ttp - T0) - gtl * (T0 - Ttm))
        sel = pl.ds(c, nt, stride=n)
        a_ref[sel, :] = -gcl * sm
        c_ref[sel, :] = -gch * sq
        b_ref[sel, :] = 1.0 + s0 * (gcl + gch)
        d_ref[sel, :] = ex
        ta_ref[sel, :] = -gtl * stm
        tc_ref[sel, :] = -gth * stp
        tb_ref[sel, :] = 1.0 + s0 * (gtl + gth + rim)

    def ld(ref, i):
        return ref[pl.ds(i, nt, stride=n), :]

    def st(ref, i, val):
        ref[pl.ds(i, nt, stride=n), :] = val

    shape = (nt, nwl)
    _factor(n, [0], ld, st, a_ref, b_ref, c_ref, r_ref, cp_ref, v_ref, w_ref, True, shape)
    _solve_rhs(n, [0], ld, st, a_ref, r_ref, cp_ref, d_ref, y_ref, True, shape)
    rws = _summary_rows(ld, 0, n, y_ref, v_ref, w_ref)
    rws += [jnp.zeros(shape, F32)] * (8 - len(rws))
    for k, val in enumerate(rws):
        sm_ref[pl.ds(k, nt, stride=8), :] = val


def prep_solve(h2, hcl, hch, z2, spray, flags, n):
    rows, nwl = h2.shape
    nt = rows // n
    shp = jax.ShapeDtypeStruct(h2.shape, F32)
    vm = pl.BlockSpec(memory_space=pltpu.VMEM)
    pad = pltpu.VMEM((rows + 2 * n, nwl), F32)
    return pl.pallas_call(compiler_params=PARAMS, kernel=
        functools.partial(_prep_kernel, n),
        out_shape=[shp] * 3 + [jax.ShapeDtypeStruct((nt * 8, nwl), F32)] + [shp] * 6,
        in_specs=[vm] * 4 + [SMEM_SPEC, SMEM_SPEC],
        scratch_shapes=[pad, pad, pad] + [pltpu.VMEM(h2.shape, F32)] * 3,
    )(h2, hcl, hch, z2, spray, flags)


def _edge_kernel(n, h_ref, hwl_ref, hwh_ref, fl_ref, a_ref, r_ref, cp_ref, y_ref, sm_ref,
                 yo_ref, smo_ref, d_ref, e_ref):
    rows, nwl = h_ref.shape
    nt = rows // n
    lane = lax.broadcasted_iota(jnp.int32, (nt, nwl), 1)
    for c in range(n):
        sel = pl.ds(c, nt, stride=n)
        T0, k0, s0 = medium_parameters(h_ref[sel, :])
        wlo = medium_parameters(hwl_ref[:, c : c + 1])
        whi = medium_parameters(hwh_ref[:, c : c + 1])
        Twm, _, Twp, _, gwl, gwh = _width_faces(n, c, T0, k0, s0, lane, wlo, whi, fl_ref)
        edge = jnp.where(lane == 0, -gwl * (T0 - Twm), jnp.where(lane == nwl - 1, gwh * (Twp - T0), 0.0))
        d_ref[sel, :] = edge

    def ld(ref, i):
        return ref[pl.ds(i, nt, stride=n), :]

    def st(ref, i, val):
        ref[pl.ds(i, nt, stride=n), :] = val

    _solve_rhs(n, [0], ld, st, a_ref, r_ref, cp_ref, d_ref, e_ref, True, (nt, nwl))
    yo_ref[...] = y_ref[...] + e_ref[...]
    smo_ref[...] = sm_ref[...]
    smo_ref[pl.ds(0, nt, stride=8), :] = sm_ref[pl.ds(0, nt, stride=8), :] + ld(e_ref, 0)
    smo_ref[pl.ds(3, nt, stride=8), :] = sm_ref[pl.ds(3, nt, stride=8), :] + ld(e_ref, n - 1)


def edge_solve(h2, hwl, hwh, flags, a, r, cp, y, sm, n):
    vm = pl.BlockSpec(memory_space=pltpu.VMEM)
    return pl.pallas_call(compiler_params=PARAMS, kernel=
        functools.partial(_edge_kernel, n),
        out_shape=[jax.ShapeDtypeStruct(y.shape, F32), jax.ShapeDtypeStruct(sm.shape, F32)],
        in_specs=[vm] * 3 + [SMEM_SPEC] + [vm] * 5,
        scratch_shapes=[pltpu.VMEM(y.shape, F32)] * 2,
    )(h2, hwl, hwh, flags, a, r, cp, y, sm)


def _wfactor_kernel(n, nsub, h_ref, hwl_ref, hwh_ref, fl_ref, a_ref, r_ref, cp_ref, v_ref, w_ref,
                    at_ref, bt_ref, ct_ref, b_ref, c_ref):
    rows, nwl = h_ref.shape
    nt = rows // n
    lane = lax.broadcasted_iota(jnp.int32, (nt, nwl), 1)
    for c in range(n):
        sel = pl.ds(c, nt, stride=n)
        T0, k0, s0 = medium_parameters(h_ref[sel, :])
        wlo = medium_parameters(hwl_ref[:, c : c + 1])
        whi = medium_parameters(hwh_ref[:, c : c + 1])
        _, swm, _, swp, gwl, gwh = _width_faces(n, c, T0, k0, s0, lane, wlo, whi, fl_ref)
        at_ref[sel, :] = -gwl * swm
        ct_ref[sel, :] = -gwh * swp
        bt_ref[sel, :] = 1.0 + s0 * (gwl + gwh)
    for src, dst in ((at_ref, a_ref), (bt_ref, b_ref), (ct_ref, c_ref)):
        for q in range(dst.shape[1]):
            dst[:, q, :] = src[q * 128 : (q + 1) * 128, :].T
    m = a_ref.shape[0] // nsub
    subs = [q * m for q in range(nsub)]
    _factor(m, subs, _lead_ld, _lead_st, a_ref, b_ref, c_ref, r_ref, cp_ref, v_ref, w_ref, 4, a_ref.shape[1:])


def wfactor(h2, hwl, hwh, flags, n, nsub):
    rows, nwl = h2.shape
    wshape = (nwl, rows // 128, 128)
    shp = jax.ShapeDtypeStruct(wshape, F32)
    vm = pl.BlockSpec(memory_space=pltpu.VMEM)
    return pl.pallas_call(compiler_params=PARAMS, kernel=
        functools.partial(_wfactor_kernel, n, nsub),
        out_shape=[shp] * 5,
        in_specs=[vm] * 3 + [SMEM_SPEC],
        scratch_shapes=[pltpu.VMEM(h2.shape, F32)] * 3 + [pltpu.VMEM(wshape, F32)] * 2,
    )(h2, hwl, hwh, flags)


def _width_kernel(nsub, yc_ref, vc_ref, wc_ref, bk_ref, a_ref, r_ref, cp_ref, v_ref, w_ref,
                  y_ref, sm_ref, d_ref):
    sc = yc_ref[...] + vc_ref[...] * bk_ref[:, 0:1, :] + wc_ref[...] * bk_ref[:, 1:2, :]
    nt, ncl, nwl = sc.shape
    sc = sc.reshape(nt * ncl, nwl)
    for q in range(d_ref.shape[1]):
        d_ref[:, q, :] = sc[q * 128 : (q + 1) * 128, :].T
    n = a_ref.shape[0] // nsub
    subs = [q * n for q in range(nsub)]
    _solve_rhs(n, subs, _lead_ld, _lead_st, a_ref, r_ref, cp_ref, d_ref, y_ref, 4, a_ref.shape[1:])
    for q, s0 in enumerate(subs):
        for k, val in enumerate(_summary_rows(_lead_ld, s0, n, y_ref, v_ref, w_ref)):
            sm_ref[q, k] = val


def _thick_kernel(nsub, tsub, nw, me_ref, *refs):
    r_refs = refs[:nw]
    (yw_ref, vw_ref, ww_ref, a_ref, r_ref, cp_ref, v_ref, w_ref, h_ref,
     o_ref, sw_ref, d_ref, y_ref) = refs[nw:]
    lrw = _width_reduce(me_ref[0], r_refs)
    m = yw_ref.shape[0] // nsub
    for q in range(nsub):
        sl = slice(q * m, (q + 1) * m)
        sw_ref[sl] = yw_ref[sl] + vw_ref[sl] * lrw[q][0] + ww_ref[sl] * lrw[q][1]
    nt, ncl, nwl = a_ref.shape
    per_q = 128 // ncl
    for q in range(sw_ref.shape[1]):
        d_ref[q * per_q : (q + 1) * per_q] = sw_ref[:, q, :].T.reshape(per_q, ncl, nwl)
    n = nt // tsub
    subs = [q * n for q in range(tsub)]
    shape = a_ref.shape[1:]
    _solve_rhs(n, subs, _lead_ld, _lead_st, a_ref, r_ref, cp_ref, d_ref, y_ref, 4, shape)
    sums = [tuple(_summary_rows(_lead_ld, s0, n, y_ref, v_ref, w_ref)) for s0 in subs]
    lrs = [None] * tsub

    def emit(p, left, right):
        lrs[p] = (left, right)

    _reduce_blocks(tsub, lambda p: sums[p], emit, jnp.zeros(shape, F32))
    for q, s0 in enumerate(subs):
        sl = slice(s0, s0 + n)
        left, right = lrs[q]
        o_ref[sl] = h_ref[sl] + (y_ref[sl] + v_ref[sl] * left + w_ref[sl] * right)


def cast_solve(a, b, c, d, n):
    shp = jax.ShapeDtypeStruct(a.shape, F32)
    m = a.shape[0] // n
    return pl.pallas_call(compiler_params=PARAMS, kernel=
        functools.partial(_cast_kernel, n),
        out_shape=[shp, shp, shp, jax.ShapeDtypeStruct((m * 8, a.shape[1]), F32)],
        scratch_shapes=[pltpu.VMEM(a.shape, F32)],
    )(a, b, c, d)


def width_solve(yc, vc, wc, bk, a, fac, nsub):
    shp = jax.ShapeDtypeStruct(a.shape, F32)
    return pl.pallas_call(compiler_params=PARAMS, kernel=
        functools.partial(_width_kernel, nsub),
        out_shape=[shp, jax.ShapeDtypeStruct((nsub, 6) + a.shape[1:], F32)],
        scratch_shapes=[pltpu.VMEM(a.shape, F32)],
    )(yc, vc, wc, bk, a, *fac)


def thick_solve(me, got, yw, vw, ww, a, fac, h, nsub, tsub):
    vm = pl.BlockSpec(memory_space=pltpu.VMEM)
    return pl.pallas_call(compiler_params=PARAMS, kernel=
        functools.partial(_thick_kernel, nsub, tsub, len(got)),
        out_shape=jax.ShapeDtypeStruct(a.shape, F32),
        in_specs=[SMEM_SPEC] + [vm] * (len(got) + 9),
        scratch_shapes=[pltpu.VMEM(yw.shape, F32)] + [pltpu.VMEM(a.shape, F32)] * 2,
    )(me, *got, yw, vw, ww, a, *fac, h)


def _reduce_blocks(nb, blk, emit, zero):
    pp, qq = zero, zero
    saved = []
    for p in range(nb):
        y0, v0, w0, yn, vn, wn = blk(p)
        rd = 1.0 / (1.0 - v0 * qq)
        fa = (y0 + v0 * pp) * rd
        fb = w0 * rd
        saved.append((fa, fb, pp, qq))
        pp, qq = yn + vn * (pp + qq * fa), wn + vn * qq * fb
    f_next = zero
    for p in range(nb - 1, -1, -1):
        fa, fb, pp, qq = saved[p]
        f = fa + fb * f_next
        emit(p, pp + qq * f, f_next)
        f_next = f


def _cast_reduced_kernel(s_ref, lr_ref):
    nb = s_ref.shape[0]
    def blk(p):
        return tuple(s_ref[p, :, k, :] for k in range(6))

    def emit(p, left, right):
        lr_ref[p, :, 0:1, :] = left[:, None]
        lr_ref[p, :, 1:2, :] = right[:, None]

    _reduce_blocks(nb, blk, emit, jnp.zeros((s_ref.shape[1], s_ref.shape[3]), F32))


def _width_reduce(me, r_refs):
    nw = len(r_refs)
    nsub = r_refs[0].shape[0]
    out = [[None, None] for _ in range(nsub)]

    def blk(b):
        dev, q = divmod(b, nsub)
        kk = (me - dev + nw) % nw
        vals = []
        for k6 in range(6):
            val = r_refs[0][q, k6]
            for k in range(1, nw):
                val = jnp.where(kk == k, r_refs[k][q, k6], val)
            vals.append(val)
        return tuple(vals)

    def emit(b, left, right):
        dev, q = divmod(b, nsub)
        mine = me == dev
        for j, val in enumerate((left, right)):
            out[q][j] = val if out[q][j] is None else jnp.where(mine, val, out[q][j])

    _reduce_blocks(nw * nsub, blk, emit, jnp.zeros(r_refs[0].shape[2:], F32))
    return out


def _surface_kernel(scale, z_ref, sp_ref, o_ref):
    z = z_ref[...]
    acc = jnp.zeros(z.shape, F32)
    for q in range(sp_ref.shape[0]):
        acc = jnp.where(z == q, sp_ref[q], acc)
    o_ref[...] = acc * scale


def medium_parameters(x):
    t = jnp.tanh(x)
    hot = x - solidification_release * t
    cond = 1.5 - 0.5 * jnp.tanh(hot)
    slope = (1.0 - solidification_release) + solidification_release * t * t
    return hot, cond, slope


def shards(h, zones, spray_coef):
    nt, ncl, nwl = h.shape
    nc, nw = lax.axis_size("cast"), lax.axis_size("width")
    ci, wi = lax.axis_index("cast"), lax.axis_index("width")
    up_c = [(i, i + 1) for i in range(nc - 1)]
    up_w = [(i, i + 1) for i in range(nw - 1)]
    even = ci % 2 == 0
    first, last = h[:, 0, :], h[:, -1, :]
    in_chip = [(i, i ^ 1) for i in range(nc)]
    across = [(i, i + 1) for i in range(1, nc - 1, 2)] + [(i + 1, i) for i in range(1, nc - 1, 2)]
    got_a = lax.ppermute(jnp.where(even, last, first), "cast", in_chip)
    got_b = lax.ppermute(jnp.where(even, first, last), "cast", across)
    h_wl = lax.ppermute(h[:, :, -1], "width", up_w)
    h_wh = lax.ppermute(h[:, :, 0], "width", [(b, a) for a, b in up_w])

    cast_low = (ci > 0).astype(F32)
    cast_high = (ci < nc - 1).astype(F32)
    width_low = (wi > 0).astype(F32)
    width_high = (wi < nw - 1).astype(F32)
    flags = jnp.stack([cast_low, cast_high, width_low, width_high, even.astype(F32)])
    h2 = h.reshape(nt * ncl, nwl)
    outs = prep_solve(h2, got_a, got_b, zones.reshape(2 * ncl, nwl), spray_coef, flags, ncl)
    y, v, w, summ, a_c, r_c, cp_c = outs[:7]
    tlo, tmd, thi = (x.reshape(nt, ncl, nwl) for x in outs[7:])
    y, summ = edge_solve(h2, h_wl, h_wh, flags, a_c, r_c, cp_c, y, summ, ncl)
    recv = lax.all_to_all(summ.reshape(nc, nt // nc, 8, nwl), "cast", 0, 0, tiled=True)
    lr_shape = recv.shape[:2] + (2, nwl)
    lr = pl.pallas_call(compiler_params=PARAMS, kernel=_cast_reduced_kernel, out_shape=jax.ShapeDtypeStruct(lr_shape, F32))(recv)
    back = lax.all_to_all(lr, "cast", 0, 0, tiled=True).reshape(nt, 2, nwl)
    y, v, w = (x.reshape(nt, ncl, nwl) for x in (y, v, w))

    lines = nt * ncl
    nsub = 4

    def wl(x):
        return jnp.transpose(x, (2, 0, 1)).reshape(nwl, lines // 128, 128)

    wa, *wfac = wfactor(h2, h_wl, h_wh, flags, ncl, nsub)
    tfac = factor(tlo, tmd, thi, 4)
    yw, summ = width_solve(y, v, w, back, wa, wfac, nsub)
    got = [summ] + [
        lax.ppermute(summ, "width", [(i, (i + q) % nw) for i in range(nw)]) for q in range(1, nw)
    ]
    me = wi.astype(jnp.int32).reshape(1)
    return thick_solve(me, got, yw, wfac[2], wfac[3], tlo, tfac, h, nsub, 4)


def solution(mesh):
    spec = P(None, "cast", "width")
    return jax.shard_map(
        shards, mesh=mesh, in_specs=(spec, spec, P()), out_specs=spec, check_vma=False
    )
```

```python
import functools

import jax
import jax.numpy as jnp
from jax import lax
from jax.experimental import pallas as pl
from jax.experimental.pallas import tpu as pltpu
from jax.sharding import PartitionSpec as P

F32 = jnp.float32
solidification_release = 0.4
quench_medium_hotness = -2.0
SMEM_SPEC = pl.BlockSpec(memory_space=pltpu.SMEM)


def _sweep(n, subs, ld, st, a_ref, b_ref, c_ref, d_ref, y_ref, v_ref, w_ref, cp_ref, unroll, shape):
    with_vw = v_ref is not None
    zero = jnp.zeros(shape, F32)
    one = jnp.ones(shape, F32)

    def fwd(i, carries):
        out = []
        for s0, (cprev, dprev, vprev) in zip(subs, carries):
            j = s0 + i
            a = ld(a_ref, j)
            r = 1.0 / (ld(b_ref, j) - a * cprev)
            cn = ld(c_ref, j) * r
            dn = (ld(d_ref, j) - a * dprev) * r
            st(cp_ref, j, cn)
            st(y_ref, j, dn)
            if with_vw:
                vprev = -(a * vprev) * r
                st(v_ref, j, vprev)
            out.append((cn, dn, vprev))
        return tuple(out)

    carries = tuple((zero, zero, one) for _ in subs)
    if unroll is True:
        for i in range(n):
            carries = fwd(i, carries)
    else:
        carries = lax.fori_loop(0, n, fwd, carries, unroll=unroll)
    if with_vw:
        for s0, (cl, _, _) in zip(subs, carries):
            st(w_ref, s0 + n - 1, -cl)

    def bwd(jj, carries):
        i = n - 2 - jj
        out = []
        for s0, (yn, vn, wn) in zip(subs, carries):
            j = s0 + i
            cp = ld(cp_ref, j)
            yn = ld(y_ref, j) - cp * yn
            st(y_ref, j, yn)
            if with_vw:
                vn = ld(v_ref, j) - cp * vn
                wn = -cp * wn
                st(v_ref, j, vn)
                st(w_ref, j, wn)
            out.append((yn, vn, wn))
        return tuple(out)

    carries = tuple((dl, vl, -cl) for cl, dl, vl in carries)
    if unroll is True:
        for jj in range(n - 1):
            carries = bwd(jj, carries)
    else:
        lax.fori_loop(0, n - 1, bwd, carries, unroll=unroll)


def _summary_rows(ld, s0, n, y_ref, v_ref, w_ref):
    return [ld(y_ref, s0), ld(v_ref, s0), ld(w_ref, s0),
            ld(y_ref, s0 + n - 1), ld(v_ref, s0 + n - 1), ld(w_ref, s0 + n - 1)]


def _cast_kernel(n, a_ref, b_ref, c_ref, d_ref, y_ref, v_ref, w_ref, sm_ref, cp_ref):
    m = a_ref.shape[0] // n

    def ld(ref, i):
        return ref[pl.ds(i, m, stride=n), :]

    def st(ref, i, val):
        ref[pl.ds(i, m, stride=n), :] = val

    shape = (m, a_ref.shape[1])
    _sweep(n, [0], ld, st, a_ref, b_ref, c_ref, d_ref, y_ref, v_ref, w_ref, cp_ref, True, shape)
    rows = _summary_rows(ld, 0, n, y_ref, v_ref, w_ref)
    rows += [jnp.zeros(shape, F32)] * (8 - len(rows))
    for k, val in enumerate(rows):
        sm_ref[pl.ds(k, m, stride=8), :] = val


def _lead_ld(ref, i):
    return ref[i]


def _lead_st(ref, i, val):
    ref[i] = val


def _loop(n, body, carry, unroll):
    if unroll is True:
        for i in range(n):
            carry = body(i, carry)
        return carry
    return lax.fori_loop(0, n, body, carry, unroll=unroll)


def _factor(n, subs, ld, st, a_ref, b_ref, c_ref, r_ref, cp_ref, v_ref, w_ref, unroll, shape):
    zero = jnp.zeros(shape, F32)
    one = jnp.ones(shape, F32)

    def fwd(i, carries):
        out = []
        for s0, (cprev, vprev) in zip(subs, carries):
            j = s0 + i
            a = ld(a_ref, j)
            r = 1.0 / (ld(b_ref, j) - a * cprev)
            cn = ld(c_ref, j) * r
            vprev = -(a * vprev) * r
            st(r_ref, j, r)
            st(cp_ref, j, cn)
            st(v_ref, j, vprev)
            out.append((cn, vprev))
        return tuple(out)

    carries = _loop(n, fwd, tuple((zero, one) for _ in subs), unroll)
    for s0, (cl, _) in zip(subs, carries):
        st(w_ref, s0 + n - 1, -cl)

    def bwd(jj, carries):
        i = n - 2 - jj
        out = []
        for s0, (vn, wn) in zip(subs, carries):
            j = s0 + i
            cp = ld(cp_ref, j)
            vn = ld(v_ref, j) - cp * vn
            wn = -cp * wn
            st(v_ref, j, vn)
            st(w_ref, j, wn)
            out.append((vn, wn))
        return tuple(out)

    _loop(n - 1, bwd, tuple((vl, -cl) for cl, vl in carries), unroll)


def _solve_rhs(n, subs, ld, st, a_ref, r_ref, cp_ref, d_ref, y_ref, unroll, shape):
    zero = jnp.zeros(shape, F32)

    def fwd(i, carries):
        out = []
        for s0, dprev in zip(subs, carries):
            j = s0 + i
            dn = (ld(d_ref, j) - ld(a_ref, j) * dprev) * ld(r_ref, j)
            st(y_ref, j, dn)
            out.append(dn)
        return tuple(out)

    carries = _loop(n, fwd, tuple(zero for _ in subs), unroll)

    def bwd(jj, carries):
        i = n - 2 - jj
        out = []
        for s0, yn in zip(subs, carries):
            j = s0 + i
            yn = ld(y_ref, j) - ld(cp_ref, j) * yn
            st(y_ref, j, yn)
            out.append(yn)
        return tuple(out)

    _loop(n - 1, bwd, carries, unroll)


def _factor_kernel(nsub, a_ref, b_ref, c_ref, r_ref, cp_ref, v_ref, w_ref):
    n = a_ref.shape[0] // nsub
    subs = [q * n for q in range(nsub)]
    _factor(n, subs, _lead_ld, _lead_st, a_ref, b_ref, c_ref, r_ref, cp_ref, v_ref, w_ref, 4, a_ref.shape[1:])


def factor(a, b, c, nsub):
    shp = jax.ShapeDtypeStruct(a.shape, F32)
    return pl.pallas_call(functools.partial(_factor_kernel, nsub), out_shape=[shp] * 4)(a, b, c)


def _width_faces(n, c, T0, k0, s0, lane, wlo, whi, fl_ref):
    nwl = T0.shape[1]
    g_w = nwl * nwl / 4.0 * 0.5
    if wlo is None:
        wlo = (T0, k0, s0)
        whi = (T0, k0, s0)
        e_lo, e_hi = 0.0, 0.0
    else:
        e_lo, e_hi = fl_ref[2], fl_ref[3]
    Twm, kwm, swm = (jnp.where(lane == 0, b, pltpu.roll(f, 1, 1)) for f, b in zip((T0, k0, s0), wlo))
    Twp, kwp, swp = (
        jnp.where(lane == nwl - 1, b, pltpu.roll(f, nwl - 1, 1)) for f, b in zip((T0, k0, s0), whi)
    )
    gwl = g_w * (k0 + kwm) * jnp.where(lane == 0, e_lo, 1.0)
    gwh = g_w * (kwp + k0) * jnp.where(lane == nwl - 1, e_hi, 1.0)
    return Twm, swm, Twp, swp, gwl, gwh


def _prep_kernel(n, h_ref, hcl_ref, hch_ref, z_ref, sp_ref, fl_ref,
                 y_ref, v_ref, w_ref, sm_ref, a_ref, r_ref, cp_ref, ta_ref, tb_ref, tc_ref,
                 tp_ref, kp_ref, sp2_ref, b_ref, c_ref, d_ref):
    rows, nwl = h_ref.shape
    nt = rows // n
    hot, cond, slope = medium_parameters(h_ref[...])
    zpad = jnp.zeros((n, nwl), F32)
    for ref, val in ((tp_ref, hot), (kp_ref, cond), (sp2_ref, slope)):
        ref[0:n] = zpad
        ref[n : n + rows] = val
        ref[n + rows : 2 * n + rows] = zpad

    def row(ref, off):
        return ref[pl.ds(off, nt, stride=n), :]

    lane = lax.broadcasted_iota(jnp.int32, (nt, nwl), 1)
    tix = lax.broadcasted_iota(jnp.int32, (nt, nwl), 0)
    even = fl_ref[4] > 0.5
    got_a, got_b = hcl_ref[...], hch_ref[...]
    cast_lo = medium_parameters(jnp.where(even, got_b, got_a))
    cast_hi = medium_parameters(jnp.where(even, got_a, got_b))
    g_c = n * n * 4.0 * 0.5
    g_t = nt * nt / 4.0 * 0.5
    nz = sp_ref.shape[0]

    def surf_row(zr):
        acc = jnp.zeros(zr.shape, F32)
        for q in range(nz):
            acc = jnp.where(zr == q, sp_ref[q], acc)
        return acc * (nt * nt / 8.0)

    for c in range(n):
        T0, k0, s0 = (row(r, n + c) for r in (tp_ref, kp_ref, sp2_ref))
        if c == 0:
            Tm, km, sm = cast_lo
        else:
            Tm, km, sm = (row(r, n + c - 1) for r in (tp_ref, kp_ref, sp2_ref))
        if c == n - 1:
            Tq, kq, sq = cast_hi
        else:
            Tq, kq, sq = (row(r, n + c + 1) for r in (tp_ref, kp_ref, sp2_ref))
        Ttm, ktm, stm = (row(r, c) for r in (tp_ref, kp_ref, sp2_ref))
        Ttp, ktp, stp = (row(r, 2 * n + c) for r in (tp_ref, kp_ref, sp2_ref))
        Twm, _, Twp, _, gwl, gwh = _width_faces(n, c, T0, k0, s0, lane, None, None, fl_ref)
        gcl = g_c * (k0 + km)
        if c == 0:
            gcl = gcl * fl_ref[0]
        gch = g_c * (kq + k0)
        if c == n - 1:
            gch = gch * fl_ref[1]
        gtl = jnp.where(tix == 0, 0.0, g_t * (k0 + ktm))
        gth = jnp.where(tix == nt - 1, 0.0, g_t * (ktp + k0))
        s_lo = surf_row(z_ref[c : c + 1, :])
        s_hi = surf_row(z_ref[n + c : n + c + 1, :])
        rim = jnp.where(tix == 0, s_lo, jnp.where(tix == nt - 1, s_hi, 0.0))
        ex = rim * (quench_medium_hotness - T0)
        ex = ex + (gch * (Tq - T0) - gcl * (T0 - Tm))
        ex = ex + (gwh * (Twp - T0) - gwl * (T0 - Twm))
        ex = ex + (gth * (Ttp - T0) - gtl * (T0 - Ttm))
        sel = pl.ds(c, nt, stride=n)
        a_ref[sel, :] = -gcl * sm
        c_ref[sel, :] = -gch * sq
        b_ref[sel, :] = 1.0 + s0 * (gcl + gch)
        d_ref[sel, :] = ex
        ta_ref[sel, :] = -gtl * stm
        tc_ref[sel, :] = -gth * stp
        tb_ref[sel, :] = 1.0 + s0 * (gtl + gth + rim)

    def ld(ref, i):
        return ref[pl.ds(i, nt, stride=n), :]

    def st(ref, i, val):
        ref[pl.ds(i, nt, stride=n), :] = val

    shape = (nt, nwl)
    _factor(n, [0], ld, st, a_ref, b_ref, c_ref, r_ref, cp_ref, v_ref, w_ref, True, shape)
    _solve_rhs(n, [0], ld, st, a_ref, r_ref, cp_ref, d_ref, y_ref, True, shape)
    rws = _summary_rows(ld, 0, n, y_ref, v_ref, w_ref)
    rws += [jnp.zeros(shape, F32)] * (8 - len(rws))
    for k, val in enumerate(rws):
        sm_ref[pl.ds(k, nt, stride=8), :] = val


def prep_solve(h2, hcl, hch, z2, spray, flags, n):
    rows, nwl = h2.shape
    nt = rows // n
    shp = jax.ShapeDtypeStruct(h2.shape, F32)
    vm = pl.BlockSpec(memory_space=pltpu.VMEM)
    pad = pltpu.VMEM((rows + 2 * n, nwl), F32)
    return pl.pallas_call(
        functools.partial(_prep_kernel, n),
        out_shape=[shp] * 3 + [jax.ShapeDtypeStruct((nt * 8, nwl), F32)] + [shp] * 6,
        in_specs=[vm] * 4 + [SMEM_SPEC, SMEM_SPEC],
        scratch_shapes=[pad, pad, pad] + [pltpu.VMEM(h2.shape, F32)] * 3,
    )(h2, hcl, hch, z2, spray, flags)


def _edge_kernel(n, h_ref, hwl_ref, hwh_ref, fl_ref, a_ref, r_ref, cp_ref, y_ref, sm_ref,
                 yo_ref, smo_ref, d_ref, e_ref):
    rows, nwl = h_ref.shape
    nt = rows // n
    lane = lax.broadcasted_iota(jnp.int32, (nt, nwl), 1)
    for c in range(n):
        sel = pl.ds(c, nt, stride=n)
        T0, k0, s0 = medium_parameters(h_ref[sel, :])
        wlo = medium_parameters(hwl_ref[:, c : c + 1])
        whi = medium_parameters(hwh_ref[:, c : c + 1])
        Twm, _, Twp, _, gwl, gwh = _width_faces(n, c, T0, k0, s0, lane, wlo, whi, fl_ref)
        edge = jnp.where(lane == 0, -gwl * (T0 - Twm), jnp.where(lane == nwl - 1, gwh * (Twp - T0), 0.0))
        d_ref[sel, :] = edge

    def ld(ref, i):
        return ref[pl.ds(i, nt, stride=n), :]

    def st(ref, i, val):
        ref[pl.ds(i, nt, stride=n), :] = val

    _solve_rhs(n, [0], ld, st, a_ref, r_ref, cp_ref, d_ref, e_ref, True, (nt, nwl))
    yo_ref[...] = y_ref[...] + e_ref[...]
    smo_ref[...] = sm_ref[...]
    smo_ref[pl.ds(0, nt, stride=8), :] = sm_ref[pl.ds(0, nt, stride=8), :] + ld(e_ref, 0)
    smo_ref[pl.ds(3, nt, stride=8), :] = sm_ref[pl.ds(3, nt, stride=8), :] + ld(e_ref, n - 1)


def edge_solve(h2, hwl, hwh, flags, a, r, cp, y, sm, n):
    vm = pl.BlockSpec(memory_space=pltpu.VMEM)
    return pl.pallas_call(
        functools.partial(_edge_kernel, n),
        out_shape=[jax.ShapeDtypeStruct(y.shape, F32), jax.ShapeDtypeStruct(sm.shape, F32)],
        in_specs=[vm] * 3 + [SMEM_SPEC] + [vm] * 5,
        scratch_shapes=[pltpu.VMEM(y.shape, F32)] * 2,
    )(h2, hwl, hwh, flags, a, r, cp, y, sm)


def _wfactor_kernel(n, nsub, h_ref, hwl_ref, hwh_ref, fl_ref, a_ref, r_ref, cp_ref, v_ref, w_ref,
                    at_ref, bt_ref, ct_ref, b_ref, c_ref):
    rows, nwl = h_ref.shape
    nt = rows // n
    lane = lax.broadcasted_iota(jnp.int32, (nt, nwl), 1)
    for c in range(n):
        sel = pl.ds(c, nt, stride=n)
        T0, k0, s0 = medium_parameters(h_ref[sel, :])
        wlo = medium_parameters(hwl_ref[:, c : c + 1])
        whi = medium_parameters(hwh_ref[:, c : c + 1])
        _, swm, _, swp, gwl, gwh = _width_faces(n, c, T0, k0, s0, lane, wlo, whi, fl_ref)
        at_ref[sel, :] = -gwl * swm
        ct_ref[sel, :] = -gwh * swp
        bt_ref[sel, :] = 1.0 + s0 * (gwl + gwh)
    for src, dst in ((at_ref, a_ref), (bt_ref, b_ref), (ct_ref, c_ref)):
        for q in range(dst.shape[1]):
            dst[:, q, :] = src[q * 128 : (q + 1) * 128, :].T
    m = a_ref.shape[0] // nsub
    subs = [q * m for q in range(nsub)]
    _factor(m, subs, _lead_ld, _lead_st, a_ref, b_ref, c_ref, r_ref, cp_ref, v_ref, w_ref, 4, a_ref.shape[1:])


def wfactor(h2, hwl, hwh, flags, n, nsub):
    rows, nwl = h2.shape
    wshape = (nwl, rows // 128, 128)
    shp = jax.ShapeDtypeStruct(wshape, F32)
    vm = pl.BlockSpec(memory_space=pltpu.VMEM)
    return pl.pallas_call(
        functools.partial(_wfactor_kernel, n, nsub),
        out_shape=[shp] * 5,
        in_specs=[vm] * 3 + [SMEM_SPEC],
        scratch_shapes=[pltpu.VMEM(h2.shape, F32)] * 3 + [pltpu.VMEM(wshape, F32)] * 2,
    )(h2, hwl, hwh, flags)


def _width_kernel(nsub, yc_ref, vc_ref, wc_ref, bk_ref, a_ref, r_ref, cp_ref, v_ref, w_ref,
                  y_ref, sm_ref, d_ref):
    sc = yc_ref[...] + vc_ref[...] * bk_ref[:, 0:1, :] + wc_ref[...] * bk_ref[:, 1:2, :]
    nt, ncl, nwl = sc.shape
    sc = sc.reshape(nt * ncl, nwl)
    for q in range(d_ref.shape[1]):
        d_ref[:, q, :] = sc[q * 128 : (q + 1) * 128, :].T
    n = a_ref.shape[0] // nsub
    subs = [q * n for q in range(nsub)]
    _solve_rhs(n, subs, _lead_ld, _lead_st, a_ref, r_ref, cp_ref, d_ref, y_ref, 4, a_ref.shape[1:])
    for q, s0 in enumerate(subs):
        for k, val in enumerate(_summary_rows(_lead_ld, s0, n, y_ref, v_ref, w_ref)):
            sm_ref[q, k] = val


def _thick_kernel(nsub, tsub, nw, me_ref, *refs):
    r_refs = refs[:nw]
    (yw_ref, vw_ref, ww_ref, a_ref, r_ref, cp_ref, v_ref, w_ref, h_ref,
     o_ref, sw_ref, d_ref, y_ref) = refs[nw:]
    lrw = _width_reduce(me_ref[0], r_refs)
    m = yw_ref.shape[0] // nsub
    for q in range(nsub):
        sl = slice(q * m, (q + 1) * m)
        sw_ref[sl] = yw_ref[sl] + vw_ref[sl] * lrw[q][0] + ww_ref[sl] * lrw[q][1]
    nt, ncl, nwl = a_ref.shape
    per_q = 128 // ncl
    for q in range(sw_ref.shape[1]):
        d_ref[q * per_q : (q + 1) * per_q] = sw_ref[:, q, :].T.reshape(per_q, ncl, nwl)
    n = nt // tsub
    subs = [q * n for q in range(tsub)]
    shape = a_ref.shape[1:]
    _solve_rhs(n, subs, _lead_ld, _lead_st, a_ref, r_ref, cp_ref, d_ref, y_ref, 4, shape)
    sums = [tuple(_summary_rows(_lead_ld, s0, n, y_ref, v_ref, w_ref)) for s0 in subs]
    lrs = [None] * tsub

    def emit(p, left, right):
        lrs[p] = (left, right)

    _reduce_blocks(tsub, lambda p: sums[p], emit, jnp.zeros(shape, F32))
    for q, s0 in enumerate(subs):
        sl = slice(s0, s0 + n)
        left, right = lrs[q]
        o_ref[sl] = h_ref[sl] + (y_ref[sl] + v_ref[sl] * left + w_ref[sl] * right)


def cast_solve(a, b, c, d, n):
    shp = jax.ShapeDtypeStruct(a.shape, F32)
    m = a.shape[0] // n
    return pl.pallas_call(
        functools.partial(_cast_kernel, n),
        out_shape=[shp, shp, shp, jax.ShapeDtypeStruct((m * 8, a.shape[1]), F32)],
        scratch_shapes=[pltpu.VMEM(a.shape, F32)],
    )(a, b, c, d)


def width_solve(yc, vc, wc, bk, a, fac, nsub):
    shp = jax.ShapeDtypeStruct(a.shape, F32)
    return pl.pallas_call(
        functools.partial(_width_kernel, nsub),
        out_shape=[shp, jax.ShapeDtypeStruct((nsub, 6) + a.shape[1:], F32)],
        scratch_shapes=[pltpu.VMEM(a.shape, F32)],
    )(yc, vc, wc, bk, a, *fac)


def thick_solve(me, got, yw, vw, ww, a, fac, h, nsub, tsub):
    vm = pl.BlockSpec(memory_space=pltpu.VMEM)
    return pl.pallas_call(
        functools.partial(_thick_kernel, nsub, tsub, len(got)),
        out_shape=jax.ShapeDtypeStruct(a.shape, F32),
        in_specs=[SMEM_SPEC] + [vm] * (len(got) + 9),
        scratch_shapes=[pltpu.VMEM(yw.shape, F32)] + [pltpu.VMEM(a.shape, F32)] * 2,
    )(me, *got, yw, vw, ww, a, *fac, h)


def _reduce_blocks(nb, blk, emit, zero):
    pp, qq = zero, zero
    saved = []
    for p in range(nb):
        y0, v0, w0, yn, vn, wn = blk(p)
        rd = 1.0 / (1.0 - v0 * qq)
        fa = (y0 + v0 * pp) * rd
        fb = w0 * rd
        saved.append((fa, fb, pp, qq))
        pp, qq = yn + vn * (pp + qq * fa), wn + vn * qq * fb
    f_next = zero
    for p in range(nb - 1, -1, -1):
        fa, fb, pp, qq = saved[p]
        f = fa + fb * f_next
        emit(p, pp + qq * f, f_next)
        f_next = f


def _merge(A, B):
    yA0, vA0, wA0, yAn, vAn, wAn = A
    yB0, vB0, wB0, yBn, vBn, wBn = B
    rd = 1.0 / (1.0 - wAn * vB0)
    ey = (yAn + wAn * yB0) * rd
    ev = vAn * rd
    ew = wAn * wB0 * rd
    fy = yB0 + vB0 * ey
    fv = vB0 * ev
    fw = wB0 + vB0 * ew
    return (yA0 + wA0 * fy, vA0 + wA0 * fv, wA0 * fw, yBn + vBn * ey, vBn * ev, wBn + vBn * ew)


def _chain(nb, blk, emit, left, right):
    pp, qq = left, jnp.zeros_like(left)
    saved = []
    for p in range(nb):
        y0, v0, w0, yn, vn, wn = blk(p)
        rd = 1.0 / (1.0 - v0 * qq)
        fa = (y0 + v0 * pp) * rd
        fb = w0 * rd
        saved.append((fa, fb, pp, qq))
        pp, qq = yn + vn * (pp + qq * fa), wn + vn * qq * fb
    f_next = right
    for p in range(nb - 1, -1, -1):
        fa, fb, pp, qq = saved[p]
        f = fa + fb * f_next
        emit(p, pp + qq * f, f_next)
        f_next = f


def _cast_reduced_kernel(s_ref, lr_ref):
    nb, g, _, nl = s_ref.shape
    ng = 8
    if g != 1 or nb % ng:
        def blk(p):
            return tuple(s_ref[p, :, k, :] for k in range(6))

        def emit(p, left, right):
            lr_ref[p, :, 0:1, :] = left[:, None]
            lr_ref[p, :, 1:2, :] = right[:, None]

        _reduce_blocks(nb, blk, emit, jnp.zeros((g, nl), F32))
        return
    m = nb // ng

    def member(j):
        return tuple(
            jnp.concatenate([s_ref[G * m + j, 0, k : k + 1, :] for G in range(ng)], 0)
            for k in range(6)
        )

    members = [member(j) for j in range(m)]
    acc = members[0]
    for j in range(1, m):
        acc = _merge(acc, members[j])
    outer = [None] * ng

    def emit_g(G, left, right):
        outer[G] = (left, right)

    zero1 = jnp.zeros((1, nl), F32)
    _chain(ng, lambda G: tuple(x[G : G + 1] for x in acc), emit_g, zero1, zero1)
    left_g = jnp.concatenate([outer[G][0] for G in range(ng)], 0)
    right_g = jnp.concatenate([outer[G][1] for G in range(ng)], 0)

    def emit(j, left, right):
        for G in range(ng):
            lr_ref[G * m + j, 0, 0:1, :] = left[G : G + 1]
            lr_ref[G * m + j, 0, 1:2, :] = right[G : G + 1]

    _chain(m, lambda j: members[j], emit, left_g, right_g)


def _width_reduce(me, r_refs):
    nw = len(r_refs)
    nsub = r_refs[0].shape[0]
    out = [[None, None] for _ in range(nsub)]

    def blk(b):
        dev, q = divmod(b, nsub)
        kk = (me - dev + nw) % nw
        vals = []
        for k6 in range(6):
            val = r_refs[0][q, k6]
            for k in range(1, nw):
                val = jnp.where(kk == k, r_refs[k][q, k6], val)
            vals.append(val)
        return tuple(vals)

    def emit(b, left, right):
        dev, q = divmod(b, nsub)
        mine = me == dev
        for j, val in enumerate((left, right)):
            out[q][j] = val if out[q][j] is None else jnp.where(mine, val, out[q][j])

    _reduce_blocks(nw * nsub, blk, emit, jnp.zeros(r_refs[0].shape[2:], F32))
    return out


def _surface_kernel(scale, z_ref, sp_ref, o_ref):
    z = z_ref[...]
    acc = jnp.zeros(z.shape, F32)
    for q in range(sp_ref.shape[0]):
        acc = jnp.where(z == q, sp_ref[q], acc)
    o_ref[...] = acc * scale


def medium_parameters(x):
    t = jnp.tanh(x)
    hot = x - solidification_release * t
    cond = 1.5 - 0.5 * jnp.tanh(hot)
    slope = (1.0 - solidification_release) + solidification_release * t * t
    return hot, cond, slope


def shards(h, zones, spray_coef):
    nt, ncl, nwl = h.shape
    nc, nw = lax.axis_size("cast"), lax.axis_size("width")
    ci, wi = lax.axis_index("cast"), lax.axis_index("width")
    up_c = [(i, i + 1) for i in range(nc - 1)]
    up_w = [(i, i + 1) for i in range(nw - 1)]
    even = ci % 2 == 0
    first, last = h[:, 0, :], h[:, -1, :]
    in_chip = [(i, i ^ 1) for i in range(nc)]
    across = [(i, i + 1) for i in range(1, nc - 1, 2)] + [(i + 1, i) for i in range(1, nc - 1, 2)]
    got_a = lax.ppermute(jnp.where(even, last, first), "cast", in_chip)
    got_b = lax.ppermute(jnp.where(even, first, last), "cast", across)
    h_wl = lax.ppermute(h[:, :, -1], "width", up_w)
    h_wh = lax.ppermute(h[:, :, 0], "width", [(b, a) for a, b in up_w])

    cast_low = (ci > 0).astype(F32)
    cast_high = (ci < nc - 1).astype(F32)
    width_low = (wi > 0).astype(F32)
    width_high = (wi < nw - 1).astype(F32)
    flags = jnp.stack([cast_low, cast_high, width_low, width_high, even.astype(F32)])
    h2 = h.reshape(nt * ncl, nwl)
    outs = prep_solve(h2, got_a, got_b, zones.reshape(2 * ncl, nwl), spray_coef, flags, ncl)
    y, v, w, summ, a_c, r_c, cp_c = outs[:7]
    tlo, tmd, thi = (x.reshape(nt, ncl, nwl) for x in outs[7:])
    y, summ = edge_solve(h2, h_wl, h_wh, flags, a_c, r_c, cp_c, y, summ, ncl)
    recv = lax.all_to_all(summ.reshape(nc, nt // nc, 8, nwl), "cast", 0, 0, tiled=True)
    lr_shape = recv.shape[:2] + (2, nwl)
    lr = pl.pallas_call(_cast_reduced_kernel, out_shape=jax.ShapeDtypeStruct(lr_shape, F32))(recv)
    back = lax.all_to_all(lr, "cast", 0, 0, tiled=True).reshape(nt, 2, nwl)
    y, v, w = (x.reshape(nt, ncl, nwl) for x in (y, v, w))

    lines = nt * ncl
    nsub = 4

    def wl(x):
        return jnp.transpose(x, (2, 0, 1)).reshape(nwl, lines // 128, 128)

    wa, *wfac = wfactor(h2, h_wl, h_wh, flags, ncl, nsub)
    tfac = factor(tlo, tmd, thi, 4)
    yw, summ = width_solve(y, v, w, back, wa, wfac, nsub)
    got = [summ] + [
        lax.ppermute(summ, "width", [(i, (i + q) % nw) for i in range(nw)]) for q in range(1, nw)
    ]
    me = wi.astype(jnp.int32).reshape(1)
    return thick_solve(me, got, yw, wfac[2], wfac[3], tlo, tfac, h, nsub, 4)


def solution(mesh):
    spec = P(None, "cast", "width")
    return jax.shard_map(
        shards, mesh=mesh, in_specs=(spec, spec, P()), out_specs=spec, check_vma=False
    )
```

```python
import functools

import jax
import jax.numpy as jnp
from jax import lax
from jax.experimental import pallas as pl
from jax.experimental.pallas import tpu as pltpu
from jax.sharding import PartitionSpec as P

F32 = jnp.float32
solidification_release = 0.4
quench_medium_hotness = -2.0
SMEM_SPEC = pl.BlockSpec(memory_space=pltpu.SMEM)


def _sweep(n, subs, ld, st, a_ref, b_ref, c_ref, d_ref, y_ref, v_ref, w_ref, cp_ref, unroll, shape):
    with_vw = v_ref is not None
    zero = jnp.zeros(shape, F32)
    one = jnp.ones(shape, F32)

    def fwd(i, carries):
        out = []
        for s0, (cprev, dprev, vprev) in zip(subs, carries):
            j = s0 + i
            a = ld(a_ref, j)
            r = 1.0 / (ld(b_ref, j) - a * cprev)
            cn = ld(c_ref, j) * r
            dn = (ld(d_ref, j) - a * dprev) * r
            st(cp_ref, j, cn)
            st(y_ref, j, dn)
            if with_vw:
                vprev = -(a * vprev) * r
                st(v_ref, j, vprev)
            out.append((cn, dn, vprev))
        return tuple(out)

    carries = tuple((zero, zero, one) for _ in subs)
    if unroll is True:
        for i in range(n):
            carries = fwd(i, carries)
    else:
        carries = lax.fori_loop(0, n, fwd, carries, unroll=unroll)
    if with_vw:
        for s0, (cl, _, _) in zip(subs, carries):
            st(w_ref, s0 + n - 1, -cl)

    def bwd(jj, carries):
        i = n - 2 - jj
        out = []
        for s0, (yn, vn, wn) in zip(subs, carries):
            j = s0 + i
            cp = ld(cp_ref, j)
            yn = ld(y_ref, j) - cp * yn
            st(y_ref, j, yn)
            if with_vw:
                vn = ld(v_ref, j) - cp * vn
                wn = -cp * wn
                st(v_ref, j, vn)
                st(w_ref, j, wn)
            out.append((yn, vn, wn))
        return tuple(out)

    carries = tuple((dl, vl, -cl) for cl, dl, vl in carries)
    if unroll is True:
        for jj in range(n - 1):
            carries = bwd(jj, carries)
    else:
        lax.fori_loop(0, n - 1, bwd, carries, unroll=unroll)


def _summary_rows(ld, s0, n, y_ref, v_ref, w_ref):
    return [ld(y_ref, s0), ld(v_ref, s0), ld(w_ref, s0),
            ld(y_ref, s0 + n - 1), ld(v_ref, s0 + n - 1), ld(w_ref, s0 + n - 1)]


def _cast_kernel(n, a_ref, b_ref, c_ref, d_ref, y_ref, v_ref, w_ref, sm_ref, cp_ref):
    m = a_ref.shape[0] // n

    def ld(ref, i):
        return ref[pl.ds(i, m, stride=n), :]

    def st(ref, i, val):
        ref[pl.ds(i, m, stride=n), :] = val

    shape = (m, a_ref.shape[1])
    _sweep(n, [0], ld, st, a_ref, b_ref, c_ref, d_ref, y_ref, v_ref, w_ref, cp_ref, True, shape)
    rows = _summary_rows(ld, 0, n, y_ref, v_ref, w_ref)
    rows += [jnp.zeros(shape, F32)] * (8 - len(rows))
    for k, val in enumerate(rows):
        sm_ref[pl.ds(k, m, stride=8), :] = val


def _lead_ld(ref, i):
    return ref[i]


def _lead_st(ref, i, val):
    ref[i] = val


def _loop(n, body, carry, unroll):
    if unroll is True:
        for i in range(n):
            carry = body(i, carry)
        return carry
    return lax.fori_loop(0, n, body, carry, unroll=unroll)


def _factor(n, subs, ld, st, a_ref, b_ref, c_ref, r_ref, cp_ref, v_ref, w_ref, unroll, shape):
    zero = jnp.zeros(shape, F32)
    one = jnp.ones(shape, F32)

    def fwd(i, carries):
        out = []
        for s0, (cprev, vprev) in zip(subs, carries):
            j = s0 + i
            a = ld(a_ref, j)
            r = 1.0 / (ld(b_ref, j) - a * cprev)
            cn = ld(c_ref, j) * r
            vprev = -(a * vprev) * r
            st(r_ref, j, r)
            st(cp_ref, j, cn)
            st(v_ref, j, vprev)
            out.append((cn, vprev))
        return tuple(out)

    carries = _loop(n, fwd, tuple((zero, one) for _ in subs), unroll)
    for s0, (cl, _) in zip(subs, carries):
        st(w_ref, s0 + n - 1, -cl)

    def bwd(jj, carries):
        i = n - 2 - jj
        out = []
        for s0, (vn, wn) in zip(subs, carries):
            j = s0 + i
            cp = ld(cp_ref, j)
            vn = ld(v_ref, j) - cp * vn
            wn = -cp * wn
            st(v_ref, j, vn)
            st(w_ref, j, wn)
            out.append((vn, wn))
        return tuple(out)

    _loop(n - 1, bwd, tuple((vl, -cl) for cl, vl in carries), unroll)


def _solve_rhs(n, subs, ld, st, a_ref, r_ref, cp_ref, d_ref, y_ref, unroll, shape):
    zero = jnp.zeros(shape, F32)

    def fwd(i, carries):
        out = []
        for s0, dprev in zip(subs, carries):
            j = s0 + i
            dn = (ld(d_ref, j) - ld(a_ref, j) * dprev) * ld(r_ref, j)
            st(y_ref, j, dn)
            out.append(dn)
        return tuple(out)

    carries = _loop(n, fwd, tuple(zero for _ in subs), unroll)

    def bwd(jj, carries):
        i = n - 2 - jj
        out = []
        for s0, yn in zip(subs, carries):
            j = s0 + i
            yn = ld(y_ref, j) - ld(cp_ref, j) * yn
            st(y_ref, j, yn)
            out.append(yn)
        return tuple(out)

    _loop(n - 1, bwd, carries, unroll)


def _factor_kernel(nsub, a_ref, b_ref, c_ref, r_ref, cp_ref, v_ref, w_ref):
    n = a_ref.shape[0] // nsub
    subs = [q * n for q in range(nsub)]
    _factor(n, subs, _lead_ld, _lead_st, a_ref, b_ref, c_ref, r_ref, cp_ref, v_ref, w_ref, 4, a_ref.shape[1:])


def factor(a, b, c, nsub):
    shp = jax.ShapeDtypeStruct(a.shape, F32)
    return pl.pallas_call(functools.partial(_factor_kernel, nsub), out_shape=[shp] * 4)(a, b, c)


def _width_faces(n, c, T0, k0, s0, lane, wlo, whi, fl_ref):
    nwl = T0.shape[1]
    g_w = nwl * nwl / 4.0 * 0.5
    if wlo is None:
        wlo = (T0, k0, s0)
        whi = (T0, k0, s0)
        e_lo, e_hi = 0.0, 0.0
    else:
        e_lo, e_hi = fl_ref[2], fl_ref[3]
    Twm, kwm, swm = (jnp.where(lane == 0, b, pltpu.roll(f, 1, 1)) for f, b in zip((T0, k0, s0), wlo))
    Twp, kwp, swp = (
        jnp.where(lane == nwl - 1, b, pltpu.roll(f, nwl - 1, 1)) for f, b in zip((T0, k0, s0), whi)
    )
    gwl = g_w * (k0 + kwm) * jnp.where(lane == 0, e_lo, 1.0)
    gwh = g_w * (kwp + k0) * jnp.where(lane == nwl - 1, e_hi, 1.0)
    return Twm, swm, Twp, swp, gwl, gwh


def _prep_kernel(n, h_ref, hcl_ref, hch_ref, z_ref, sp_ref, fl_ref,
                 y_ref, v_ref, w_ref, sm_ref, a_ref, r_ref, cp_ref, ta_ref, tb_ref, tc_ref,
                 tp_ref, kp_ref, sp2_ref, b_ref, c_ref, d_ref):
    rows, nwl = h_ref.shape
    nt = rows // n
    hot, cond, slope = medium_parameters(h_ref[...])
    zpad = jnp.zeros((n, nwl), F32)
    for ref, val in ((tp_ref, hot), (kp_ref, cond), (sp2_ref, slope)):
        ref[0:n] = zpad
        ref[n : n + rows] = val
        ref[n + rows : 2 * n + rows] = zpad

    def row(ref, off):
        return ref[pl.ds(off, nt, stride=n), :]

    lane = lax.broadcasted_iota(jnp.int32, (nt, nwl), 1)
    tix = lax.broadcasted_iota(jnp.int32, (nt, nwl), 0)
    even = fl_ref[4] > 0.5
    got_a, got_b = hcl_ref[...], hch_ref[...]
    cast_lo = medium_parameters(jnp.where(even, got_b, got_a))
    cast_hi = medium_parameters(jnp.where(even, got_a, got_b))
    g_c = n * n * 4.0 * 0.5
    g_t = nt * nt / 4.0 * 0.5
    nz = sp_ref.shape[0]

    def surf_row(zr):
        acc = jnp.zeros(zr.shape, F32)
        for q in range(nz):
            acc = jnp.where(zr == q, sp_ref[q], acc)
        return acc * (nt * nt / 8.0)

    for c in range(n):
        T0, k0, s0 = (row(r, n + c) for r in (tp_ref, kp_ref, sp2_ref))
        if c == 0:
            Tm, km, sm = cast_lo
        else:
            Tm, km, sm = (row(r, n + c - 1) for r in (tp_ref, kp_ref, sp2_ref))
        if c == n - 1:
            Tq, kq, sq = cast_hi
        else:
            Tq, kq, sq = (row(r, n + c + 1) for r in (tp_ref, kp_ref, sp2_ref))
        Ttm, ktm, stm = (row(r, c) for r in (tp_ref, kp_ref, sp2_ref))
        Ttp, ktp, stp = (row(r, 2 * n + c) for r in (tp_ref, kp_ref, sp2_ref))
        Twm, _, Twp, _, gwl, gwh = _width_faces(n, c, T0, k0, s0, lane, None, None, fl_ref)
        gcl = g_c * (k0 + km)
        if c == 0:
            gcl = gcl * fl_ref[0]
        gch = g_c * (kq + k0)
        if c == n - 1:
            gch = gch * fl_ref[1]
        gtl = jnp.where(tix == 0, 0.0, g_t * (k0 + ktm))
        gth = jnp.where(tix == nt - 1, 0.0, g_t * (ktp + k0))
        s_lo = surf_row(z_ref[c : c + 1, :])
        s_hi = surf_row(z_ref[n + c : n + c + 1, :])
        rim = jnp.where(tix == 0, s_lo, jnp.where(tix == nt - 1, s_hi, 0.0))
        ex = rim * (quench_medium_hotness - T0)
        ex = ex + (gch * (Tq - T0) - gcl * (T0 - Tm))
        ex = ex + (gwh * (Twp - T0) - gwl * (T0 - Twm))
        ex = ex + (gth * (Ttp - T0) - gtl * (T0 - Ttm))
        sel = pl.ds(c, nt, stride=n)
        a_ref[sel, :] = -gcl * sm
        c_ref[sel, :] = -gch * sq
        b_ref[sel, :] = 1.0 + s0 * (gcl + gch)
        d_ref[sel, :] = ex
        ta_ref[sel, :] = -gtl * stm
        tc_ref[sel, :] = -gth * stp
        tb_ref[sel, :] = 1.0 + s0 * (gtl + gth + rim)

    def ld(ref, i):
        return ref[pl.ds(i, nt, stride=n), :]

    def st(ref, i, val):
        ref[pl.ds(i, nt, stride=n), :] = val

    shape = (nt, nwl)
    _factor(n, [0], ld, st, a_ref, b_ref, c_ref, r_ref, cp_ref, v_ref, w_ref, True, shape)
    _solve_rhs(n, [0], ld, st, a_ref, r_ref, cp_ref, d_ref, y_ref, True, shape)
    rws = _summary_rows(ld, 0, n, y_ref, v_ref, w_ref)
    rws += [jnp.zeros(shape, F32)] * (8 - len(rws))
    for k, val in enumerate(rws):
        sm_ref[pl.ds(k, nt, stride=8), :] = val


def prep_solve(h2, hcl, hch, z2, spray, flags, n):
    rows, nwl = h2.shape
    nt = rows // n
    shp = jax.ShapeDtypeStruct(h2.shape, F32)
    vm = pl.BlockSpec(memory_space=pltpu.VMEM)
    pad = pltpu.VMEM((rows + 2 * n, nwl), F32)
    return pl.pallas_call(
        functools.partial(_prep_kernel, n),
        out_shape=[shp] * 3 + [jax.ShapeDtypeStruct((nt * 8, nwl), F32)] + [shp] * 6,
        in_specs=[vm] * 4 + [SMEM_SPEC, SMEM_SPEC],
        scratch_shapes=[pad, pad, pad] + [pltpu.VMEM(h2.shape, F32)] * 3,
    )(h2, hcl, hch, z2, spray, flags)


def _edge_kernel(n, h_ref, hwl_ref, hwh_ref, fl_ref, a_ref, r_ref, cp_ref, y_ref, sm_ref,
                 yo_ref, smo_ref, d_ref, e_ref):
    rows, nwl = h_ref.shape
    nt = rows // n
    lane = lax.broadcasted_iota(jnp.int32, (nt, nwl), 1)
    for c in range(n):
        sel = pl.ds(c, nt, stride=n)
        T0, k0, s0 = medium_parameters(h_ref[sel, :])
        wlo = medium_parameters(hwl_ref[:, c : c + 1])
        whi = medium_parameters(hwh_ref[:, c : c + 1])
        Twm, _, Twp, _, gwl, gwh = _width_faces(n, c, T0, k0, s0, lane, wlo, whi, fl_ref)
        edge = jnp.where(lane == 0, -gwl * (T0 - Twm), jnp.where(lane == nwl - 1, gwh * (Twp - T0), 0.0))
        d_ref[sel, :] = edge

    def ld(ref, i):
        return ref[pl.ds(i, nt, stride=n), :]

    def st(ref, i, val):
        ref[pl.ds(i, nt, stride=n), :] = val

    _solve_rhs(n, [0], ld, st, a_ref, r_ref, cp_ref, d_ref, e_ref, True, (nt, nwl))
    yo_ref[...] = y_ref[...] + e_ref[...]
    smo_ref[...] = sm_ref[...]
    smo_ref[pl.ds(0, nt, stride=8), :] = sm_ref[pl.ds(0, nt, stride=8), :] + ld(e_ref, 0)
    smo_ref[pl.ds(3, nt, stride=8), :] = sm_ref[pl.ds(3, nt, stride=8), :] + ld(e_ref, n - 1)


def edge_solve(h2, hwl, hwh, flags, a, r, cp, y, sm, n):
    vm = pl.BlockSpec(memory_space=pltpu.VMEM)
    return pl.pallas_call(
        functools.partial(_edge_kernel, n),
        out_shape=[jax.ShapeDtypeStruct(y.shape, F32), jax.ShapeDtypeStruct(sm.shape, F32)],
        in_specs=[vm] * 3 + [SMEM_SPEC] + [vm] * 5,
        scratch_shapes=[pltpu.VMEM(y.shape, F32)] * 2,
    )(h2, hwl, hwh, flags, a, r, cp, y, sm)


def _wfactor_kernel(n, nsub, h_ref, hwl_ref, hwh_ref, fl_ref, a_ref, r_ref, cp_ref, v_ref, w_ref,
                    at_ref, bt_ref, ct_ref, b_ref, c_ref):
    rows, nwl = h_ref.shape
    nt = rows // n
    lane = lax.broadcasted_iota(jnp.int32, (nt, nwl), 1)
    for c in range(n):
        sel = pl.ds(c, nt, stride=n)
        T0, k0, s0 = medium_parameters(h_ref[sel, :])
        wlo = medium_parameters(hwl_ref[:, c : c + 1])
        whi = medium_parameters(hwh_ref[:, c : c + 1])
        _, swm, _, swp, gwl, gwh = _width_faces(n, c, T0, k0, s0, lane, wlo, whi, fl_ref)
        at_ref[sel, :] = -gwl * swm
        ct_ref[sel, :] = -gwh * swp
        bt_ref[sel, :] = 1.0 + s0 * (gwl + gwh)
    for src, dst in ((at_ref, a_ref), (bt_ref, b_ref), (ct_ref, c_ref)):
        for q in range(dst.shape[1]):
            dst[:, q, :] = src[q * 128 : (q + 1) * 128, :].T
    m = a_ref.shape[0] // nsub
    subs = [q * m for q in range(nsub)]
    _factor(m, subs, _lead_ld, _lead_st, a_ref, b_ref, c_ref, r_ref, cp_ref, v_ref, w_ref, 4, a_ref.shape[1:])


def wfactor(h2, hwl, hwh, flags, n, nsub):
    rows, nwl = h2.shape
    wshape = (nwl, rows // 128, 128)
    shp = jax.ShapeDtypeStruct(wshape, F32)
    vm = pl.BlockSpec(memory_space=pltpu.VMEM)
    return pl.pallas_call(
        functools.partial(_wfactor_kernel, n, nsub),
        out_shape=[shp] * 5,
        in_specs=[vm] * 3 + [SMEM_SPEC],
        scratch_shapes=[pltpu.VMEM(h2.shape, F32)] * 3 + [pltpu.VMEM(wshape, F32)] * 2,
    )(h2, hwl, hwh, flags)


def _width_kernel(nsub, yc_ref, vc_ref, wc_ref, bk_ref, a_ref, r_ref, cp_ref, v_ref, w_ref,
                  y_ref, sm_ref, d_ref):
    sc = yc_ref[...] + vc_ref[...] * bk_ref[:, 0:1, :] + wc_ref[...] * bk_ref[:, 1:2, :]
    nt, ncl, nwl = sc.shape
    sc = sc.reshape(nt * ncl, nwl)
    for q in range(d_ref.shape[1]):
        d_ref[:, q, :] = sc[q * 128 : (q + 1) * 128, :].T
    n = a_ref.shape[0] // nsub
    subs = [q * n for q in range(nsub)]
    _solve_rhs(n, subs, _lead_ld, _lead_st, a_ref, r_ref, cp_ref, d_ref, y_ref, 4, a_ref.shape[1:])
    for q, s0 in enumerate(subs):
        for k, val in enumerate(_summary_rows(_lead_ld, s0, n, y_ref, v_ref, w_ref)):
            sm_ref[q, k] = val


def _thick_kernel(nsub, tsub, nw, me_ref, *refs):
    r_refs = refs[:nw]
    (yw_ref, vw_ref, ww_ref, a_ref, r_ref, cp_ref, v_ref, w_ref, h_ref,
     o_ref, sw_ref, d_ref, y_ref) = refs[nw:]
    lrw = _width_reduce(me_ref[0], r_refs)
    m = yw_ref.shape[0] // nsub
    for q in range(nsub):
        sl = slice(q * m, (q + 1) * m)
        sw_ref[sl] = yw_ref[sl] + vw_ref[sl] * lrw[q][0] + ww_ref[sl] * lrw[q][1]
    nt, ncl, nwl = a_ref.shape
    per_q = 128 // ncl
    for q in range(sw_ref.shape[1]):
        d_ref[q * per_q : (q + 1) * per_q] = sw_ref[:, q, :].T.reshape(per_q, ncl, nwl)
    n = nt // tsub
    subs = [q * n for q in range(tsub)]
    shape = a_ref.shape[1:]
    _solve_rhs(n, subs, _lead_ld, _lead_st, a_ref, r_ref, cp_ref, d_ref, y_ref, 4, shape)
    sums = [tuple(_summary_rows(_lead_ld, s0, n, y_ref, v_ref, w_ref)) for s0 in subs]
    lrs = [None] * tsub

    def emit(p, left, right):
        lrs[p] = (left, right)

    _reduce_blocks(tsub, lambda p: sums[p], emit, jnp.zeros(shape, F32))
    for q, s0 in enumerate(subs):
        sl = slice(s0, s0 + n)
        left, right = lrs[q]
        o_ref[sl] = h_ref[sl] + (y_ref[sl] + v_ref[sl] * left + w_ref[sl] * right)


def cast_solve(a, b, c, d, n):
    shp = jax.ShapeDtypeStruct(a.shape, F32)
    m = a.shape[0] // n
    return pl.pallas_call(
        functools.partial(_cast_kernel, n),
        out_shape=[shp, shp, shp, jax.ShapeDtypeStruct((m * 8, a.shape[1]), F32)],
        scratch_shapes=[pltpu.VMEM(a.shape, F32)],
    )(a, b, c, d)


def width_solve(yc, vc, wc, bk, a, fac, nsub):
    shp = jax.ShapeDtypeStruct(a.shape, F32)
    return pl.pallas_call(
        functools.partial(_width_kernel, nsub),
        out_shape=[shp, jax.ShapeDtypeStruct((nsub, 6) + a.shape[1:], F32)],
        scratch_shapes=[pltpu.VMEM(a.shape, F32)],
    )(yc, vc, wc, bk, a, *fac)


def thick_solve(me, got, yw, vw, ww, a, fac, h, nsub, tsub):
    vm = pl.BlockSpec(memory_space=pltpu.VMEM)
    return pl.pallas_call(
        functools.partial(_thick_kernel, nsub, tsub, len(got)),
        out_shape=jax.ShapeDtypeStruct(a.shape, F32),
        in_specs=[SMEM_SPEC] + [vm] * (len(got) + 9),
        scratch_shapes=[pltpu.VMEM(yw.shape, F32)] + [pltpu.VMEM(a.shape, F32)] * 2,
    )(me, *got, yw, vw, ww, a, *fac, h)


def _reduce_blocks(nb, blk, emit, zero):
    pp, qq = zero, zero
    saved = []
    for p in range(nb):
        y0, v0, w0, yn, vn, wn = blk(p)
        rd = 1.0 / (1.0 - v0 * qq)
        fa = (y0 + v0 * pp) * rd
        fb = w0 * rd
        saved.append((fa, fb, pp, qq))
        pp, qq = yn + vn * (pp + qq * fa), wn + vn * qq * fb
    f_next = zero
    for p in range(nb - 1, -1, -1):
        fa, fb, pp, qq = saved[p]
        f = fa + fb * f_next
        emit(p, pp + qq * f, f_next)
        f_next = f


def _merge(A, B):
    yA0, vA0, wA0, yAn, vAn, wAn = A
    yB0, vB0, wB0, yBn, vBn, wBn = B
    rd = 1.0 / (1.0 - wAn * vB0)
    ey = (yAn + wAn * yB0) * rd
    ev = vAn * rd
    ew = wAn * wB0 * rd
    fy = yB0 + vB0 * ey
    fv = vB0 * ev
    fw = wB0 + vB0 * ew
    return (yA0 + wA0 * fy, vA0 + wA0 * fv, wA0 * fw, yBn + vBn * ey, vBn * ev, wBn + vBn * ew)


def _chain(nb, blk, emit, left, right):
    pp, qq = left, jnp.zeros_like(left)
    saved = []
    for p in range(nb):
        y0, v0, w0, yn, vn, wn = blk(p)
        rd = 1.0 / (1.0 - v0 * qq)
        fa = (y0 + v0 * pp) * rd
        fb = w0 * rd
        saved.append((fa, fb, pp, qq))
        pp, qq = yn + vn * (pp + qq * fa), wn + vn * qq * fb
    f_next = right
    for p in range(nb - 1, -1, -1):
        fa, fb, pp, qq = saved[p]
        f = fa + fb * f_next
        emit(p, pp + qq * f, f_next)
        f_next = f


def _cast_reduced_kernel(s_ref, lr_ref):
    nb, g, _, nl = s_ref.shape
    ng = 8
    if g != 1 or nb % ng:
        def blk(p):
            return tuple(s_ref[p, :, k, :] for k in range(6))

        def emit(p, left, right):
            lr_ref[p, :, 0:1, :] = left[:, None]
            lr_ref[p, :, 1:2, :] = right[:, None]

        _reduce_blocks(nb, blk, emit, jnp.zeros((g, nl), F32))
        return
    m = nb // ng

    def member(j):
        return tuple(
            jnp.concatenate([s_ref[G * m + j, 0, k : k + 1, :] for G in range(ng)], 0)
            for k in range(6)
        )

    members = [member(j) for j in range(m)]
    acc = members[0]
    for j in range(1, m):
        acc = _merge(acc, members[j])
    outer = [None] * ng

    def emit_g(G, left, right):
        outer[G] = (left, right)

    zero1 = jnp.zeros((1, nl), F32)
    _chain(ng, lambda G: tuple(x[G : G + 1] for x in acc), emit_g, zero1, zero1)
    left_g = jnp.concatenate([outer[G][0] for G in range(ng)], 0)
    right_g = jnp.concatenate([outer[G][1] for G in range(ng)], 0)

    def emit(j, left, right):
        for G in range(ng):
            lr_ref[G * m + j, 0, 0:1, :] = left[G : G + 1]
            lr_ref[G * m + j, 0, 1:2, :] = right[G : G + 1]

    _chain(m, lambda j: members[j], emit, left_g, right_g)


def _width_reduce(me, r_refs):
    nw = len(r_refs)
    nsub = r_refs[0].shape[0]
    out = [[None, None] for _ in range(nsub)]

    def blk(b):
        dev, q = divmod(b, nsub)
        kk = (me - dev + nw) % nw
        vals = []
        for k6 in range(6):
            val = r_refs[0][q, k6]
            for k in range(1, nw):
                val = jnp.where(kk == k, r_refs[k][q, k6], val)
            vals.append(val)
        return tuple(vals)

    def emit(b, left, right):
        dev, q = divmod(b, nsub)
        mine = me == dev
        for j, val in enumerate((left, right)):
            out[q][j] = val if out[q][j] is None else jnp.where(mine, val, out[q][j])

    _reduce_blocks(nw * nsub, blk, emit, jnp.zeros(r_refs[0].shape[2:], F32))
    return out


def _surface_kernel(scale, z_ref, sp_ref, o_ref):
    z = z_ref[...]
    acc = jnp.zeros(z.shape, F32)
    for q in range(sp_ref.shape[0]):
        acc = jnp.where(z == q, sp_ref[q], acc)
    o_ref[...] = acc * scale


def medium_parameters(x):
    t = jnp.tanh(x)
    hot = x - solidification_release * t
    cond = 1.5 - 0.5 * jnp.tanh(hot)
    slope = (1.0 - solidification_release) + solidification_release * t * t
    return hot, cond, slope


def shards(h, zones, spray_coef):
    nt, ncl, nwl = h.shape
    nc, nw = lax.axis_size("cast"), lax.axis_size("width")
    ci, wi = lax.axis_index("cast"), lax.axis_index("width")
    up_c = [(i, i + 1) for i in range(nc - 1)]
    up_w = [(i, i + 1) for i in range(nw - 1)]
    even = ci % 2 == 0
    first, last = h[:, 0, :], h[:, -1, :]
    in_chip = [(i, i ^ 1) for i in range(nc)]
    across = [(i, i + 1) for i in range(1, nc - 1, 2)] + [(i + 1, i) for i in range(1, nc - 1, 2)]
    got_a = lax.ppermute(jnp.where(even, last, first), "cast", in_chip)
    got_b = lax.ppermute(jnp.where(even, first, last), "cast", across)
    h_wl = lax.ppermute(h[:, :, -1], "width", up_w)
    h_wh = lax.ppermute(h[:, :, 0], "width", [(b, a) for a, b in up_w])

    cast_low = (ci > 0).astype(F32)
    cast_high = (ci < nc - 1).astype(F32)
    width_low = (wi > 0).astype(F32)
    width_high = (wi < nw - 1).astype(F32)
    flags = jnp.stack([cast_low, cast_high, width_low, width_high, even.astype(F32)])
    h2 = h.reshape(nt * ncl, nwl)
    outs = prep_solve(h2, got_a, got_b, zones.reshape(2 * ncl, nwl), spray_coef, flags, ncl)
    y, v, w, summ, a_c, r_c, cp_c = outs[:7]
    tlo, tmd, thi = (x.reshape(nt, ncl, nwl) for x in outs[7:])
    y, summ = edge_solve(h2, h_wl, h_wh, flags, a_c, r_c, cp_c, y, summ, ncl)
    recv = lax.all_to_all(summ.reshape(nc, nt // nc, 8, nwl), "cast", 0, 0, tiled=True)
    lr_shape = recv.shape[:2] + (2, nwl)
    lr = pl.pallas_call(_cast_reduced_kernel, out_shape=jax.ShapeDtypeStruct(lr_shape, F32))(recv)
    back = lax.all_to_all(lr, "cast", 0, 0, tiled=True).reshape(nt, 2, nwl)
    y, v, w = (x.reshape(nt, ncl, nwl) for x in (y, v, w))

    lines = nt * ncl
    nsub = 4

    def wl(x):
        return jnp.transpose(x, (2, 0, 1)).reshape(nwl, lines // 128, 128)

    wa, *wfac = wfactor(h2, h_wl, h_wh, flags, ncl, nsub)
    tfac = factor(tlo, tmd, thi, 8)
    yw, summ = width_solve(y, v, w, back, wa, wfac, nsub)
    got = [summ] + [
        lax.ppermute(summ, "width", [(i, (i + q) % nw) for i in range(nw)]) for q in range(1, nw)
    ]
    me = wi.astype(jnp.int32).reshape(1)
    return thick_solve(me, got, yw, wfac[2], wfac[3], tlo, tfac, h, nsub, 8)


def solution(mesh):
    spec = P(None, "cast", "width")
    return jax.shard_map(
        shards, mesh=mesh, in_specs=(spec, spec, P()), out_specs=spec, check_vma=False
    )
```

```python
import functools

import jax
import jax.numpy as jnp
from jax import lax
from jax.experimental import pallas as pl
from jax.experimental.pallas import tpu as pltpu
from jax.sharding import PartitionSpec as P

F32 = jnp.float32
solidification_release = 0.4
quench_medium_hotness = -2.0
SMEM_SPEC = pl.BlockSpec(memory_space=pltpu.SMEM)


def _sweep(n, subs, ld, st, a_ref, b_ref, c_ref, d_ref, y_ref, v_ref, w_ref, cp_ref, unroll, shape):
    with_vw = v_ref is not None
    zero = jnp.zeros(shape, F32)
    one = jnp.ones(shape, F32)

    def fwd(i, carries):
        out = []
        for s0, (cprev, dprev, vprev) in zip(subs, carries):
            j = s0 + i
            a = ld(a_ref, j)
            r = 1.0 / (ld(b_ref, j) - a * cprev)
            cn = ld(c_ref, j) * r
            dn = (ld(d_ref, j) - a * dprev) * r
            st(cp_ref, j, cn)
            st(y_ref, j, dn)
            if with_vw:
                vprev = -(a * vprev) * r
                st(v_ref, j, vprev)
            out.append((cn, dn, vprev))
        return tuple(out)

    carries = tuple((zero, zero, one) for _ in subs)
    if unroll is True:
        for i in range(n):
            carries = fwd(i, carries)
    else:
        carries = lax.fori_loop(0, n, fwd, carries, unroll=unroll)
    if with_vw:
        for s0, (cl, _, _) in zip(subs, carries):
            st(w_ref, s0 + n - 1, -cl)

    def bwd(jj, carries):
        i = n - 2 - jj
        out = []
        for s0, (yn, vn, wn) in zip(subs, carries):
            j = s0 + i
            cp = ld(cp_ref, j)
            yn = ld(y_ref, j) - cp * yn
            st(y_ref, j, yn)
            if with_vw:
                vn = ld(v_ref, j) - cp * vn
                wn = -cp * wn
                st(v_ref, j, vn)
                st(w_ref, j, wn)
            out.append((yn, vn, wn))
        return tuple(out)

    carries = tuple((dl, vl, -cl) for cl, dl, vl in carries)
    if unroll is True:
        for jj in range(n - 1):
            carries = bwd(jj, carries)
    else:
        lax.fori_loop(0, n - 1, bwd, carries, unroll=unroll)


def _summary_rows(ld, s0, n, y_ref, v_ref, w_ref):
    return [ld(y_ref, s0), ld(v_ref, s0), ld(w_ref, s0),
            ld(y_ref, s0 + n - 1), ld(v_ref, s0 + n - 1), ld(w_ref, s0 + n - 1)]


def _cast_kernel(n, a_ref, b_ref, c_ref, d_ref, y_ref, v_ref, w_ref, sm_ref, cp_ref):
    m = a_ref.shape[0] // n

    def ld(ref, i):
        return ref[pl.ds(i, m, stride=n), :]

    def st(ref, i, val):
        ref[pl.ds(i, m, stride=n), :] = val

    shape = (m, a_ref.shape[1])
    _sweep(n, [0], ld, st, a_ref, b_ref, c_ref, d_ref, y_ref, v_ref, w_ref, cp_ref, True, shape)
    rows = _summary_rows(ld, 0, n, y_ref, v_ref, w_ref)
    rows += [jnp.zeros(shape, F32)] * (8 - len(rows))
    for k, val in enumerate(rows):
        sm_ref[pl.ds(k, m, stride=8), :] = val


def _lead_ld(ref, i):
    return ref[i]


def _lead_st(ref, i, val):
    ref[i] = val


def _loop(n, body, carry, unroll):
    if unroll is True:
        for i in range(n):
            carry = body(i, carry)
        return carry
    return lax.fori_loop(0, n, body, carry, unroll=unroll)


def _factor(n, subs, ld, st, a_ref, b_ref, c_ref, r_ref, cp_ref, v_ref, w_ref, unroll, shape):
    zero = jnp.zeros(shape, F32)
    one = jnp.ones(shape, F32)

    def fwd(i, carries):
        out = []
        for s0, (cprev, vprev) in zip(subs, carries):
            j = s0 + i
            a = ld(a_ref, j)
            r = 1.0 / (ld(b_ref, j) - a * cprev)
            cn = ld(c_ref, j) * r
            vprev = -(a * vprev) * r
            st(r_ref, j, r)
            st(cp_ref, j, cn)
            st(v_ref, j, vprev)
            out.append((cn, vprev))
        return tuple(out)

    carries = _loop(n, fwd, tuple((zero, one) for _ in subs), unroll)
    for s0, (cl, _) in zip(subs, carries):
        st(w_ref, s0 + n - 1, -cl)

    def bwd(jj, carries):
        i = n - 2 - jj
        out = []
        for s0, (vn, wn) in zip(subs, carries):
            j = s0 + i
            cp = ld(cp_ref, j)
            vn = ld(v_ref, j) - cp * vn
            wn = -cp * wn
            st(v_ref, j, vn)
            st(w_ref, j, wn)
            out.append((vn, wn))
        return tuple(out)

    _loop(n - 1, bwd, tuple((vl, -cl) for cl, vl in carries), unroll)


def _solve_rhs(n, subs, ld, st, a_ref, r_ref, cp_ref, d_ref, y_ref, unroll, shape):
    zero = jnp.zeros(shape, F32)

    def fwd(i, carries):
        out = []
        for s0, dprev in zip(subs, carries):
            j = s0 + i
            dn = (ld(d_ref, j) - ld(a_ref, j) * dprev) * ld(r_ref, j)
            st(y_ref, j, dn)
            out.append(dn)
        return tuple(out)

    carries = _loop(n, fwd, tuple(zero for _ in subs), unroll)

    def bwd(jj, carries):
        i = n - 2 - jj
        out = []
        for s0, yn in zip(subs, carries):
            j = s0 + i
            yn = ld(y_ref, j) - ld(cp_ref, j) * yn
            st(y_ref, j, yn)
            out.append(yn)
        return tuple(out)

    _loop(n - 1, bwd, carries, unroll)


def _factor_kernel(nsub, a_ref, b_ref, c_ref, r_ref, cp_ref, v_ref, w_ref):
    n = a_ref.shape[0] // nsub
    subs = [q * n for q in range(nsub)]
    _factor(n, subs, _lead_ld, _lead_st, a_ref, b_ref, c_ref, r_ref, cp_ref, v_ref, w_ref, 4, a_ref.shape[1:])


def factor(a, b, c, nsub):
    shp = jax.ShapeDtypeStruct(a.shape, F32)
    return pl.pallas_call(functools.partial(_factor_kernel, nsub), out_shape=[shp] * 4)(a, b, c)


def _width_faces(n, c, T0, k0, s0, lane, wlo, whi, fl_ref):
    nwl = T0.shape[1]
    g_w = nwl * nwl / 4.0 * 0.5
    if wlo is None:
        wlo = (T0, k0, s0)
        whi = (T0, k0, s0)
        e_lo, e_hi = 0.0, 0.0
    else:
        e_lo, e_hi = fl_ref[2], fl_ref[3]
    Twm, kwm, swm = (jnp.where(lane == 0, b, pltpu.roll(f, 1, 1)) for f, b in zip((T0, k0, s0), wlo))
    Twp, kwp, swp = (
        jnp.where(lane == nwl - 1, b, pltpu.roll(f, nwl - 1, 1)) for f, b in zip((T0, k0, s0), whi)
    )
    gwl = g_w * (k0 + kwm) * jnp.where(lane == 0, e_lo, 1.0)
    gwh = g_w * (kwp + k0) * jnp.where(lane == nwl - 1, e_hi, 1.0)
    return Twm, swm, Twp, swp, gwl, gwh


def _prep_kernel(n, h_ref, hcl_ref, hch_ref, z_ref, sp_ref, fl_ref,
                 y_ref, v_ref, w_ref, sm_ref, a_ref, r_ref, cp_ref, ta_ref, tb_ref, tc_ref,
                 tp_ref, kp_ref, sp2_ref, b_ref, c_ref, d_ref):
    rows, nwl = h_ref.shape
    nt = rows // n
    hot, cond, slope = medium_parameters(h_ref[...])
    zpad = jnp.zeros((n, nwl), F32)
    for ref, val in ((tp_ref, hot), (kp_ref, cond), (sp2_ref, slope)):
        ref[0:n] = zpad
        ref[n : n + rows] = val
        ref[n + rows : 2 * n + rows] = zpad

    def row(ref, off):
        return ref[pl.ds(off, nt, stride=n), :]

    lane = lax.broadcasted_iota(jnp.int32, (nt, nwl), 1)
    tix = lax.broadcasted_iota(jnp.int32, (nt, nwl), 0)
    even = fl_ref[4] > 0.5
    got_a, got_b = hcl_ref[...], hch_ref[...]
    cast_lo = medium_parameters(jnp.where(even, got_b, got_a))
    cast_hi = medium_parameters(jnp.where(even, got_a, got_b))
    g_c = n * n * 4.0 * 0.5
    g_t = nt * nt / 4.0 * 0.5
    nz = sp_ref.shape[0]

    def surf_row(zr):
        acc = jnp.zeros(zr.shape, F32)
        for q in range(nz):
            acc = jnp.where(zr == q, sp_ref[q], acc)
        return acc * (nt * nt / 8.0)

    for c in range(n):
        T0, k0, s0 = (row(r, n + c) for r in (tp_ref, kp_ref, sp2_ref))
        if c == 0:
            Tm, km, sm = cast_lo
        else:
            Tm, km, sm = (row(r, n + c - 1) for r in (tp_ref, kp_ref, sp2_ref))
        if c == n - 1:
            Tq, kq, sq = cast_hi
        else:
            Tq, kq, sq = (row(r, n + c + 1) for r in (tp_ref, kp_ref, sp2_ref))
        Ttm, ktm, stm = (row(r, c) for r in (tp_ref, kp_ref, sp2_ref))
        Ttp, ktp, stp = (row(r, 2 * n + c) for r in (tp_ref, kp_ref, sp2_ref))
        Twm, _, Twp, _, gwl, gwh = _width_faces(n, c, T0, k0, s0, lane, None, None, fl_ref)
        gcl = g_c * (k0 + km)
        if c == 0:
            gcl = gcl * fl_ref[0]
        gch = g_c * (kq + k0)
        if c == n - 1:
            gch = gch * fl_ref[1]
        gtl = jnp.where(tix == 0, 0.0, g_t * (k0 + ktm))
        gth = jnp.where(tix == nt - 1, 0.0, g_t * (ktp + k0))
        s_lo = surf_row(z_ref[c : c + 1, :])
        s_hi = surf_row(z_ref[n + c : n + c + 1, :])
        rim = jnp.where(tix == 0, s_lo, jnp.where(tix == nt - 1, s_hi, 0.0))
        ex = rim * (quench_medium_hotness - T0)
        ex = ex + (gch * (Tq - T0) - gcl * (T0 - Tm))
        ex = ex + (gwh * (Twp - T0) - gwl * (T0 - Twm))
        ex = ex + (gth * (Ttp - T0) - gtl * (T0 - Ttm))
        sel = pl.ds(c, nt, stride=n)
        a_ref[sel, :] = -gcl * sm
        c_ref[sel, :] = -gch * sq
        b_ref[sel, :] = 1.0 + s0 * (gcl + gch)
        d_ref[sel, :] = ex
        ta_ref[sel, :] = -gtl * stm
        tc_ref[sel, :] = -gth * stp
        tb_ref[sel, :] = 1.0 + s0 * (gtl + gth + rim)

    def ld(ref, i):
        return ref[pl.ds(i, nt, stride=n), :]

    def st(ref, i, val):
        ref[pl.ds(i, nt, stride=n), :] = val

    shape = (nt, nwl)
    _factor(n, [0], ld, st, a_ref, b_ref, c_ref, r_ref, cp_ref, v_ref, w_ref, True, shape)
    _solve_rhs(n, [0], ld, st, a_ref, r_ref, cp_ref, d_ref, y_ref, True, shape)
    rws = _summary_rows(ld, 0, n, y_ref, v_ref, w_ref)
    rws += [jnp.zeros(shape, F32)] * (8 - len(rws))
    for k, val in enumerate(rws):
        sm_ref[pl.ds(k, nt, stride=8), :] = val


def prep_solve(h2, hcl, hch, z2, spray, flags, n):
    rows, nwl = h2.shape
    nt = rows // n
    shp = jax.ShapeDtypeStruct(h2.shape, F32)
    vm = pl.BlockSpec(memory_space=pltpu.VMEM)
    pad = pltpu.VMEM((rows + 2 * n, nwl), F32)
    return pl.pallas_call(
        functools.partial(_prep_kernel, n),
        out_shape=[shp] * 3 + [jax.ShapeDtypeStruct((nt * 8, nwl), F32)] + [shp] * 6,
        in_specs=[vm] * 4 + [SMEM_SPEC, SMEM_SPEC],
        scratch_shapes=[pad, pad, pad] + [pltpu.VMEM(h2.shape, F32)] * 3,
    )(h2, hcl, hch, z2, spray, flags)


def _edge_kernel(n, h_ref, hwl_ref, hwh_ref, fl_ref, a_ref, r_ref, cp_ref, y_ref, sm_ref,
                 yo_ref, smo_ref, d_ref, e_ref):
    rows, nwl = h_ref.shape
    nt = rows // n
    lane = lax.broadcasted_iota(jnp.int32, (nt, nwl), 1)
    for c in range(n):
        sel = pl.ds(c, nt, stride=n)
        T0, k0, s0 = medium_parameters(h_ref[sel, :])
        wlo = medium_parameters(hwl_ref[:, c : c + 1])
        whi = medium_parameters(hwh_ref[:, c : c + 1])
        Twm, _, Twp, _, gwl, gwh = _width_faces(n, c, T0, k0, s0, lane, wlo, whi, fl_ref)
        edge = jnp.where(lane == 0, -gwl * (T0 - Twm), jnp.where(lane == nwl - 1, gwh * (Twp - T0), 0.0))
        d_ref[sel, :] = edge

    def ld(ref, i):
        return ref[pl.ds(i, nt, stride=n), :]

    def st(ref, i, val):
        ref[pl.ds(i, nt, stride=n), :] = val

    _solve_rhs(n, [0], ld, st, a_ref, r_ref, cp_ref, d_ref, e_ref, True, (nt, nwl))
    yo_ref[...] = y_ref[...] + e_ref[...]
    smo_ref[...] = sm_ref[...]
    smo_ref[pl.ds(0, nt, stride=8), :] = sm_ref[pl.ds(0, nt, stride=8), :] + ld(e_ref, 0)
    smo_ref[pl.ds(3, nt, stride=8), :] = sm_ref[pl.ds(3, nt, stride=8), :] + ld(e_ref, n - 1)


def edge_solve(h2, hwl, hwh, flags, a, r, cp, y, sm, n):
    vm = pl.BlockSpec(memory_space=pltpu.VMEM)
    return pl.pallas_call(
        functools.partial(_edge_kernel, n),
        out_shape=[jax.ShapeDtypeStruct(y.shape, F32), jax.ShapeDtypeStruct(sm.shape, F32)],
        in_specs=[vm] * 3 + [SMEM_SPEC] + [vm] * 5,
        scratch_shapes=[pltpu.VMEM(y.shape, F32)] * 2,
    )(h2, hwl, hwh, flags, a, r, cp, y, sm)


def _wfactor_kernel(n, nsub, h_ref, hwl_ref, hwh_ref, fl_ref, a_ref, r_ref, cp_ref, v_ref, w_ref,
                    at_ref, bt_ref, ct_ref, b_ref, c_ref):
    rows, nwl = h_ref.shape
    nt = rows // n
    lane = lax.broadcasted_iota(jnp.int32, (nt, nwl), 1)
    for c in range(n):
        sel = pl.ds(c, nt, stride=n)
        T0, k0, s0 = medium_parameters(h_ref[sel, :])
        wlo = medium_parameters(hwl_ref[:, c : c + 1])
        whi = medium_parameters(hwh_ref[:, c : c + 1])
        _, swm, _, swp, gwl, gwh = _width_faces(n, c, T0, k0, s0, lane, wlo, whi, fl_ref)
        at_ref[sel, :] = -gwl * swm
        ct_ref[sel, :] = -gwh * swp
        bt_ref[sel, :] = 1.0 + s0 * (gwl + gwh)
    for src, dst in ((at_ref, a_ref), (bt_ref, b_ref), (ct_ref, c_ref)):
        for q in range(dst.shape[1]):
            dst[:, q, :] = src[q * 128 : (q + 1) * 128, :].T
    m = a_ref.shape[0] // nsub
    subs = [q * m for q in range(nsub)]
    _factor(m, subs, _lead_ld, _lead_st, a_ref, b_ref, c_ref, r_ref, cp_ref, v_ref, w_ref, 4, a_ref.shape[1:])


def wfactor(h2, hwl, hwh, flags, n, nsub):
    rows, nwl = h2.shape
    wshape = (nwl, rows // 128, 128)
    shp = jax.ShapeDtypeStruct(wshape, F32)
    vm = pl.BlockSpec(memory_space=pltpu.VMEM)
    return pl.pallas_call(
        functools.partial(_wfactor_kernel, n, nsub),
        out_shape=[shp] * 5,
        in_specs=[vm] * 3 + [SMEM_SPEC],
        scratch_shapes=[pltpu.VMEM(h2.shape, F32)] * 3 + [pltpu.VMEM(wshape, F32)] * 2,
    )(h2, hwl, hwh, flags)


def _width_kernel(nsub, yc_ref, vc_ref, wc_ref, bk_ref, a_ref, r_ref, cp_ref, v_ref, w_ref,
                  y_ref, sm_ref, d_ref):
    sc = yc_ref[...] + vc_ref[...] * bk_ref[:, 0:1, :] + wc_ref[...] * bk_ref[:, 1:2, :]
    nt, ncl, nwl = sc.shape
    sc = sc.reshape(nt * ncl, nwl)
    for q in range(d_ref.shape[1]):
        d_ref[:, q, :] = sc[q * 128 : (q + 1) * 128, :].T
    n = a_ref.shape[0] // nsub
    subs = [q * n for q in range(nsub)]
    _solve_rhs(n, subs, _lead_ld, _lead_st, a_ref, r_ref, cp_ref, d_ref, y_ref, 4, a_ref.shape[1:])
    for q, s0 in enumerate(subs):
        for k, val in enumerate(_summary_rows(_lead_ld, s0, n, y_ref, v_ref, w_ref)):
            sm_ref[q, k] = val


def _thick_kernel(nsub, tsub, nw, me_ref, *refs):
    r_refs = refs[:nw]
    (yw_ref, vw_ref, ww_ref, a_ref, r_ref, cp_ref, v_ref, w_ref, h_ref,
     o_ref, sw_ref, d_ref, y_ref) = refs[nw:]
    lrw = _width_reduce(me_ref[0], r_refs)
    m = yw_ref.shape[0] // nsub
    for q in range(nsub):
        sl = slice(q * m, (q + 1) * m)
        sw_ref[sl] = yw_ref[sl] + vw_ref[sl] * lrw[q][0] + ww_ref[sl] * lrw[q][1]
    nt, ncl, nwl = a_ref.shape
    per_q = 128 // ncl
    for q in range(sw_ref.shape[1]):
        d_ref[q * per_q : (q + 1) * per_q] = sw_ref[:, q, :].T.reshape(per_q, ncl, nwl)
    n = nt // tsub
    subs = [q * n for q in range(tsub)]
    shape = a_ref.shape[1:]
    _solve_rhs(n, subs, _lead_ld, _lead_st, a_ref, r_ref, cp_ref, d_ref, y_ref, 4, shape)
    sums = [tuple(_summary_rows(_lead_ld, s0, n, y_ref, v_ref, w_ref)) for s0 in subs]
    lrs = [None] * tsub

    def emit(p, left, right):
        lrs[p] = (left, right)

    _reduce_blocks(tsub, lambda p: sums[p], emit, jnp.zeros(shape, F32))
    for q, s0 in enumerate(subs):
        sl = slice(s0, s0 + n)
        left, right = lrs[q]
        o_ref[sl] = h_ref[sl] + (y_ref[sl] + v_ref[sl] * left + w_ref[sl] * right)


def cast_solve(a, b, c, d, n):
    shp = jax.ShapeDtypeStruct(a.shape, F32)
    m = a.shape[0] // n
    return pl.pallas_call(
        functools.partial(_cast_kernel, n),
        out_shape=[shp, shp, shp, jax.ShapeDtypeStruct((m * 8, a.shape[1]), F32)],
        scratch_shapes=[pltpu.VMEM(a.shape, F32)],
    )(a, b, c, d)


def width_solve(yc, vc, wc, bk, a, fac, nsub):
    shp = jax.ShapeDtypeStruct(a.shape, F32)
    return pl.pallas_call(
        functools.partial(_width_kernel, nsub),
        out_shape=[shp, jax.ShapeDtypeStruct((nsub, 6) + a.shape[1:], F32)],
        scratch_shapes=[pltpu.VMEM(a.shape, F32)],
    )(yc, vc, wc, bk, a, *fac)


def thick_solve(me, got, yw, vw, ww, a, fac, h, nsub, tsub):
    vm = pl.BlockSpec(memory_space=pltpu.VMEM)
    return pl.pallas_call(
        functools.partial(_thick_kernel, nsub, tsub, len(got)),
        out_shape=jax.ShapeDtypeStruct(a.shape, F32),
        in_specs=[SMEM_SPEC] + [vm] * (len(got) + 9),
        scratch_shapes=[pltpu.VMEM(yw.shape, F32)] + [pltpu.VMEM(a.shape, F32)] * 2,
    )(me, *got, yw, vw, ww, a, *fac, h)


def _reduce_blocks(nb, blk, emit, zero):
    pp, qq = zero, zero
    saved = []
    for p in range(nb):
        y0, v0, w0, yn, vn, wn = blk(p)
        rd = 1.0 / (1.0 - v0 * qq)
        fa = (y0 + v0 * pp) * rd
        fb = w0 * rd
        saved.append((fa, fb, pp, qq))
        pp, qq = yn + vn * (pp + qq * fa), wn + vn * qq * fb
    f_next = zero
    for p in range(nb - 1, -1, -1):
        fa, fb, pp, qq = saved[p]
        f = fa + fb * f_next
        emit(p, pp + qq * f, f_next)
        f_next = f


def _merge(A, B):
    yA0, vA0, wA0, yAn, vAn, wAn = A
    yB0, vB0, wB0, yBn, vBn, wBn = B
    rd = 1.0 / (1.0 - wAn * vB0)
    ey = (yAn + wAn * yB0) * rd
    ev = vAn * rd
    ew = wAn * wB0 * rd
    fy = yB0 + vB0 * ey
    fv = vB0 * ev
    fw = wB0 + vB0 * ew
    return (yA0 + wA0 * fy, vA0 + wA0 * fv, wA0 * fw, yBn + vBn * ey, vBn * ev, wBn + vBn * ew)


def _chain(nb, blk, emit, left, right):
    pp, qq = left, jnp.zeros_like(left)
    saved = []
    for p in range(nb):
        y0, v0, w0, yn, vn, wn = blk(p)
        rd = 1.0 / (1.0 - v0 * qq)
        fa = (y0 + v0 * pp) * rd
        fb = w0 * rd
        saved.append((fa, fb, pp, qq))
        pp, qq = yn + vn * (pp + qq * fa), wn + vn * qq * fb
    f_next = right
    for p in range(nb - 1, -1, -1):
        fa, fb, pp, qq = saved[p]
        f = fa + fb * f_next
        emit(p, pp + qq * f, f_next)
        f_next = f


def _cast_reduced_kernel(s_ref, lr_ref):
    nb, g, _, nl = s_ref.shape
    ng = 8
    if g != 1 or nb % ng:
        def blk(p):
            return tuple(s_ref[p, :, k, :] for k in range(6))

        def emit(p, left, right):
            lr_ref[p, :, 0:1, :] = left[:, None]
            lr_ref[p, :, 1:2, :] = right[:, None]

        _reduce_blocks(nb, blk, emit, jnp.zeros((g, nl), F32))
        return
    m = nb // ng

    def member(j):
        return tuple(
            jnp.concatenate([s_ref[G * m + j, 0, k : k + 1, :] for G in range(ng)], 0)
            for k in range(6)
        )

    members = [member(j) for j in range(m)]
    acc = members[0]
    for j in range(1, m):
        acc = _merge(acc, members[j])
    outer = [None] * ng

    def emit_g(G, left, right):
        outer[G] = (left, right)

    zero1 = jnp.zeros((1, nl), F32)
    _chain(ng, lambda G: tuple(x[G : G + 1] for x in acc), emit_g, zero1, zero1)
    left_g = jnp.concatenate([outer[G][0] for G in range(ng)], 0)
    right_g = jnp.concatenate([outer[G][1] for G in range(ng)], 0)

    def emit(j, left, right):
        for G in range(ng):
            lr_ref[G * m + j, 0, 0:1, :] = left[G : G + 1]
            lr_ref[G * m + j, 0, 1:2, :] = right[G : G + 1]

    _chain(m, lambda j: members[j], emit, left_g, right_g)


def _width_reduce(me, r_refs):
    nw = len(r_refs)
    nsub = r_refs[0].shape[0]
    out = [[None, None] for _ in range(nsub)]

    def blk(b):
        dev, q = divmod(b, nsub)
        kk = (me - dev + nw) % nw
        vals = []
        for k6 in range(6):
            val = r_refs[0][q, k6]
            for k in range(1, nw):
                val = jnp.where(kk == k, r_refs[k][q, k6], val)
            vals.append(val)
        return tuple(vals)

    def emit(b, left, right):
        dev, q = divmod(b, nsub)
        mine = me == dev
        for j, val in enumerate((left, right)):
            out[q][j] = val if out[q][j] is None else jnp.where(mine, val, out[q][j])

    _reduce_blocks(nw * nsub, blk, emit, jnp.zeros(r_refs[0].shape[2:], F32))
    return out


def _surface_kernel(scale, z_ref, sp_ref, o_ref):
    z = z_ref[...]
    acc = jnp.zeros(z.shape, F32)
    for q in range(sp_ref.shape[0]):
        acc = jnp.where(z == q, sp_ref[q], acc)
    o_ref[...] = acc * scale


def medium_parameters(x):
    t = jnp.tanh(x)
    hot = x - solidification_release * t
    cond = 1.5 - 0.5 * jnp.tanh(hot)
    slope = (1.0 - solidification_release) + solidification_release * t * t
    return hot, cond, slope


def shards(h, zones, spray_coef):
    nt, ncl, nwl = h.shape
    nc, nw = lax.axis_size("cast"), lax.axis_size("width")
    ci, wi = lax.axis_index("cast"), lax.axis_index("width")
    up_c = [(i, i + 1) for i in range(nc - 1)]
    up_w = [(i, i + 1) for i in range(nw - 1)]
    even = ci % 2 == 0
    first, last = h[:, 0, :], h[:, -1, :]
    in_chip = [(i, i ^ 1) for i in range(nc)]
    across = [(i, i + 1) for i in range(1, nc - 1, 2)] + [(i + 1, i) for i in range(1, nc - 1, 2)]
    got_a = lax.ppermute(jnp.where(even, last, first), "cast", in_chip)
    got_b = lax.ppermute(jnp.where(even, first, last), "cast", across)
    h_wl = lax.ppermute(h[:, :, -1], "width", up_w)
    h_wh = lax.ppermute(h[:, :, 0], "width", [(b, a) for a, b in up_w])

    cast_low = (ci > 0).astype(F32)
    cast_high = (ci < nc - 1).astype(F32)
    width_low = (wi > 0).astype(F32)
    width_high = (wi < nw - 1).astype(F32)
    flags = jnp.stack([cast_low, cast_high, width_low, width_high, even.astype(F32)])
    h2 = h.reshape(nt * ncl, nwl)
    outs = prep_solve(h2, got_a, got_b, zones.reshape(2 * ncl, nwl), spray_coef, flags, ncl)
    y, v, w, summ, a_c, r_c, cp_c = outs[:7]
    tlo, tmd, thi = (x.reshape(nt, ncl, nwl) for x in outs[7:])
    y, summ = edge_solve(h2, h_wl, h_wh, flags, a_c, r_c, cp_c, y, summ, ncl)
    recv = lax.all_to_all(summ.reshape(nc, nt // nc, 8, nwl), "cast", 0, 0, tiled=True)
    lr_shape = recv.shape[:2] + (2, nwl)
    lr = pl.pallas_call(_cast_reduced_kernel, out_shape=jax.ShapeDtypeStruct(lr_shape, F32))(recv)
    back = lax.all_to_all(lr, "cast", 0, 0, tiled=True).reshape(nt, 2, nwl)
    y, v, w = (x.reshape(nt, ncl, nwl) for x in (y, v, w))

    lines = nt * ncl
    nsub = 8

    def wl(x):
        return jnp.transpose(x, (2, 0, 1)).reshape(nwl, lines // 128, 128)

    wa, *wfac = wfactor(h2, h_wl, h_wh, flags, ncl, nsub)
    tfac = factor(tlo, tmd, thi, 8)
    yw, summ = width_solve(y, v, w, back, wa, wfac, nsub)
    got = [summ] + [
        lax.ppermute(summ, "width", [(i, (i + q) % nw) for i in range(nw)]) for q in range(1, nw)
    ]
    me = wi.astype(jnp.int32).reshape(1)
    return thick_solve(me, got, yw, wfac[2], wfac[3], tlo, tfac, h, nsub, 8)


def solution(mesh):
    spec = P(None, "cast", "width")
    return jax.shard_map(
        shards, mesh=mesh, in_specs=(spec, spec, P()), out_specs=spec, check_vma=False
    )
```

```python
import functools

import jax
import jax.numpy as jnp
from jax import lax
from jax.experimental import pallas as pl
from jax.experimental.pallas import tpu as pltpu
from jax.sharding import PartitionSpec as P

F32 = jnp.float32
solidification_release = 0.4
quench_medium_hotness = -2.0
SMEM_SPEC = pl.BlockSpec(memory_space=pltpu.SMEM)


def _sweep(n, subs, ld, st, a_ref, b_ref, c_ref, d_ref, y_ref, v_ref, w_ref, cp_ref, unroll, shape):
    with_vw = v_ref is not None
    zero = jnp.zeros(shape, F32)
    one = jnp.ones(shape, F32)

    def fwd(i, carries):
        out = []
        for s0, (cprev, dprev, vprev) in zip(subs, carries):
            j = s0 + i
            a = ld(a_ref, j)
            r = 1.0 / (ld(b_ref, j) - a * cprev)
            cn = ld(c_ref, j) * r
            dn = (ld(d_ref, j) - a * dprev) * r
            st(cp_ref, j, cn)
            st(y_ref, j, dn)
            if with_vw:
                vprev = -(a * vprev) * r
                st(v_ref, j, vprev)
            out.append((cn, dn, vprev))
        return tuple(out)

    carries = tuple((zero, zero, one) for _ in subs)
    if unroll is True:
        for i in range(n):
            carries = fwd(i, carries)
    else:
        carries = lax.fori_loop(0, n, fwd, carries, unroll=unroll)
    if with_vw:
        for s0, (cl, _, _) in zip(subs, carries):
            st(w_ref, s0 + n - 1, -cl)

    def bwd(jj, carries):
        i = n - 2 - jj
        out = []
        for s0, (yn, vn, wn) in zip(subs, carries):
            j = s0 + i
            cp = ld(cp_ref, j)
            yn = ld(y_ref, j) - cp * yn
            st(y_ref, j, yn)
            if with_vw:
                vn = ld(v_ref, j) - cp * vn
                wn = -cp * wn
                st(v_ref, j, vn)
                st(w_ref, j, wn)
            out.append((yn, vn, wn))
        return tuple(out)

    carries = tuple((dl, vl, -cl) for cl, dl, vl in carries)
    if unroll is True:
        for jj in range(n - 1):
            carries = bwd(jj, carries)
    else:
        lax.fori_loop(0, n - 1, bwd, carries, unroll=unroll)


def _summary_rows(ld, s0, n, y_ref, v_ref, w_ref):
    return [ld(y_ref, s0), ld(v_ref, s0), ld(w_ref, s0),
            ld(y_ref, s0 + n - 1), ld(v_ref, s0 + n - 1), ld(w_ref, s0 + n - 1)]


def _cast_kernel(n, a_ref, b_ref, c_ref, d_ref, y_ref, v_ref, w_ref, sm_ref, cp_ref):
    m = a_ref.shape[0] // n

    def ld(ref, i):
        return ref[pl.ds(i, m, stride=n), :]

    def st(ref, i, val):
        ref[pl.ds(i, m, stride=n), :] = val

    shape = (m, a_ref.shape[1])
    _sweep(n, [0], ld, st, a_ref, b_ref, c_ref, d_ref, y_ref, v_ref, w_ref, cp_ref, True, shape)
    rows = _summary_rows(ld, 0, n, y_ref, v_ref, w_ref)
    rows += [jnp.zeros(shape, F32)] * (8 - len(rows))
    for k, val in enumerate(rows):
        sm_ref[pl.ds(k, m, stride=8), :] = val


def _lead_ld(ref, i):
    return ref[i]


def _lead_st(ref, i, val):
    ref[i] = val


def _loop(n, body, carry, unroll):
    if unroll is True:
        for i in range(n):
            carry = body(i, carry)
        return carry
    return lax.fori_loop(0, n, body, carry, unroll=unroll)


def _factor(n, subs, ld, st, a_ref, b_ref, c_ref, r_ref, cp_ref, v_ref, w_ref, unroll, shape):
    zero = jnp.zeros(shape, F32)
    one = jnp.ones(shape, F32)

    def fwd(i, carries):
        out = []
        for s0, (cprev, vprev) in zip(subs, carries):
            j = s0 + i
            a = ld(a_ref, j)
            r = 1.0 / (ld(b_ref, j) - a * cprev)
            cn = ld(c_ref, j) * r
            vprev = -(a * vprev) * r
            st(r_ref, j, r)
            st(cp_ref, j, cn)
            st(v_ref, j, vprev)
            out.append((cn, vprev))
        return tuple(out)

    carries = _loop(n, fwd, tuple((zero, one) for _ in subs), unroll)
    for s0, (cl, _) in zip(subs, carries):
        st(w_ref, s0 + n - 1, -cl)

    def bwd(jj, carries):
        i = n - 2 - jj
        out = []
        for s0, (vn, wn) in zip(subs, carries):
            j = s0 + i
            cp = ld(cp_ref, j)
            vn = ld(v_ref, j) - cp * vn
            wn = -cp * wn
            st(v_ref, j, vn)
            st(w_ref, j, wn)
            out.append((vn, wn))
        return tuple(out)

    _loop(n - 1, bwd, tuple((vl, -cl) for cl, vl in carries), unroll)


def _solve_rhs(n, subs, ld, st, a_ref, r_ref, cp_ref, d_ref, y_ref, unroll, shape):
    zero = jnp.zeros(shape, F32)

    def fwd(i, carries):
        out = []
        for s0, dprev in zip(subs, carries):
            j = s0 + i
            dn = (ld(d_ref, j) - ld(a_ref, j) * dprev) * ld(r_ref, j)
            st(y_ref, j, dn)
            out.append(dn)
        return tuple(out)

    carries = _loop(n, fwd, tuple(zero for _ in subs), unroll)

    def bwd(jj, carries):
        i = n - 2 - jj
        out = []
        for s0, yn in zip(subs, carries):
            j = s0 + i
            yn = ld(y_ref, j) - ld(cp_ref, j) * yn
            st(y_ref, j, yn)
            out.append(yn)
        return tuple(out)

    _loop(n - 1, bwd, carries, unroll)


def _factor_kernel(nsub, a_ref, b_ref, c_ref, r_ref, cp_ref, v_ref, w_ref):
    n = a_ref.shape[0] // nsub
    subs = [q * n for q in range(nsub)]
    _factor(n, subs, _lead_ld, _lead_st, a_ref, b_ref, c_ref, r_ref, cp_ref, v_ref, w_ref, 4, a_ref.shape[1:])


def factor(a, b, c, nsub):
    shp = jax.ShapeDtypeStruct(a.shape, F32)
    return pl.pallas_call(functools.partial(_factor_kernel, nsub), out_shape=[shp] * 4)(a, b, c)


def _width_faces(n, c, T0, k0, s0, lane, wlo, whi, fl_ref):
    nwl = T0.shape[1]
    g_w = nwl * nwl / 4.0 * 0.5
    if wlo is None:
        wlo = (T0, k0, s0)
        whi = (T0, k0, s0)
        e_lo, e_hi = 0.0, 0.0
    else:
        e_lo, e_hi = fl_ref[2], fl_ref[3]
    Twm, kwm, swm = (jnp.where(lane == 0, b, pltpu.roll(f, 1, 1)) for f, b in zip((T0, k0, s0), wlo))
    Twp, kwp, swp = (
        jnp.where(lane == nwl - 1, b, pltpu.roll(f, nwl - 1, 1)) for f, b in zip((T0, k0, s0), whi)
    )
    gwl = g_w * (k0 + kwm) * jnp.where(lane == 0, e_lo, 1.0)
    gwh = g_w * (kwp + k0) * jnp.where(lane == nwl - 1, e_hi, 1.0)
    return Twm, swm, Twp, swp, gwl, gwh


def _prep_kernel(n, h_ref, hcl_ref, hch_ref, z_ref, sp_ref, fl_ref,
                 y_ref, v_ref, w_ref, sm_ref, a_ref, r_ref, cp_ref, ta_ref, tb_ref, tc_ref,
                 tp_ref, kp_ref, sp2_ref, b_ref, c_ref, d_ref):
    rows, nwl = h_ref.shape
    nt = rows // n
    hot, cond, slope = medium_parameters(h_ref[...])
    zpad = jnp.zeros((n, nwl), F32)
    for ref, val in ((tp_ref, hot), (kp_ref, cond), (sp2_ref, slope)):
        ref[0:n] = zpad
        ref[n : n + rows] = val
        ref[n + rows : 2 * n + rows] = zpad

    def row(ref, off):
        return ref[pl.ds(off, nt, stride=n), :]

    lane = lax.broadcasted_iota(jnp.int32, (nt, nwl), 1)
    tix = lax.broadcasted_iota(jnp.int32, (nt, nwl), 0)
    even = fl_ref[4] > 0.5
    got_a, got_b = hcl_ref[...], hch_ref[...]
    cast_lo = medium_parameters(jnp.where(even, got_b, got_a))
    cast_hi = medium_parameters(jnp.where(even, got_a, got_b))
    g_c = n * n * 4.0 * 0.5
    g_t = nt * nt / 4.0 * 0.5
    nz = sp_ref.shape[0]

    def surf_row(zr):
        acc = jnp.zeros(zr.shape, F32)
        for q in range(nz):
            acc = jnp.where(zr == q, sp_ref[q], acc)
        return acc * (nt * nt / 8.0)

    for c in range(n):
        T0, k0, s0 = (row(r, n + c) for r in (tp_ref, kp_ref, sp2_ref))
        if c == 0:
            Tm, km, sm = cast_lo
        else:
            Tm, km, sm = (row(r, n + c - 1) for r in (tp_ref, kp_ref, sp2_ref))
        if c == n - 1:
            Tq, kq, sq = cast_hi
        else:
            Tq, kq, sq = (row(r, n + c + 1) for r in (tp_ref, kp_ref, sp2_ref))
        Ttm, ktm, stm = (row(r, c) for r in (tp_ref, kp_ref, sp2_ref))
        Ttp, ktp, stp = (row(r, 2 * n + c) for r in (tp_ref, kp_ref, sp2_ref))
        Twm, _, Twp, _, gwl, gwh = _width_faces(n, c, T0, k0, s0, lane, None, None, fl_ref)
        gcl = g_c * (k0 + km)
        if c == 0:
            gcl = gcl * fl_ref[0]
        gch = g_c * (kq + k0)
        if c == n - 1:
            gch = gch * fl_ref[1]
        gtl = jnp.where(tix == 0, 0.0, g_t * (k0 + ktm))
        gth = jnp.where(tix == nt - 1, 0.0, g_t * (ktp + k0))
        s_lo = surf_row(z_ref[c : c + 1, :])
        s_hi = surf_row(z_ref[n + c : n + c + 1, :])
        rim = jnp.where(tix == 0, s_lo, jnp.where(tix == nt - 1, s_hi, 0.0))
        ex = rim * (quench_medium_hotness - T0)
        ex = ex + (gch * (Tq - T0) - gcl * (T0 - Tm))
        ex = ex + (gwh * (Twp - T0) - gwl * (T0 - Twm))
        ex = ex + (gth * (Ttp - T0) - gtl * (T0 - Ttm))
        sel = pl.ds(c, nt, stride=n)
        a_ref[sel, :] = -gcl * sm
        c_ref[sel, :] = -gch * sq
        b_ref[sel, :] = 1.0 + s0 * (gcl + gch)
        d_ref[sel, :] = ex
        ta_ref[sel, :] = -gtl * stm
        tc_ref[sel, :] = -gth * stp
        tb_ref[sel, :] = 1.0 + s0 * (gtl + gth + rim)

    def ld(ref, i):
        return ref[pl.ds(i, nt, stride=n), :]

    def st(ref, i, val):
        ref[pl.ds(i, nt, stride=n), :] = val

    shape = (nt, nwl)
    _factor(n, [0], ld, st, a_ref, b_ref, c_ref, r_ref, cp_ref, v_ref, w_ref, True, shape)
    _solve_rhs(n, [0], ld, st, a_ref, r_ref, cp_ref, d_ref, y_ref, True, shape)
    rws = _summary_rows(ld, 0, n, y_ref, v_ref, w_ref)
    rws += [jnp.zeros(shape, F32)] * (8 - len(rws))
    for k, val in enumerate(rws):
        sm_ref[pl.ds(k, nt, stride=8), :] = val


def prep_solve(h2, hcl, hch, z2, spray, flags, n):
    rows, nwl = h2.shape
    nt = rows // n
    shp = jax.ShapeDtypeStruct(h2.shape, F32)
    vm = pl.BlockSpec(memory_space=pltpu.VMEM)
    pad = pltpu.VMEM((rows + 2 * n, nwl), F32)
    return pl.pallas_call(
        functools.partial(_prep_kernel, n),
        out_shape=[shp] * 3 + [jax.ShapeDtypeStruct((nt * 8, nwl), F32)] + [shp] * 6,
        in_specs=[vm] * 4 + [SMEM_SPEC, SMEM_SPEC],
        scratch_shapes=[pad, pad, pad] + [pltpu.VMEM(h2.shape, F32)] * 3,
    )(h2, hcl, hch, z2, spray, flags)


def _edge_kernel(n, h_ref, hwl_ref, hwh_ref, fl_ref, a_ref, r_ref, cp_ref, y_ref, sm_ref,
                 yo_ref, smo_ref, d_ref, e_ref):
    rows, nwl = h_ref.shape
    nt = rows // n
    lane = lax.broadcasted_iota(jnp.int32, (nt, nwl), 1)
    for c in range(n):
        sel = pl.ds(c, nt, stride=n)
        T0, k0, s0 = medium_parameters(h_ref[sel, :])
        wlo = medium_parameters(hwl_ref[:, c : c + 1])
        whi = medium_parameters(hwh_ref[:, c : c + 1])
        Twm, _, Twp, _, gwl, gwh = _width_faces(n, c, T0, k0, s0, lane, wlo, whi, fl_ref)
        edge = jnp.where(lane == 0, -gwl * (T0 - Twm), jnp.where(lane == nwl - 1, gwh * (Twp - T0), 0.0))
        d_ref[sel, :] = edge

    def ld(ref, i):
        return ref[pl.ds(i, nt, stride=n), :]

    def st(ref, i, val):
        ref[pl.ds(i, nt, stride=n), :] = val

    _solve_rhs(n, [0], ld, st, a_ref, r_ref, cp_ref, d_ref, e_ref, True, (nt, nwl))
    yo_ref[...] = y_ref[...] + e_ref[...]
    smo_ref[...] = sm_ref[...]
    smo_ref[pl.ds(0, nt, stride=8), :] = sm_ref[pl.ds(0, nt, stride=8), :] + ld(e_ref, 0)
    smo_ref[pl.ds(3, nt, stride=8), :] = sm_ref[pl.ds(3, nt, stride=8), :] + ld(e_ref, n - 1)


def edge_solve(h2, hwl, hwh, flags, a, r, cp, y, sm, n):
    vm = pl.BlockSpec(memory_space=pltpu.VMEM)
    return pl.pallas_call(
        functools.partial(_edge_kernel, n),
        out_shape=[jax.ShapeDtypeStruct(y.shape, F32), jax.ShapeDtypeStruct(sm.shape, F32)],
        in_specs=[vm] * 3 + [SMEM_SPEC] + [vm] * 5,
        scratch_shapes=[pltpu.VMEM(y.shape, F32)] * 2,
    )(h2, hwl, hwh, flags, a, r, cp, y, sm)


def _wfactor_kernel(n, nsub, h_ref, hwl_ref, hwh_ref, fl_ref, a_ref, r_ref, cp_ref, v_ref, w_ref,
                    vws_ref, at_ref, bt_ref, ct_ref, b_ref, c_ref):
    rows, nwl = h_ref.shape
    nt = rows // n
    lane = lax.broadcasted_iota(jnp.int32, (nt, nwl), 1)
    for c in range(n):
        sel = pl.ds(c, nt, stride=n)
        T0, k0, s0 = medium_parameters(h_ref[sel, :])
        wlo = medium_parameters(hwl_ref[:, c : c + 1])
        whi = medium_parameters(hwh_ref[:, c : c + 1])
        _, swm, _, swp, gwl, gwh = _width_faces(n, c, T0, k0, s0, lane, wlo, whi, fl_ref)
        at_ref[sel, :] = -gwl * swm
        ct_ref[sel, :] = -gwh * swp
        bt_ref[sel, :] = 1.0 + s0 * (gwl + gwh)
    for src, dst in ((at_ref, a_ref), (bt_ref, b_ref), (ct_ref, c_ref)):
        for q in range(dst.shape[1]):
            dst[:, q, :] = src[q * 128 : (q + 1) * 128, :].T
    m = a_ref.shape[0] // nsub
    subs = [q * m for q in range(nsub)]
    _factor(m, subs, _lead_ld, _lead_st, a_ref, b_ref, c_ref, r_ref, cp_ref, v_ref, w_ref, 4, a_ref.shape[1:])
    for q, s0 in enumerate(subs):
        for k, val in enumerate((v_ref[s0], w_ref[s0], v_ref[s0 + m - 1], w_ref[s0 + m - 1])):
            vws_ref[q, k] = val


def wfactor(h2, hwl, hwh, flags, n, nsub):
    rows, nwl = h2.shape
    wshape = (nwl, rows // 128, 128)
    shp = jax.ShapeDtypeStruct(wshape, F32)
    vm = pl.BlockSpec(memory_space=pltpu.VMEM)
    return pl.pallas_call(
        functools.partial(_wfactor_kernel, n, nsub),
        out_shape=[shp] * 5 + [jax.ShapeDtypeStruct((nsub, 4) + wshape[1:], F32)],
        in_specs=[vm] * 3 + [SMEM_SPEC],
        scratch_shapes=[pltpu.VMEM(h2.shape, F32)] * 3 + [pltpu.VMEM(wshape, F32)] * 2,
    )(h2, hwl, hwh, flags)


def _width_kernel(nsub, yc_ref, vc_ref, wc_ref, bk_ref, a_ref, r_ref, cp_ref, vws_ref,
                  y_ref, sm_ref, d_ref):
    sc = yc_ref[...] + vc_ref[...] * bk_ref[:, 0:1, :] + wc_ref[...] * bk_ref[:, 1:2, :]
    nt, ncl, nwl = sc.shape
    sc = sc.reshape(nt * ncl, nwl)
    for q in range(d_ref.shape[1]):
        d_ref[:, q, :] = sc[q * 128 : (q + 1) * 128, :].T
    n = a_ref.shape[0] // nsub
    subs = [q * n for q in range(nsub)]
    _solve_rhs(n, subs, _lead_ld, _lead_st, a_ref, r_ref, cp_ref, d_ref, y_ref, 4, a_ref.shape[1:])
    for q, s0 in enumerate(subs):
        rows = (y_ref[s0], vws_ref[q, 0], vws_ref[q, 1], y_ref[s0 + n - 1], vws_ref[q, 2], vws_ref[q, 3])
        for k, val in enumerate(rows):
            sm_ref[q, k] = val


def _thick_kernel(nsub, tsub, nw, me_ref, *refs):
    r_refs = refs[:nw]
    (yw_ref, vw_ref, ww_ref, a_ref, r_ref, cp_ref, v_ref, w_ref, h_ref,
     o_ref, sw_ref, d_ref, y_ref) = refs[nw:]
    lrw = _width_reduce(me_ref[0], r_refs)
    m = yw_ref.shape[0] // nsub
    for q in range(nsub):
        sl = slice(q * m, (q + 1) * m)
        sw_ref[sl] = yw_ref[sl] + vw_ref[sl] * lrw[q][0] + ww_ref[sl] * lrw[q][1]
    nt, ncl, nwl = a_ref.shape
    per_q = 128 // ncl
    for q in range(sw_ref.shape[1]):
        d_ref[q * per_q : (q + 1) * per_q] = sw_ref[:, q, :].T.reshape(per_q, ncl, nwl)
    n = nt // tsub
    subs = [q * n for q in range(tsub)]
    shape = a_ref.shape[1:]
    _solve_rhs(n, subs, _lead_ld, _lead_st, a_ref, r_ref, cp_ref, d_ref, y_ref, 4, shape)
    sums = [tuple(_summary_rows(_lead_ld, s0, n, y_ref, v_ref, w_ref)) for s0 in subs]
    lrs = [None] * tsub

    def emit(p, left, right):
        lrs[p] = (left, right)

    _reduce_blocks(tsub, lambda p: sums[p], emit, jnp.zeros(shape, F32))
    for q, s0 in enumerate(subs):
        sl = slice(s0, s0 + n)
        left, right = lrs[q]
        o_ref[sl] = h_ref[sl] + (y_ref[sl] + v_ref[sl] * left + w_ref[sl] * right)


def cast_solve(a, b, c, d, n):
    shp = jax.ShapeDtypeStruct(a.shape, F32)
    m = a.shape[0] // n
    return pl.pallas_call(
        functools.partial(_cast_kernel, n),
        out_shape=[shp, shp, shp, jax.ShapeDtypeStruct((m * 8, a.shape[1]), F32)],
        scratch_shapes=[pltpu.VMEM(a.shape, F32)],
    )(a, b, c, d)


def width_solve(yc, vc, wc, bk, a, fac, nsub):
    shp = jax.ShapeDtypeStruct(a.shape, F32)
    return pl.pallas_call(
        functools.partial(_width_kernel, nsub),
        out_shape=[shp, jax.ShapeDtypeStruct((nsub, 6) + a.shape[1:], F32)],
        scratch_shapes=[pltpu.VMEM(a.shape, F32)],
    )(yc, vc, wc, bk, a, *fac)


def thick_solve(me, got, yw, vw, ww, a, fac, h, nsub, tsub):
    vm = pl.BlockSpec(memory_space=pltpu.VMEM)
    return pl.pallas_call(
        functools.partial(_thick_kernel, nsub, tsub, len(got)),
        out_shape=jax.ShapeDtypeStruct(a.shape, F32),
        in_specs=[SMEM_SPEC] + [vm] * (len(got) + 9),
        scratch_shapes=[pltpu.VMEM(yw.shape, F32)] + [pltpu.VMEM(a.shape, F32)] * 2,
    )(me, *got, yw, vw, ww, a, *fac, h)


def _reduce_blocks(nb, blk, emit, zero):
    pp, qq = zero, zero
    saved = []
    for p in range(nb):
        y0, v0, w0, yn, vn, wn = blk(p)
        rd = 1.0 / (1.0 - v0 * qq)
        fa = (y0 + v0 * pp) * rd
        fb = w0 * rd
        saved.append((fa, fb, pp, qq))
        pp, qq = yn + vn * (pp + qq * fa), wn + vn * qq * fb
    f_next = zero
    for p in range(nb - 1, -1, -1):
        fa, fb, pp, qq = saved[p]
        f = fa + fb * f_next
        emit(p, pp + qq * f, f_next)
        f_next = f


def _merge(A, B):
    yA0, vA0, wA0, yAn, vAn, wAn = A
    yB0, vB0, wB0, yBn, vBn, wBn = B
    rd = 1.0 / (1.0 - wAn * vB0)
    ey = (yAn + wAn * yB0) * rd
    ev = vAn * rd
    ew = wAn * wB0 * rd
    fy = yB0 + vB0 * ey
    fv = vB0 * ev
    fw = wB0 + vB0 * ew
    return (yA0 + wA0 * fy, vA0 + wA0 * fv, wA0 * fw, yBn + vBn * ey, vBn * ev, wBn + vBn * ew)


def _chain(nb, blk, emit, left, right):
    pp, qq = left, jnp.zeros_like(left)
    saved = []
    for p in range(nb):
        y0, v0, w0, yn, vn, wn = blk(p)
        rd = 1.0 / (1.0 - v0 * qq)
        fa = (y0 + v0 * pp) * rd
        fb = w0 * rd
        saved.append((fa, fb, pp, qq))
        pp, qq = yn + vn * (pp + qq * fa), wn + vn * qq * fb
    f_next = right
    for p in range(nb - 1, -1, -1):
        fa, fb, pp, qq = saved[p]
        f = fa + fb * f_next
        emit(p, pp + qq * f, f_next)
        f_next = f


def _cast_reduced_kernel(s_ref, lr_ref):
    nb, g, _, nl = s_ref.shape
    ng = 8
    if g != 1 or nb % ng:
        def blk(p):
            return tuple(s_ref[p, :, k, :] for k in range(6))

        def emit(p, left, right):
            lr_ref[p, :, 0:1, :] = left[:, None]
            lr_ref[p, :, 1:2, :] = right[:, None]

        _reduce_blocks(nb, blk, emit, jnp.zeros((g, nl), F32))
        return
    m = nb // ng

    def member(j):
        return tuple(
            jnp.concatenate([s_ref[G * m + j, 0, k : k + 1, :] for G in range(ng)], 0)
            for k in range(6)
        )

    members = [member(j) for j in range(m)]
    acc = members[0]
    for j in range(1, m):
        acc = _merge(acc, members[j])
    outer = [None] * ng

    def emit_g(G, left, right):
        outer[G] = (left, right)

    zero1 = jnp.zeros((1, nl), F32)
    _chain(ng, lambda G: tuple(x[G : G + 1] for x in acc), emit_g, zero1, zero1)
    left_g = jnp.concatenate([outer[G][0] for G in range(ng)], 0)
    right_g = jnp.concatenate([outer[G][1] for G in range(ng)], 0)

    def emit(j, left, right):
        for G in range(ng):
            lr_ref[G * m + j, 0, 0:1, :] = left[G : G + 1]
            lr_ref[G * m + j, 0, 1:2, :] = right[G : G + 1]

    _chain(m, lambda j: members[j], emit, left_g, right_g)


def _width_reduce(me, r_refs):
    nw = len(r_refs)
    nsub = r_refs[0].shape[0]
    out = [[None, None] for _ in range(nsub)]

    def blk(b):
        dev, q = divmod(b, nsub)
        kk = (me - dev + nw) % nw
        vals = []
        for k6 in range(6):
            val = r_refs[0][q, k6]
            for k in range(1, nw):
                val = jnp.where(kk == k, r_refs[k][q, k6], val)
            vals.append(val)
        return tuple(vals)

    def emit(b, left, right):
        dev, q = divmod(b, nsub)
        mine = me == dev
        for j, val in enumerate((left, right)):
            out[q][j] = val if out[q][j] is None else jnp.where(mine, val, out[q][j])

    _reduce_blocks(nw * nsub, blk, emit, jnp.zeros(r_refs[0].shape[2:], F32))
    return out


def _surface_kernel(scale, z_ref, sp_ref, o_ref):
    z = z_ref[...]
    acc = jnp.zeros(z.shape, F32)
    for q in range(sp_ref.shape[0]):
        acc = jnp.where(z == q, sp_ref[q], acc)
    o_ref[...] = acc * scale


def medium_parameters(x):
    t = jnp.tanh(x)
    hot = x - solidification_release * t
    cond = 1.5 - 0.5 * jnp.tanh(hot)
    slope = (1.0 - solidification_release) + solidification_release * t * t
    return hot, cond, slope


def shards(h, zones, spray_coef):
    nt, ncl, nwl = h.shape
    nc, nw = lax.axis_size("cast"), lax.axis_size("width")
    ci, wi = lax.axis_index("cast"), lax.axis_index("width")
    up_c = [(i, i + 1) for i in range(nc - 1)]
    up_w = [(i, i + 1) for i in range(nw - 1)]
    even = ci % 2 == 0
    first, last = h[:, 0, :], h[:, -1, :]
    in_chip = [(i, i ^ 1) for i in range(nc)]
    across = [(i, i + 1) for i in range(1, nc - 1, 2)] + [(i + 1, i) for i in range(1, nc - 1, 2)]
    got_a = lax.ppermute(jnp.where(even, last, first), "cast", in_chip)
    got_b = lax.ppermute(jnp.where(even, first, last), "cast", across)
    h_wl = lax.ppermute(h[:, :, -1], "width", up_w)
    h_wh = lax.ppermute(h[:, :, 0], "width", [(b, a) for a, b in up_w])

    cast_low = (ci > 0).astype(F32)
    cast_high = (ci < nc - 1).astype(F32)
    width_low = (wi > 0).astype(F32)
    width_high = (wi < nw - 1).astype(F32)
    flags = jnp.stack([cast_low, cast_high, width_low, width_high, even.astype(F32)])
    h2 = h.reshape(nt * ncl, nwl)
    outs = prep_solve(h2, got_a, got_b, zones.reshape(2 * ncl, nwl), spray_coef, flags, ncl)
    y, v, w, summ, a_c, r_c, cp_c = outs[:7]
    tlo, tmd, thi = (x.reshape(nt, ncl, nwl) for x in outs[7:])
    y, summ = edge_solve(h2, h_wl, h_wh, flags, a_c, r_c, cp_c, y, summ, ncl)
    recv = lax.all_to_all(summ.reshape(nc, nt // nc, 8, nwl), "cast", 0, 0, tiled=True)
    lr_shape = recv.shape[:2] + (2, nwl)
    lr = pl.pallas_call(_cast_reduced_kernel, out_shape=jax.ShapeDtypeStruct(lr_shape, F32))(recv)
    back = lax.all_to_all(lr, "cast", 0, 0, tiled=True).reshape(nt, 2, nwl)
    y, v, w = (x.reshape(nt, ncl, nwl) for x in (y, v, w))

    lines = nt * ncl
    nsub = 4

    def wl(x):
        return jnp.transpose(x, (2, 0, 1)).reshape(nwl, lines // 128, 128)

    wa, r_w, cp_w, v_w, w_w, vws = wfactor(h2, h_wl, h_wh, flags, ncl, nsub)
    wfac = (r_w, cp_w, v_w, w_w)
    tfac = factor(tlo, tmd, thi, 8)
    yw, summ = width_solve(y, v, w, back, wa, (r_w, cp_w, vws), nsub)
    got = [summ] + [
        lax.ppermute(summ, "width", [(i, (i + q) % nw) for i in range(nw)]) for q in range(1, nw)
    ]
    me = wi.astype(jnp.int32).reshape(1)
    return thick_solve(me, got, yw, wfac[2], wfac[3], tlo, tfac, h, nsub, 8)


def solution(mesh):
    spec = P(None, "cast", "width")
    return jax.shard_map(
        shards, mesh=mesh, in_specs=(spec, spec, P()), out_specs=spec, check_vma=False
    )
```

```python
import functools

import jax
import jax.numpy as jnp
from jax import lax
from jax.experimental import pallas as pl
from jax.experimental.pallas import tpu as pltpu
from jax.sharding import PartitionSpec as P

F32 = jnp.float32
solidification_release = 0.4
quench_medium_hotness = -2.0
SMEM_SPEC = pl.BlockSpec(memory_space=pltpu.SMEM)


def _sweep(n, subs, ld, st, a_ref, b_ref, c_ref, d_ref, y_ref, v_ref, w_ref, cp_ref, unroll, shape):
    with_vw = v_ref is not None
    zero = jnp.zeros(shape, F32)
    one = jnp.ones(shape, F32)

    def fwd(i, carries):
        out = []
        for s0, (cprev, dprev, vprev) in zip(subs, carries):
            j = s0 + i
            a = ld(a_ref, j)
            r = 1.0 / (ld(b_ref, j) - a * cprev)
            cn = ld(c_ref, j) * r
            dn = (ld(d_ref, j) - a * dprev) * r
            st(cp_ref, j, cn)
            st(y_ref, j, dn)
            if with_vw:
                vprev = -(a * vprev) * r
                st(v_ref, j, vprev)
            out.append((cn, dn, vprev))
        return tuple(out)

    carries = tuple((zero, zero, one) for _ in subs)
    if unroll is True:
        for i in range(n):
            carries = fwd(i, carries)
    else:
        carries = lax.fori_loop(0, n, fwd, carries, unroll=unroll)
    if with_vw:
        for s0, (cl, _, _) in zip(subs, carries):
            st(w_ref, s0 + n - 1, -cl)

    def bwd(jj, carries):
        i = n - 2 - jj
        out = []
        for s0, (yn, vn, wn) in zip(subs, carries):
            j = s0 + i
            cp = ld(cp_ref, j)
            yn = ld(y_ref, j) - cp * yn
            st(y_ref, j, yn)
            if with_vw:
                vn = ld(v_ref, j) - cp * vn
                wn = -cp * wn
                st(v_ref, j, vn)
                st(w_ref, j, wn)
            out.append((yn, vn, wn))
        return tuple(out)

    carries = tuple((dl, vl, -cl) for cl, dl, vl in carries)
    if unroll is True:
        for jj in range(n - 1):
            carries = bwd(jj, carries)
    else:
        lax.fori_loop(0, n - 1, bwd, carries, unroll=unroll)


def _summary_rows(ld, s0, n, y_ref, v_ref, w_ref):
    return [ld(y_ref, s0), ld(v_ref, s0), ld(w_ref, s0),
            ld(y_ref, s0 + n - 1), ld(v_ref, s0 + n - 1), ld(w_ref, s0 + n - 1)]


def _cast_kernel(n, a_ref, b_ref, c_ref, d_ref, y_ref, v_ref, w_ref, sm_ref, cp_ref):
    m = a_ref.shape[0] // n

    def ld(ref, i):
        return ref[pl.ds(i, m, stride=n), :]

    def st(ref, i, val):
        ref[pl.ds(i, m, stride=n), :] = val

    shape = (m, a_ref.shape[1])
    _sweep(n, [0], ld, st, a_ref, b_ref, c_ref, d_ref, y_ref, v_ref, w_ref, cp_ref, True, shape)
    rows = _summary_rows(ld, 0, n, y_ref, v_ref, w_ref)
    rows += [jnp.zeros(shape, F32)] * (8 - len(rows))
    for k, val in enumerate(rows):
        sm_ref[pl.ds(k, m, stride=8), :] = val


def _lead_ld(ref, i):
    return ref[i]


def _lead_st(ref, i, val):
    ref[i] = val


def _loop(n, body, carry, unroll):
    if unroll is True:
        for i in range(n):
            carry = body(i, carry)
        return carry
    return lax.fori_loop(0, n, body, carry, unroll=unroll)


def _factor(n, subs, ld, st, a_ref, b_ref, c_ref, r_ref, cp_ref, v_ref, w_ref, unroll, shape):
    zero = jnp.zeros(shape, F32)
    one = jnp.ones(shape, F32)

    def fwd(i, carries):
        out = []
        for s0, (cprev, vprev) in zip(subs, carries):
            j = s0 + i
            a = ld(a_ref, j)
            r = 1.0 / (ld(b_ref, j) - a * cprev)
            cn = ld(c_ref, j) * r
            vprev = -(a * vprev) * r
            st(r_ref, j, r)
            st(cp_ref, j, cn)
            st(v_ref, j, vprev)
            out.append((cn, vprev))
        return tuple(out)

    carries = _loop(n, fwd, tuple((zero, one) for _ in subs), unroll)
    for s0, (cl, _) in zip(subs, carries):
        st(w_ref, s0 + n - 1, -cl)

    def bwd(jj, carries):
        i = n - 2 - jj
        out = []
        for s0, (vn, wn) in zip(subs, carries):
            j = s0 + i
            cp = ld(cp_ref, j)
            vn = ld(v_ref, j) - cp * vn
            wn = -cp * wn
            st(v_ref, j, vn)
            st(w_ref, j, wn)
            out.append((vn, wn))
        return tuple(out)

    _loop(n - 1, bwd, tuple((vl, -cl) for cl, vl in carries), unroll)


def _solve_rhs(n, subs, ld, st, a_ref, r_ref, cp_ref, d_ref, y_ref, unroll, shape):
    zero = jnp.zeros(shape, F32)

    def fwd(i, carries):
        out = []
        for s0, dprev in zip(subs, carries):
            j = s0 + i
            dn = (ld(d_ref, j) - ld(a_ref, j) * dprev) * ld(r_ref, j)
            st(y_ref, j, dn)
            out.append(dn)
        return tuple(out)

    carries = _loop(n, fwd, tuple(zero for _ in subs), unroll)

    def bwd(jj, carries):
        i = n - 2 - jj
        out = []
        for s0, yn in zip(subs, carries):
            j = s0 + i
            yn = ld(y_ref, j) - ld(cp_ref, j) * yn
            st(y_ref, j, yn)
            out.append(yn)
        return tuple(out)

    _loop(n - 1, bwd, carries, unroll)


def _factor_kernel(nsub, a_ref, b_ref, c_ref, r_ref, cp_ref, v_ref, w_ref):
    n = a_ref.shape[0] // nsub
    subs = [q * n for q in range(nsub)]
    _factor(n, subs, _lead_ld, _lead_st, a_ref, b_ref, c_ref, r_ref, cp_ref, v_ref, w_ref, 4, a_ref.shape[1:])


def factor(a, b, c, nsub):
    shp = jax.ShapeDtypeStruct(a.shape, F32)
    return pl.pallas_call(functools.partial(_factor_kernel, nsub), out_shape=[shp] * 4)(a, b, c)


def _width_faces(n, c, T0, k0, s0, lane, wlo, whi, fl_ref):
    nwl = T0.shape[1]
    g_w = nwl * nwl / 4.0 * 0.5
    if wlo is None:
        wlo = (T0, k0, s0)
        whi = (T0, k0, s0)
        e_lo, e_hi = 0.0, 0.0
    else:
        e_lo, e_hi = fl_ref[2], fl_ref[3]
    Twm, kwm, swm = (jnp.where(lane == 0, b, pltpu.roll(f, 1, 1)) for f, b in zip((T0, k0, s0), wlo))
    Twp, kwp, swp = (
        jnp.where(lane == nwl - 1, b, pltpu.roll(f, nwl - 1, 1)) for f, b in zip((T0, k0, s0), whi)
    )
    gwl = g_w * (k0 + kwm) * jnp.where(lane == 0, e_lo, 1.0)
    gwh = g_w * (kwp + k0) * jnp.where(lane == nwl - 1, e_hi, 1.0)
    return Twm, swm, Twp, swp, gwl, gwh


def _prep_kernel(n, h_ref, hcl_ref, hch_ref, z_ref, sp_ref, fl_ref,
                 y_ref, v_ref, w_ref, sm_ref, a_ref, r_ref, cp_ref, ta_ref, tb_ref, tc_ref,
                 tp_ref, kp_ref, sp2_ref, b_ref, c_ref, d_ref):
    rows, nwl = h_ref.shape
    nt = rows // n
    hot, cond, slope = medium_parameters(h_ref[...])
    zpad = jnp.zeros((n, nwl), F32)
    for ref, val in ((tp_ref, hot), (kp_ref, cond), (sp2_ref, slope)):
        ref[0:n] = zpad
        ref[n : n + rows] = val
        ref[n + rows : 2 * n + rows] = zpad

    def row(ref, off):
        return ref[pl.ds(off, nt, stride=n), :]

    lane = lax.broadcasted_iota(jnp.int32, (nt, nwl), 1)
    tix = lax.broadcasted_iota(jnp.int32, (nt, nwl), 0)
    even = fl_ref[4] > 0.5
    got_a, got_b = hcl_ref[...], hch_ref[...]
    cast_lo = medium_parameters(jnp.where(even, got_b, got_a))
    cast_hi = medium_parameters(jnp.where(even, got_a, got_b))
    g_c = n * n * 4.0 * 0.5
    g_t = nt * nt / 4.0 * 0.5
    nz = sp_ref.shape[0]

    def surf_row(zr):
        acc = jnp.zeros(zr.shape, F32)
        for q in range(nz):
            acc = jnp.where(zr == q, sp_ref[q], acc)
        return acc * (nt * nt / 8.0)

    for c in range(n):
        T0, k0, s0 = (row(r, n + c) for r in (tp_ref, kp_ref, sp2_ref))
        if c == 0:
            Tm, km, sm = cast_lo
        else:
            Tm, km, sm = (row(r, n + c - 1) for r in (tp_ref, kp_ref, sp2_ref))
        if c == n - 1:
            Tq, kq, sq = cast_hi
        else:
            Tq, kq, sq = (row(r, n + c + 1) for r in (tp_ref, kp_ref, sp2_ref))
        Ttm, ktm, stm = (row(r, c) for r in (tp_ref, kp_ref, sp2_ref))
        Ttp, ktp, stp = (row(r, 2 * n + c) for r in (tp_ref, kp_ref, sp2_ref))
        Twm, _, Twp, _, gwl, gwh = _width_faces(n, c, T0, k0, s0, lane, None, None, fl_ref)
        gcl = g_c * (k0 + km)
        if c == 0:
            gcl = gcl * fl_ref[0]
        gch = g_c * (kq + k0)
        if c == n - 1:
            gch = gch * fl_ref[1]
        gtl = jnp.where(tix == 0, 0.0, g_t * (k0 + ktm))
        gth = jnp.where(tix == nt - 1, 0.0, g_t * (ktp + k0))
        s_lo = surf_row(z_ref[c : c + 1, :])
        s_hi = surf_row(z_ref[n + c : n + c + 1, :])
        rim = jnp.where(tix == 0, s_lo, jnp.where(tix == nt - 1, s_hi, 0.0))
        ex = rim * (quench_medium_hotness - T0)
        ex = ex + (gch * (Tq - T0) - gcl * (T0 - Tm))
        ex = ex + (gwh * (Twp - T0) - gwl * (T0 - Twm))
        ex = ex + (gth * (Ttp - T0) - gtl * (T0 - Ttm))
        sel = pl.ds(c, nt, stride=n)
        a_ref[sel, :] = -gcl * sm
        c_ref[sel, :] = -gch * sq
        b_ref[sel, :] = 1.0 + s0 * (gcl + gch)
        d_ref[sel, :] = ex
        ta_ref[sel, :] = -gtl * stm
        tc_ref[sel, :] = -gth * stp
        tb_ref[sel, :] = 1.0 + s0 * (gtl + gth + rim)

    def ld(ref, i):
        return ref[pl.ds(i, nt, stride=n), :]

    def st(ref, i, val):
        ref[pl.ds(i, nt, stride=n), :] = val

    shape = (nt, nwl)
    _factor(n, [0], ld, st, a_ref, b_ref, c_ref, r_ref, cp_ref, v_ref, w_ref, True, shape)
    _solve_rhs(n, [0], ld, st, a_ref, r_ref, cp_ref, d_ref, y_ref, True, shape)
    rws = _summary_rows(ld, 0, n, y_ref, v_ref, w_ref)
    rws += [jnp.zeros(shape, F32)] * (8 - len(rws))
    for k, val in enumerate(rws):
        sm_ref[pl.ds(k, nt, stride=8), :] = val


def prep_solve(h2, hcl, hch, z2, spray, flags, n):
    rows, nwl = h2.shape
    nt = rows // n
    shp = jax.ShapeDtypeStruct(h2.shape, F32)
    vm = pl.BlockSpec(memory_space=pltpu.VMEM)
    pad = pltpu.VMEM((rows + 2 * n, nwl), F32)
    return pl.pallas_call(
        functools.partial(_prep_kernel, n),
        out_shape=[shp] * 3 + [jax.ShapeDtypeStruct((nt * 8, nwl), F32)] + [shp] * 6,
        in_specs=[vm] * 4 + [SMEM_SPEC, SMEM_SPEC],
        scratch_shapes=[pad, pad, pad] + [pltpu.VMEM(h2.shape, F32)] * 3,
    )(h2, hcl, hch, z2, spray, flags)


def _edge_kernel(n, h_ref, hwl_ref, hwh_ref, fl_ref, a_ref, r_ref, cp_ref, y_ref, sm_ref,
                 yo_ref, smo_ref, d_ref, e_ref):
    rows, nwl = h_ref.shape
    nt = rows // n
    lane = lax.broadcasted_iota(jnp.int32, (nt, nwl), 1)
    for c in range(n):
        sel = pl.ds(c, nt, stride=n)
        T0, k0, s0 = medium_parameters(h_ref[sel, :])
        wlo = medium_parameters(hwl_ref[:, c : c + 1])
        whi = medium_parameters(hwh_ref[:, c : c + 1])
        Twm, _, Twp, _, gwl, gwh = _width_faces(n, c, T0, k0, s0, lane, wlo, whi, fl_ref)
        edge = jnp.where(lane == 0, -gwl * (T0 - Twm), jnp.where(lane == nwl - 1, gwh * (Twp - T0), 0.0))
        d_ref[sel, :] = edge

    def ld(ref, i):
        return ref[pl.ds(i, nt, stride=n), :]

    def st(ref, i, val):
        ref[pl.ds(i, nt, stride=n), :] = val

    _solve_rhs(n, [0], ld, st, a_ref, r_ref, cp_ref, d_ref, e_ref, True, (nt, nwl))
    yo_ref[...] = y_ref[...] + e_ref[...]
    smo_ref[...] = sm_ref[...]
    smo_ref[pl.ds(0, nt, stride=8), :] = sm_ref[pl.ds(0, nt, stride=8), :] + ld(e_ref, 0)
    smo_ref[pl.ds(3, nt, stride=8), :] = sm_ref[pl.ds(3, nt, stride=8), :] + ld(e_ref, n - 1)


def edge_solve(h2, hwl, hwh, flags, a, r, cp, y, sm, n):
    vm = pl.BlockSpec(memory_space=pltpu.VMEM)
    return pl.pallas_call(
        functools.partial(_edge_kernel, n),
        out_shape=[jax.ShapeDtypeStruct(y.shape, F32), jax.ShapeDtypeStruct(sm.shape, F32)],
        in_specs=[vm] * 3 + [SMEM_SPEC] + [vm] * 5,
        scratch_shapes=[pltpu.VMEM(y.shape, F32)] * 2,
    )(h2, hwl, hwh, flags, a, r, cp, y, sm)


def _wfactor_kernel(n, nsub, h_ref, hwl_ref, hwh_ref, fl_ref, a_ref, r_ref, cp_ref, v_ref, w_ref,
                    vws_ref, at_ref, bt_ref, ct_ref, b_ref, c_ref):
    rows, nwl = h_ref.shape
    nt = rows // n
    lane = lax.broadcasted_iota(jnp.int32, (nt, nwl), 1)
    for c in range(n):
        sel = pl.ds(c, nt, stride=n)
        T0, k0, s0 = medium_parameters(h_ref[sel, :])
        wlo = medium_parameters(hwl_ref[:, c : c + 1])
        whi = medium_parameters(hwh_ref[:, c : c + 1])
        _, swm, _, swp, gwl, gwh = _width_faces(n, c, T0, k0, s0, lane, wlo, whi, fl_ref)
        at_ref[sel, :] = -gwl * swm
        ct_ref[sel, :] = -gwh * swp
        bt_ref[sel, :] = 1.0 + s0 * (gwl + gwh)
    for src, dst in ((at_ref, a_ref), (bt_ref, b_ref), (ct_ref, c_ref)):
        for q in range(dst.shape[1]):
            dst[:, q, :] = src[q * 128 : (q + 1) * 128, :].T
    m = a_ref.shape[0] // nsub
    subs = [q * m for q in range(nsub)]
    _factor(m, subs, _lead_ld, _lead_st, a_ref, b_ref, c_ref, r_ref, cp_ref, v_ref, w_ref, 4, a_ref.shape[1:])
    for q, s0 in enumerate(subs):
        for k, val in enumerate((v_ref[s0], w_ref[s0], v_ref[s0 + m - 1], w_ref[s0 + m - 1])):
            vws_ref[q, k] = val


def wfactor(h2, hwl, hwh, flags, n, nsub):
    rows, nwl = h2.shape
    wshape = (nwl, rows // 128, 128)
    shp = jax.ShapeDtypeStruct(wshape, F32)
    vm = pl.BlockSpec(memory_space=pltpu.VMEM)
    return pl.pallas_call(
        functools.partial(_wfactor_kernel, n, nsub),
        out_shape=[shp] * 5 + [jax.ShapeDtypeStruct((nsub, 4) + wshape[1:], F32)],
        in_specs=[vm] * 3 + [SMEM_SPEC],
        scratch_shapes=[pltpu.VMEM(h2.shape, F32)] * 3 + [pltpu.VMEM(wshape, F32)] * 2,
    )(h2, hwl, hwh, flags)


def _width_kernel(nsub, yc_ref, vc_ref, wc_ref, bk_ref, a_ref, r_ref, cp_ref, vws_ref,
                  y_ref, sm_ref, d_ref):
    sc = yc_ref[...] + vc_ref[...] * bk_ref[:, 0:1, :] + wc_ref[...] * bk_ref[:, 1:2, :]
    nt, ncl, nwl = sc.shape
    sc = sc.reshape(nt * ncl, nwl)
    for q in range(d_ref.shape[1]):
        d_ref[:, q, :] = sc[q * 128 : (q + 1) * 128, :].T
    n = a_ref.shape[0] // nsub
    subs = [q * n for q in range(nsub)]
    _solve_rhs(n, subs, _lead_ld, _lead_st, a_ref, r_ref, cp_ref, d_ref, y_ref, 4, a_ref.shape[1:])
    for q, s0 in enumerate(subs):
        rows = (y_ref[s0], vws_ref[q, 0], vws_ref[q, 1], y_ref[s0 + n - 1], vws_ref[q, 2], vws_ref[q, 3])
        for k, val in enumerate(rows):
            sm_ref[q, k] = val


def _thick_kernel(nsub, tsub, nw, me_ref, *refs):
    r_refs = refs[:nw]
    (yw_ref, vw_ref, ww_ref, a_ref, r_ref, cp_ref, v_ref, w_ref, h_ref,
     o_ref, sw_ref, d_ref, y_ref) = refs[nw:]
    lrw = _width_reduce(me_ref[0], r_refs)
    m = yw_ref.shape[0] // nsub
    for q in range(nsub):
        sl = slice(q * m, (q + 1) * m)
        sw_ref[sl] = yw_ref[sl] + vw_ref[sl] * lrw[q][0] + ww_ref[sl] * lrw[q][1]
    nt, ncl, nwl = a_ref.shape
    per_q = 128 // ncl
    for q in range(sw_ref.shape[1]):
        d_ref[q * per_q : (q + 1) * per_q] = sw_ref[:, q, :].T.reshape(per_q, ncl, nwl)
    n = nt // tsub
    subs = [q * n for q in range(tsub)]
    shape = a_ref.shape[1:]
    _solve_rhs(n, subs, _lead_ld, _lead_st, a_ref, r_ref, cp_ref, d_ref, y_ref, 4, shape)
    sums = [tuple(_summary_rows(_lead_ld, s0, n, y_ref, v_ref, w_ref)) for s0 in subs]
    lrs = [None] * tsub

    def emit(p, left, right):
        lrs[p] = (left, right)

    _reduce_blocks(tsub, lambda p: sums[p], emit, jnp.zeros(shape, F32))
    for q, s0 in enumerate(subs):
        sl = slice(s0, s0 + n)
        left, right = lrs[q]
        o_ref[sl] = h_ref[sl] + (y_ref[sl] + v_ref[sl] * left + w_ref[sl] * right)


def cast_solve(a, b, c, d, n):
    shp = jax.ShapeDtypeStruct(a.shape, F32)
    m = a.shape[0] // n
    return pl.pallas_call(
        functools.partial(_cast_kernel, n),
        out_shape=[shp, shp, shp, jax.ShapeDtypeStruct((m * 8, a.shape[1]), F32)],
        scratch_shapes=[pltpu.VMEM(a.shape, F32)],
    )(a, b, c, d)


def width_solve(yc, vc, wc, bk, a, fac, nsub):
    shp = jax.ShapeDtypeStruct(a.shape, F32)
    return pl.pallas_call(
        functools.partial(_width_kernel, nsub),
        out_shape=[shp, jax.ShapeDtypeStruct((nsub, 6) + a.shape[1:], F32)],
        scratch_shapes=[pltpu.VMEM(a.shape, F32)],
    )(yc, vc, wc, bk, a, *fac)


def thick_solve(me, got, yw, vw, ww, a, fac, h, nsub, tsub):
    vm = pl.BlockSpec(memory_space=pltpu.VMEM)
    return pl.pallas_call(
        functools.partial(_thick_kernel, nsub, tsub, len(got)),
        out_shape=jax.ShapeDtypeStruct(a.shape, F32),
        in_specs=[SMEM_SPEC] + [vm] * (len(got) + 9),
        scratch_shapes=[pltpu.VMEM(yw.shape, F32)] + [pltpu.VMEM(a.shape, F32)] * 2,
    )(me, *got, yw, vw, ww, a, *fac, h)


def _reduce_blocks(nb, blk, emit, zero):
    pp, qq = zero, zero
    saved = []
    for p in range(nb):
        y0, v0, w0, yn, vn, wn = blk(p)
        rd = 1.0 / (1.0 - v0 * qq)
        fa = (y0 + v0 * pp) * rd
        fb = w0 * rd
        saved.append((fa, fb, pp, qq))
        pp, qq = yn + vn * (pp + qq * fa), wn + vn * qq * fb
    f_next = zero
    for p in range(nb - 1, -1, -1):
        fa, fb, pp, qq = saved[p]
        f = fa + fb * f_next
        emit(p, pp + qq * f, f_next)
        f_next = f


def _merge(A, B):
    yA0, vA0, wA0, yAn, vAn, wAn = A
    yB0, vB0, wB0, yBn, vBn, wBn = B
    rd = 1.0 / (1.0 - wAn * vB0)
    ey = (yAn + wAn * yB0) * rd
    ev = vAn * rd
    ew = wAn * wB0 * rd
    fy = yB0 + vB0 * ey
    fv = vB0 * ev
    fw = wB0 + vB0 * ew
    return (yA0 + wA0 * fy, vA0 + wA0 * fv, wA0 * fw, yBn + vBn * ey, vBn * ev, wBn + vBn * ew)


def _chain(nb, blk, emit, left, right):
    pp, qq = left, jnp.zeros_like(left)
    saved = []
    for p in range(nb):
        y0, v0, w0, yn, vn, wn = blk(p)
        rd = 1.0 / (1.0 - v0 * qq)
        fa = (y0 + v0 * pp) * rd
        fb = w0 * rd
        saved.append((fa, fb, pp, qq))
        pp, qq = yn + vn * (pp + qq * fa), wn + vn * qq * fb
    f_next = right
    for p in range(nb - 1, -1, -1):
        fa, fb, pp, qq = saved[p]
        f = fa + fb * f_next
        emit(p, pp + qq * f, f_next)
        f_next = f


def _cast_reduced_kernel(s_ref, lr_ref):
    nb, g, _, nl = s_ref.shape
    ng = 8
    if g != 1 or nb % ng:
        def blk(p):
            return tuple(s_ref[p, :, k, :] for k in range(6))

        def emit(p, left, right):
            lr_ref[p, :, 0:1, :] = left[:, None]
            lr_ref[p, :, 1:2, :] = right[:, None]

        _reduce_blocks(nb, blk, emit, jnp.zeros((g, nl), F32))
        return
    m = nb // ng

    def member(j):
        return tuple(
            jnp.concatenate([s_ref[G * m + j, 0, k : k + 1, :] for G in range(ng)], 0)
            for k in range(6)
        )

    members = [member(j) for j in range(m)]
    acc = members[0]
    for j in range(1, m):
        acc = _merge(acc, members[j])
    outer = [None] * ng

    def emit_g(G, left, right):
        outer[G] = (left, right)

    zero1 = jnp.zeros((1, nl), F32)
    _chain(ng, lambda G: tuple(x[G : G + 1] for x in acc), emit_g, zero1, zero1)
    left_g = jnp.concatenate([outer[G][0] for G in range(ng)], 0)
    right_g = jnp.concatenate([outer[G][1] for G in range(ng)], 0)

    def emit(j, left, right):
        for G in range(ng):
            lr_ref[G * m + j, 0, 0:1, :] = left[G : G + 1]
            lr_ref[G * m + j, 0, 1:2, :] = right[G : G + 1]

    _chain(m, lambda j: members[j], emit, left_g, right_g)


def _width_reduce(me, r_refs):
    nw = len(r_refs)
    nsub = r_refs[0].shape[0]
    out = [[None, None] for _ in range(nsub)]

    def blk(b):
        dev, q = divmod(b, nsub)
        kk = (me - dev + nw) % nw
        vals = []
        for k6 in range(6):
            val = r_refs[0][q, k6]
            for k in range(1, nw):
                val = jnp.where(kk == k, r_refs[k][q, k6], val)
            vals.append(val)
        return tuple(vals)

    def emit(b, left, right):
        dev, q = divmod(b, nsub)
        mine = me == dev
        for j, val in enumerate((left, right)):
            out[q][j] = val if out[q][j] is None else jnp.where(mine, val, out[q][j])

    _reduce_blocks(nw * nsub, blk, emit, jnp.zeros(r_refs[0].shape[2:], F32))
    return out


def _surface_kernel(scale, z_ref, sp_ref, o_ref):
    z = z_ref[...]
    acc = jnp.zeros(z.shape, F32)
    for q in range(sp_ref.shape[0]):
        acc = jnp.where(z == q, sp_ref[q], acc)
    o_ref[...] = acc * scale


def medium_parameters(x):
    t = jnp.tanh(x)
    hot = x - solidification_release * t
    cond = 1.5 - 0.5 * jnp.tanh(hot)
    slope = (1.0 - solidification_release) + solidification_release * t * t
    return hot, cond, slope


def shards(h, zones, spray_coef):
    nt, ncl, nwl = h.shape
    nc, nw = lax.axis_size("cast"), lax.axis_size("width")
    ci, wi = lax.axis_index("cast"), lax.axis_index("width")
    up_c = [(i, i + 1) for i in range(nc - 1)]
    up_w = [(i, i + 1) for i in range(nw - 1)]
    even = ci % 2 == 0
    first, last = h[:, 0, :], h[:, -1, :]
    in_chip = [(i, i ^ 1) for i in range(nc)]
    across = [(i, i + 1) for i in range(1, nc - 1, 2)] + [(i + 1, i) for i in range(1, nc - 1, 2)]
    got_a = lax.ppermute(jnp.where(even, last, first), "cast", in_chip)
    got_b = lax.ppermute(jnp.where(even, first, last), "cast", across)
    h_wl = lax.ppermute(h[:, :, -1], "width", up_w)
    h_wh = lax.ppermute(h[:, :, 0], "width", [(b, a) for a, b in up_w])

    cast_low = (ci > 0).astype(F32)
    cast_high = (ci < nc - 1).astype(F32)
    width_low = (wi > 0).astype(F32)
    width_high = (wi < nw - 1).astype(F32)
    flags = jnp.stack([cast_low, cast_high, width_low, width_high, even.astype(F32)])
    h2 = h.reshape(nt * ncl, nwl)
    outs = prep_solve(h2, got_a, got_b, zones.reshape(2 * ncl, nwl), spray_coef, flags, ncl)
    y, v, w, summ, a_c, r_c, cp_c = outs[:7]
    tlo, tmd, thi = (x.reshape(nt, ncl, nwl) for x in outs[7:])
    y, summ = edge_solve(h2, h_wl, h_wh, flags, a_c, r_c, cp_c, y, summ, ncl)
    recv = lax.all_to_all(summ.reshape(nc, nt // nc, 8, nwl), "cast", 0, 0, tiled=True)
    lr_shape = recv.shape[:2] + (2, nwl)
    lr = pl.pallas_call(_cast_reduced_kernel, out_shape=jax.ShapeDtypeStruct(lr_shape, F32))(recv)
    back = lax.all_to_all(lr, "cast", 0, 0, tiled=True).reshape(nt, 2, nwl)
    y, v, w = (x.reshape(nt, ncl, nwl) for x in (y, v, w))

    lines = nt * ncl
    nsub = 4

    def wl(x):
        return jnp.transpose(x, (2, 0, 1)).reshape(nwl, lines // 128, 128)

    wa, r_w, cp_w, v_w, w_w, vws = wfactor(h2, h_wl, h_wh, flags, ncl, nsub)
    wfac = (r_w, cp_w, v_w, w_w)
    tfac = factor(tlo, tmd, thi, 16)
    yw, summ = width_solve(y, v, w, back, wa, (r_w, cp_w, vws), nsub)
    got = [summ] + [
        lax.ppermute(summ, "width", [(i, (i + q) % nw) for i in range(nw)]) for q in range(1, nw)
    ]
    me = wi.astype(jnp.int32).reshape(1)
    return thick_solve(me, got, yw, wfac[2], wfac[3], tlo, tfac, h, nsub, 16)


def solution(mesh):
    spec = P(None, "cast", "width")
    return jax.shard_map(
        shards, mesh=mesh, in_specs=(spec, spec, P()), out_specs=spec, check_vma=False
    )
```

```python
import functools

import jax
import jax.numpy as jnp
from jax import lax
from jax.experimental import pallas as pl
from jax.experimental.pallas import tpu as pltpu
from jax.sharding import PartitionSpec as P

F32 = jnp.float32
solidification_release = 0.4
quench_medium_hotness = -2.0
SMEM_SPEC = pl.BlockSpec(memory_space=pltpu.SMEM)


def _sweep(n, subs, ld, st, a_ref, b_ref, c_ref, d_ref, y_ref, v_ref, w_ref, cp_ref, unroll, shape):
    with_vw = v_ref is not None
    zero = jnp.zeros(shape, F32)
    one = jnp.ones(shape, F32)

    def fwd(i, carries):
        out = []
        for s0, (cprev, dprev, vprev) in zip(subs, carries):
            j = s0 + i
            a = ld(a_ref, j)
            r = 1.0 / (ld(b_ref, j) - a * cprev)
            cn = ld(c_ref, j) * r
            dn = (ld(d_ref, j) - a * dprev) * r
            st(cp_ref, j, cn)
            st(y_ref, j, dn)
            if with_vw:
                vprev = -(a * vprev) * r
                st(v_ref, j, vprev)
            out.append((cn, dn, vprev))
        return tuple(out)

    carries = tuple((zero, zero, one) for _ in subs)
    if unroll is True:
        for i in range(n):
            carries = fwd(i, carries)
    else:
        carries = lax.fori_loop(0, n, fwd, carries, unroll=unroll)
    if with_vw:
        for s0, (cl, _, _) in zip(subs, carries):
            st(w_ref, s0 + n - 1, -cl)

    def bwd(jj, carries):
        i = n - 2 - jj
        out = []
        for s0, (yn, vn, wn) in zip(subs, carries):
            j = s0 + i
            cp = ld(cp_ref, j)
            yn = ld(y_ref, j) - cp * yn
            st(y_ref, j, yn)
            if with_vw:
                vn = ld(v_ref, j) - cp * vn
                wn = -cp * wn
                st(v_ref, j, vn)
                st(w_ref, j, wn)
            out.append((yn, vn, wn))
        return tuple(out)

    carries = tuple((dl, vl, -cl) for cl, dl, vl in carries)
    if unroll is True:
        for jj in range(n - 1):
            carries = bwd(jj, carries)
    else:
        lax.fori_loop(0, n - 1, bwd, carries, unroll=unroll)


def _summary_rows(ld, s0, n, y_ref, v_ref, w_ref):
    return [ld(y_ref, s0), ld(v_ref, s0), ld(w_ref, s0),
            ld(y_ref, s0 + n - 1), ld(v_ref, s0 + n - 1), ld(w_ref, s0 + n - 1)]


def _cast_kernel(n, a_ref, b_ref, c_ref, d_ref, y_ref, v_ref, w_ref, sm_ref, cp_ref):
    m = a_ref.shape[0] // n

    def ld(ref, i):
        return ref[pl.ds(i, m, stride=n), :]

    def st(ref, i, val):
        ref[pl.ds(i, m, stride=n), :] = val

    shape = (m, a_ref.shape[1])
    _sweep(n, [0], ld, st, a_ref, b_ref, c_ref, d_ref, y_ref, v_ref, w_ref, cp_ref, True, shape)
    rows = _summary_rows(ld, 0, n, y_ref, v_ref, w_ref)
    rows += [jnp.zeros(shape, F32)] * (8 - len(rows))
    for k, val in enumerate(rows):
        sm_ref[pl.ds(k, m, stride=8), :] = val


def _lead_ld(ref, i):
    return ref[i]


def _lead_st(ref, i, val):
    ref[i] = val


def _loop(n, body, carry, unroll):
    if unroll is True:
        for i in range(n):
            carry = body(i, carry)
        return carry
    return lax.fori_loop(0, n, body, carry, unroll=unroll)


def _factor(n, subs, ld, st, a_ref, b_ref, c_ref, r_ref, cp_ref, v_ref, w_ref, unroll, shape):
    zero = jnp.zeros(shape, F32)
    one = jnp.ones(shape, F32)

    def fwd(i, carries):
        out = []
        for s0, (cprev, vprev) in zip(subs, carries):
            j = s0 + i
            a = ld(a_ref, j)
            r = 1.0 / (ld(b_ref, j) - a * cprev)
            cn = ld(c_ref, j) * r
            vprev = -(a * vprev) * r
            st(r_ref, j, r)
            st(cp_ref, j, cn)
            st(v_ref, j, vprev)
            out.append((cn, vprev))
        return tuple(out)

    carries = _loop(n, fwd, tuple((zero, one) for _ in subs), unroll)
    for s0, (cl, _) in zip(subs, carries):
        st(w_ref, s0 + n - 1, -cl)

    def bwd(jj, carries):
        i = n - 2 - jj
        out = []
        for s0, (vn, wn) in zip(subs, carries):
            j = s0 + i
            cp = ld(cp_ref, j)
            vn = ld(v_ref, j) - cp * vn
            wn = -cp * wn
            st(v_ref, j, vn)
            st(w_ref, j, wn)
            out.append((vn, wn))
        return tuple(out)

    _loop(n - 1, bwd, tuple((vl, -cl) for cl, vl in carries), unroll)


def _solve_rhs(n, subs, ld, st, a_ref, r_ref, cp_ref, d_ref, y_ref, unroll, shape):
    zero = jnp.zeros(shape, F32)

    def fwd(i, carries):
        out = []
        for s0, dprev in zip(subs, carries):
            j = s0 + i
            dn = (ld(d_ref, j) - ld(a_ref, j) * dprev) * ld(r_ref, j)
            st(y_ref, j, dn)
            out.append(dn)
        return tuple(out)

    carries = _loop(n, fwd, tuple(zero for _ in subs), unroll)

    def bwd(jj, carries):
        i = n - 2 - jj
        out = []
        for s0, yn in zip(subs, carries):
            j = s0 + i
            yn = ld(y_ref, j) - ld(cp_ref, j) * yn
            st(y_ref, j, yn)
            out.append(yn)
        return tuple(out)

    _loop(n - 1, bwd, carries, unroll)


def _factor_kernel(nsub, a_ref, b_ref, c_ref, r_ref, cp_ref, v_ref, w_ref):
    n = a_ref.shape[0] // nsub
    subs = [q * n for q in range(nsub)]
    _factor(n, subs, _lead_ld, _lead_st, a_ref, b_ref, c_ref, r_ref, cp_ref, v_ref, w_ref, 4, a_ref.shape[1:])


def factor(a, b, c, nsub):
    shp = jax.ShapeDtypeStruct(a.shape, F32)
    return pl.pallas_call(functools.partial(_factor_kernel, nsub), out_shape=[shp] * 4)(a, b, c)


def _width_faces(n, c, T0, k0, s0, lane, wlo, whi, fl_ref):
    nwl = T0.shape[1]
    g_w = nwl * nwl / 4.0 * 0.5
    if wlo is None:
        wlo = (T0, k0, s0)
        whi = (T0, k0, s0)
        e_lo, e_hi = 0.0, 0.0
    else:
        e_lo, e_hi = fl_ref[2], fl_ref[3]
    Twm, kwm, swm = (jnp.where(lane == 0, b, pltpu.roll(f, 1, 1)) for f, b in zip((T0, k0, s0), wlo))
    Twp, kwp, swp = (
        jnp.where(lane == nwl - 1, b, pltpu.roll(f, nwl - 1, 1)) for f, b in zip((T0, k0, s0), whi)
    )
    gwl = g_w * (k0 + kwm) * jnp.where(lane == 0, e_lo, 1.0)
    gwh = g_w * (kwp + k0) * jnp.where(lane == nwl - 1, e_hi, 1.0)
    return Twm, swm, Twp, swp, gwl, gwh


def _prep_kernel(n, h_ref, hcl_ref, hch_ref, z_ref, sp_ref, fl_ref,
                 y_ref, v_ref, w_ref, sm_ref, a_ref, r_ref, cp_ref, ta_ref, tb_ref, tc_ref,
                 tp_ref, kp_ref, sp2_ref, b_ref, c_ref, d_ref):
    rows, nwl = h_ref.shape
    nt = rows // n
    hot, cond, slope = medium_parameters(h_ref[...])
    zpad = jnp.zeros((n, nwl), F32)
    for ref, val in ((tp_ref, hot), (kp_ref, cond), (sp2_ref, slope)):
        ref[0:n] = zpad
        ref[n : n + rows] = val
        ref[n + rows : 2 * n + rows] = zpad

    def row(ref, off):
        return ref[pl.ds(off, nt, stride=n), :]

    lane = lax.broadcasted_iota(jnp.int32, (nt, nwl), 1)
    tix = lax.broadcasted_iota(jnp.int32, (nt, nwl), 0)
    even = fl_ref[4] > 0.5
    got_a, got_b = hcl_ref[...], hch_ref[...]
    cast_lo = medium_parameters(jnp.where(even, got_b, got_a))
    cast_hi = medium_parameters(jnp.where(even, got_a, got_b))
    g_c = n * n * 4.0 * 0.5
    g_t = nt * nt / 4.0 * 0.5
    nz = sp_ref.shape[0]

    def surf_row(zr):
        acc = jnp.zeros(zr.shape, F32)
        for q in range(nz):
            acc = jnp.where(zr == q, sp_ref[q], acc)
        return acc * (nt * nt / 8.0)

    for c in range(n):
        T0, k0, s0 = (row(r, n + c) for r in (tp_ref, kp_ref, sp2_ref))
        if c == 0:
            Tm, km, sm = cast_lo
        else:
            Tm, km, sm = (row(r, n + c - 1) for r in (tp_ref, kp_ref, sp2_ref))
        if c == n - 1:
            Tq, kq, sq = cast_hi
        else:
            Tq, kq, sq = (row(r, n + c + 1) for r in (tp_ref, kp_ref, sp2_ref))
        Ttm, ktm, stm = (row(r, c) for r in (tp_ref, kp_ref, sp2_ref))
        Ttp, ktp, stp = (row(r, 2 * n + c) for r in (tp_ref, kp_ref, sp2_ref))
        Twm, _, Twp, _, gwl, gwh = _width_faces(n, c, T0, k0, s0, lane, None, None, fl_ref)
        gcl = g_c * (k0 + km)
        if c == 0:
            gcl = gcl * fl_ref[0]
        gch = g_c * (kq + k0)
        if c == n - 1:
            gch = gch * fl_ref[1]
        gtl = jnp.where(tix == 0, 0.0, g_t * (k0 + ktm))
        gth = jnp.where(tix == nt - 1, 0.0, g_t * (ktp + k0))
        s_lo = surf_row(z_ref[c : c + 1, :])
        s_hi = surf_row(z_ref[n + c : n + c + 1, :])
        rim = jnp.where(tix == 0, s_lo, jnp.where(tix == nt - 1, s_hi, 0.0))
        ex = rim * (quench_medium_hotness - T0)
        ex = ex + (gch * (Tq - T0) - gcl * (T0 - Tm))
        ex = ex + (gwh * (Twp - T0) - gwl * (T0 - Twm))
        ex = ex + (gth * (Ttp - T0) - gtl * (T0 - Ttm))
        sel = pl.ds(c, nt, stride=n)
        a_ref[sel, :] = -gcl * sm
        c_ref[sel, :] = -gch * sq
        b_ref[sel, :] = 1.0 + s0 * (gcl + gch)
        d_ref[sel, :] = ex
        ta_ref[sel, :] = -gtl * stm
        tc_ref[sel, :] = -gth * stp
        tb_ref[sel, :] = 1.0 + s0 * (gtl + gth + rim)

    def ld(ref, i):
        return ref[pl.ds(i, nt, stride=n), :]

    def st(ref, i, val):
        ref[pl.ds(i, nt, stride=n), :] = val

    shape = (nt, nwl)
    _factor(n, [0], ld, st, a_ref, b_ref, c_ref, r_ref, cp_ref, v_ref, w_ref, True, shape)
    _solve_rhs(n, [0], ld, st, a_ref, r_ref, cp_ref, d_ref, y_ref, True, shape)
    rws = _summary_rows(ld, 0, n, y_ref, v_ref, w_ref)
    rws += [jnp.zeros(shape, F32)] * (8 - len(rws))
    for k, val in enumerate(rws):
        sm_ref[pl.ds(k, nt, stride=8), :] = val


def prep_solve(h2, hcl, hch, z2, spray, flags, n):
    rows, nwl = h2.shape
    nt = rows // n
    shp = jax.ShapeDtypeStruct(h2.shape, F32)
    vm = pl.BlockSpec(memory_space=pltpu.VMEM)
    pad = pltpu.VMEM((rows + 2 * n, nwl), F32)
    return pl.pallas_call(
        functools.partial(_prep_kernel, n),
        out_shape=[shp] * 3 + [jax.ShapeDtypeStruct((nt * 8, nwl), F32)] + [shp] * 6,
        in_specs=[vm] * 4 + [SMEM_SPEC, SMEM_SPEC],
        scratch_shapes=[pad, pad, pad] + [pltpu.VMEM(h2.shape, F32)] * 3,
    )(h2, hcl, hch, z2, spray, flags)


def _edge_kernel(n, h_ref, hwl_ref, hwh_ref, fl_ref, a_ref, r_ref, cp_ref, y_ref, sm_ref,
                 yo_ref, smo_ref, d_ref, e_ref):
    rows, nwl = h_ref.shape
    nt = rows // n
    lane = lax.broadcasted_iota(jnp.int32, (nt, nwl), 1)
    for c in range(n):
        sel = pl.ds(c, nt, stride=n)
        T0, k0, s0 = medium_parameters(h_ref[sel, :])
        wlo = medium_parameters(hwl_ref[:, c : c + 1])
        whi = medium_parameters(hwh_ref[:, c : c + 1])
        Twm, _, Twp, _, gwl, gwh = _width_faces(n, c, T0, k0, s0, lane, wlo, whi, fl_ref)
        edge = jnp.where(lane == 0, -gwl * (T0 - Twm), jnp.where(lane == nwl - 1, gwh * (Twp - T0), 0.0))
        d_ref[sel, :] = edge

    def ld(ref, i):
        return ref[pl.ds(i, nt, stride=n), :]

    def st(ref, i, val):
        ref[pl.ds(i, nt, stride=n), :] = val

    _solve_rhs(n, [0], ld, st, a_ref, r_ref, cp_ref, d_ref, e_ref, True, (nt, nwl))
    yo_ref[...] = y_ref[...] + e_ref[...]
    smo_ref[...] = sm_ref[...]
    smo_ref[pl.ds(0, nt, stride=8), :] = sm_ref[pl.ds(0, nt, stride=8), :] + ld(e_ref, 0)
    smo_ref[pl.ds(3, nt, stride=8), :] = sm_ref[pl.ds(3, nt, stride=8), :] + ld(e_ref, n - 1)


def edge_solve(h2, hwl, hwh, flags, a, r, cp, y, sm, n):
    vm = pl.BlockSpec(memory_space=pltpu.VMEM)
    return pl.pallas_call(
        functools.partial(_edge_kernel, n),
        out_shape=[jax.ShapeDtypeStruct(y.shape, F32), jax.ShapeDtypeStruct(sm.shape, F32)],
        in_specs=[vm] * 3 + [SMEM_SPEC] + [vm] * 5,
        scratch_shapes=[pltpu.VMEM(y.shape, F32)] * 2,
    )(h2, hwl, hwh, flags, a, r, cp, y, sm)


def _wfactor_kernel(n, nsub, h_ref, hwl_ref, hwh_ref, fl_ref, a_ref, r_ref, cp_ref, v_ref, w_ref,
                    vws_ref, at_ref, bt_ref, ct_ref, b_ref, c_ref):
    rows, nwl = h_ref.shape
    nt = rows // n
    lane = lax.broadcasted_iota(jnp.int32, (nt, nwl), 1)
    for c in range(n):
        sel = pl.ds(c, nt, stride=n)
        T0, k0, s0 = medium_parameters(h_ref[sel, :])
        wlo = medium_parameters(hwl_ref[:, c : c + 1])
        whi = medium_parameters(hwh_ref[:, c : c + 1])
        _, swm, _, swp, gwl, gwh = _width_faces(n, c, T0, k0, s0, lane, wlo, whi, fl_ref)
        at_ref[sel, :] = -gwl * swm
        ct_ref[sel, :] = -gwh * swp
        bt_ref[sel, :] = 1.0 + s0 * (gwl + gwh)
    for src, dst in ((at_ref, a_ref), (bt_ref, b_ref), (ct_ref, c_ref)):
        for q in range(dst.shape[1]):
            dst[:, q, :] = src[q * 128 : (q + 1) * 128, :].T
    m = a_ref.shape[0] // nsub
    subs = [q * m for q in range(nsub)]
    _factor(m, subs, _lead_ld, _lead_st, a_ref, b_ref, c_ref, r_ref, cp_ref, v_ref, w_ref, 4, a_ref.shape[1:])
    for q, s0 in enumerate(subs):
        for k, val in enumerate((v_ref[s0], w_ref[s0], v_ref[s0 + m - 1], w_ref[s0 + m - 1])):
            vws_ref[q, k] = val


def wfactor(h2, hwl, hwh, flags, n, nsub):
    rows, nwl = h2.shape
    wshape = (nwl, rows // 128, 128)
    shp = jax.ShapeDtypeStruct(wshape, F32)
    vm = pl.BlockSpec(memory_space=pltpu.VMEM)
    return pl.pallas_call(
        functools.partial(_wfactor_kernel, n, nsub),
        out_shape=[shp] * 5 + [jax.ShapeDtypeStruct((nsub, 4) + wshape[1:], F32)],
        in_specs=[vm] * 3 + [SMEM_SPEC],
        scratch_shapes=[pltpu.VMEM(h2.shape, F32)] * 3 + [pltpu.VMEM(wshape, F32)] * 2,
    )(h2, hwl, hwh, flags)


def _width_kernel(nsub, yc_ref, vc_ref, wc_ref, bk_ref, a_ref, r_ref, cp_ref, vws_ref,
                  y_ref, sm_ref, d_ref):
    sc = yc_ref[...] + vc_ref[...] * bk_ref[:, 0:1, :] + wc_ref[...] * bk_ref[:, 1:2, :]
    nt, ncl, nwl = sc.shape
    sc = sc.reshape(nt * ncl, nwl)
    for q in range(d_ref.shape[1]):
        d_ref[:, q, :] = sc[q * 128 : (q + 1) * 128, :].T
    n = a_ref.shape[0] // nsub
    subs = [q * n for q in range(nsub)]
    _solve_rhs(n, subs, _lead_ld, _lead_st, a_ref, r_ref, cp_ref, d_ref, y_ref, 4, a_ref.shape[1:])
    for q, s0 in enumerate(subs):
        rows = (y_ref[s0], vws_ref[q, 0], vws_ref[q, 1], y_ref[s0 + n - 1], vws_ref[q, 2], vws_ref[q, 3])
        for k, val in enumerate(rows):
            sm_ref[q, k] = val


def _thick_kernel(nsub, tsub, nw, me_ref, *refs):
    r_refs = refs[:nw]
    (yw_ref, vw_ref, ww_ref, a_ref, r_ref, cp_ref, v_ref, w_ref, h_ref,
     o_ref, sw_ref, d_ref, y_ref) = refs[nw:]
    lrw = _width_reduce(me_ref[0], r_refs)
    m = yw_ref.shape[0] // nsub
    for q in range(nsub):
        sl = slice(q * m, (q + 1) * m)
        sw_ref[sl] = yw_ref[sl] + vw_ref[sl] * lrw[q][0] + ww_ref[sl] * lrw[q][1]
    nt, ncl, nwl = a_ref.shape
    per_q = 128 // ncl
    for q in range(sw_ref.shape[1]):
        d_ref[q * per_q : (q + 1) * per_q] = sw_ref[:, q, :].T.reshape(per_q, ncl, nwl)
    n = nt // tsub
    subs = [q * n for q in range(tsub)]
    shape = a_ref.shape[1:]
    _solve_rhs(n, subs, _lead_ld, _lead_st, a_ref, r_ref, cp_ref, d_ref, y_ref, 4, shape)
    sums = [tuple(_summary_rows(_lead_ld, s0, n, y_ref, v_ref, w_ref)) for s0 in subs]
    lrs = [None] * tsub

    def emit(p, left, right):
        lrs[p] = (left, right)

    _reduce_blocks(tsub, lambda p: sums[p], emit, jnp.zeros(shape, F32))
    for q, s0 in enumerate(subs):
        sl = slice(s0, s0 + n)
        left, right = lrs[q]
        o_ref[sl] = h_ref[sl] + (y_ref[sl] + v_ref[sl] * left + w_ref[sl] * right)


def cast_solve(a, b, c, d, n):
    shp = jax.ShapeDtypeStruct(a.shape, F32)
    m = a.shape[0] // n
    return pl.pallas_call(
        functools.partial(_cast_kernel, n),
        out_shape=[shp, shp, shp, jax.ShapeDtypeStruct((m * 8, a.shape[1]), F32)],
        scratch_shapes=[pltpu.VMEM(a.shape, F32)],
    )(a, b, c, d)


def width_solve(yc, vc, wc, bk, a, fac, nsub):
    shp = jax.ShapeDtypeStruct(a.shape, F32)
    return pl.pallas_call(
        functools.partial(_width_kernel, nsub),
        out_shape=[shp, jax.ShapeDtypeStruct((nsub, 6) + a.shape[1:], F32)],
        scratch_shapes=[pltpu.VMEM(a.shape, F32)],
    )(yc, vc, wc, bk, a, *fac)


def thick_solve(me, got, yw, vw, ww, a, fac, h, nsub, tsub):
    vm = pl.BlockSpec(memory_space=pltpu.VMEM)
    return pl.pallas_call(
        functools.partial(_thick_kernel, nsub, tsub, len(got)),
        out_shape=jax.ShapeDtypeStruct(a.shape, F32),
        in_specs=[SMEM_SPEC] + [vm] * (len(got) + 9),
        scratch_shapes=[pltpu.VMEM(yw.shape, F32)] + [pltpu.VMEM(a.shape, F32)] * 2,
    )(me, *got, yw, vw, ww, a, *fac, h)


def _reduce_blocks(nb, blk, emit, zero):
    pp, qq = zero, zero
    saved = []
    for p in range(nb):
        y0, v0, w0, yn, vn, wn = blk(p)
        rd = 1.0 / (1.0 - v0 * qq)
        fa = (y0 + v0 * pp) * rd
        fb = w0 * rd
        saved.append((fa, fb, pp, qq))
        pp, qq = yn + vn * (pp + qq * fa), wn + vn * qq * fb
    f_next = zero
    for p in range(nb - 1, -1, -1):
        fa, fb, pp, qq = saved[p]
        f = fa + fb * f_next
        emit(p, pp + qq * f, f_next)
        f_next = f


def _merge(A, B):
    yA0, vA0, wA0, yAn, vAn, wAn = A
    yB0, vB0, wB0, yBn, vBn, wBn = B
    rd = 1.0 / (1.0 - wAn * vB0)
    ey = (yAn + wAn * yB0) * rd
    ev = vAn * rd
    ew = wAn * wB0 * rd
    fy = yB0 + vB0 * ey
    fv = vB0 * ev
    fw = wB0 + vB0 * ew
    return (yA0 + wA0 * fy, vA0 + wA0 * fv, wA0 * fw, yBn + vBn * ey, vBn * ev, wBn + vBn * ew)


def _chain(nb, blk, emit, left, right):
    pp, qq = left, jnp.zeros_like(left)
    saved = []
    for p in range(nb):
        y0, v0, w0, yn, vn, wn = blk(p)
        rd = 1.0 / (1.0 - v0 * qq)
        fa = (y0 + v0 * pp) * rd
        fb = w0 * rd
        saved.append((fa, fb, pp, qq))
        pp, qq = yn + vn * (pp + qq * fa), wn + vn * qq * fb
    f_next = right
    for p in range(nb - 1, -1, -1):
        fa, fb, pp, qq = saved[p]
        f = fa + fb * f_next
        emit(p, pp + qq * f, f_next)
        f_next = f


def _cast_reduced_kernel(s_ref, lr_ref):
    nb, g, _, nl = s_ref.shape
    ng = 8
    if g != 1 or nb % ng:
        def blk(p):
            return tuple(s_ref[p, :, k, :] for k in range(6))

        def emit(p, left, right):
            lr_ref[p, :, 0:1, :] = left[:, None]
            lr_ref[p, :, 1:2, :] = right[:, None]

        _reduce_blocks(nb, blk, emit, jnp.zeros((g, nl), F32))
        return
    m = nb // ng

    def member(j):
        return tuple(
            jnp.concatenate([s_ref[G * m + j, 0, k : k + 1, :] for G in range(ng)], 0)
            for k in range(6)
        )

    members = [member(j) for j in range(m)]
    acc = members[0]
    for j in range(1, m):
        acc = _merge(acc, members[j])
    outer = [None] * ng

    def emit_g(G, left, right):
        outer[G] = (left, right)

    zero1 = jnp.zeros((1, nl), F32)
    _chain(ng, lambda G: tuple(x[G : G + 1] for x in acc), emit_g, zero1, zero1)
    left_g = jnp.concatenate([outer[G][0] for G in range(ng)], 0)
    right_g = jnp.concatenate([outer[G][1] for G in range(ng)], 0)

    def emit(j, left, right):
        for G in range(ng):
            lr_ref[G * m + j, 0, 0:1, :] = left[G : G + 1]
            lr_ref[G * m + j, 0, 1:2, :] = right[G : G + 1]

    _chain(m, lambda j: members[j], emit, left_g, right_g)


def _width_reduce(me, r_refs):
    nw = len(r_refs)
    nsub = r_refs[0].shape[0]
    out = [[None, None] for _ in range(nsub)]

    def blk(b):
        dev, q = divmod(b, nsub)
        kk = (me - dev + nw) % nw
        vals = []
        for k6 in range(6):
            val = r_refs[0][q, k6]
            for k in range(1, nw):
                val = jnp.where(kk == k, r_refs[k][q, k6], val)
            vals.append(val)
        return tuple(vals)

    def emit(b, left, right):
        dev, q = divmod(b, nsub)
        mine = me == dev
        for j, val in enumerate((left, right)):
            out[q][j] = val if out[q][j] is None else jnp.where(mine, val, out[q][j])

    _reduce_blocks(nw * nsub, blk, emit, jnp.zeros(r_refs[0].shape[2:], F32))
    return out


def _surface_kernel(scale, z_ref, sp_ref, o_ref):
    z = z_ref[...]
    acc = jnp.zeros(z.shape, F32)
    for q in range(sp_ref.shape[0]):
        acc = jnp.where(z == q, sp_ref[q], acc)
    o_ref[...] = acc * scale


def medium_parameters(x):
    t = jnp.tanh(x)
    hot = x - solidification_release * t
    cond = 1.5 - 0.5 * jnp.tanh(hot)
    slope = (1.0 - solidification_release) + solidification_release * t * t
    return hot, cond, slope


def shards(h, zones, spray_coef):
    nt, ncl, nwl = h.shape
    nc, nw = lax.axis_size("cast"), lax.axis_size("width")
    ci, wi = lax.axis_index("cast"), lax.axis_index("width")
    up_c = [(i, i + 1) for i in range(nc - 1)]
    up_w = [(i, i + 1) for i in range(nw - 1)]
    even = ci % 2 == 0
    first, last = h[:, 0, :], h[:, -1, :]
    in_chip = [(i, i ^ 1) for i in range(nc)]
    across = [(i, i + 1) for i in range(1, nc - 1, 2)] + [(i + 1, i) for i in range(1, nc - 1, 2)]
    got_a = lax.ppermute(jnp.where(even, last, first), "cast", in_chip)
    got_b = lax.ppermute(jnp.where(even, first, last), "cast", across)
    h_wl = lax.ppermute(h[:, :, -1], "width", up_w)
    h_wh = lax.ppermute(h[:, :, 0], "width", [(b, a) for a, b in up_w])

    cast_low = (ci > 0).astype(F32)
    cast_high = (ci < nc - 1).astype(F32)
    width_low = (wi > 0).astype(F32)
    width_high = (wi < nw - 1).astype(F32)
    flags = jnp.stack([cast_low, cast_high, width_low, width_high, even.astype(F32)])
    h2 = h.reshape(nt * ncl, nwl)
    outs = prep_solve(h2, got_a, got_b, zones.reshape(2 * ncl, nwl), spray_coef, flags, ncl)
    y, v, w, summ, a_c, r_c, cp_c = outs[:7]
    tlo, tmd, thi = (x.reshape(nt, ncl, nwl) for x in outs[7:])
    y, summ = edge_solve(h2, h_wl, h_wh, flags, a_c, r_c, cp_c, y, summ, ncl)
    recv = lax.all_to_all(summ.reshape(nc, nt // nc, 8, nwl), "cast", 0, 0, tiled=True)
    lr_shape = recv.shape[:2] + (2, nwl)
    lr = pl.pallas_call(_cast_reduced_kernel, out_shape=jax.ShapeDtypeStruct(lr_shape, F32))(recv)
    back = lax.all_to_all(lr, "cast", 0, 0, tiled=True).reshape(nt, 2, nwl)
    y, v, w = (x.reshape(nt, ncl, nwl) for x in (y, v, w))

    lines = nt * ncl
    nsub = 2

    def wl(x):
        return jnp.transpose(x, (2, 0, 1)).reshape(nwl, lines // 128, 128)

    wa, r_w, cp_w, v_w, w_w, vws = wfactor(h2, h_wl, h_wh, flags, ncl, nsub)
    wfac = (r_w, cp_w, v_w, w_w)
    tfac = factor(tlo, tmd, thi, 8)
    yw, summ = width_solve(y, v, w, back, wa, (r_w, cp_w, vws), nsub)
    got = [summ] + [
        lax.ppermute(summ, "width", [(i, (i + q) % nw) for i in range(nw)]) for q in range(1, nw)
    ]
    me = wi.astype(jnp.int32).reshape(1)
    return thick_solve(me, got, yw, wfac[2], wfac[3], tlo, tfac, h, nsub, 8)


def solution(mesh):
    spec = P(None, "cast", "width")
    return jax.shard_map(
        shards, mesh=mesh, in_specs=(spec, spec, P()), out_specs=spec, check_vma=False
    )
```

```python
import functools

import jax
import jax.numpy as jnp
from jax import lax
from jax.experimental import pallas as pl
from jax.experimental.pallas import tpu as pltpu
from jax.sharding import PartitionSpec as P

F32 = jnp.float32
solidification_release = 0.4
quench_medium_hotness = -2.0
SMEM_SPEC = pl.BlockSpec(memory_space=pltpu.SMEM)


def _sweep(n, subs, ld, st, a_ref, b_ref, c_ref, d_ref, y_ref, v_ref, w_ref, cp_ref, unroll, shape):
    with_vw = v_ref is not None
    zero = jnp.zeros(shape, F32)
    one = jnp.ones(shape, F32)

    def fwd(i, carries):
        out = []
        for s0, (cprev, dprev, vprev) in zip(subs, carries):
            j = s0 + i
            a = ld(a_ref, j)
            r = 1.0 / (ld(b_ref, j) - a * cprev)
            cn = ld(c_ref, j) * r
            dn = (ld(d_ref, j) - a * dprev) * r
            st(cp_ref, j, cn)
            st(y_ref, j, dn)
            if with_vw:
                vprev = -(a * vprev) * r
                st(v_ref, j, vprev)
            out.append((cn, dn, vprev))
        return tuple(out)

    carries = tuple((zero, zero, one) for _ in subs)
    if unroll is True:
        for i in range(n):
            carries = fwd(i, carries)
    else:
        carries = lax.fori_loop(0, n, fwd, carries, unroll=unroll)
    if with_vw:
        for s0, (cl, _, _) in zip(subs, carries):
            st(w_ref, s0 + n - 1, -cl)

    def bwd(jj, carries):
        i = n - 2 - jj
        out = []
        for s0, (yn, vn, wn) in zip(subs, carries):
            j = s0 + i
            cp = ld(cp_ref, j)
            yn = ld(y_ref, j) - cp * yn
            st(y_ref, j, yn)
            if with_vw:
                vn = ld(v_ref, j) - cp * vn
                wn = -cp * wn
                st(v_ref, j, vn)
                st(w_ref, j, wn)
            out.append((yn, vn, wn))
        return tuple(out)

    carries = tuple((dl, vl, -cl) for cl, dl, vl in carries)
    if unroll is True:
        for jj in range(n - 1):
            carries = bwd(jj, carries)
    else:
        lax.fori_loop(0, n - 1, bwd, carries, unroll=unroll)


def _summary_rows(ld, s0, n, y_ref, v_ref, w_ref):
    return [ld(y_ref, s0), ld(v_ref, s0), ld(w_ref, s0),
            ld(y_ref, s0 + n - 1), ld(v_ref, s0 + n - 1), ld(w_ref, s0 + n - 1)]


def _cast_kernel(n, a_ref, b_ref, c_ref, d_ref, y_ref, v_ref, w_ref, sm_ref, cp_ref):
    m = a_ref.shape[0] // n

    def ld(ref, i):
        return ref[pl.ds(i, m, stride=n), :]

    def st(ref, i, val):
        ref[pl.ds(i, m, stride=n), :] = val

    shape = (m, a_ref.shape[1])
    _sweep(n, [0], ld, st, a_ref, b_ref, c_ref, d_ref, y_ref, v_ref, w_ref, cp_ref, True, shape)
    rows = _summary_rows(ld, 0, n, y_ref, v_ref, w_ref)
    rows += [jnp.zeros(shape, F32)] * (8 - len(rows))
    for k, val in enumerate(rows):
        sm_ref[pl.ds(k, m, stride=8), :] = val


def _lead_ld(ref, i):
    return ref[i]


def _lead_st(ref, i, val):
    ref[i] = val


def _loop(n, body, carry, unroll):
    if unroll is True:
        for i in range(n):
            carry = body(i, carry)
        return carry
    return lax.fori_loop(0, n, body, carry, unroll=unroll)


def _factor(n, subs, ld, st, a_ref, b_ref, c_ref, r_ref, cp_ref, v_ref, w_ref, unroll, shape):
    zero = jnp.zeros(shape, F32)
    one = jnp.ones(shape, F32)

    def fwd(i, carries):
        out = []
        for s0, (cprev, vprev) in zip(subs, carries):
            j = s0 + i
            a = ld(a_ref, j)
            r = 1.0 / (ld(b_ref, j) - a * cprev)
            cn = ld(c_ref, j) * r
            vprev = -(a * vprev) * r
            st(r_ref, j, r)
            st(cp_ref, j, cn)
            st(v_ref, j, vprev)
            out.append((cn, vprev))
        return tuple(out)

    carries = _loop(n, fwd, tuple((zero, one) for _ in subs), unroll)
    for s0, (cl, _) in zip(subs, carries):
        st(w_ref, s0 + n - 1, -cl)

    def bwd(jj, carries):
        i = n - 2 - jj
        out = []
        for s0, (vn, wn) in zip(subs, carries):
            j = s0 + i
            cp = ld(cp_ref, j)
            vn = ld(v_ref, j) - cp * vn
            wn = -cp * wn
            st(v_ref, j, vn)
            st(w_ref, j, wn)
            out.append((vn, wn))
        return tuple(out)

    _loop(n - 1, bwd, tuple((vl, -cl) for cl, vl in carries), unroll)


def _solve_rhs(n, subs, ld, st, a_ref, r_ref, cp_ref, d_ref, y_ref, unroll, shape):
    zero = jnp.zeros(shape, F32)

    def fwd(i, carries):
        out = []
        for s0, dprev in zip(subs, carries):
            j = s0 + i
            dn = (ld(d_ref, j) - ld(a_ref, j) * dprev) * ld(r_ref, j)
            st(y_ref, j, dn)
            out.append(dn)
        return tuple(out)

    carries = _loop(n, fwd, tuple(zero for _ in subs), unroll)

    def bwd(jj, carries):
        i = n - 2 - jj
        out = []
        for s0, yn in zip(subs, carries):
            j = s0 + i
            yn = ld(y_ref, j) - ld(cp_ref, j) * yn
            st(y_ref, j, yn)
            out.append(yn)
        return tuple(out)

    _loop(n - 1, bwd, carries, unroll)


def _factor_kernel(nsub, a_ref, b_ref, c_ref, r_ref, cp_ref, v_ref, w_ref):
    n = a_ref.shape[0] // nsub
    subs = [q * n for q in range(nsub)]
    _factor(n, subs, _lead_ld, _lead_st, a_ref, b_ref, c_ref, r_ref, cp_ref, v_ref, w_ref, True, a_ref.shape[1:])


def factor(a, b, c, nsub):
    shp = jax.ShapeDtypeStruct(a.shape, F32)
    return pl.pallas_call(functools.partial(_factor_kernel, nsub), out_shape=[shp] * 4)(a, b, c)


def _width_faces(n, c, T0, k0, s0, lane, wlo, whi, fl_ref):
    nwl = T0.shape[1]
    g_w = nwl * nwl / 4.0 * 0.5
    if wlo is None:
        wlo = (T0, k0, s0)
        whi = (T0, k0, s0)
        e_lo, e_hi = 0.0, 0.0
    else:
        e_lo, e_hi = fl_ref[2], fl_ref[3]
    Twm, kwm, swm = (jnp.where(lane == 0, b, pltpu.roll(f, 1, 1)) for f, b in zip((T0, k0, s0), wlo))
    Twp, kwp, swp = (
        jnp.where(lane == nwl - 1, b, pltpu.roll(f, nwl - 1, 1)) for f, b in zip((T0, k0, s0), whi)
    )
    gwl = g_w * (k0 + kwm) * jnp.where(lane == 0, e_lo, 1.0)
    gwh = g_w * (kwp + k0) * jnp.where(lane == nwl - 1, e_hi, 1.0)
    return Twm, swm, Twp, swp, gwl, gwh


def _prep_kernel(n, h_ref, hcl_ref, hch_ref, z_ref, sp_ref, fl_ref,
                 y_ref, v_ref, w_ref, sm_ref, a_ref, r_ref, cp_ref, ta_ref, tb_ref, tc_ref,
                 tp_ref, kp_ref, sp2_ref, b_ref, c_ref, d_ref):
    rows, nwl = h_ref.shape
    nt = rows // n
    hot, cond, slope = medium_parameters(h_ref[...])
    zpad = jnp.zeros((n, nwl), F32)
    for ref, val in ((tp_ref, hot), (kp_ref, cond), (sp2_ref, slope)):
        ref[0:n] = zpad
        ref[n : n + rows] = val
        ref[n + rows : 2 * n + rows] = zpad

    def row(ref, off):
        return ref[pl.ds(off, nt, stride=n), :]

    lane = lax.broadcasted_iota(jnp.int32, (nt, nwl), 1)
    tix = lax.broadcasted_iota(jnp.int32, (nt, nwl), 0)
    even = fl_ref[4] > 0.5
    got_a, got_b = hcl_ref[...], hch_ref[...]
    cast_lo = medium_parameters(jnp.where(even, got_b, got_a))
    cast_hi = medium_parameters(jnp.where(even, got_a, got_b))
    g_c = n * n * 4.0 * 0.5
    g_t = nt * nt / 4.0 * 0.5
    nz = sp_ref.shape[0]

    def surf_row(zr):
        acc = jnp.zeros(zr.shape, F32)
        for q in range(nz):
            acc = jnp.where(zr == q, sp_ref[q], acc)
        return acc * (nt * nt / 8.0)

    for c in range(n):
        T0, k0, s0 = (row(r, n + c) for r in (tp_ref, kp_ref, sp2_ref))
        if c == 0:
            Tm, km, sm = cast_lo
        else:
            Tm, km, sm = (row(r, n + c - 1) for r in (tp_ref, kp_ref, sp2_ref))
        if c == n - 1:
            Tq, kq, sq = cast_hi
        else:
            Tq, kq, sq = (row(r, n + c + 1) for r in (tp_ref, kp_ref, sp2_ref))
        Ttm, ktm, stm = (row(r, c) for r in (tp_ref, kp_ref, sp2_ref))
        Ttp, ktp, stp = (row(r, 2 * n + c) for r in (tp_ref, kp_ref, sp2_ref))
        Twm, _, Twp, _, gwl, gwh = _width_faces(n, c, T0, k0, s0, lane, None, None, fl_ref)
        gcl = g_c * (k0 + km)
        if c == 0:
            gcl = gcl * fl_ref[0]
        gch = g_c * (kq + k0)
        if c == n - 1:
            gch = gch * fl_ref[1]
        gtl = jnp.where(tix == 0, 0.0, g_t * (k0 + ktm))
        gth = jnp.where(tix == nt - 1, 0.0, g_t * (ktp + k0))
        s_lo = surf_row(z_ref[c : c + 1, :])
        s_hi = surf_row(z_ref[n + c : n + c + 1, :])
        rim = jnp.where(tix == 0, s_lo, jnp.where(tix == nt - 1, s_hi, 0.0))
        ex = rim * (quench_medium_hotness - T0)
        ex = ex + (gch * (Tq - T0) - gcl * (T0 - Tm))
        ex = ex + (gwh * (Twp - T0) - gwl * (T0 - Twm))
        ex = ex + (gth * (Ttp - T0) - gtl * (T0 - Ttm))
        sel = pl.ds(c, nt, stride=n)
        a_ref[sel, :] = -gcl * sm
        c_ref[sel, :] = -gch * sq
        b_ref[sel, :] = 1.0 + s0 * (gcl + gch)
        d_ref[sel, :] = ex
        ta_ref[sel, :] = -gtl * stm
        tc_ref[sel, :] = -gth * stp
        tb_ref[sel, :] = 1.0 + s0 * (gtl + gth + rim)

    def ld(ref, i):
        return ref[pl.ds(i, nt, stride=n), :]

    def st(ref, i, val):
        ref[pl.ds(i, nt, stride=n), :] = val

    shape = (nt, nwl)
    _factor(n, [0], ld, st, a_ref, b_ref, c_ref, r_ref, cp_ref, v_ref, w_ref, True, shape)
    _solve_rhs(n, [0], ld, st, a_ref, r_ref, cp_ref, d_ref, y_ref, True, shape)
    rws = _summary_rows(ld, 0, n, y_ref, v_ref, w_ref)
    rws += [jnp.zeros(shape, F32)] * (8 - len(rws))
    for k, val in enumerate(rws):
        sm_ref[pl.ds(k, nt, stride=8), :] = val


def prep_solve(h2, hcl, hch, z2, spray, flags, n):
    rows, nwl = h2.shape
    nt = rows // n
    shp = jax.ShapeDtypeStruct(h2.shape, F32)
    vm = pl.BlockSpec(memory_space=pltpu.VMEM)
    pad = pltpu.VMEM((rows + 2 * n, nwl), F32)
    return pl.pallas_call(
        functools.partial(_prep_kernel, n),
        out_shape=[shp] * 3 + [jax.ShapeDtypeStruct((nt * 8, nwl), F32)] + [shp] * 6,
        in_specs=[vm] * 4 + [SMEM_SPEC, SMEM_SPEC],
        scratch_shapes=[pad, pad, pad] + [pltpu.VMEM(h2.shape, F32)] * 3,
    )(h2, hcl, hch, z2, spray, flags)


def _edge_kernel(n, h_ref, hwl_ref, hwh_ref, fl_ref, a_ref, r_ref, cp_ref, y_ref, sm_ref,
                 yo_ref, smo_ref, d_ref, e_ref):
    rows, nwl = h_ref.shape
    nt = rows // n
    lane = lax.broadcasted_iota(jnp.int32, (nt, nwl), 1)
    for c in range(n):
        sel = pl.ds(c, nt, stride=n)
        T0, k0, s0 = medium_parameters(h_ref[sel, :])
        wlo = medium_parameters(hwl_ref[:, c : c + 1])
        whi = medium_parameters(hwh_ref[:, c : c + 1])
        Twm, _, Twp, _, gwl, gwh = _width_faces(n, c, T0, k0, s0, lane, wlo, whi, fl_ref)
        edge = jnp.where(lane == 0, -gwl * (T0 - Twm), jnp.where(lane == nwl - 1, gwh * (Twp - T0), 0.0))
        d_ref[sel, :] = edge

    def ld(ref, i):
        return ref[pl.ds(i, nt, stride=n), :]

    def st(ref, i, val):
        ref[pl.ds(i, nt, stride=n), :] = val

    _solve_rhs(n, [0], ld, st, a_ref, r_ref, cp_ref, d_ref, e_ref, True, (nt, nwl))
    yo_ref[...] = y_ref[...] + e_ref[...]
    smo_ref[...] = sm_ref[...]
    smo_ref[pl.ds(0, nt, stride=8), :] = sm_ref[pl.ds(0, nt, stride=8), :] + ld(e_ref, 0)
    smo_ref[pl.ds(3, nt, stride=8), :] = sm_ref[pl.ds(3, nt, stride=8), :] + ld(e_ref, n - 1)


def edge_solve(h2, hwl, hwh, flags, a, r, cp, y, sm, n):
    vm = pl.BlockSpec(memory_space=pltpu.VMEM)
    return pl.pallas_call(
        functools.partial(_edge_kernel, n),
        out_shape=[jax.ShapeDtypeStruct(y.shape, F32), jax.ShapeDtypeStruct(sm.shape, F32)],
        in_specs=[vm] * 3 + [SMEM_SPEC] + [vm] * 5,
        scratch_shapes=[pltpu.VMEM(y.shape, F32)] * 2,
    )(h2, hwl, hwh, flags, a, r, cp, y, sm)


def _wfactor_kernel(n, nsub, h_ref, hwl_ref, hwh_ref, fl_ref, a_ref, r_ref, cp_ref, v_ref, w_ref,
                    vws_ref, at_ref, bt_ref, ct_ref, b_ref, c_ref):
    rows, nwl = h_ref.shape
    nt = rows // n
    lane = lax.broadcasted_iota(jnp.int32, (nt, nwl), 1)
    for c in range(n):
        sel = pl.ds(c, nt, stride=n)
        T0, k0, s0 = medium_parameters(h_ref[sel, :])
        wlo = medium_parameters(hwl_ref[:, c : c + 1])
        whi = medium_parameters(hwh_ref[:, c : c + 1])
        _, swm, _, swp, gwl, gwh = _width_faces(n, c, T0, k0, s0, lane, wlo, whi, fl_ref)
        at_ref[sel, :] = -gwl * swm
        ct_ref[sel, :] = -gwh * swp
        bt_ref[sel, :] = 1.0 + s0 * (gwl + gwh)
    for src, dst in ((at_ref, a_ref), (bt_ref, b_ref), (ct_ref, c_ref)):
        for q in range(dst.shape[1]):
            dst[:, q, :] = src[q * 128 : (q + 1) * 128, :].T
    m = a_ref.shape[0] // nsub
    subs = [q * m for q in range(nsub)]
    _factor(m, subs, _lead_ld, _lead_st, a_ref, b_ref, c_ref, r_ref, cp_ref, v_ref, w_ref, True, a_ref.shape[1:])
    for q, s0 in enumerate(subs):
        for k, val in enumerate((v_ref[s0], w_ref[s0], v_ref[s0 + m - 1], w_ref[s0 + m - 1])):
            vws_ref[q, k] = val


def wfactor(h2, hwl, hwh, flags, n, nsub):
    rows, nwl = h2.shape
    wshape = (nwl, rows // 128, 128)
    shp = jax.ShapeDtypeStruct(wshape, F32)
    vm = pl.BlockSpec(memory_space=pltpu.VMEM)
    return pl.pallas_call(
        functools.partial(_wfactor_kernel, n, nsub),
        out_shape=[shp] * 5 + [jax.ShapeDtypeStruct((nsub, 4) + wshape[1:], F32)],
        in_specs=[vm] * 3 + [SMEM_SPEC],
        scratch_shapes=[pltpu.VMEM(h2.shape, F32)] * 3 + [pltpu.VMEM(wshape, F32)] * 2,
    )(h2, hwl, hwh, flags)


def _width_kernel(nsub, yc_ref, vc_ref, wc_ref, bk_ref, a_ref, r_ref, cp_ref, vws_ref,
                  y_ref, sm_ref, d_ref):
    sc = yc_ref[...] + vc_ref[...] * bk_ref[:, 0:1, :] + wc_ref[...] * bk_ref[:, 1:2, :]
    nt, ncl, nwl = sc.shape
    sc = sc.reshape(nt * ncl, nwl)
    for q in range(d_ref.shape[1]):
        d_ref[:, q, :] = sc[q * 128 : (q + 1) * 128, :].T
    n = a_ref.shape[0] // nsub
    subs = [q * n for q in range(nsub)]
    _solve_rhs(n, subs, _lead_ld, _lead_st, a_ref, r_ref, cp_ref, d_ref, y_ref, True, a_ref.shape[1:])
    for q, s0 in enumerate(subs):
        rows = (y_ref[s0], vws_ref[q, 0], vws_ref[q, 1], y_ref[s0 + n - 1], vws_ref[q, 2], vws_ref[q, 3])
        for k, val in enumerate(rows):
            sm_ref[q, k] = val


def _thick_kernel(nsub, tsub, nw, me_ref, *refs):
    r_refs = refs[:nw]
    (yw_ref, vw_ref, ww_ref, a_ref, r_ref, cp_ref, v_ref, w_ref, h_ref,
     o_ref, sw_ref, d_ref, y_ref) = refs[nw:]
    lrw = _width_reduce(me_ref[0], r_refs)
    m = yw_ref.shape[0] // nsub
    for q in range(nsub):
        sl = slice(q * m, (q + 1) * m)
        sw_ref[sl] = yw_ref[sl] + vw_ref[sl] * lrw[q][0] + ww_ref[sl] * lrw[q][1]
    nt, ncl, nwl = a_ref.shape
    per_q = 128 // ncl
    for q in range(sw_ref.shape[1]):
        d_ref[q * per_q : (q + 1) * per_q] = sw_ref[:, q, :].T.reshape(per_q, ncl, nwl)
    n = nt // tsub
    subs = [q * n for q in range(tsub)]
    shape = a_ref.shape[1:]
    _solve_rhs(n, subs, _lead_ld, _lead_st, a_ref, r_ref, cp_ref, d_ref, y_ref, True, shape)
    sums = [tuple(_summary_rows(_lead_ld, s0, n, y_ref, v_ref, w_ref)) for s0 in subs]
    lrs = [None] * tsub

    def emit(p, left, right):
        lrs[p] = (left, right)

    _reduce_blocks(tsub, lambda p: sums[p], emit, jnp.zeros(shape, F32))
    for q, s0 in enumerate(subs):
        sl = slice(s0, s0 + n)
        left, right = lrs[q]
        o_ref[sl] = h_ref[sl] + (y_ref[sl] + v_ref[sl] * left + w_ref[sl] * right)


def cast_solve(a, b, c, d, n):
    shp = jax.ShapeDtypeStruct(a.shape, F32)
    m = a.shape[0] // n
    return pl.pallas_call(
        functools.partial(_cast_kernel, n),
        out_shape=[shp, shp, shp, jax.ShapeDtypeStruct((m * 8, a.shape[1]), F32)],
        scratch_shapes=[pltpu.VMEM(a.shape, F32)],
    )(a, b, c, d)


def width_solve(yc, vc, wc, bk, a, fac, nsub):
    shp = jax.ShapeDtypeStruct(a.shape, F32)
    return pl.pallas_call(
        functools.partial(_width_kernel, nsub),
        out_shape=[shp, jax.ShapeDtypeStruct((nsub, 6) + a.shape[1:], F32)],
        scratch_shapes=[pltpu.VMEM(a.shape, F32)],
    )(yc, vc, wc, bk, a, *fac)


def thick_solve(me, got, yw, vw, ww, a, fac, h, nsub, tsub):
    vm = pl.BlockSpec(memory_space=pltpu.VMEM)
    return pl.pallas_call(
        functools.partial(_thick_kernel, nsub, tsub, len(got)),
        out_shape=jax.ShapeDtypeStruct(a.shape, F32),
        in_specs=[SMEM_SPEC] + [vm] * (len(got) + 9),
        scratch_shapes=[pltpu.VMEM(yw.shape, F32)] + [pltpu.VMEM(a.shape, F32)] * 2,
    )(me, *got, yw, vw, ww, a, *fac, h)


def _reduce_blocks(nb, blk, emit, zero):
    pp, qq = zero, zero
    saved = []
    for p in range(nb):
        y0, v0, w0, yn, vn, wn = blk(p)
        rd = 1.0 / (1.0 - v0 * qq)
        fa = (y0 + v0 * pp) * rd
        fb = w0 * rd
        saved.append((fa, fb, pp, qq))
        pp, qq = yn + vn * (pp + qq * fa), wn + vn * qq * fb
    f_next = zero
    for p in range(nb - 1, -1, -1):
        fa, fb, pp, qq = saved[p]
        f = fa + fb * f_next
        emit(p, pp + qq * f, f_next)
        f_next = f


def _merge(A, B):
    yA0, vA0, wA0, yAn, vAn, wAn = A
    yB0, vB0, wB0, yBn, vBn, wBn = B
    rd = 1.0 / (1.0 - wAn * vB0)
    ey = (yAn + wAn * yB0) * rd
    ev = vAn * rd
    ew = wAn * wB0 * rd
    fy = yB0 + vB0 * ey
    fv = vB0 * ev
    fw = wB0 + vB0 * ew
    return (yA0 + wA0 * fy, vA0 + wA0 * fv, wA0 * fw, yBn + vBn * ey, vBn * ev, wBn + vBn * ew)


def _chain(nb, blk, emit, left, right):
    pp, qq = left, jnp.zeros_like(left)
    saved = []
    for p in range(nb):
        y0, v0, w0, yn, vn, wn = blk(p)
        rd = 1.0 / (1.0 - v0 * qq)
        fa = (y0 + v0 * pp) * rd
        fb = w0 * rd
        saved.append((fa, fb, pp, qq))
        pp, qq = yn + vn * (pp + qq * fa), wn + vn * qq * fb
    f_next = right
    for p in range(nb - 1, -1, -1):
        fa, fb, pp, qq = saved[p]
        f = fa + fb * f_next
        emit(p, pp + qq * f, f_next)
        f_next = f


def _cast_reduced_kernel(s_ref, lr_ref):
    nb, g, _, nl = s_ref.shape
    ng = 8
    if g != 1 or nb % ng:
        def blk(p):
            return tuple(s_ref[p, :, k, :] for k in range(6))

        def emit(p, left, right):
            lr_ref[p, :, 0:1, :] = left[:, None]
            lr_ref[p, :, 1:2, :] = right[:, None]

        _reduce_blocks(nb, blk, emit, jnp.zeros((g, nl), F32))
        return
    m = nb // ng

    def member(j):
        return tuple(
            jnp.concatenate([s_ref[G * m + j, 0, k : k + 1, :] for G in range(ng)], 0)
            for k in range(6)
        )

    members = [member(j) for j in range(m)]
    acc = members[0]
    for j in range(1, m):
        acc = _merge(acc, members[j])
    outer = [None] * ng

    def emit_g(G, left, right):
        outer[G] = (left, right)

    zero1 = jnp.zeros((1, nl), F32)
    _chain(ng, lambda G: tuple(x[G : G + 1] for x in acc), emit_g, zero1, zero1)
    left_g = jnp.concatenate([outer[G][0] for G in range(ng)], 0)
    right_g = jnp.concatenate([outer[G][1] for G in range(ng)], 0)

    def emit(j, left, right):
        for G in range(ng):
            lr_ref[G * m + j, 0, 0:1, :] = left[G : G + 1]
            lr_ref[G * m + j, 0, 1:2, :] = right[G : G + 1]

    _chain(m, lambda j: members[j], emit, left_g, right_g)


def _width_reduce(me, r_refs):
    nw = len(r_refs)
    nsub = r_refs[0].shape[0]
    out = [[None, None] for _ in range(nsub)]

    def blk(b):
        dev, q = divmod(b, nsub)
        kk = (me - dev + nw) % nw
        vals = []
        for k6 in range(6):
            val = r_refs[0][q, k6]
            for k in range(1, nw):
                val = jnp.where(kk == k, r_refs[k][q, k6], val)
            vals.append(val)
        return tuple(vals)

    def emit(b, left, right):
        dev, q = divmod(b, nsub)
        mine = me == dev
        for j, val in enumerate((left, right)):
            out[q][j] = val if out[q][j] is None else jnp.where(mine, val, out[q][j])

    _reduce_blocks(nw * nsub, blk, emit, jnp.zeros(r_refs[0].shape[2:], F32))
    return out


def _surface_kernel(scale, z_ref, sp_ref, o_ref):
    z = z_ref[...]
    acc = jnp.zeros(z.shape, F32)
    for q in range(sp_ref.shape[0]):
        acc = jnp.where(z == q, sp_ref[q], acc)
    o_ref[...] = acc * scale


def medium_parameters(x):
    t = jnp.tanh(x)
    hot = x - solidification_release * t
    cond = 1.5 - 0.5 * jnp.tanh(hot)
    slope = (1.0 - solidification_release) + solidification_release * t * t
    return hot, cond, slope


def shards(h, zones, spray_coef):
    nt, ncl, nwl = h.shape
    nc, nw = lax.axis_size("cast"), lax.axis_size("width")
    ci, wi = lax.axis_index("cast"), lax.axis_index("width")
    up_c = [(i, i + 1) for i in range(nc - 1)]
    up_w = [(i, i + 1) for i in range(nw - 1)]
    even = ci % 2 == 0
    first, last = h[:, 0, :], h[:, -1, :]
    in_chip = [(i, i ^ 1) for i in range(nc)]
    across = [(i, i + 1) for i in range(1, nc - 1, 2)] + [(i + 1, i) for i in range(1, nc - 1, 2)]
    got_a = lax.ppermute(jnp.where(even, last, first), "cast", in_chip)
    got_b = lax.ppermute(jnp.where(even, first, last), "cast", across)
    h_wl = lax.ppermute(h[:, :, -1], "width", up_w)
    h_wh = lax.ppermute(h[:, :, 0], "width", [(b, a) for a, b in up_w])

    cast_low = (ci > 0).astype(F32)
    cast_high = (ci < nc - 1).astype(F32)
    width_low = (wi > 0).astype(F32)
    width_high = (wi < nw - 1).astype(F32)
    flags = jnp.stack([cast_low, cast_high, width_low, width_high, even.astype(F32)])
    h2 = h.reshape(nt * ncl, nwl)
    outs = prep_solve(h2, got_a, got_b, zones.reshape(2 * ncl, nwl), spray_coef, flags, ncl)
    y, v, w, summ, a_c, r_c, cp_c = outs[:7]
    tlo, tmd, thi = (x.reshape(nt, ncl, nwl) for x in outs[7:])
    y, summ = edge_solve(h2, h_wl, h_wh, flags, a_c, r_c, cp_c, y, summ, ncl)
    recv = lax.all_to_all(summ.reshape(nc, nt // nc, 8, nwl), "cast", 0, 0, tiled=True)
    lr_shape = recv.shape[:2] + (2, nwl)
    lr = pl.pallas_call(_cast_reduced_kernel, out_shape=jax.ShapeDtypeStruct(lr_shape, F32))(recv)
    back = lax.all_to_all(lr, "cast", 0, 0, tiled=True).reshape(nt, 2, nwl)
    y, v, w = (x.reshape(nt, ncl, nwl) for x in (y, v, w))

    lines = nt * ncl
    nsub = 4

    def wl(x):
        return jnp.transpose(x, (2, 0, 1)).reshape(nwl, lines // 128, 128)

    wa, r_w, cp_w, v_w, w_w, vws = wfactor(h2, h_wl, h_wh, flags, ncl, nsub)
    wfac = (r_w, cp_w, v_w, w_w)
    tfac = factor(tlo, tmd, thi, 8)
    yw, summ = width_solve(y, v, w, back, wa, (r_w, cp_w, vws), nsub)
    got = [summ] + [
        lax.ppermute(summ, "width", [(i, (i + q) % nw) for i in range(nw)]) for q in range(1, nw)
    ]
    me = wi.astype(jnp.int32).reshape(1)
    return thick_solve(me, got, yw, wfac[2], wfac[3], tlo, tfac, h, nsub, 8)


def solution(mesh):
    spec = P(None, "cast", "width")
    return jax.shard_map(
        shards, mesh=mesh, in_specs=(spec, spec, P()), out_specs=spec, check_vma=False
    )
```

```python
import functools

import jax
import jax.numpy as jnp
from jax import lax
from jax.experimental import pallas as pl
from jax.experimental.pallas import tpu as pltpu
from jax.sharding import PartitionSpec as P

F32 = jnp.float32
solidification_release = 0.4
quench_medium_hotness = -2.0
SMEM_SPEC = pl.BlockSpec(memory_space=pltpu.SMEM)


def _sweep(n, subs, ld, st, a_ref, b_ref, c_ref, d_ref, y_ref, v_ref, w_ref, cp_ref, unroll, shape):
    with_vw = v_ref is not None
    zero = jnp.zeros(shape, F32)
    one = jnp.ones(shape, F32)

    def fwd(i, carries):
        out = []
        for s0, (cprev, dprev, vprev) in zip(subs, carries):
            j = s0 + i
            a = ld(a_ref, j)
            r = 1.0 / (ld(b_ref, j) - a * cprev)
            cn = ld(c_ref, j) * r
            dn = (ld(d_ref, j) - a * dprev) * r
            st(cp_ref, j, cn)
            st(y_ref, j, dn)
            if with_vw:
                vprev = -(a * vprev) * r
                st(v_ref, j, vprev)
            out.append((cn, dn, vprev))
        return tuple(out)

    carries = tuple((zero, zero, one) for _ in subs)
    if unroll is True:
        for i in range(n):
            carries = fwd(i, carries)
    else:
        carries = lax.fori_loop(0, n, fwd, carries, unroll=unroll)
    if with_vw:
        for s0, (cl, _, _) in zip(subs, carries):
            st(w_ref, s0 + n - 1, -cl)

    def bwd(jj, carries):
        i = n - 2 - jj
        out = []
        for s0, (yn, vn, wn) in zip(subs, carries):
            j = s0 + i
            cp = ld(cp_ref, j)
            yn = ld(y_ref, j) - cp * yn
            st(y_ref, j, yn)
            if with_vw:
                vn = ld(v_ref, j) - cp * vn
                wn = -cp * wn
                st(v_ref, j, vn)
                st(w_ref, j, wn)
            out.append((yn, vn, wn))
        return tuple(out)

    carries = tuple((dl, vl, -cl) for cl, dl, vl in carries)
    if unroll is True:
        for jj in range(n - 1):
            carries = bwd(jj, carries)
    else:
        lax.fori_loop(0, n - 1, bwd, carries, unroll=unroll)


def _summary_rows(ld, s0, n, y_ref, v_ref, w_ref):
    return [ld(y_ref, s0), ld(v_ref, s0), ld(w_ref, s0),
            ld(y_ref, s0 + n - 1), ld(v_ref, s0 + n - 1), ld(w_ref, s0 + n - 1)]


def _cast_kernel(n, a_ref, b_ref, c_ref, d_ref, y_ref, v_ref, w_ref, sm_ref, cp_ref):
    m = a_ref.shape[0] // n

    def ld(ref, i):
        return ref[pl.ds(i, m, stride=n), :]

    def st(ref, i, val):
        ref[pl.ds(i, m, stride=n), :] = val

    shape = (m, a_ref.shape[1])
    _sweep(n, [0], ld, st, a_ref, b_ref, c_ref, d_ref, y_ref, v_ref, w_ref, cp_ref, True, shape)
    rows = _summary_rows(ld, 0, n, y_ref, v_ref, w_ref)
    rows += [jnp.zeros(shape, F32)] * (8 - len(rows))
    for k, val in enumerate(rows):
        sm_ref[pl.ds(k, m, stride=8), :] = val


def _lead_ld(ref, i):
    return ref[i]


def _lead_st(ref, i, val):
    ref[i] = val


def _loop(n, body, carry, unroll):
    if unroll is True:
        for i in range(n):
            carry = body(i, carry)
        return carry
    return lax.fori_loop(0, n, body, carry, unroll=unroll)


def _factor(n, subs, ld, st, a_ref, b_ref, c_ref, r_ref, cp_ref, v_ref, w_ref, unroll, shape):
    zero = jnp.zeros(shape, F32)
    one = jnp.ones(shape, F32)

    def fwd(i, carries):
        out = []
        for s0, (cprev, vprev) in zip(subs, carries):
            j = s0 + i
            a = ld(a_ref, j)
            r = 1.0 / (ld(b_ref, j) - a * cprev)
            cn = ld(c_ref, j) * r
            vprev = -(a * vprev) * r
            st(r_ref, j, r)
            st(cp_ref, j, cn)
            st(v_ref, j, vprev)
            out.append((cn, vprev))
        return tuple(out)

    carries = _loop(n, fwd, tuple((zero, one) for _ in subs), unroll)
    for s0, (cl, _) in zip(subs, carries):
        st(w_ref, s0 + n - 1, -cl)

    def bwd(jj, carries):
        i = n - 2 - jj
        out = []
        for s0, (vn, wn) in zip(subs, carries):
            j = s0 + i
            cp = ld(cp_ref, j)
            vn = ld(v_ref, j) - cp * vn
            wn = -cp * wn
            st(v_ref, j, vn)
            st(w_ref, j, wn)
            out.append((vn, wn))
        return tuple(out)

    _loop(n - 1, bwd, tuple((vl, -cl) for cl, vl in carries), unroll)


def _solve_rhs(n, subs, ld, st, a_ref, r_ref, cp_ref, d_ref, y_ref, unroll, shape):
    zero = jnp.zeros(shape, F32)

    def fwd(i, carries):
        out = []
        for s0, dprev in zip(subs, carries):
            j = s0 + i
            dn = (ld(d_ref, j) - ld(a_ref, j) * dprev) * ld(r_ref, j)
            st(y_ref, j, dn)
            out.append(dn)
        return tuple(out)

    carries = _loop(n, fwd, tuple(zero for _ in subs), unroll)

    def bwd(jj, carries):
        i = n - 2 - jj
        out = []
        for s0, yn in zip(subs, carries):
            j = s0 + i
            yn = ld(y_ref, j) - ld(cp_ref, j) * yn
            st(y_ref, j, yn)
            out.append(yn)
        return tuple(out)

    _loop(n - 1, bwd, carries, unroll)


def _factor_kernel(nsub, a_ref, b_ref, c_ref, r_ref, cp_ref, v_ref, w_ref):
    n = a_ref.shape[0] // nsub
    subs = [q * n for q in range(nsub)]
    _factor(n, subs, _lead_ld, _lead_st, a_ref, b_ref, c_ref, r_ref, cp_ref, v_ref, w_ref, True, a_ref.shape[1:])


def factor(a, b, c, nsub):
    shp = jax.ShapeDtypeStruct(a.shape, F32)
    return pl.pallas_call(functools.partial(_factor_kernel, nsub), out_shape=[shp] * 4)(a, b, c)


def _width_faces(n, c, T0, k0, s0, lane, wlo, whi, fl_ref):
    nwl = T0.shape[1]
    g_w = nwl * nwl / 4.0 * 0.5
    if wlo is None:
        wlo = (T0, k0, s0)
        whi = (T0, k0, s0)
        e_lo, e_hi = 0.0, 0.0
    else:
        e_lo, e_hi = fl_ref[2], fl_ref[3]
    Twm, kwm, swm = (jnp.where(lane == 0, b, pltpu.roll(f, 1, 1)) for f, b in zip((T0, k0, s0), wlo))
    Twp, kwp, swp = (
        jnp.where(lane == nwl - 1, b, pltpu.roll(f, nwl - 1, 1)) for f, b in zip((T0, k0, s0), whi)
    )
    gwl = g_w * (k0 + kwm) * jnp.where(lane == 0, e_lo, 1.0)
    gwh = g_w * (kwp + k0) * jnp.where(lane == nwl - 1, e_hi, 1.0)
    return Twm, swm, Twp, swp, gwl, gwh


def _prep_kernel(n, h_ref, hcl_ref, hch_ref, z_ref, sp_ref, fl_ref,
                 y_ref, v_ref, w_ref, sm_ref, a_ref, r_ref, cp_ref, ta_ref, tb_ref, tc_ref,
                 tp_ref, kp_ref, sp2_ref, b_ref, c_ref, d_ref):
    rows, nwl = h_ref.shape
    nt = rows // n
    hot, cond, slope = medium_parameters(h_ref[...])
    zpad = jnp.zeros((n, nwl), F32)
    for ref, val in ((tp_ref, hot), (kp_ref, cond), (sp2_ref, slope)):
        ref[0:n] = zpad
        ref[n : n + rows] = val
        ref[n + rows : 2 * n + rows] = zpad

    def row(ref, off):
        return ref[pl.ds(off, nt, stride=n), :]

    lane = lax.broadcasted_iota(jnp.int32, (nt, nwl), 1)
    tix = lax.broadcasted_iota(jnp.int32, (nt, nwl), 0)
    even = fl_ref[4] > 0.5
    got_a, got_b = hcl_ref[...], hch_ref[...]
    cast_lo = medium_parameters(jnp.where(even, got_b, got_a))
    cast_hi = medium_parameters(jnp.where(even, got_a, got_b))
    g_c = n * n * 4.0 * 0.5
    g_t = nt * nt / 4.0 * 0.5
    nz = sp_ref.shape[0]

    def surf_row(zr):
        acc = jnp.zeros(zr.shape, F32)
        for q in range(nz):
            acc = jnp.where(zr == q, sp_ref[q], acc)
        return acc * (nt * nt / 8.0)

    for c in range(n):
        T0, k0, s0 = (row(r, n + c) for r in (tp_ref, kp_ref, sp2_ref))
        if c == 0:
            Tm, km, sm = cast_lo
        else:
            Tm, km, sm = (row(r, n + c - 1) for r in (tp_ref, kp_ref, sp2_ref))
        if c == n - 1:
            Tq, kq, sq = cast_hi
        else:
            Tq, kq, sq = (row(r, n + c + 1) for r in (tp_ref, kp_ref, sp2_ref))
        Ttm, ktm, stm = (row(r, c) for r in (tp_ref, kp_ref, sp2_ref))
        Ttp, ktp, stp = (row(r, 2 * n + c) for r in (tp_ref, kp_ref, sp2_ref))
        Twm, _, Twp, _, gwl, gwh = _width_faces(n, c, T0, k0, s0, lane, None, None, fl_ref)
        gcl = g_c * (k0 + km)
        if c == 0:
            gcl = gcl * fl_ref[0]
        gch = g_c * (kq + k0)
        if c == n - 1:
            gch = gch * fl_ref[1]
        gtl = jnp.where(tix == 0, 0.0, g_t * (k0 + ktm))
        gth = jnp.where(tix == nt - 1, 0.0, g_t * (ktp + k0))
        s_lo = surf_row(z_ref[c : c + 1, :])
        s_hi = surf_row(z_ref[n + c : n + c + 1, :])
        rim = jnp.where(tix == 0, s_lo, jnp.where(tix == nt - 1, s_hi, 0.0))
        ex = rim * (quench_medium_hotness - T0)
        ex = ex + (gch * (Tq - T0) - gcl * (T0 - Tm))
        ex = ex + (gwh * (Twp - T0) - gwl * (T0 - Twm))
        ex = ex + (gth * (Ttp - T0) - gtl * (T0 - Ttm))
        sel = pl.ds(c, nt, stride=n)
        a_ref[sel, :] = -gcl * sm
        c_ref[sel, :] = -gch * sq
        b_ref[sel, :] = 1.0 + s0 * (gcl + gch)
        d_ref[sel, :] = ex
        ta_ref[sel, :] = -gtl * stm
        tc_ref[sel, :] = -gth * stp
        tb_ref[sel, :] = 1.0 + s0 * (gtl + gth + rim)

    def ld(ref, i):
        return ref[pl.ds(i, nt, stride=n), :]

    def st(ref, i, val):
        ref[pl.ds(i, nt, stride=n), :] = val

    shape = (nt, nwl)
    _factor(n, [0], ld, st, a_ref, b_ref, c_ref, r_ref, cp_ref, v_ref, w_ref, True, shape)
    _solve_rhs(n, [0], ld, st, a_ref, r_ref, cp_ref, d_ref, y_ref, True, shape)
    rws = _summary_rows(ld, 0, n, y_ref, v_ref, w_ref)
    rws += [jnp.zeros(shape, F32)] * (8 - len(rws))
    for k, val in enumerate(rws):
        sm_ref[pl.ds(k, nt, stride=8), :] = val


def prep_solve(h2, hcl, hch, z2, spray, flags, n):
    rows, nwl = h2.shape
    nt = rows // n
    shp = jax.ShapeDtypeStruct(h2.shape, F32)
    vm = pl.BlockSpec(memory_space=pltpu.VMEM)
    pad = pltpu.VMEM((rows + 2 * n, nwl), F32)
    return pl.pallas_call(
        functools.partial(_prep_kernel, n),
        out_shape=[shp] * 3 + [jax.ShapeDtypeStruct((nt * 8, nwl), F32)] + [shp] * 6,
        in_specs=[vm] * 4 + [SMEM_SPEC, SMEM_SPEC],
        scratch_shapes=[pad, pad, pad] + [pltpu.VMEM(h2.shape, F32)] * 3,
    )(h2, hcl, hch, z2, spray, flags)


def _edge_kernel(n, h_ref, hwl_ref, hwh_ref, fl_ref, a_ref, r_ref, cp_ref, y_ref, sm_ref,
                 yo_ref, smo_ref, d_ref, e_ref):
    rows, nwl = h_ref.shape
    nt = rows // n
    lane = lax.broadcasted_iota(jnp.int32, (nt, nwl), 1)
    for c in range(n):
        sel = pl.ds(c, nt, stride=n)
        T0, k0, s0 = medium_parameters(h_ref[sel, :])
        wlo = medium_parameters(hwl_ref[:, c : c + 1])
        whi = medium_parameters(hwh_ref[:, c : c + 1])
        Twm, _, Twp, _, gwl, gwh = _width_faces(n, c, T0, k0, s0, lane, wlo, whi, fl_ref)
        edge = jnp.where(lane == 0, -gwl * (T0 - Twm), jnp.where(lane == nwl - 1, gwh * (Twp - T0), 0.0))
        d_ref[sel, :] = edge

    def ld(ref, i):
        return ref[pl.ds(i, nt, stride=n), :]

    def st(ref, i, val):
        ref[pl.ds(i, nt, stride=n), :] = val

    _solve_rhs(n, [0], ld, st, a_ref, r_ref, cp_ref, d_ref, e_ref, True, (nt, nwl))
    yo_ref[...] = y_ref[...] + e_ref[...]
    smo_ref[...] = sm_ref[...]
    smo_ref[pl.ds(0, nt, stride=8), :] = sm_ref[pl.ds(0, nt, stride=8), :] + ld(e_ref, 0)
    smo_ref[pl.ds(3, nt, stride=8), :] = sm_ref[pl.ds(3, nt, stride=8), :] + ld(e_ref, n - 1)


def edge_solve(h2, hwl, hwh, flags, a, r, cp, y, sm, n):
    vm = pl.BlockSpec(memory_space=pltpu.VMEM)
    return pl.pallas_call(
        functools.partial(_edge_kernel, n),
        out_shape=[jax.ShapeDtypeStruct(y.shape, F32), jax.ShapeDtypeStruct(sm.shape, F32)],
        in_specs=[vm] * 3 + [SMEM_SPEC] + [vm] * 5,
        scratch_shapes=[pltpu.VMEM(y.shape, F32)] * 2,
    )(h2, hwl, hwh, flags, a, r, cp, y, sm)


def _wfactor_kernel(n, nsub, h_ref, hwl_ref, hwh_ref, fl_ref, a_ref, r_ref, cp_ref, v_ref, w_ref,
                    vws_ref, at_ref, bt_ref, ct_ref, b_ref, c_ref):
    rows, nwl = h_ref.shape
    nt = rows // n
    lane = lax.broadcasted_iota(jnp.int32, (nt, nwl), 1)
    for c in range(n):
        sel = pl.ds(c, nt, stride=n)
        T0, k0, s0 = medium_parameters(h_ref[sel, :])
        wlo = medium_parameters(hwl_ref[:, c : c + 1])
        whi = medium_parameters(hwh_ref[:, c : c + 1])
        _, swm, _, swp, gwl, gwh = _width_faces(n, c, T0, k0, s0, lane, wlo, whi, fl_ref)
        at_ref[sel, :] = -gwl * swm
        ct_ref[sel, :] = -gwh * swp
        bt_ref[sel, :] = 1.0 + s0 * (gwl + gwh)
    for src, dst in ((at_ref, a_ref), (bt_ref, b_ref), (ct_ref, c_ref)):
        for q in range(dst.shape[1]):
            dst[:, q, :] = src[q * 128 : (q + 1) * 128, :].T
    m = a_ref.shape[0] // nsub
    subs = [q * m for q in range(nsub)]
    _factor(m, subs, _lead_ld, _lead_st, a_ref, b_ref, c_ref, r_ref, cp_ref, v_ref, w_ref, True, a_ref.shape[1:])
    for q, s0 in enumerate(subs):
        for k, val in enumerate((v_ref[s0], w_ref[s0], v_ref[s0 + m - 1], w_ref[s0 + m - 1])):
            vws_ref[q, k] = val


def wfactor(h2, hwl, hwh, flags, n, nsub):
    rows, nwl = h2.shape
    wshape = (nwl, rows // 128, 128)
    shp = jax.ShapeDtypeStruct(wshape, F32)
    vm = pl.BlockSpec(memory_space=pltpu.VMEM)
    return pl.pallas_call(
        functools.partial(_wfactor_kernel, n, nsub),
        out_shape=[shp] * 5 + [jax.ShapeDtypeStruct((nsub, 4) + wshape[1:], F32)],
        in_specs=[vm] * 3 + [SMEM_SPEC],
        scratch_shapes=[pltpu.VMEM(h2.shape, F32)] * 3 + [pltpu.VMEM(wshape, F32)] * 2,
    )(h2, hwl, hwh, flags)


def _width_kernel(nsub, yc_ref, vc_ref, wc_ref, bk_ref, a_ref, r_ref, cp_ref, vws_ref,
                  y_ref, sm_ref, d_ref):
    sc = yc_ref[...] + vc_ref[...] * bk_ref[:, 0:1, :] + wc_ref[...] * bk_ref[:, 1:2, :]
    nt, ncl, nwl = sc.shape
    sc = sc.reshape(nt * ncl, nwl)
    for q in range(d_ref.shape[1]):
        d_ref[:, q, :] = sc[q * 128 : (q + 1) * 128, :].T
    n = a_ref.shape[0] // nsub
    subs = [q * n for q in range(nsub)]
    _solve_rhs(n, subs, _lead_ld, _lead_st, a_ref, r_ref, cp_ref, d_ref, y_ref, True, a_ref.shape[1:])
    for q, s0 in enumerate(subs):
        rows = (y_ref[s0], vws_ref[q, 0], vws_ref[q, 1], y_ref[s0 + n - 1], vws_ref[q, 2], vws_ref[q, 3])
        for k, val in enumerate(rows):
            sm_ref[q, k] = val


def _thick_kernel(nsub, tsub, nw, me_ref, *refs):
    r_refs = refs[:nw]
    (yw_ref, vw_ref, ww_ref, a_ref, r_ref, cp_ref, v_ref, w_ref, h_ref,
     o_ref, sw_ref, d_ref, y_ref) = refs[nw:]
    lrw = _width_reduce(me_ref[0], r_refs)
    m = yw_ref.shape[0] // nsub
    for q in range(nsub):
        sl = slice(q * m, (q + 1) * m)
        sw_ref[sl] = yw_ref[sl] + vw_ref[sl] * lrw[q][0] + ww_ref[sl] * lrw[q][1]
    nt, ncl, nwl = a_ref.shape
    per_q = 128 // ncl
    for q in range(sw_ref.shape[1]):
        d_ref[q * per_q : (q + 1) * per_q] = sw_ref[:, q, :].T.reshape(per_q, ncl, nwl)
    n = nt // tsub
    subs = [q * n for q in range(tsub)]
    shape = a_ref.shape[1:]
    _solve_rhs(n, subs, _lead_ld, _lead_st, a_ref, r_ref, cp_ref, d_ref, y_ref, True, shape)
    sums = [tuple(_summary_rows(_lead_ld, s0, n, y_ref, v_ref, w_ref)) for s0 in subs]
    lrs = [None] * tsub

    def emit(p, left, right):
        lrs[p] = (left, right)

    _reduce_blocks(tsub, lambda p: sums[p], emit, jnp.zeros(shape, F32))
    for q, s0 in enumerate(subs):
        sl = slice(s0, s0 + n)
        left, right = lrs[q]
        o_ref[sl] = h_ref[sl] + (y_ref[sl] + v_ref[sl] * left + w_ref[sl] * right)


def cast_solve(a, b, c, d, n):
    shp = jax.ShapeDtypeStruct(a.shape, F32)
    m = a.shape[0] // n
    return pl.pallas_call(
        functools.partial(_cast_kernel, n),
        out_shape=[shp, shp, shp, jax.ShapeDtypeStruct((m * 8, a.shape[1]), F32)],
        scratch_shapes=[pltpu.VMEM(a.shape, F32)],
    )(a, b, c, d)


def width_solve(yc, vc, wc, bk, a, fac, nsub):
    shp = jax.ShapeDtypeStruct(a.shape, F32)
    return pl.pallas_call(
        functools.partial(_width_kernel, nsub),
        out_shape=[shp, jax.ShapeDtypeStruct((nsub, 6) + a.shape[1:], F32)],
        scratch_shapes=[pltpu.VMEM(a.shape, F32)],
    )(yc, vc, wc, bk, a, *fac)


def thick_solve(me, got, yw, vw, ww, a, fac, h, nsub, tsub):
    vm = pl.BlockSpec(memory_space=pltpu.VMEM)
    return pl.pallas_call(
        functools.partial(_thick_kernel, nsub, tsub, len(got)),
        out_shape=jax.ShapeDtypeStruct(a.shape, F32),
        in_specs=[SMEM_SPEC] + [vm] * (len(got) + 9),
        scratch_shapes=[pltpu.VMEM(yw.shape, F32)] + [pltpu.VMEM(a.shape, F32)] * 2,
    )(me, *got, yw, vw, ww, a, *fac, h)


def _reduce_blocks(nb, blk, emit, zero):
    pp, qq = zero, zero
    saved = []
    for p in range(nb):
        y0, v0, w0, yn, vn, wn = blk(p)
        rd = 1.0 / (1.0 - v0 * qq)
        fa = (y0 + v0 * pp) * rd
        fb = w0 * rd
        saved.append((fa, fb, pp, qq))
        pp, qq = yn + vn * (pp + qq * fa), wn + vn * qq * fb
    f_next = zero
    for p in range(nb - 1, -1, -1):
        fa, fb, pp, qq = saved[p]
        f = fa + fb * f_next
        emit(p, pp + qq * f, f_next)
        f_next = f


def _merge(A, B):
    yA0, vA0, wA0, yAn, vAn, wAn = A
    yB0, vB0, wB0, yBn, vBn, wBn = B
    rd = 1.0 / (1.0 - wAn * vB0)
    ey = (yAn + wAn * yB0) * rd
    ev = vAn * rd
    ew = wAn * wB0 * rd
    fy = yB0 + vB0 * ey
    fv = vB0 * ev
    fw = wB0 + vB0 * ew
    return (yA0 + wA0 * fy, vA0 + wA0 * fv, wA0 * fw, yBn + vBn * ey, vBn * ev, wBn + vBn * ew)


def _chain(nb, blk, emit, left, right):
    pp, qq = left, jnp.zeros_like(left)
    saved = []
    for p in range(nb):
        y0, v0, w0, yn, vn, wn = blk(p)
        rd = 1.0 / (1.0 - v0 * qq)
        fa = (y0 + v0 * pp) * rd
        fb = w0 * rd
        saved.append((fa, fb, pp, qq))
        pp, qq = yn + vn * (pp + qq * fa), wn + vn * qq * fb
    f_next = right
    for p in range(nb - 1, -1, -1):
        fa, fb, pp, qq = saved[p]
        f = fa + fb * f_next
        emit(p, pp + qq * f, f_next)
        f_next = f


def _cast_reduced_kernel(s_ref, lr_ref):
    nb, g, _, nl = s_ref.shape
    ng = 8
    if g != 1 or nb % ng:
        def blk(p):
            return tuple(s_ref[p, :, k, :] for k in range(6))

        def emit(p, left, right):
            lr_ref[p, :, 0:1, :] = left[:, None]
            lr_ref[p, :, 1:2, :] = right[:, None]

        _reduce_blocks(nb, blk, emit, jnp.zeros((g, nl), F32))
        return
    m = nb // ng

    def member(j):
        return tuple(
            jnp.concatenate([s_ref[G * m + j, 0, k : k + 1, :] for G in range(ng)], 0)
            for k in range(6)
        )

    members = [member(j) for j in range(m)]
    acc = members[0]
    for j in range(1, m):
        acc = _merge(acc, members[j])
    outer = [None] * ng

    def emit_g(G, left, right):
        outer[G] = (left, right)

    zero1 = jnp.zeros((1, nl), F32)
    _chain(ng, lambda G: tuple(x[G : G + 1] for x in acc), emit_g, zero1, zero1)
    left_g = jnp.concatenate([outer[G][0] for G in range(ng)], 0)
    right_g = jnp.concatenate([outer[G][1] for G in range(ng)], 0)

    def emit(j, left, right):
        for G in range(ng):
            lr_ref[G * m + j, 0, 0:1, :] = left[G : G + 1]
            lr_ref[G * m + j, 0, 1:2, :] = right[G : G + 1]

    _chain(m, lambda j: members[j], emit, left_g, right_g)


def _width_reduce(me, r_refs):
    nw = len(r_refs)
    nsub = r_refs[0].shape[0]
    out = [[None, None] for _ in range(nsub)]

    def blk(b):
        dev, q = divmod(b, nsub)
        kk = (me - dev + nw) % nw
        vals = []
        for k6 in range(6):
            val = r_refs[0][q, k6]
            for k in range(1, nw):
                val = jnp.where(kk == k, r_refs[k][q, k6], val)
            vals.append(val)
        return tuple(vals)

    def emit(b, left, right):
        dev, q = divmod(b, nsub)
        mine = me == dev
        for j, val in enumerate((left, right)):
            out[q][j] = val if out[q][j] is None else jnp.where(mine, val, out[q][j])

    _reduce_blocks(nw * nsub, blk, emit, jnp.zeros(r_refs[0].shape[2:], F32))
    return out


def _surface_kernel(scale, z_ref, sp_ref, o_ref):
    z = z_ref[...]
    acc = jnp.zeros(z.shape, F32)
    for q in range(sp_ref.shape[0]):
        acc = jnp.where(z == q, sp_ref[q], acc)
    o_ref[...] = acc * scale


def medium_parameters(x):
    t = jnp.tanh(x)
    hot = x - solidification_release * t
    cond = 1.5 - 0.5 * jnp.tanh(hot)
    slope = (1.0 - solidification_release) + solidification_release * t * t
    return hot, cond, slope


def shards(h, zones, spray_coef):
    nt, ncl, nwl = h.shape
    nc, nw = lax.axis_size("cast"), lax.axis_size("width")
    ci, wi = lax.axis_index("cast"), lax.axis_index("width")
    up_c = [(i, i + 1) for i in range(nc - 1)]
    up_w = [(i, i + 1) for i in range(nw - 1)]
    even = ci % 2 == 0
    first, last = h[:, 0, :], h[:, -1, :]
    in_chip = [(i, i ^ 1) for i in range(nc)]
    across = [(i, i + 1) for i in range(1, nc - 1, 2)] + [(i + 1, i) for i in range(1, nc - 1, 2)]
    got_a = lax.ppermute(jnp.where(even, last, first), "cast", in_chip)
    got_b = lax.ppermute(jnp.where(even, first, last), "cast", across)
    h_wl = lax.ppermute(h[:, :, -1], "width", up_w)
    h_wh = lax.ppermute(h[:, :, 0], "width", [(b, a) for a, b in up_w])

    cast_low = (ci > 0).astype(F32)
    cast_high = (ci < nc - 1).astype(F32)
    width_low = (wi > 0).astype(F32)
    width_high = (wi < nw - 1).astype(F32)
    flags = jnp.stack([cast_low, cast_high, width_low, width_high, even.astype(F32)])
    h2 = h.reshape(nt * ncl, nwl)
    outs = prep_solve(h2, got_a, got_b, zones.reshape(2 * ncl, nwl), spray_coef, flags, ncl)
    y, v, w, summ, a_c, r_c, cp_c = outs[:7]
    tlo, tmd, thi = (x.reshape(nt, ncl, nwl) for x in outs[7:])
    y, summ = edge_solve(h2, h_wl, h_wh, flags, a_c, r_c, cp_c, y, summ, ncl)
    recv = lax.all_to_all(summ.reshape(nc, nt // nc, 8, nwl), "cast", 0, 0, tiled=True)
    lr_shape = recv.shape[:2] + (2, nwl)
    lr = pl.pallas_call(_cast_reduced_kernel, out_shape=jax.ShapeDtypeStruct(lr_shape, F32))(recv)
    back = lax.all_to_all(lr, "cast", 0, 0, tiled=True).reshape(nt, 2, nwl)
    y, v, w = (x.reshape(nt, ncl, nwl) for x in (y, v, w))

    lines = nt * ncl
    nsub = 4

    def wl(x):
        return jnp.transpose(x, (2, 0, 1)).reshape(nwl, lines // 128, 128)

    wa, r_w, cp_w, v_w, w_w, vws = wfactor(h2, h_wl, h_wh, flags, ncl, nsub)
    wfac = (r_w, cp_w, v_w, w_w)
    tfac = factor(tlo, tmd, thi, 16)
    yw, summ = width_solve(y, v, w, back, wa, (r_w, cp_w, vws), nsub)
    got = [summ] + [
        lax.ppermute(summ, "width", [(i, (i + q) % nw) for i in range(nw)]) for q in range(1, nw)
    ]
    me = wi.astype(jnp.int32).reshape(1)
    return thick_solve(me, got, yw, wfac[2], wfac[3], tlo, tfac, h, nsub, 16)


def solution(mesh):
    spec = P(None, "cast", "width")
    return jax.shard_map(
        shards, mesh=mesh, in_specs=(spec, spec, P()), out_specs=spec, check_vma=False
    )
```

```python
import functools

import jax
import jax.numpy as jnp
from jax import lax
from jax.experimental import pallas as pl
from jax.experimental.pallas import tpu as pltpu
from jax.sharding import PartitionSpec as P

F32 = jnp.float32
solidification_release = 0.4
quench_medium_hotness = -2.0
SMEM_SPEC = pl.BlockSpec(memory_space=pltpu.SMEM)


def _sweep(n, subs, ld, st, a_ref, b_ref, c_ref, d_ref, y_ref, v_ref, w_ref, cp_ref, unroll, shape):
    with_vw = v_ref is not None
    zero = jnp.zeros(shape, F32)
    one = jnp.ones(shape, F32)

    def fwd(i, carries):
        out = []
        for s0, (cprev, dprev, vprev) in zip(subs, carries):
            j = s0 + i
            a = ld(a_ref, j)
            r = 1.0 / (ld(b_ref, j) - a * cprev)
            cn = ld(c_ref, j) * r
            dn = (ld(d_ref, j) - a * dprev) * r
            st(cp_ref, j, cn)
            st(y_ref, j, dn)
            if with_vw:
                vprev = -(a * vprev) * r
                st(v_ref, j, vprev)
            out.append((cn, dn, vprev))
        return tuple(out)

    carries = tuple((zero, zero, one) for _ in subs)
    if unroll is True:
        for i in range(n):
            carries = fwd(i, carries)
    else:
        carries = lax.fori_loop(0, n, fwd, carries, unroll=unroll)
    if with_vw:
        for s0, (cl, _, _) in zip(subs, carries):
            st(w_ref, s0 + n - 1, -cl)

    def bwd(jj, carries):
        i = n - 2 - jj
        out = []
        for s0, (yn, vn, wn) in zip(subs, carries):
            j = s0 + i
            cp = ld(cp_ref, j)
            yn = ld(y_ref, j) - cp * yn
            st(y_ref, j, yn)
            if with_vw:
                vn = ld(v_ref, j) - cp * vn
                wn = -cp * wn
                st(v_ref, j, vn)
                st(w_ref, j, wn)
            out.append((yn, vn, wn))
        return tuple(out)

    carries = tuple((dl, vl, -cl) for cl, dl, vl in carries)
    if unroll is True:
        for jj in range(n - 1):
            carries = bwd(jj, carries)
    else:
        lax.fori_loop(0, n - 1, bwd, carries, unroll=unroll)


def _summary_rows(ld, s0, n, y_ref, v_ref, w_ref):
    return [ld(y_ref, s0), ld(v_ref, s0), ld(w_ref, s0),
            ld(y_ref, s0 + n - 1), ld(v_ref, s0 + n - 1), ld(w_ref, s0 + n - 1)]


def _cast_kernel(n, a_ref, b_ref, c_ref, d_ref, y_ref, v_ref, w_ref, sm_ref, cp_ref):
    m = a_ref.shape[0] // n

    def ld(ref, i):
        return ref[pl.ds(i, m, stride=n), :]

    def st(ref, i, val):
        ref[pl.ds(i, m, stride=n), :] = val

    shape = (m, a_ref.shape[1])
    _sweep(n, [0], ld, st, a_ref, b_ref, c_ref, d_ref, y_ref, v_ref, w_ref, cp_ref, True, shape)
    rows = _summary_rows(ld, 0, n, y_ref, v_ref, w_ref)
    rows += [jnp.zeros(shape, F32)] * (8 - len(rows))
    for k, val in enumerate(rows):
        sm_ref[pl.ds(k, m, stride=8), :] = val


def _lead_ld(ref, i):
    return ref[i]


def _lead_st(ref, i, val):
    ref[i] = val


def _loop(n, body, carry, unroll):
    if unroll is True:
        for i in range(n):
            carry = body(i, carry)
        return carry
    return lax.fori_loop(0, n, body, carry, unroll=unroll)


def _factor(n, subs, ld, st, a_ref, b_ref, c_ref, r_ref, cp_ref, v_ref, w_ref, unroll, shape):
    zero = jnp.zeros(shape, F32)
    one = jnp.ones(shape, F32)

    def fwd(i, carries):
        out = []
        for s0, (cprev, vprev) in zip(subs, carries):
            j = s0 + i
            a = ld(a_ref, j)
            r = 1.0 / (ld(b_ref, j) - a * cprev)
            cn = ld(c_ref, j) * r
            vprev = -(a * vprev) * r
            st(r_ref, j, r)
            st(cp_ref, j, cn)
            st(v_ref, j, vprev)
            out.append((cn, vprev))
        return tuple(out)

    carries = _loop(n, fwd, tuple((zero, one) for _ in subs), unroll)
    for s0, (cl, _) in zip(subs, carries):
        st(w_ref, s0 + n - 1, -cl)

    def bwd(jj, carries):
        i = n - 2 - jj
        out = []
        for s0, (vn, wn) in zip(subs, carries):
            j = s0 + i
            cp = ld(cp_ref, j)
            vn = ld(v_ref, j) - cp * vn
            wn = -cp * wn
            st(v_ref, j, vn)
            st(w_ref, j, wn)
            out.append((vn, wn))
        return tuple(out)

    _loop(n - 1, bwd, tuple((vl, -cl) for cl, vl in carries), unroll)


def _solve_rhs(n, subs, ld, st, a_ref, r_ref, cp_ref, d_ref, y_ref, unroll, shape):
    zero = jnp.zeros(shape, F32)

    def fwd(i, carries):
        out = []
        for s0, dprev in zip(subs, carries):
            j = s0 + i
            dn = (ld(d_ref, j) - ld(a_ref, j) * dprev) * ld(r_ref, j)
            st(y_ref, j, dn)
            out.append(dn)
        return tuple(out)

    carries = _loop(n, fwd, tuple(zero for _ in subs), unroll)

    def bwd(jj, carries):
        i = n - 2 - jj
        out = []
        for s0, yn in zip(subs, carries):
            j = s0 + i
            yn = ld(y_ref, j) - ld(cp_ref, j) * yn
            st(y_ref, j, yn)
            out.append(yn)
        return tuple(out)

    _loop(n - 1, bwd, carries, unroll)


def _factor_kernel(nsub, a_ref, b_ref, c_ref, r_ref, cp_ref, v_ref, w_ref):
    n = a_ref.shape[0] // nsub
    subs = [q * n for q in range(nsub)]
    _factor(n, subs, _lead_ld, _lead_st, a_ref, b_ref, c_ref, r_ref, cp_ref, v_ref, w_ref, True, a_ref.shape[1:])


def factor(a, b, c, nsub):
    shp = jax.ShapeDtypeStruct(a.shape, F32)
    return pl.pallas_call(functools.partial(_factor_kernel, nsub), out_shape=[shp] * 4)(a, b, c)


def _width_faces(n, c, T0, k0, s0, lane, wlo, whi, fl_ref):
    nwl = T0.shape[1]
    g_w = nwl * nwl / 4.0 * 0.5
    if wlo is None:
        wlo = (T0, k0, s0)
        whi = (T0, k0, s0)
        e_lo, e_hi = 0.0, 0.0
    else:
        e_lo, e_hi = fl_ref[2], fl_ref[3]
    Twm, kwm, swm = (jnp.where(lane == 0, b, pltpu.roll(f, 1, 1)) for f, b in zip((T0, k0, s0), wlo))
    Twp, kwp, swp = (
        jnp.where(lane == nwl - 1, b, pltpu.roll(f, nwl - 1, 1)) for f, b in zip((T0, k0, s0), whi)
    )
    gwl = g_w * (k0 + kwm) * jnp.where(lane == 0, e_lo, 1.0)
    gwh = g_w * (kwp + k0) * jnp.where(lane == nwl - 1, e_hi, 1.0)
    return Twm, swm, Twp, swp, gwl, gwh


def _prep_kernel(n, h_ref, hcl_ref, hch_ref, z_ref, sp_ref, fl_ref,
                 y_ref, v_ref, w_ref, sm_ref, a_ref, r_ref, cp_ref, ta_ref, tb_ref, tc_ref,
                 tp_ref, kp_ref, sp2_ref, b_ref, c_ref, d_ref):
    rows, nwl = h_ref.shape
    nt = rows // n
    hot, cond, slope = medium_parameters(h_ref[...])
    zpad = jnp.zeros((n, nwl), F32)
    for ref, val in ((tp_ref, hot), (kp_ref, cond), (sp2_ref, slope)):
        ref[0:n] = zpad
        ref[n : n + rows] = val
        ref[n + rows : 2 * n + rows] = zpad

    def row(ref, off):
        return ref[pl.ds(off, nt, stride=n), :]

    lane = lax.broadcasted_iota(jnp.int32, (nt, nwl), 1)
    tix = lax.broadcasted_iota(jnp.int32, (nt, nwl), 0)
    even = fl_ref[4] > 0.5
    got_a, got_b = hcl_ref[...], hch_ref[...]
    cast_lo = medium_parameters(jnp.where(even, got_b, got_a))
    cast_hi = medium_parameters(jnp.where(even, got_a, got_b))
    g_c = n * n * 4.0 * 0.5
    g_t = nt * nt / 4.0 * 0.5
    nz = sp_ref.shape[0]

    def surf_row(zr):
        acc = jnp.zeros(zr.shape, F32)
        for q in range(nz):
            acc = jnp.where(zr == q, sp_ref[q], acc)
        return acc * (nt * nt / 8.0)

    for c in range(n):
        T0, k0, s0 = (row(r, n + c) for r in (tp_ref, kp_ref, sp2_ref))
        if c == 0:
            Tm, km, sm = cast_lo
        else:
            Tm, km, sm = (row(r, n + c - 1) for r in (tp_ref, kp_ref, sp2_ref))
        if c == n - 1:
            Tq, kq, sq = cast_hi
        else:
            Tq, kq, sq = (row(r, n + c + 1) for r in (tp_ref, kp_ref, sp2_ref))
        Ttm, ktm, stm = (row(r, c) for r in (tp_ref, kp_ref, sp2_ref))
        Ttp, ktp, stp = (row(r, 2 * n + c) for r in (tp_ref, kp_ref, sp2_ref))
        Twm, _, Twp, _, gwl, gwh = _width_faces(n, c, T0, k0, s0, lane, None, None, fl_ref)
        gcl = g_c * (k0 + km)
        if c == 0:
            gcl = gcl * fl_ref[0]
        gch = g_c * (kq + k0)
        if c == n - 1:
            gch = gch * fl_ref[1]
        gtl = jnp.where(tix == 0, 0.0, g_t * (k0 + ktm))
        gth = jnp.where(tix == nt - 1, 0.0, g_t * (ktp + k0))
        s_lo = surf_row(z_ref[c : c + 1, :])
        s_hi = surf_row(z_ref[n + c : n + c + 1, :])
        rim = jnp.where(tix == 0, s_lo, jnp.where(tix == nt - 1, s_hi, 0.0))
        ex = rim * (quench_medium_hotness - T0)
        ex = ex + (gch * (Tq - T0) - gcl * (T0 - Tm))
        ex = ex + (gwh * (Twp - T0) - gwl * (T0 - Twm))
        ex = ex + (gth * (Ttp - T0) - gtl * (T0 - Ttm))
        sel = pl.ds(c, nt, stride=n)
        a_ref[sel, :] = -gcl * sm
        c_ref[sel, :] = -gch * sq
        b_ref[sel, :] = 1.0 + s0 * (gcl + gch)
        d_ref[sel, :] = ex
        ta_ref[sel, :] = -gtl * stm
        tc_ref[sel, :] = -gth * stp
        tb_ref[sel, :] = 1.0 + s0 * (gtl + gth + rim)

    def ld(ref, i):
        return ref[pl.ds(i, nt, stride=n), :]

    def st(ref, i, val):
        ref[pl.ds(i, nt, stride=n), :] = val

    shape = (nt, nwl)
    _factor(n, [0], ld, st, a_ref, b_ref, c_ref, r_ref, cp_ref, v_ref, w_ref, True, shape)
    _solve_rhs(n, [0], ld, st, a_ref, r_ref, cp_ref, d_ref, y_ref, True, shape)
    rws = _summary_rows(ld, 0, n, y_ref, v_ref, w_ref)
    rws += [jnp.zeros(shape, F32)] * (8 - len(rws))
    for k, val in enumerate(rws):
        sm_ref[pl.ds(k, nt, stride=8), :] = val


def prep_solve(h2, hcl, hch, z2, spray, flags, n):
    rows, nwl = h2.shape
    nt = rows // n
    shp = jax.ShapeDtypeStruct(h2.shape, F32)
    vm = pl.BlockSpec(memory_space=pltpu.VMEM)
    pad = pltpu.VMEM((rows + 2 * n, nwl), F32)
    return pl.pallas_call(
        functools.partial(_prep_kernel, n),
        out_shape=[shp] * 3 + [jax.ShapeDtypeStruct((nt * 8, nwl), F32)] + [shp] * 6,
        in_specs=[vm] * 4 + [SMEM_SPEC, SMEM_SPEC],
        scratch_shapes=[pad, pad, pad] + [pltpu.VMEM(h2.shape, F32)] * 3,
    )(h2, hcl, hch, z2, spray, flags)


def _edge_kernel(n, h_ref, hwl_ref, hwh_ref, fl_ref, a_ref, r_ref, cp_ref, y_ref, sm_ref,
                 yo_ref, smo_ref, d_ref, e_ref):
    rows, nwl = h_ref.shape
    nt = rows // n
    lane = lax.broadcasted_iota(jnp.int32, (nt, nwl), 1)
    for c in range(n):
        sel = pl.ds(c, nt, stride=n)
        T0, k0, s0 = medium_parameters(h_ref[sel, :])
        wlo = medium_parameters(hwl_ref[:, c : c + 1])
        whi = medium_parameters(hwh_ref[:, c : c + 1])
        Twm, _, Twp, _, gwl, gwh = _width_faces(n, c, T0, k0, s0, lane, wlo, whi, fl_ref)
        edge = jnp.where(lane == 0, -gwl * (T0 - Twm), jnp.where(lane == nwl - 1, gwh * (Twp - T0), 0.0))
        d_ref[sel, :] = edge

    def ld(ref, i):
        return ref[pl.ds(i, nt, stride=n), :]

    def st(ref, i, val):
        ref[pl.ds(i, nt, stride=n), :] = val

    _solve_rhs(n, [0], ld, st, a_ref, r_ref, cp_ref, d_ref, e_ref, True, (nt, nwl))
    yo_ref[...] = y_ref[...] + e_ref[...]
    smo_ref[...] = sm_ref[...]
    smo_ref[pl.ds(0, nt, stride=8), :] = sm_ref[pl.ds(0, nt, stride=8), :] + ld(e_ref, 0)
    smo_ref[pl.ds(3, nt, stride=8), :] = sm_ref[pl.ds(3, nt, stride=8), :] + ld(e_ref, n - 1)


def edge_solve(h2, hwl, hwh, flags, a, r, cp, y, sm, n):
    vm = pl.BlockSpec(memory_space=pltpu.VMEM)
    return pl.pallas_call(
        functools.partial(_edge_kernel, n),
        out_shape=[jax.ShapeDtypeStruct(y.shape, F32), jax.ShapeDtypeStruct(sm.shape, F32)],
        in_specs=[vm] * 3 + [SMEM_SPEC] + [vm] * 5,
        scratch_shapes=[pltpu.VMEM(y.shape, F32)] * 2,
    )(h2, hwl, hwh, flags, a, r, cp, y, sm)


def _wfactor_kernel(n, nsub, h_ref, hwl_ref, hwh_ref, fl_ref, a_ref, r_ref, cp_ref, v_ref, w_ref,
                    vws_ref, at_ref, bt_ref, ct_ref, b_ref, c_ref):
    rows, nwl = h_ref.shape
    nt = rows // n
    lane = lax.broadcasted_iota(jnp.int32, (nt, nwl), 1)
    for c in range(n):
        sel = pl.ds(c, nt, stride=n)
        T0, k0, s0 = medium_parameters(h_ref[sel, :])
        wlo = medium_parameters(hwl_ref[:, c : c + 1])
        whi = medium_parameters(hwh_ref[:, c : c + 1])
        _, swm, _, swp, gwl, gwh = _width_faces(n, c, T0, k0, s0, lane, wlo, whi, fl_ref)
        at_ref[sel, :] = -gwl * swm
        ct_ref[sel, :] = -gwh * swp
        bt_ref[sel, :] = 1.0 + s0 * (gwl + gwh)
    for src, dst in ((at_ref, a_ref), (bt_ref, b_ref), (ct_ref, c_ref)):
        for q in range(dst.shape[1]):
            dst[:, q, :] = src[q * 128 : (q + 1) * 128, :].T
    m = a_ref.shape[0] // nsub
    subs = [q * m for q in range(nsub)]
    _factor(m, subs, _lead_ld, _lead_st, a_ref, b_ref, c_ref, r_ref, cp_ref, v_ref, w_ref, True, a_ref.shape[1:])
    for q, s0 in enumerate(subs):
        for k, val in enumerate((v_ref[s0], w_ref[s0], v_ref[s0 + m - 1], w_ref[s0 + m - 1])):
            vws_ref[q, k] = val


def wfactor(h2, hwl, hwh, flags, n, nsub):
    rows, nwl = h2.shape
    wshape = (nwl, rows // 128, 128)
    shp = jax.ShapeDtypeStruct(wshape, F32)
    vm = pl.BlockSpec(memory_space=pltpu.VMEM)
    return pl.pallas_call(
        functools.partial(_wfactor_kernel, n, nsub),
        out_shape=[shp] * 5 + [jax.ShapeDtypeStruct((nsub, 4) + wshape[1:], F32)],
        in_specs=[vm] * 3 + [SMEM_SPEC],
        scratch_shapes=[pltpu.VMEM(h2.shape, F32)] * 3 + [pltpu.VMEM(wshape, F32)] * 2,
    )(h2, hwl, hwh, flags)


def _width_kernel(nsub, yc_ref, vc_ref, wc_ref, bk_ref, a_ref, r_ref, cp_ref, vws_ref,
                  y_ref, sm_ref, d_ref):
    sc = yc_ref[...] + vc_ref[...] * bk_ref[:, 0:1, :] + wc_ref[...] * bk_ref[:, 1:2, :]
    nt, ncl, nwl = sc.shape
    sc = sc.reshape(nt * ncl, nwl)
    for q in range(d_ref.shape[1]):
        d_ref[:, q, :] = sc[q * 128 : (q + 1) * 128, :].T
    n = a_ref.shape[0] // nsub
    subs = [q * n for q in range(nsub)]
    _solve_rhs(n, subs, _lead_ld, _lead_st, a_ref, r_ref, cp_ref, d_ref, y_ref, True, a_ref.shape[1:])
    for q, s0 in enumerate(subs):
        rows = (y_ref[s0], vws_ref[q, 0], vws_ref[q, 1], y_ref[s0 + n - 1], vws_ref[q, 2], vws_ref[q, 3])
        for k, val in enumerate(rows):
            sm_ref[q, k] = val


def _thick_kernel(nsub, tsub, nw, me_ref, *refs):
    r_refs = refs[:nw]
    (yw_ref, vw_ref, ww_ref, a_ref, r_ref, cp_ref, v_ref, w_ref, h_ref,
     o_ref, sw_ref, d_ref, y_ref) = refs[nw:]
    lrw = _width_reduce(me_ref[0], r_refs)
    m = yw_ref.shape[0] // nsub
    for q in range(nsub):
        sl = slice(q * m, (q + 1) * m)
        sw_ref[sl] = yw_ref[sl] + vw_ref[sl] * lrw[q][0] + ww_ref[sl] * lrw[q][1]
    nt, ncl, nwl = a_ref.shape
    per_q = 128 // ncl
    for q in range(sw_ref.shape[1]):
        d_ref[q * per_q : (q + 1) * per_q] = sw_ref[:, q, :].T.reshape(per_q, ncl, nwl)
    n = nt // tsub
    subs = [q * n for q in range(tsub)]
    shape = a_ref.shape[1:]
    _solve_rhs(n, subs, _lead_ld, _lead_st, a_ref, r_ref, cp_ref, d_ref, y_ref, True, shape)
    sums = [tuple(_summary_rows(_lead_ld, s0, n, y_ref, v_ref, w_ref)) for s0 in subs]
    lrs = [None] * tsub

    def emit(p, left, right):
        lrs[p] = (left, right)

    _reduce_blocks(tsub, lambda p: sums[p], emit, jnp.zeros(shape, F32))
    for q, s0 in enumerate(subs):
        sl = slice(s0, s0 + n)
        left, right = lrs[q]
        o_ref[sl] = h_ref[sl] + (y_ref[sl] + v_ref[sl] * left + w_ref[sl] * right)


def cast_solve(a, b, c, d, n):
    shp = jax.ShapeDtypeStruct(a.shape, F32)
    m = a.shape[0] // n
    return pl.pallas_call(
        functools.partial(_cast_kernel, n),
        out_shape=[shp, shp, shp, jax.ShapeDtypeStruct((m * 8, a.shape[1]), F32)],
        scratch_shapes=[pltpu.VMEM(a.shape, F32)],
    )(a, b, c, d)


def width_solve(yc, vc, wc, bk, a, fac, nsub):
    shp = jax.ShapeDtypeStruct(a.shape, F32)
    return pl.pallas_call(
        functools.partial(_width_kernel, nsub),
        out_shape=[shp, jax.ShapeDtypeStruct((nsub, 6) + a.shape[1:], F32)],
        scratch_shapes=[pltpu.VMEM(a.shape, F32)],
    )(yc, vc, wc, bk, a, *fac)


def thick_solve(me, got, yw, vw, ww, a, fac, h, nsub, tsub):
    vm = pl.BlockSpec(memory_space=pltpu.VMEM)
    return pl.pallas_call(
        functools.partial(_thick_kernel, nsub, tsub, len(got)),
        out_shape=jax.ShapeDtypeStruct(a.shape, F32),
        in_specs=[SMEM_SPEC] + [vm] * (len(got) + 9),
        scratch_shapes=[pltpu.VMEM(yw.shape, F32)] + [pltpu.VMEM(a.shape, F32)] * 2,
    )(me, *got, yw, vw, ww, a, *fac, h)


def _reduce_blocks(nb, blk, emit, zero):
    pp, qq = zero, zero
    saved = []
    for p in range(nb):
        y0, v0, w0, yn, vn, wn = blk(p)
        rd = 1.0 / (1.0 - v0 * qq)
        fa = (y0 + v0 * pp) * rd
        fb = w0 * rd
        saved.append((fa, fb, pp, qq))
        pp, qq = yn + vn * (pp + qq * fa), wn + vn * qq * fb
    f_next = zero
    for p in range(nb - 1, -1, -1):
        fa, fb, pp, qq = saved[p]
        f = fa + fb * f_next
        emit(p, pp + qq * f, f_next)
        f_next = f


def _merge(A, B):
    yA0, vA0, wA0, yAn, vAn, wAn = A
    yB0, vB0, wB0, yBn, vBn, wBn = B
    rd = 1.0 / (1.0 - wAn * vB0)
    ey = (yAn + wAn * yB0) * rd
    ev = vAn * rd
    ew = wAn * wB0 * rd
    fy = yB0 + vB0 * ey
    fv = vB0 * ev
    fw = wB0 + vB0 * ew
    return (yA0 + wA0 * fy, vA0 + wA0 * fv, wA0 * fw, yBn + vBn * ey, vBn * ev, wBn + vBn * ew)


def _chain(nb, blk, emit, left, right):
    pp, qq = left, jnp.zeros_like(left)
    saved = []
    for p in range(nb):
        y0, v0, w0, yn, vn, wn = blk(p)
        rd = 1.0 / (1.0 - v0 * qq)
        fa = (y0 + v0 * pp) * rd
        fb = w0 * rd
        saved.append((fa, fb, pp, qq))
        pp, qq = yn + vn * (pp + qq * fa), wn + vn * qq * fb
    f_next = right
    for p in range(nb - 1, -1, -1):
        fa, fb, pp, qq = saved[p]
        f = fa + fb * f_next
        emit(p, pp + qq * f, f_next)
        f_next = f


def _cast_reduced_kernel(s_ref, lr_ref):
    nb, g, _, nl = s_ref.shape
    ng = 8
    if g != 1 or nb % ng:
        def blk(p):
            return tuple(s_ref[p, :, k, :] for k in range(6))

        def emit(p, left, right):
            lr_ref[p, :, 0:1, :] = left[:, None]
            lr_ref[p, :, 1:2, :] = right[:, None]

        _reduce_blocks(nb, blk, emit, jnp.zeros((g, nl), F32))
        return
    m = nb // ng

    def member(j):
        return tuple(
            jnp.concatenate([s_ref[G * m + j, 0, k : k + 1, :] for G in range(ng)], 0)
            for k in range(6)
        )

    members = [member(j) for j in range(m)]
    acc = members[0]
    for j in range(1, m):
        acc = _merge(acc, members[j])
    outer = [None] * ng

    def emit_g(G, left, right):
        outer[G] = (left, right)

    zero1 = jnp.zeros((1, nl), F32)
    _chain(ng, lambda G: tuple(x[G : G + 1] for x in acc), emit_g, zero1, zero1)
    left_g = jnp.concatenate([outer[G][0] for G in range(ng)], 0)
    right_g = jnp.concatenate([outer[G][1] for G in range(ng)], 0)

    def emit(j, left, right):
        for G in range(ng):
            lr_ref[G * m + j, 0, 0:1, :] = left[G : G + 1]
            lr_ref[G * m + j, 0, 1:2, :] = right[G : G + 1]

    _chain(m, lambda j: members[j], emit, left_g, right_g)


def _width_reduce(me, r_refs):
    nw = len(r_refs)
    nsub = r_refs[0].shape[0]
    out = [[None, None] for _ in range(nsub)]

    def blk(b):
        dev, q = divmod(b, nsub)
        kk = (me - dev + nw) % nw
        vals = []
        for k6 in range(6):
            val = r_refs[0][q, k6]
            for k in range(1, nw):
                val = jnp.where(kk == k, r_refs[k][q, k6], val)
            vals.append(val)
        return tuple(vals)

    def emit(b, left, right):
        dev, q = divmod(b, nsub)
        mine = me == dev
        for j, val in enumerate((left, right)):
            out[q][j] = val if out[q][j] is None else jnp.where(mine, val, out[q][j])

    _reduce_blocks(nw * nsub, blk, emit, jnp.zeros(r_refs[0].shape[2:], F32))
    return out


def _surface_kernel(scale, z_ref, sp_ref, o_ref):
    z = z_ref[...]
    acc = jnp.zeros(z.shape, F32)
    for q in range(sp_ref.shape[0]):
        acc = jnp.where(z == q, sp_ref[q], acc)
    o_ref[...] = acc * scale


def medium_parameters(x):
    t = jnp.tanh(x)
    hot = x - solidification_release * t
    cond = 1.5 - 0.5 * jnp.tanh(hot)
    slope = (1.0 - solidification_release) + solidification_release * t * t
    return hot, cond, slope


def shards(h, zones, spray_coef):
    nt, ncl, nwl = h.shape
    nc, nw = lax.axis_size("cast"), lax.axis_size("width")
    ci, wi = lax.axis_index("cast"), lax.axis_index("width")
    up_c = [(i, i + 1) for i in range(nc - 1)]
    up_w = [(i, i + 1) for i in range(nw - 1)]
    even = ci % 2 == 0
    first, last = h[:, 0, :], h[:, -1, :]
    in_chip = [(i, i ^ 1) for i in range(nc)]
    across = [(i, i + 1) for i in range(1, nc - 1, 2)] + [(i + 1, i) for i in range(1, nc - 1, 2)]
    got_a = lax.ppermute(jnp.where(even, last, first), "cast", in_chip)
    got_b = lax.ppermute(jnp.where(even, first, last), "cast", across)
    h_wl = lax.ppermute(h[:, :, -1], "width", up_w)
    h_wh = lax.ppermute(h[:, :, 0], "width", [(b, a) for a, b in up_w])

    cast_low = (ci > 0).astype(F32)
    cast_high = (ci < nc - 1).astype(F32)
    width_low = (wi > 0).astype(F32)
    width_high = (wi < nw - 1).astype(F32)
    flags = jnp.stack([cast_low, cast_high, width_low, width_high, even.astype(F32)])
    h2 = h.reshape(nt * ncl, nwl)
    outs = prep_solve(h2, got_a, got_b, zones.reshape(2 * ncl, nwl), spray_coef, flags, ncl)
    y, v, w, summ, a_c, r_c, cp_c = outs[:7]
    tlo, tmd, thi = (x.reshape(nt, ncl, nwl) for x in outs[7:])
    y, summ = edge_solve(h2, h_wl, h_wh, flags, a_c, r_c, cp_c, y, summ, ncl)
    recv = lax.all_to_all(summ.reshape(nc, nt // nc, 8, nwl), "cast", 0, 0, tiled=True)
    lr_shape = recv.shape[:2] + (2, nwl)
    lr = pl.pallas_call(_cast_reduced_kernel, out_shape=jax.ShapeDtypeStruct(lr_shape, F32))(recv)
    back = lax.all_to_all(lr, "cast", 0, 0, tiled=True).reshape(nt, 2, nwl)
    y, v, w = (x.reshape(nt, ncl, nwl) for x in (y, v, w))

    lines = nt * ncl
    nsub = 2

    def wl(x):
        return jnp.transpose(x, (2, 0, 1)).reshape(nwl, lines // 128, 128)

    wa, r_w, cp_w, v_w, w_w, vws = wfactor(h2, h_wl, h_wh, flags, ncl, nsub)
    wfac = (r_w, cp_w, v_w, w_w)
    tfac = factor(tlo, tmd, thi, 8)
    yw, summ = width_solve(y, v, w, back, wa, (r_w, cp_w, vws), nsub)
    got = [summ] + [
        lax.ppermute(summ, "width", [(i, (i + q) % nw) for i in range(nw)]) for q in range(1, nw)
    ]
    me = wi.astype(jnp.int32).reshape(1)
    return thick_solve(me, got, yw, wfac[2], wfac[3], tlo, tfac, h, nsub, 8)


def solution(mesh):
    spec = P(None, "cast", "width")
    return jax.shard_map(
        shards, mesh=mesh, in_specs=(spec, spec, P()), out_specs=spec, check_vma=False
    )
```
